32 devices in a mesh: groups: 2 (over y), seq: 4 (over z), heads: 2 (over x), pair: 2 (over core).
Axes of the slice: x: 2, y: 2, z: 4, core: 2. Of those that a mesh axis runs over, the one named last changes fastest.
Arguments:
- queries: bfloat16 [6656, 2048], P(('groups', 'seq'), ('heads', 'pair')), parts along dimension 0, may hold values from -25 to 25
- key_rows: bfloat16 [6656, 2048], P(('groups', 'seq'), ('heads', 'pair')), parts along dimension 0, may hold values from -9 to 9
- value_rows: bfloat16 [6656, 2048], P(('groups', 'seq'), ('heads', 'pair')), parts along dimension 0, may hold values from -6 to 6
- out_grad: bfloat16 [6656, 2048], P(('groups', 'seq'), ('heads', 'pair')), parts along dimension 0, may hold values from -96 to 96
- random_device: int32 [104, 2], P('groups'), parts along dimension 0, may hold values from 0 to 3, all different within a row; in each aligned block of 13 rows (0 to 12, 13 to 25, ...) at most 9 rows name the same one
- random_block: int32 [104, 2], P('groups'), parts along dimension 0, may hold values from 0 to 12
Outputs:
- query_gradient: bfloat16 [6656, 2048], P(('groups', 'seq'), ('heads', 'pair')), parts along dimension 0
- key_grad: bfloat16 [6656, 2048], P(('groups', 'seq'), ('heads', 'pair')), parts along dimension 0
- value_grad: bfloat16 [6656, 2048], P(('groups', 'seq'), ('heads', 'pair')), parts along dimension 0
The draws below stay inside these ranges and needn't reach their ends.
There are 2 independent parts, one for each index of `groups`. The reference program is written for one: setup_inputs(seed, part) draws one part's arguments, and reference() takes and returns one part's arrays. A program takes and returns all parts, laid end to end along the dimension named above; each array names one. Nothing has to cross between parts.
Inputs may be any that keep to these rules, and one draw needn't show every extreme that they name: `random_device`: in the 13 rows of one index of seq (aligned blocks of rows) no device number appears more than 9 times, and in every draw some number appears exactly 9 times in some device's rows; the 2 entries of a row differ.
All inputs are finite; a program needn't handle non-finite values.
Results may differ from the reference program's by a relative error of at most 0.02.
Values may be sent and summed in bfloat16 or wider, within the bound.
No kernel may reach another device: no remote copies, remote signals or barrier semaphores. Data moves between devices by JAX's collectives and lax.ppermute only.
A program may use at most 128 MiB of HBM per device.

```python
import math
import jax
import jax.numpy as jnp
import numpy as np
from jax import lax

HEADS = 16
DH = 128
D = 2048
BLOCK = 64
RAND = 2
BLK_DEV = 13
SEQ = 3328
QBLOCKS = 52
CAP = 9
N_SEQ = 4


def draw_key_rows(key, part):
    return jnp.clip(jax.random.normal(jax.random.fold_in(key, 11), (SEQ, D), jnp.float32), -4.0, 4.0).astype(jnp.bfloat16)


def draw_queries(key, part):
    return jnp.clip(jax.random.normal(jax.random.fold_in(key, 12), (SEQ, D), jnp.float32), -4.0, 4.0).astype(jnp.bfloat16)


def place_ends(values, own_key, least, high):
    place = [jax.random.randint(jax.random.fold_in(own_key, axis), (), 0, length) for axis, length in enumerate(values.shape)]
    main_axis = values.shape.index(max(values.shape))
    next_to = place[:main_axis] + [(place[main_axis] + 1) % values.shape[main_axis]] + place[main_axis + 1:]
    return values.at[tuple(place)].set(least).at[tuple(next_to)].set(high)


def steps_of(key, dims, split, smallest, largest):
    level = 1.0
    for dim, parts in split:
        steps = jax.random.uniform(jax.random.fold_in(jax.random.fold_in(key, 6), dim), (parts,), jnp.float32, smallest / len(split), largest / len(split))
        level = level * jnp.repeat(jnp.exp(steps), dims[dim] // parts).reshape((-1,) + (1,) * (len(dims) - 1 - dim))
    return level


def shared_out(own_key, own, number, rows, amount, top, bound, slope):
    order = jax.random.permutation(own_key, amount)
    crowded, ordinary = shares(amount, rows * top, bound, slope, True), shares(amount, rows * top, bound, slope, False)
    places = jnp.arange(amount)

    def named(tallies, rotation):
        used = int((tallies > 0).sum())
        fixed = max(1, used // 4)
        shifted = fixed + (places - fixed + rotation * (used - fixed)) % max(1, amount - fixed)
        return jnp.zeros((amount,), jnp.int32).at[order[jnp.where(places < fixed, places, shifted)]].set(jnp.asarray(tallies, jnp.int32))

    tallies = jnp.where(number % 4 == 0, named(crowded, number // 4), named(ordinary, number - number // 4 - 1))
    mixed = jax.random.permutation(jax.random.fold_in(own, 3), amount)
    source_of, receiver = mixed[0:amount // 2 * 2:2], mixed[1:amount // 2 * 2:2]
    margin = jnp.minimum(tallies[source_of] - 1, bound - tallies[receiver]) // 2
    margin = jnp.where((source_of == order[0]) | (receiver == order[0]) | (tallies[receiver] == 0), 0, jnp.maximum(margin, 0))
    shifted = jax.random.randint(jax.random.fold_in(own, 4), (amount // 2,), 0, 1 << 20) % (margin + 1)
    tallies = tallies.at[source_of].add(-shifted).at[receiver].add(shifted)
    members = jnp.searchsorted(jnp.cumsum(tallies), jnp.arange(rows * top), side="right").astype(jnp.int32)
    grid = members.reshape(top, rows).T
    grid = grid[jax.random.permutation(jax.random.fold_in(own, 1), rows)]
    rotation = jax.random.randint(jax.random.fold_in(own, 2), (rows, 1), 0, top)
    return jnp.take_along_axis(grid, (jnp.arange(top)[None, :] + rotation) % top, axis=1)


def shares(number_of, total, most, skew, full):
    loads = [(1 << 20) // math.isqrt(grade ** skew) + 1 for grade in range(1, number_of + 1)]
    largest = most if full else min(most, max(-(-total // number_of), total * loads[0] // sum(loads)))
    least = 1 if total - largest >= number_of - 1 else 0
    given, surplus = [largest] + [least] * (number_of - 1), total - largest - least * (number_of - 1)
    while surplus > 0:
        free = [i for i in range(1, number_of) if given[i] < largest] or [i for i in range(1, number_of) if given[i] < most]
        whole, left = sum([loads[i] for i in free]), surplus
        for i in free:
            extra = min(most - given[i], max(1, left * loads[i] // whole), surplus)
            given[i] = given[i] + extra
            surplus = surplus - extra
    return np.array(given)


def centred(rng, dims, scale, most, pieces=(), kind=jnp.bfloat16):
    result = jax.random.normal(rng, dims, jnp.float32) * scale
    if len(pieces) > 0:
        result = steps_of(rng, dims, pieces, -0.22, 0.18) * result
    return jnp.clip(result, min=-most, max=most).astype(kind)


def setup_inputs(seed: int = 0, part: int = 0) -> dict:
    key_list = jax.random.split(jax.random.key(seed), 7)
    part_splits = jax.random.split(jax.random.fold_in(key_list[6], part), 7)
    queries = draw_queries(jax.random.fold_in(jax.random.fold_in(key_list[6], part), 71), part)
    key_rows = draw_key_rows(jax.random.fold_in(jax.random.fold_in(key_list[6], part), 71), part)
    value_rows = centred(part_splits[2], (SEQ, D), 1.0, 6.0, ((0, 4), (1, 4)))
    out_grad = centred(part_splits[3], (SEQ, D), 16.0, 96.0, ((0, 4), (1, 4)))
    random_device_keys = jax.random.split(jax.random.fold_in(part_splits[4], 1), QBLOCKS // BLK_DEV)
    random_device_turns = jax.random.permutation(jax.random.fold_in(part_splits[4], 3), QBLOCKS // BLK_DEV)
    random_device = jax.vmap(lambda own, number: shared_out(jax.random.fold_in(part_splits[4], 2), own, number, BLK_DEV, N_SEQ, RAND, CAP, 1))(random_device_keys, random_device_turns).reshape((QBLOCKS, RAND))
    random_block = place_ends(jax.random.randint(part_splits[5], (QBLOCKS, RAND), 0, BLK_DEV), jax.random.fold_in(part_splits[5], 1), 0, BLK_DEV - 1).astype(jnp.int32)
    return dict(queries=queries, key_rows=key_rows, value_rows=value_rows, out_grad=out_grad, random_device=random_device, random_block=random_block)


def rounded_scores(array):
    return lax.optimization_barrier(array.astype(jnp.bfloat16)).astype(jnp.float32)

def one_head(operands, random_device, random_block):
    query_rows, key_part, value_part, grad_rows = operands
    block_count = SEQ // BLOCK
    logit_scale = 1.0 / math.sqrt(DH)
    query_tiles = query_rows.reshape(block_count, BLOCK, DH).astype(jnp.float32)
    key_blocks = key_part.reshape(block_count, BLOCK, DH)
    value_blocks = value_part.reshape(block_count, BLOCK, DH)
    gradient_tiles = grad_rows.reshape(block_count, BLOCK, DH).astype(jnp.float32)
    block_ids = jnp.arange(block_count, dtype=jnp.int32)
    chosen = (random_device * BLK_DEV + random_block).astype(jnp.int32)
    context_ids = jnp.concatenate([jnp.clip(block_ids - 1, 0, block_count - 1)[:, None], block_ids[:, None], jnp.clip(block_ids + 1, 0, block_count - 1)[:, None], chosen], axis=1)
    gathered_key_rows = key_blocks[context_ids].reshape(block_count, (3 + RAND) * BLOCK, DH).astype(jnp.float32)
    gathered_value_rows = value_blocks[context_ids].reshape(block_count, (3 + RAND) * BLOCK, DH).astype(jnp.float32)
    slot_ids = jnp.arange(3 + RAND, dtype=jnp.int32)[None, :]
    missing = (slot_ids == 0) & (block_ids[:, None] == 0) | (slot_ids == 2) & (block_ids[:, None] == block_count - 1)
    usable = jnp.repeat(jnp.logical_not(missing), BLOCK, axis=1)
    attention_logits = jnp.einsum('nje,nxe->njx', query_tiles, gathered_key_rows) * logit_scale
    attention_logits = jnp.where(usable[:, None, :], attention_logits, -jnp.inf)
    row_max = lax.optimization_barrier(jnp.max(attention_logits, axis=-1, keepdims=True))
    exponent = jnp.exp(attention_logits - row_max)
    row_total = lax.optimization_barrier(jnp.sum(exponent, axis=-1, keepdims=True))
    probability = exponent / row_total
    softmax_weights = rounded_scores(probability)
    attended_output = rounded_scores(jnp.einsum('zxp,zph->zxh', softmax_weights, gathered_value_rows))
    row_delta = lax.optimization_barrier(jnp.sum(gradient_tiles * attended_output, axis=-1, keepdims=True))
    probability_gradient = jnp.einsum('nje,nxe->njx', gradient_tiles, gathered_value_rows)
    score_gradient = rounded_scores(probability * (probability_gradient - row_delta))
    query_gradient = (logit_scale * jnp.einsum('zxp,zph->zxh', score_gradient, gathered_key_rows)).astype(jnp.bfloat16)
    key_contributions = logit_scale * jnp.einsum('fec,few->fcw', score_gradient, query_tiles)
    value_contributions = jnp.einsum('fec,few->fcw', softmax_weights, gradient_tiles)
    all_terms = jnp.concatenate([key_contributions, value_contributions], axis=-1).reshape(block_count, 3 + RAND, BLOCK, 2 * DH)
    zero_block = jnp.zeros((1, BLOCK, 2 * DH), jnp.float32)
    summed = all_terms[:, 1] + jnp.concatenate([all_terms[1:, 0], zero_block], axis=0) + jnp.concatenate([zero_block, all_terms[:-1, 2]], axis=0)
    far_terms = rounded_scores(all_terms[:, 3:]).reshape(block_count * RAND, BLOCK, 2 * DH)
    summed = summed.at[chosen.reshape(-1)].add(far_terms)
    summed = summed.reshape(SEQ, 2 * DH)
    return (query_gradient.reshape(SEQ, DH), summed[:, :DH].astype(jnp.bfloat16), summed[:, DH:].astype(jnp.bfloat16))

def reference(queries, key_rows, value_rows, out_grad, random_device, random_block):

    def heads_first(array):
        return array.reshape(SEQ, HEADS, DH).transpose(1, 0, 2)

    def heads_last(array):
        return array.transpose(1, 0, 2).reshape(SEQ, HEADS * DH)
    stacked = (heads_first(queries), heads_first(key_rows), heads_first(value_rows), heads_first(out_grad))
    results = lax.map(lambda operands: one_head(operands, random_device, random_block), stacked)
    return (heads_last(results[0]), heads_last(results[1]), heads_last(results[2]))
```

```python
import math

import jax
import jax.numpy as jnp
from jax import lax
from jax.experimental import pallas as pl
from jax.experimental.pallas import tpu as pltpu
from jax.sharding import PartitionSpec as P

DH = 128
BLOCK = 64
RAND = 2


def extended(block, sides, width):
    for axis, dim in sides:
        count = lax.axis_size(axis)
        forward = [(i, i + 1) for i in range(count - 1)]
        backward = [(target, source) for source, target in forward]
        low = lax.ppermute(
            lax.slice_in_dim(block, block.shape[dim] - width, None, axis=dim), axis, forward
        )
        high = lax.ppermute(lax.slice_in_dim(block, 0, width, axis=dim), axis, backward)
        block = jnp.concatenate([low, block, high], axis=dim)
    return block


def routing(random_device, random_block, own_index, seq_size, blocks_dev, capacity):
    entries = blocks_dev * RAND
    wanted_from = random_device.reshape(seq_size, entries)
    wanted_block = random_block.reshape(seq_size, entries)
    from_me = (wanted_from == own_index).astype(jnp.int32)
    rank_out = jnp.cumsum(from_me, axis=1) - from_me
    slot_hits = from_me[:, None, :] * (
        rank_out[:, None, :] == jnp.arange(capacity, dtype=jnp.int32)[None, :, None]
    ).astype(jnp.int32)
    block_hits = (
        wanted_block[:, :, None] == jnp.arange(blocks_dev, dtype=jnp.int32)[None, None, :]
    ).astype(jnp.float32)
    selector = jnp.einsum("sce,sej->scj", slot_hits.astype(jnp.float32), block_hits)
    selector = selector.reshape(seq_size * capacity, blocks_dev).astype(jnp.bfloat16)
    own_sources = lax.dynamic_slice_in_dim(
        random_device, own_index * blocks_dev, blocks_dev, 0
    ).reshape(entries)
    peer_hits = (own_sources[:, None] == jnp.arange(seq_size, dtype=jnp.int32)[None, :]).astype(
        jnp.int32
    )
    earlier = jnp.cumsum(peer_hits, axis=0) - peer_hits
    rank_in = jnp.sum(earlier * peer_hits, axis=1)
    slot_index = own_sources * capacity + rank_in
    return (selector, slot_index)


def far_context(arrived, slot_index, blocks_dev):
    picked = jnp.take(arrived, slot_index, axis=0)
    return picked.reshape(blocks_dev, RAND, arrived.shape[1], arrived.shape[2])


def usable_mask(own_index, seq_size, blocks_dev):
    block_ids = jnp.arange(blocks_dev, dtype=jnp.int32)[:, None]
    slot_ids = jnp.arange(3 + RAND, dtype=jnp.int32)[None, :]
    global_block = own_index * blocks_dev + block_ids
    missing = (slot_ids == 0) & (global_block == 0) | (slot_ids == 2) & (
        global_block == seq_size * blocks_dev - 1
    )
    return jnp.repeat(jnp.logical_not(missing), BLOCK, axis=1)


def slot_pieces(haloed, far_blocks, blocks_dev, start_col):
    pieces = []
    for slot in range(3):
        pieces.append(haloed[slot : slot + blocks_dev, :, start_col : start_col + DH])
    far_part = far_blocks[:, :, :, start_col : start_col + DH]
    return (pieces, far_part)


def forward_head(query_tiles, key_pieces, key_far, value_pieces, value_far, usable):
    blocks_dev = query_tiles.shape[0]
    logit_parts = [
        jnp.einsum("bje,bxe->bjx", query_tiles, piece, preferred_element_type=jnp.float32)
        for piece in key_pieces
    ]
    far_logits = jnp.einsum(
        "bje,brxe->bjrx", query_tiles, key_far, preferred_element_type=jnp.float32
    )
    logit_parts.append(far_logits.reshape(blocks_dev, BLOCK, RAND * BLOCK))
    attention_logits = jnp.concatenate(logit_parts, axis=-1) * (1.0 / math.sqrt(DH))
    attention_logits = jnp.where(usable[:, None, :], attention_logits, -jnp.inf)
    row_max = jnp.max(attention_logits, axis=-1, keepdims=True)
    exponent = jnp.exp(attention_logits - row_max)
    row_total = jnp.sum(exponent, axis=-1, keepdims=True)
    probability = exponent / row_total
    softmax_weights = probability.astype(jnp.bfloat16)
    attended = jnp.einsum(
        "bjx,bxe->bje",
        softmax_weights[:, :, :BLOCK],
        value_pieces[0],
        preferred_element_type=jnp.float32,
    )
    for slot in range(1, 3):
        attended = attended + jnp.einsum(
            "bjx,bxe->bje",
            softmax_weights[:, :, slot * BLOCK : (slot + 1) * BLOCK],
            value_pieces[slot],
            preferred_element_type=jnp.float32,
        )
    far_weights = softmax_weights[:, :, 3 * BLOCK :].reshape(blocks_dev, BLOCK, RAND, BLOCK)
    attended = attended + jnp.einsum(
        "bjrx,brxe->bje", far_weights, value_far, preferred_element_type=jnp.float32
    )
    return (probability, attended.astype(jnp.bfloat16))


def backward_head(
    query_tiles, key_pieces, key_far, value_pieces, value_far, gradient_tiles, forward_state
):
    probability, attended_output = forward_state
    blocks_dev = query_tiles.shape[0]
    logit_scale = 1.0 / math.sqrt(DH)
    softmax_weights = probability.astype(jnp.bfloat16)
    row_delta = jnp.sum(
        gradient_tiles.astype(jnp.float32) * attended_output.astype(jnp.float32),
        axis=-1,
        keepdims=True,
    )
    grad_parts = [
        jnp.einsum("bje,bxe->bjx", gradient_tiles, piece, preferred_element_type=jnp.float32)
        for piece in value_pieces
    ]
    far_grad = jnp.einsum(
        "bje,brxe->bjrx", gradient_tiles, value_far, preferred_element_type=jnp.float32
    )
    grad_parts.append(far_grad.reshape(blocks_dev, BLOCK, RAND * BLOCK))
    probability_gradient = jnp.concatenate(grad_parts, axis=-1)
    score_gradient = (probability * (probability_gradient - row_delta)).astype(jnp.bfloat16)
    query_sum = jnp.einsum(
        "bjx,bxe->bje",
        score_gradient[:, :, :BLOCK],
        key_pieces[0],
        preferred_element_type=jnp.float32,
    )
    for slot in range(1, 3):
        query_sum = query_sum + jnp.einsum(
            "bjx,bxe->bje",
            score_gradient[:, :, slot * BLOCK : (slot + 1) * BLOCK],
            key_pieces[slot],
            preferred_element_type=jnp.float32,
        )
    far_scores = score_gradient[:, :, 3 * BLOCK :].reshape(blocks_dev, BLOCK, RAND, BLOCK)
    query_sum = query_sum + jnp.einsum(
        "bjrx,brxe->bje", far_scores, key_far, preferred_element_type=jnp.float32
    )
    query_gradient = (logit_scale * query_sum).astype(jnp.bfloat16)
    key_window, value_window = ([], [])
    for slot in range(3):
        columns = slice(slot * BLOCK, (slot + 1) * BLOCK)
        key_window.append(
            logit_scale
            * jnp.einsum(
                "bjx,bje->bxe",
                score_gradient[:, :, columns],
                query_tiles,
                preferred_element_type=jnp.float32,
            )
        )
        value_window.append(
            jnp.einsum(
                "bjx,bje->bxe",
                softmax_weights[:, :, columns],
                gradient_tiles,
                preferred_element_type=jnp.float32,
            )
        )
    far_weights = softmax_weights[:, :, 3 * BLOCK :].reshape(blocks_dev, BLOCK, RAND, BLOCK)
    key_far_terms = (
        logit_scale
        * jnp.einsum("bjrx,bje->brxe", far_scores, query_tiles, preferred_element_type=jnp.float32)
    ).astype(jnp.bfloat16)
    value_far_terms = jnp.einsum(
        "bjrx,bje->brxe", far_weights, gradient_tiles, preferred_element_type=jnp.float32
    ).astype(jnp.bfloat16)
    return (query_gradient, key_window, value_window, key_far_terms, value_far_terms)


def exchanged_shards(queries, key_rows, value_rows, out_grad, random_device, random_block):
    seq_size = lax.axis_size("seq")
    own_index = lax.axis_index("seq")
    tokens, row_width = queries.shape
    blocks_dev = tokens // BLOCK
    heads_dev = row_width // DH
    capacity = max(2, 3 * blocks_dev // seq_size)
    selector, slot_index = routing(
        random_device, random_block, own_index, seq_size, blocks_dev, capacity
    )
    packed = jnp.concatenate([key_rows, value_rows], axis=1).reshape(
        blocks_dev, BLOCK, 2 * row_width
    )
    flattened = packed.reshape(blocks_dev, BLOCK * 2 * row_width)
    outgoing_blocks = jnp.dot(selector, flattened, preferred_element_type=jnp.float32).astype(
        jnp.bfloat16
    )
    outgoing_blocks = outgoing_blocks.reshape(seq_size * capacity, BLOCK, 2 * row_width)
    haloed = extended(packed, (("seq", 0),), 1)
    arrived = lax.all_to_all(outgoing_blocks, "seq", split_axis=0, concat_axis=0, tiled=True)
    far_blocks = far_context(arrived, slot_index, blocks_dev)
    usable = usable_mask(own_index, seq_size, blocks_dev)
    query_tiles = queries.reshape(blocks_dev, BLOCK, row_width)
    gradient_tiles = out_grad.reshape(blocks_dev, BLOCK, row_width)
    states = []
    for head_index in range(heads_dev):
        key_pieces, key_far = slot_pieces(haloed, far_blocks, blocks_dev, head_index * DH)
        value_pieces, value_far = slot_pieces(
            haloed, far_blocks, blocks_dev, row_width + head_index * DH
        )
        query_head = query_tiles[:, :, head_index * DH : (head_index + 1) * DH]
        states.append(
            forward_head(query_head, key_pieces, key_far, value_pieces, value_far, usable)
        )
    query_parts = []
    window_lists = [[], [], []]
    value_lists = [[], [], []]
    far_keys, far_values = ([], [])
    for head_index in range(heads_dev):
        key_pieces, key_far = slot_pieces(haloed, far_blocks, blocks_dev, head_index * DH)
        value_pieces, value_far = slot_pieces(
            haloed, far_blocks, blocks_dev, row_width + head_index * DH
        )
        query_head = query_tiles[:, :, head_index * DH : (head_index + 1) * DH]
        gradient_head = gradient_tiles[:, :, head_index * DH : (head_index + 1) * DH]
        query_gradient, key_window, value_window, key_far_terms, value_far_terms = backward_head(
            query_head,
            key_pieces,
            key_far,
            value_pieces,
            value_far,
            gradient_head,
            states[head_index],
        )
        query_parts.append(query_gradient)
        for slot in range(3):
            window_lists[slot].append(key_window[slot])
            value_lists[slot].append(value_window[slot])
        far_keys.append(key_far_terms)
        far_values.append(value_far_terms)
    slot_terms = [
        jnp.concatenate(window_lists[slot] + value_lists[slot], axis=-1) for slot in range(3)
    ]
    left_terms = slot_terms[0]
    right_terms = slot_terms[2]
    far_terms = jnp.concatenate(far_keys + far_values, axis=-1).reshape(
        blocks_dev * RAND, BLOCK, 2 * row_width
    )
    edge_terms = jnp.stack([left_terms[0], right_terms[-1]])
    edge_haloed = extended(edge_terms.astype(jnp.bfloat16), (("seq", 0),), 1).astype(
        edge_terms.dtype
    )
    summed = (
        slot_terms[1]
        + jnp.concatenate([left_terms[1:], edge_haloed[3:]], axis=0)
        + jnp.concatenate([edge_haloed[:1], right_terms[:-1]], axis=0)
    )
    returning = (
        jnp.zeros((seq_size * capacity, BLOCK, 2 * row_width), jnp.bfloat16)
        .at[slot_index]
        .set(far_terms)
    )
    returned = lax.all_to_all(returning, "seq", split_axis=0, concat_axis=0, tiled=True)
    gathered_terms = jnp.dot(
        selector.T,
        returned.reshape(seq_size * capacity, BLOCK * 2 * row_width),
        preferred_element_type=jnp.float32,
    )
    summed = summed + gathered_terms.reshape(blocks_dev, BLOCK, 2 * row_width)
    summed = summed.reshape(tokens, 2 * row_width)
    query_out = jnp.concatenate(query_parts, axis=-1).reshape(tokens, row_width)
    return (
        query_out,
        summed[:, :row_width].astype(jnp.bfloat16),
        summed[:, row_width:].astype(jnp.bfloat16),
    )


SLOTS = 3 + RAND


def block_kernel(ids_ref, valid_ref, q_ref, g_ref, *rest):
    kv_refs = rest[:SLOTS]
    dq_ref, terms_ref = rest[SLOTS:]
    step = pl.program_id(0)
    width = q_ref.shape[1]
    logit_scale = 1.0 / math.sqrt(DH)
    context = jnp.concatenate([ref[0] for ref in kv_refs], axis=0)
    slot_of = lax.broadcasted_iota(jnp.int32, (1, SLOTS * BLOCK), 1) // BLOCK
    usable = slot_of < 0
    for slot in range(SLOTS):
        usable = usable | ((slot_of == slot) & (valid_ref[step * SLOTS + slot] > 0))
    for head in range(width // DH):
        cols = slice(head * DH, (head + 1) * DH)
        vcols = slice(width + head * DH, width + (head + 1) * DH)
        query = q_ref[:, cols]
        grad = g_ref[:, cols]
        keys = context[:, cols]
        values = context[:, vcols]
        logits = lax.dot_general(
            query, keys, (((1,), (1,)), ((), ())), preferred_element_type=jnp.float32
        ) * logit_scale
        logits = jnp.where(usable, logits, -jnp.inf)
        row_max = jnp.max(logits, axis=-1, keepdims=True)
        exponent = jnp.exp(logits - row_max)
        row_total = jnp.sum(exponent, axis=-1, keepdims=True)
        probability = exponent / row_total
        weights = probability.astype(jnp.bfloat16)
        attended = jnp.dot(weights, values, preferred_element_type=jnp.float32).astype(
            jnp.bfloat16
        )
        row_delta = jnp.sum(
            grad.astype(jnp.float32) * attended.astype(jnp.float32), axis=-1, keepdims=True
        )
        prob_grad = lax.dot_general(
            grad, values, (((1,), (1,)), ((), ())), preferred_element_type=jnp.float32
        )
        score_grad = (probability * (prob_grad - row_delta)).astype(jnp.bfloat16)
        query_grad = logit_scale * jnp.dot(
            score_grad, keys, preferred_element_type=jnp.float32
        )
        dq_ref[:, cols] = query_grad.astype(jnp.bfloat16)
        key_terms = logit_scale * lax.dot_general(
            score_grad, query, (((0,), (0,)), ((), ())), preferred_element_type=jnp.float32
        )
        value_terms = lax.dot_general(
            weights, grad, (((0,), (0,)), ((), ())), preferred_element_type=jnp.float32
        )
        for slot in range(SLOTS):
            rows = slice(slot * BLOCK, (slot + 1) * BLOCK)
            terms_ref[0, slot, :, cols] = key_terms[rows]
            terms_ref[0, slot, :, vcols] = value_terms[rows]


def block_attention(ids, valid, queries, out_grad, source):
    tokens, width = queries.shape
    blocks_dev = tokens // BLOCK

    def context_spec(slot):
        return pl.BlockSpec(
            (1, BLOCK, 2 * width), lambda i, ids, valid: (ids[i * SLOTS + slot], 0, 0)
        )

    row_spec = pl.BlockSpec((BLOCK, width), lambda i, ids, valid: (i, 0))
    grid_spec = pltpu.PrefetchScalarGridSpec(
        num_scalar_prefetch=2,
        grid=(blocks_dev,),
        in_specs=[row_spec, row_spec] + [context_spec(s) for s in range(SLOTS)],
        out_specs=[
            row_spec,
            pl.BlockSpec(
                (1, SLOTS, BLOCK, 2 * width), lambda i, ids, valid: (i, 0, 0, 0)
            ),
        ],
    )
    return pl.pallas_call(
        block_kernel,
        grid_spec=grid_spec,
        out_shape=[
            jax.ShapeDtypeStruct((tokens, width), jnp.bfloat16),
            jax.ShapeDtypeStruct((blocks_dev, SLOTS, BLOCK, 2 * width), jnp.float32),
        ],
    )(ids, valid, queries, out_grad, *([source] * SLOTS))


def gathered_shards(queries, key_rows, value_rows, out_grad, random_device, random_block):
    seq_size = lax.axis_size("seq")
    own_index = lax.axis_index("seq")
    tokens, width = queries.shape
    blocks_dev = tokens // BLOCK
    total = seq_size * blocks_dev
    first = own_index * blocks_dev
    packed = jnp.concatenate([key_rows, value_rows], axis=1)
    source = lax.all_gather(packed, "seq", axis=0, tiled=True).reshape(total, BLOCK, 2 * width)
    block_ids = first + jnp.arange(blocks_dev, dtype=jnp.int32)
    own_device = lax.dynamic_slice_in_dim(random_device, first, blocks_dev, 0)
    own_block = lax.dynamic_slice_in_dim(random_block, first, blocks_dev, 0)
    chosen = (own_device * blocks_dev + own_block).astype(jnp.int32)
    window = jnp.stack(
        [jnp.clip(block_ids - 1, 0, total - 1), block_ids, jnp.clip(block_ids + 1, 0, total - 1)],
        axis=1,
    )
    ids = jnp.concatenate([window, chosen], axis=1)
    always = jnp.ones_like(block_ids, dtype=jnp.bool_)
    valid = jnp.stack([block_ids > 0, always, block_ids < total - 1] + [always] * RAND, axis=1)
    query_out, terms = block_attention(
        ids.reshape(-1), valid.astype(jnp.int32).reshape(-1), queries, out_grad, source
    )
    zero_block = jnp.zeros((1, BLOCK, 2 * width), jnp.float32)
    own_sum = (
        terms[:, 1]
        + jnp.concatenate([terms[1:, 0], zero_block], axis=0)
        + jnp.concatenate([zero_block, terms[:-1, 2]], axis=0)
    )
    far_terms = terms[:, 3:].astype(jnp.bfloat16).reshape(blocks_dev * RAND, BLOCK * 2 * width)
    edge_terms = jnp.stack([terms[0, 0], terms[-1, 2]]).astype(jnp.bfloat16)
    sent = jnp.concatenate([far_terms, edge_terms.reshape(2, BLOCK * 2 * width)], axis=0)
    targets = jnp.concatenate([chosen.reshape(-1), jnp.stack([first - 1, first + blocks_dev])])
    target_ok = jnp.concatenate(
        [jnp.ones((blocks_dev * RAND,), jnp.bool_), jnp.stack([first > 0, first + blocks_dev < total])]
    )
    placement = (
        (targets[None, :] == jnp.arange(total, dtype=jnp.int32)[:, None]) & target_ok[None, :]
    ).astype(jnp.bfloat16)
    spread = jnp.dot(placement, sent, preferred_element_type=jnp.float32).astype(jnp.bfloat16)
    spread = spread.reshape(total * BLOCK, 2 * width)
    returned = lax.psum_scatter(spread, "seq", scatter_dimension=0, tiled=True)
    summed = own_sum.reshape(tokens, 2 * width) + returned.astype(jnp.float32)
    return (
        query_out,
        summed[:, :width].astype(jnp.bfloat16),
        summed[:, width:].astype(jnp.bfloat16),
    )


def shards(queries, key_rows, value_rows, out_grad, random_device, random_block):
    if lax.axis_size("seq") <= 8:
        return gathered_shards(queries, key_rows, value_rows, out_grad, random_device, random_block)
    return exchanged_shards(queries, key_rows, value_rows, out_grad, random_device, random_block)


def solution(mesh):
    return jax.shard_map(
        shards,
        mesh=mesh,
        in_specs=(
            P(("groups", "seq"), ("heads", "pair")),
            P(("groups", "seq"), ("heads", "pair")),
            P(("groups", "seq"), ("heads", "pair")),
            P(("groups", "seq"), ("heads", "pair")),
            P("groups", None),
            P("groups", None),
        ),
        out_specs=(
            P(("groups", "seq"), ("heads", "pair")),
            P(("groups", "seq"), ("heads", "pair")),
            P(("groups", "seq"), ("heads", "pair")),
        ),
        check_vma=False,
    )
```

```python
import math

import jax
import jax.numpy as jnp
from jax import lax
from jax.experimental import pallas as pl
from jax.experimental.pallas import tpu as pltpu
from jax.sharding import PartitionSpec as P

DH = 128
BLOCK = 64
RAND = 2


def extended(block, sides, width):
    for axis, dim in sides:
        count = lax.axis_size(axis)
        forward = [(i, i + 1) for i in range(count - 1)]
        backward = [(target, source) for source, target in forward]
        low = lax.ppermute(
            lax.slice_in_dim(block, block.shape[dim] - width, None, axis=dim), axis, forward
        )
        high = lax.ppermute(lax.slice_in_dim(block, 0, width, axis=dim), axis, backward)
        block = jnp.concatenate([low, block, high], axis=dim)
    return block


def routing(random_device, random_block, own_index, seq_size, blocks_dev, capacity):
    entries = blocks_dev * RAND
    wanted_from = random_device.reshape(seq_size, entries)
    wanted_block = random_block.reshape(seq_size, entries)
    from_me = (wanted_from == own_index).astype(jnp.int32)
    rank_out = jnp.cumsum(from_me, axis=1) - from_me
    slot_hits = from_me[:, None, :] * (
        rank_out[:, None, :] == jnp.arange(capacity, dtype=jnp.int32)[None, :, None]
    ).astype(jnp.int32)
    block_hits = (
        wanted_block[:, :, None] == jnp.arange(blocks_dev, dtype=jnp.int32)[None, None, :]
    ).astype(jnp.float32)
    selector = jnp.einsum("sce,sej->scj", slot_hits.astype(jnp.float32), block_hits)
    selector = selector.reshape(seq_size * capacity, blocks_dev).astype(jnp.bfloat16)
    own_sources = lax.dynamic_slice_in_dim(
        random_device, own_index * blocks_dev, blocks_dev, 0
    ).reshape(entries)
    peer_hits = (own_sources[:, None] == jnp.arange(seq_size, dtype=jnp.int32)[None, :]).astype(
        jnp.int32
    )
    earlier = jnp.cumsum(peer_hits, axis=0) - peer_hits
    rank_in = jnp.sum(earlier * peer_hits, axis=1)
    slot_index = own_sources * capacity + rank_in
    return (selector, slot_index)


def far_context(arrived, slot_index, blocks_dev):
    picked = jnp.take(arrived, slot_index, axis=0)
    return picked.reshape(blocks_dev, RAND, arrived.shape[1], arrived.shape[2])


def usable_mask(own_index, seq_size, blocks_dev):
    block_ids = jnp.arange(blocks_dev, dtype=jnp.int32)[:, None]
    slot_ids = jnp.arange(3 + RAND, dtype=jnp.int32)[None, :]
    global_block = own_index * blocks_dev + block_ids
    missing = (slot_ids == 0) & (global_block == 0) | (slot_ids == 2) & (
        global_block == seq_size * blocks_dev - 1
    )
    return jnp.repeat(jnp.logical_not(missing), BLOCK, axis=1)


def slot_pieces(haloed, far_blocks, blocks_dev, start_col):
    pieces = []
    for slot in range(3):
        pieces.append(haloed[slot : slot + blocks_dev, :, start_col : start_col + DH])
    far_part = far_blocks[:, :, :, start_col : start_col + DH]
    return (pieces, far_part)


def forward_head(query_tiles, key_pieces, key_far, value_pieces, value_far, usable):
    blocks_dev = query_tiles.shape[0]
    logit_parts = [
        jnp.einsum("bje,bxe->bjx", query_tiles, piece, preferred_element_type=jnp.float32)
        for piece in key_pieces
    ]
    far_logits = jnp.einsum(
        "bje,brxe->bjrx", query_tiles, key_far, preferred_element_type=jnp.float32
    )
    logit_parts.append(far_logits.reshape(blocks_dev, BLOCK, RAND * BLOCK))
    attention_logits = jnp.concatenate(logit_parts, axis=-1) * (1.0 / math.sqrt(DH))
    attention_logits = jnp.where(usable[:, None, :], attention_logits, -jnp.inf)
    row_max = jnp.max(attention_logits, axis=-1, keepdims=True)
    exponent = jnp.exp(attention_logits - row_max)
    row_total = jnp.sum(exponent, axis=-1, keepdims=True)
    probability = exponent / row_total
    softmax_weights = probability.astype(jnp.bfloat16)
    attended = jnp.einsum(
        "bjx,bxe->bje",
        softmax_weights[:, :, :BLOCK],
        value_pieces[0],
        preferred_element_type=jnp.float32,
    )
    for slot in range(1, 3):
        attended = attended + jnp.einsum(
            "bjx,bxe->bje",
            softmax_weights[:, :, slot * BLOCK : (slot + 1) * BLOCK],
            value_pieces[slot],
            preferred_element_type=jnp.float32,
        )
    far_weights = softmax_weights[:, :, 3 * BLOCK :].reshape(blocks_dev, BLOCK, RAND, BLOCK)
    attended = attended + jnp.einsum(
        "bjrx,brxe->bje", far_weights, value_far, preferred_element_type=jnp.float32
    )
    return (probability, attended.astype(jnp.bfloat16))


def backward_head(
    query_tiles, key_pieces, key_far, value_pieces, value_far, gradient_tiles, forward_state
):
    probability, attended_output = forward_state
    blocks_dev = query_tiles.shape[0]
    logit_scale = 1.0 / math.sqrt(DH)
    softmax_weights = probability.astype(jnp.bfloat16)
    row_delta = jnp.sum(
        gradient_tiles.astype(jnp.float32) * attended_output.astype(jnp.float32),
        axis=-1,
        keepdims=True,
    )
    grad_parts = [
        jnp.einsum("bje,bxe->bjx", gradient_tiles, piece, preferred_element_type=jnp.float32)
        for piece in value_pieces
    ]
    far_grad = jnp.einsum(
        "bje,brxe->bjrx", gradient_tiles, value_far, preferred_element_type=jnp.float32
    )
    grad_parts.append(far_grad.reshape(blocks_dev, BLOCK, RAND * BLOCK))
    probability_gradient = jnp.concatenate(grad_parts, axis=-1)
    score_gradient = (probability * (probability_gradient - row_delta)).astype(jnp.bfloat16)
    query_sum = jnp.einsum(
        "bjx,bxe->bje",
        score_gradient[:, :, :BLOCK],
        key_pieces[0],
        preferred_element_type=jnp.float32,
    )
    for slot in range(1, 3):
        query_sum = query_sum + jnp.einsum(
            "bjx,bxe->bje",
            score_gradient[:, :, slot * BLOCK : (slot + 1) * BLOCK],
            key_pieces[slot],
            preferred_element_type=jnp.float32,
        )
    far_scores = score_gradient[:, :, 3 * BLOCK :].reshape(blocks_dev, BLOCK, RAND, BLOCK)
    query_sum = query_sum + jnp.einsum(
        "bjrx,brxe->bje", far_scores, key_far, preferred_element_type=jnp.float32
    )
    query_gradient = (logit_scale * query_sum).astype(jnp.bfloat16)
    key_window, value_window = ([], [])
    for slot in range(3):
        columns = slice(slot * BLOCK, (slot + 1) * BLOCK)
        key_window.append(
            logit_scale
            * jnp.einsum(
                "bjx,bje->bxe",
                score_gradient[:, :, columns],
                query_tiles,
                preferred_element_type=jnp.float32,
            )
        )
        value_window.append(
            jnp.einsum(
                "bjx,bje->bxe",
                softmax_weights[:, :, columns],
                gradient_tiles,
                preferred_element_type=jnp.float32,
            )
        )
    far_weights = softmax_weights[:, :, 3 * BLOCK :].reshape(blocks_dev, BLOCK, RAND, BLOCK)
    key_far_terms = (
        logit_scale
        * jnp.einsum("bjrx,bje->brxe", far_scores, query_tiles, preferred_element_type=jnp.float32)
    ).astype(jnp.bfloat16)
    value_far_terms = jnp.einsum(
        "bjrx,bje->brxe", far_weights, gradient_tiles, preferred_element_type=jnp.float32
    ).astype(jnp.bfloat16)
    return (query_gradient, key_window, value_window, key_far_terms, value_far_terms)


def exchanged_shards(queries, key_rows, value_rows, out_grad, random_device, random_block):
    seq_size = lax.axis_size("seq")
    own_index = lax.axis_index("seq")
    tokens, row_width = queries.shape
    blocks_dev = tokens // BLOCK
    heads_dev = row_width // DH
    capacity = max(2, 3 * blocks_dev // seq_size)
    selector, slot_index = routing(
        random_device, random_block, own_index, seq_size, blocks_dev, capacity
    )
    packed = jnp.concatenate([key_rows, value_rows], axis=1).reshape(
        blocks_dev, BLOCK, 2 * row_width
    )
    flattened = packed.reshape(blocks_dev, BLOCK * 2 * row_width)
    outgoing_blocks = jnp.dot(selector, flattened, preferred_element_type=jnp.float32).astype(
        jnp.bfloat16
    )
    outgoing_blocks = outgoing_blocks.reshape(seq_size * capacity, BLOCK, 2 * row_width)
    haloed = extended(packed, (("seq", 0),), 1)
    arrived = lax.all_to_all(outgoing_blocks, "seq", split_axis=0, concat_axis=0, tiled=True)
    far_blocks = far_context(arrived, slot_index, blocks_dev)
    usable = usable_mask(own_index, seq_size, blocks_dev)
    query_tiles = queries.reshape(blocks_dev, BLOCK, row_width)
    gradient_tiles = out_grad.reshape(blocks_dev, BLOCK, row_width)
    states = []
    for head_index in range(heads_dev):
        key_pieces, key_far = slot_pieces(haloed, far_blocks, blocks_dev, head_index * DH)
        value_pieces, value_far = slot_pieces(
            haloed, far_blocks, blocks_dev, row_width + head_index * DH
        )
        query_head = query_tiles[:, :, head_index * DH : (head_index + 1) * DH]
        states.append(
            forward_head(query_head, key_pieces, key_far, value_pieces, value_far, usable)
        )
    query_parts = []
    window_lists = [[], [], []]
    value_lists = [[], [], []]
    far_keys, far_values = ([], [])
    for head_index in range(heads_dev):
        key_pieces, key_far = slot_pieces(haloed, far_blocks, blocks_dev, head_index * DH)
        value_pieces, value_far = slot_pieces(
            haloed, far_blocks, blocks_dev, row_width + head_index * DH
        )
        query_head = query_tiles[:, :, head_index * DH : (head_index + 1) * DH]
        gradient_head = gradient_tiles[:, :, head_index * DH : (head_index + 1) * DH]
        query_gradient, key_window, value_window, key_far_terms, value_far_terms = backward_head(
            query_head,
            key_pieces,
            key_far,
            value_pieces,
            value_far,
            gradient_head,
            states[head_index],
        )
        query_parts.append(query_gradient)
        for slot in range(3):
            window_lists[slot].append(key_window[slot])
            value_lists[slot].append(value_window[slot])
        far_keys.append(key_far_terms)
        far_values.append(value_far_terms)
    slot_terms = [
        jnp.concatenate(window_lists[slot] + value_lists[slot], axis=-1) for slot in range(3)
    ]
    left_terms = slot_terms[0]
    right_terms = slot_terms[2]
    far_terms = jnp.concatenate(far_keys + far_values, axis=-1).reshape(
        blocks_dev * RAND, BLOCK, 2 * row_width
    )
    edge_terms = jnp.stack([left_terms[0], right_terms[-1]])
    edge_haloed = extended(edge_terms.astype(jnp.bfloat16), (("seq", 0),), 1).astype(
        edge_terms.dtype
    )
    summed = (
        slot_terms[1]
        + jnp.concatenate([left_terms[1:], edge_haloed[3:]], axis=0)
        + jnp.concatenate([edge_haloed[:1], right_terms[:-1]], axis=0)
    )
    returning = (
        jnp.zeros((seq_size * capacity, BLOCK, 2 * row_width), jnp.bfloat16)
        .at[slot_index]
        .set(far_terms)
    )
    returned = lax.all_to_all(returning, "seq", split_axis=0, concat_axis=0, tiled=True)
    gathered_terms = jnp.dot(
        selector.T,
        returned.reshape(seq_size * capacity, BLOCK * 2 * row_width),
        preferred_element_type=jnp.float32,
    )
    summed = summed + gathered_terms.reshape(blocks_dev, BLOCK, 2 * row_width)
    summed = summed.reshape(tokens, 2 * row_width)
    query_out = jnp.concatenate(query_parts, axis=-1).reshape(tokens, row_width)
    return (
        query_out,
        summed[:, :row_width].astype(jnp.bfloat16),
        summed[:, row_width:].astype(jnp.bfloat16),
    )


SLOTS = 3 + RAND


def block_kernel(ids_ref, valid_ref, first_ref, q_ref, g_ref, *rest):
    kv_refs = rest[:SLOTS]
    own_ref, spread_ref, dq_ref, acc_ref = rest[SLOTS:]
    step = pl.program_id(0)
    steps = pl.num_programs(0)
    width = q_ref.shape[1]
    blocks_dev = own_ref.shape[0]
    logit_scale = 1.0 / math.sqrt(DH)

    @pl.when(step == 0)
    def _():
        acc_ref[...] = jnp.zeros(acc_ref.shape, jnp.float32)

    context = jnp.concatenate([ref[0] for ref in kv_refs], axis=0)
    slot_of = lax.broadcasted_iota(jnp.int32, (SLOTS * BLOCK, 1), 0) // BLOCK
    usable = slot_of < 0
    for slot in range(SLOTS):
        usable = usable | ((slot_of == slot) & (valid_ref[step * SLOTS + slot] > 0))
    key_parts, value_parts = [], []
    for head in range(width // DH):
        cols = slice(head * DH, (head + 1) * DH)
        vcols = slice(width + head * DH, width + (head + 1) * DH)
        query = q_ref[:, cols]
        grad = g_ref[:, cols]
        keys = context[:, cols]
        values = context[:, vcols]
        logits = lax.dot_general(
            keys, query, (((1,), (1,)), ((), ())), preferred_element_type=jnp.float32
        ) * logit_scale
        logits = jnp.where(usable, logits, -jnp.inf)
        row_max = jnp.max(logits, axis=0, keepdims=True)
        exponent = jnp.exp(logits - row_max)
        row_total = jnp.sum(exponent, axis=0, keepdims=True)
        probability = exponent / row_total
        weights = probability.astype(jnp.bfloat16)
        attended = lax.dot_general(
            weights, values, (((0,), (0,)), ((), ())), preferred_element_type=jnp.float32
        ).astype(jnp.bfloat16)
        product = grad.astype(jnp.float32) * attended.astype(jnp.float32)
        row_delta = jnp.sum(product.T, axis=0, keepdims=True)
        prob_grad = lax.dot_general(
            values, grad, (((1,), (1,)), ((), ())), preferred_element_type=jnp.float32
        )
        score_grad = (probability * (prob_grad - row_delta)).astype(jnp.bfloat16)
        query_grad = logit_scale * lax.dot_general(
            score_grad, keys, (((0,), (0,)), ((), ())), preferred_element_type=jnp.float32
        )
        dq_ref[:, cols] = query_grad.astype(jnp.bfloat16)
        key_parts.append(
            logit_scale * jnp.dot(score_grad, query, preferred_element_type=jnp.float32)
        )
        value_parts.append(jnp.dot(weights, grad, preferred_element_type=jnp.float32))
    terms = jnp.concatenate(key_parts + value_parts, axis=1)
    for slot in range(SLOTS):
        piece = terms[slot * BLOCK : (slot + 1) * BLOCK]
        if slot >= 3:
            piece = piece.astype(jnp.bfloat16).astype(jnp.float32)
        target = ids_ref[step * SLOTS + slot]
        acc_ref[target] = acc_ref[target] + piece

    @pl.when(step == steps - 1)
    def _():
        first = first_ref[0]
        spread_ref[...] = acc_ref[...].astype(jnp.bfloat16)
        for block in range(blocks_dev):
            own_ref[block] = acc_ref[first + block]
            spread_ref[first + block] = jnp.zeros(spread_ref.shape[1:], jnp.bfloat16)


def block_attention(ids, valid, first, queries, out_grad, source):
    tokens, width = queries.shape
    blocks_dev = tokens // BLOCK
    total = source.shape[0]

    def context_spec(slot):
        return pl.BlockSpec(
            (1, BLOCK, 2 * width), lambda i, ids, valid, first: (ids[i * SLOTS + slot], 0, 0)
        )

    row_spec = pl.BlockSpec((BLOCK, width), lambda i, ids, valid, first: (i, 0))
    grid_spec = pltpu.PrefetchScalarGridSpec(
        num_scalar_prefetch=3,
        grid=(blocks_dev,),
        in_specs=[row_spec, row_spec] + [context_spec(s) for s in range(SLOTS)],
        out_specs=[
            pl.BlockSpec(
                (blocks_dev, BLOCK, 2 * width), lambda i, ids, valid, first: (0, 0, 0)
            ),
            pl.BlockSpec((total, BLOCK, 2 * width), lambda i, ids, valid, first: (0, 0, 0)),
            row_spec,
        ],
        scratch_shapes=[pltpu.VMEM((total, BLOCK, 2 * width), jnp.float32)],
    )
    return pl.pallas_call(
        block_kernel,
        grid_spec=grid_spec,
        out_shape=[
            jax.ShapeDtypeStruct((blocks_dev, BLOCK, 2 * width), jnp.float32),
            jax.ShapeDtypeStruct((total, BLOCK, 2 * width), jnp.bfloat16),
            jax.ShapeDtypeStruct((tokens, width), jnp.bfloat16),
        ],
        compiler_params=pltpu.CompilerParams(vmem_limit_bytes=60 * 1024 * 1024),
    )(ids, valid, first, queries, out_grad, *([source] * SLOTS))


def gathered_shards(queries, key_rows, value_rows, out_grad, random_device, random_block):
    seq_size = lax.axis_size("seq")
    own_index = lax.axis_index("seq")
    tokens, width = queries.shape
    blocks_dev = tokens // BLOCK
    total = seq_size * blocks_dev
    first = own_index * blocks_dev
    packed = jnp.concatenate([key_rows, value_rows], axis=1)
    source = lax.all_gather(packed, "seq", axis=0, tiled=True).reshape(total, BLOCK, 2 * width)
    block_ids = first + jnp.arange(blocks_dev, dtype=jnp.int32)
    own_device = lax.dynamic_slice_in_dim(random_device, first, blocks_dev, 0)
    own_block = lax.dynamic_slice_in_dim(random_block, first, blocks_dev, 0)
    chosen = (own_device * blocks_dev + own_block).astype(jnp.int32)
    window = jnp.stack(
        [jnp.clip(block_ids - 1, 0, total - 1), block_ids, jnp.clip(block_ids + 1, 0, total - 1)],
        axis=1,
    )
    ids = jnp.concatenate([window, chosen], axis=1)
    always = jnp.ones_like(block_ids, dtype=jnp.bool_)
    valid = jnp.stack([block_ids > 0, always, block_ids < total - 1] + [always] * RAND, axis=1)
    own_sum, spread, query_out = block_attention(
        ids.reshape(-1),
        valid.astype(jnp.int32).reshape(-1),
        first.reshape(1).astype(jnp.int32),
        queries,
        out_grad,
        source,
    )
    returned = lax.psum_scatter(
        spread.reshape(total * BLOCK, 2 * width), "seq", scatter_dimension=0, tiled=True
    )
    summed = own_sum.reshape(tokens, 2 * width) + returned.astype(jnp.float32)
    return (
        query_out,
        summed[:, :width].astype(jnp.bfloat16),
        summed[:, width:].astype(jnp.bfloat16),
    )


def shards(queries, key_rows, value_rows, out_grad, random_device, random_block):
    if lax.axis_size("seq") <= 8:
        return gathered_shards(queries, key_rows, value_rows, out_grad, random_device, random_block)
    return exchanged_shards(queries, key_rows, value_rows, out_grad, random_device, random_block)


def solution(mesh):
    return jax.shard_map(
        shards,
        mesh=mesh,
        in_specs=(
            P(("groups", "seq"), ("heads", "pair")),
            P(("groups", "seq"), ("heads", "pair")),
            P(("groups", "seq"), ("heads", "pair")),
            P(("groups", "seq"), ("heads", "pair")),
            P("groups", None),
            P("groups", None),
        ),
        out_specs=(
            P(("groups", "seq"), ("heads", "pair")),
            P(("groups", "seq"), ("heads", "pair")),
            P(("groups", "seq"), ("heads", "pair")),
        ),
        check_vma=False,
    )
```

```python
import math

import jax
import jax.numpy as jnp
from jax import lax
from jax.experimental import pallas as pl
from jax.experimental.pallas import tpu as pltpu
from jax.sharding import PartitionSpec as P

DH = 128
BLOCK = 64
RAND = 2


def extended(block, sides, width):
    for axis, dim in sides:
        count = lax.axis_size(axis)
        forward = [(i, i + 1) for i in range(count - 1)]
        backward = [(target, source) for source, target in forward]
        low = lax.ppermute(
            lax.slice_in_dim(block, block.shape[dim] - width, None, axis=dim), axis, forward
        )
        high = lax.ppermute(lax.slice_in_dim(block, 0, width, axis=dim), axis, backward)
        block = jnp.concatenate([low, block, high], axis=dim)
    return block


def routing(random_device, random_block, own_index, seq_size, blocks_dev, capacity):
    entries = blocks_dev * RAND
    wanted_from = random_device.reshape(seq_size, entries)
    wanted_block = random_block.reshape(seq_size, entries)
    from_me = (wanted_from == own_index).astype(jnp.int32)
    rank_out = jnp.cumsum(from_me, axis=1) - from_me
    slot_hits = from_me[:, None, :] * (
        rank_out[:, None, :] == jnp.arange(capacity, dtype=jnp.int32)[None, :, None]
    ).astype(jnp.int32)
    block_hits = (
        wanted_block[:, :, None] == jnp.arange(blocks_dev, dtype=jnp.int32)[None, None, :]
    ).astype(jnp.float32)
    selector = jnp.einsum("sce,sej->scj", slot_hits.astype(jnp.float32), block_hits)
    selector = selector.reshape(seq_size * capacity, blocks_dev).astype(jnp.bfloat16)
    own_sources = lax.dynamic_slice_in_dim(
        random_device, own_index * blocks_dev, blocks_dev, 0
    ).reshape(entries)
    peer_hits = (own_sources[:, None] == jnp.arange(seq_size, dtype=jnp.int32)[None, :]).astype(
        jnp.int32
    )
    earlier = jnp.cumsum(peer_hits, axis=0) - peer_hits
    rank_in = jnp.sum(earlier * peer_hits, axis=1)
    slot_index = own_sources * capacity + rank_in
    return (selector, slot_index)


def far_context(arrived, slot_index, blocks_dev):
    picked = jnp.take(arrived, slot_index, axis=0)
    return picked.reshape(blocks_dev, RAND, arrived.shape[1], arrived.shape[2])


def usable_mask(own_index, seq_size, blocks_dev):
    block_ids = jnp.arange(blocks_dev, dtype=jnp.int32)[:, None]
    slot_ids = jnp.arange(3 + RAND, dtype=jnp.int32)[None, :]
    global_block = own_index * blocks_dev + block_ids
    missing = (slot_ids == 0) & (global_block == 0) | (slot_ids == 2) & (
        global_block == seq_size * blocks_dev - 1
    )
    return jnp.repeat(jnp.logical_not(missing), BLOCK, axis=1)


def slot_pieces(haloed, far_blocks, blocks_dev, start_col):
    pieces = []
    for slot in range(3):
        pieces.append(haloed[slot : slot + blocks_dev, :, start_col : start_col + DH])
    far_part = far_blocks[:, :, :, start_col : start_col + DH]
    return (pieces, far_part)


def forward_head(query_tiles, key_pieces, key_far, value_pieces, value_far, usable):
    blocks_dev = query_tiles.shape[0]
    logit_parts = [
        jnp.einsum("bje,bxe->bjx", query_tiles, piece, preferred_element_type=jnp.float32)
        for piece in key_pieces
    ]
    far_logits = jnp.einsum(
        "bje,brxe->bjrx", query_tiles, key_far, preferred_element_type=jnp.float32
    )
    logit_parts.append(far_logits.reshape(blocks_dev, BLOCK, RAND * BLOCK))
    attention_logits = jnp.concatenate(logit_parts, axis=-1) * (1.0 / math.sqrt(DH))
    attention_logits = jnp.where(usable[:, None, :], attention_logits, -jnp.inf)
    row_max = jnp.max(attention_logits, axis=-1, keepdims=True)
    exponent = jnp.exp(attention_logits - row_max)
    row_total = jnp.sum(exponent, axis=-1, keepdims=True)
    probability = exponent / row_total
    softmax_weights = probability.astype(jnp.bfloat16)
    attended = jnp.einsum(
        "bjx,bxe->bje",
        softmax_weights[:, :, :BLOCK],
        value_pieces[0],
        preferred_element_type=jnp.float32,
    )
    for slot in range(1, 3):
        attended = attended + jnp.einsum(
            "bjx,bxe->bje",
            softmax_weights[:, :, slot * BLOCK : (slot + 1) * BLOCK],
            value_pieces[slot],
            preferred_element_type=jnp.float32,
        )
    far_weights = softmax_weights[:, :, 3 * BLOCK :].reshape(blocks_dev, BLOCK, RAND, BLOCK)
    attended = attended + jnp.einsum(
        "bjrx,brxe->bje", far_weights, value_far, preferred_element_type=jnp.float32
    )
    return (probability, attended.astype(jnp.bfloat16))


def backward_head(
    query_tiles, key_pieces, key_far, value_pieces, value_far, gradient_tiles, forward_state
):
    probability, attended_output = forward_state
    blocks_dev = query_tiles.shape[0]
    logit_scale = 1.0 / math.sqrt(DH)
    softmax_weights = probability.astype(jnp.bfloat16)
    row_delta = jnp.sum(
        gradient_tiles.astype(jnp.float32) * attended_output.astype(jnp.float32),
        axis=-1,
        keepdims=True,
    )
    grad_parts = [
        jnp.einsum("bje,bxe->bjx", gradient_tiles, piece, preferred_element_type=jnp.float32)
        for piece in value_pieces
    ]
    far_grad = jnp.einsum(
        "bje,brxe->bjrx", gradient_tiles, value_far, preferred_element_type=jnp.float32
    )
    grad_parts.append(far_grad.reshape(blocks_dev, BLOCK, RAND * BLOCK))
    probability_gradient = jnp.concatenate(grad_parts, axis=-1)
    score_gradient = (probability * (probability_gradient - row_delta)).astype(jnp.bfloat16)
    query_sum = jnp.einsum(
        "bjx,bxe->bje",
        score_gradient[:, :, :BLOCK],
        key_pieces[0],
        preferred_element_type=jnp.float32,
    )
    for slot in range(1, 3):
        query_sum = query_sum + jnp.einsum(
            "bjx,bxe->bje",
            score_gradient[:, :, slot * BLOCK : (slot + 1) * BLOCK],
            key_pieces[slot],
            preferred_element_type=jnp.float32,
        )
    far_scores = score_gradient[:, :, 3 * BLOCK :].reshape(blocks_dev, BLOCK, RAND, BLOCK)
    query_sum = query_sum + jnp.einsum(
        "bjrx,brxe->bje", far_scores, key_far, preferred_element_type=jnp.float32
    )
    query_gradient = (logit_scale * query_sum).astype(jnp.bfloat16)
    key_window, value_window = ([], [])
    for slot in range(3):
        columns = slice(slot * BLOCK, (slot + 1) * BLOCK)
        key_window.append(
            logit_scale
            * jnp.einsum(
                "bjx,bje->bxe",
                score_gradient[:, :, columns],
                query_tiles,
                preferred_element_type=jnp.float32,
            )
        )
        value_window.append(
            jnp.einsum(
                "bjx,bje->bxe",
                softmax_weights[:, :, columns],
                gradient_tiles,
                preferred_element_type=jnp.float32,
            )
        )
    far_weights = softmax_weights[:, :, 3 * BLOCK :].reshape(blocks_dev, BLOCK, RAND, BLOCK)
    key_far_terms = (
        logit_scale
        * jnp.einsum("bjrx,bje->brxe", far_scores, query_tiles, preferred_element_type=jnp.float32)
    ).astype(jnp.bfloat16)
    value_far_terms = jnp.einsum(
        "bjrx,bje->brxe", far_weights, gradient_tiles, preferred_element_type=jnp.float32
    ).astype(jnp.bfloat16)
    return (query_gradient, key_window, value_window, key_far_terms, value_far_terms)


def exchanged_shards(queries, key_rows, value_rows, out_grad, random_device, random_block):
    seq_size = lax.axis_size("seq")
    own_index = lax.axis_index("seq")
    tokens, row_width = queries.shape
    blocks_dev = tokens // BLOCK
    heads_dev = row_width // DH
    capacity = max(2, 3 * blocks_dev // seq_size)
    selector, slot_index = routing(
        random_device, random_block, own_index, seq_size, blocks_dev, capacity
    )
    packed = jnp.concatenate([key_rows, value_rows], axis=1).reshape(
        blocks_dev, BLOCK, 2 * row_width
    )
    flattened = packed.reshape(blocks_dev, BLOCK * 2 * row_width)
    outgoing_blocks = jnp.dot(selector, flattened, preferred_element_type=jnp.float32).astype(
        jnp.bfloat16
    )
    outgoing_blocks = outgoing_blocks.reshape(seq_size * capacity, BLOCK, 2 * row_width)
    haloed = extended(packed, (("seq", 0),), 1)
    arrived = lax.all_to_all(outgoing_blocks, "seq", split_axis=0, concat_axis=0, tiled=True)
    far_blocks = far_context(arrived, slot_index, blocks_dev)
    usable = usable_mask(own_index, seq_size, blocks_dev)
    query_tiles = queries.reshape(blocks_dev, BLOCK, row_width)
    gradient_tiles = out_grad.reshape(blocks_dev, BLOCK, row_width)
    states = []
    for head_index in range(heads_dev):
        key_pieces, key_far = slot_pieces(haloed, far_blocks, blocks_dev, head_index * DH)
        value_pieces, value_far = slot_pieces(
            haloed, far_blocks, blocks_dev, row_width + head_index * DH
        )
        query_head = query_tiles[:, :, head_index * DH : (head_index + 1) * DH]
        states.append(
            forward_head(query_head, key_pieces, key_far, value_pieces, value_far, usable)
        )
    query_parts = []
    window_lists = [[], [], []]
    value_lists = [[], [], []]
    far_keys, far_values = ([], [])
    for head_index in range(heads_dev):
        key_pieces, key_far = slot_pieces(haloed, far_blocks, blocks_dev, head_index * DH)
        value_pieces, value_far = slot_pieces(
            haloed, far_blocks, blocks_dev, row_width + head_index * DH
        )
        query_head = query_tiles[:, :, head_index * DH : (head_index + 1) * DH]
        gradient_head = gradient_tiles[:, :, head_index * DH : (head_index + 1) * DH]
        query_gradient, key_window, value_window, key_far_terms, value_far_terms = backward_head(
            query_head,
            key_pieces,
            key_far,
            value_pieces,
            value_far,
            gradient_head,
            states[head_index],
        )
        query_parts.append(query_gradient)
        for slot in range(3):
            window_lists[slot].append(key_window[slot])
            value_lists[slot].append(value_window[slot])
        far_keys.append(key_far_terms)
        far_values.append(value_far_terms)
    slot_terms = [
        jnp.concatenate(window_lists[slot] + value_lists[slot], axis=-1) for slot in range(3)
    ]
    left_terms = slot_terms[0]
    right_terms = slot_terms[2]
    far_terms = jnp.concatenate(far_keys + far_values, axis=-1).reshape(
        blocks_dev * RAND, BLOCK, 2 * row_width
    )
    edge_terms = jnp.stack([left_terms[0], right_terms[-1]])
    edge_haloed = extended(edge_terms.astype(jnp.bfloat16), (("seq", 0),), 1).astype(
        edge_terms.dtype
    )
    summed = (
        slot_terms[1]
        + jnp.concatenate([left_terms[1:], edge_haloed[3:]], axis=0)
        + jnp.concatenate([edge_haloed[:1], right_terms[:-1]], axis=0)
    )
    returning = (
        jnp.zeros((seq_size * capacity, BLOCK, 2 * row_width), jnp.bfloat16)
        .at[slot_index]
        .set(far_terms)
    )
    returned = lax.all_to_all(returning, "seq", split_axis=0, concat_axis=0, tiled=True)
    gathered_terms = jnp.dot(
        selector.T,
        returned.reshape(seq_size * capacity, BLOCK * 2 * row_width),
        preferred_element_type=jnp.float32,
    )
    summed = summed + gathered_terms.reshape(blocks_dev, BLOCK, 2 * row_width)
    summed = summed.reshape(tokens, 2 * row_width)
    query_out = jnp.concatenate(query_parts, axis=-1).reshape(tokens, row_width)
    return (
        query_out,
        summed[:, :row_width].astype(jnp.bfloat16),
        summed[:, row_width:].astype(jnp.bfloat16),
    )


SLOTS = 3 + RAND


def block_kernel(ids_ref, valid_ref, first_ref, q_ref, g_ref, *rest):
    kv_refs = rest[:SLOTS]
    own_ref, spread_ref, dq_ref, acc_ref = rest[SLOTS:]
    step = pl.program_id(0)
    steps = pl.num_programs(0)
    width = q_ref.shape[1]
    blocks_dev = own_ref.shape[0]
    logit_scale = 1.0 / math.sqrt(DH)

    @pl.when(step == 0)
    def _():
        acc_ref[...] = jnp.zeros(acc_ref.shape, jnp.float32)

    context = jnp.concatenate([ref[0] for ref in kv_refs], axis=0)
    slot_of = lax.broadcasted_iota(jnp.int32, (SLOTS * BLOCK, 1), 0) // BLOCK
    usable = slot_of < 0
    for slot in range(SLOTS):
        usable = usable | ((slot_of == slot) & (valid_ref[step * SLOTS + slot] > 0))
    key_parts, value_parts = [], []
    for head in range(width // DH):
        cols = slice(head * DH, (head + 1) * DH)
        vcols = slice(width + head * DH, width + (head + 1) * DH)
        query = q_ref[:, cols]
        grad = g_ref[:, cols]
        keys = context[:, cols]
        values = context[:, vcols]
        logits = lax.dot_general(
            keys, query, (((1,), (1,)), ((), ())), preferred_element_type=jnp.float32
        ) * logit_scale
        logits = jnp.where(usable, logits, -jnp.inf)
        row_max = jnp.max(logits, axis=0, keepdims=True)
        exponent = jnp.exp(logits - row_max)
        row_total = jnp.sum(exponent, axis=0, keepdims=True)
        probability = exponent / row_total
        weights = probability.astype(jnp.bfloat16)
        attended = lax.dot_general(
            weights, values, (((0,), (0,)), ((), ())), preferred_element_type=jnp.float32
        ).astype(jnp.bfloat16)
        product = grad.astype(jnp.float32) * attended.astype(jnp.float32)
        row_delta = jnp.sum(product.T, axis=0, keepdims=True)
        prob_grad = lax.dot_general(
            values, grad, (((1,), (1,)), ((), ())), preferred_element_type=jnp.float32
        )
        score_grad = (probability * (prob_grad - row_delta)).astype(jnp.bfloat16)
        query_grad = logit_scale * lax.dot_general(
            score_grad, keys, (((0,), (0,)), ((), ())), preferred_element_type=jnp.float32
        )
        dq_ref[:, cols] = query_grad.astype(jnp.bfloat16)
        key_parts.append(
            logit_scale * jnp.dot(score_grad, query, preferred_element_type=jnp.float32)
        )
        value_parts.append(jnp.dot(weights, grad, preferred_element_type=jnp.float32))
    terms = jnp.concatenate(key_parts + value_parts, axis=1)
    for slot in range(SLOTS):
        piece = terms[slot * BLOCK : (slot + 1) * BLOCK]
        if slot >= 3:
            piece = piece.astype(jnp.bfloat16).astype(jnp.float32)
        target = ids_ref[step * SLOTS + slot]
        acc_ref[target] = acc_ref[target] + piece

    @pl.when(step == steps - 1)
    def _():
        first = first_ref[0]
        spread_ref[...] = acc_ref[...].astype(jnp.bfloat16)
        for block in range(blocks_dev):
            own_ref[block] = acc_ref[first + block]
            spread_ref[first + block] = jnp.zeros(spread_ref.shape[1:], jnp.bfloat16)


def block_attention(ids, valid, first, queries, out_grad, source, chunk, width):
    tokens = queries.shape[0]
    blocks_dev = tokens // BLOCK
    total = source.shape[0]

    def context_spec(slot):
        return pl.BlockSpec(
            (1, BLOCK, 2 * width), lambda i, ids, valid, first: (ids[i * SLOTS + slot], 0, 0)
        )

    column_spec = pl.BlockSpec((BLOCK, width), lambda i, ids, valid, first: (i, chunk))
    row_spec = pl.BlockSpec((BLOCK, width), lambda i, ids, valid, first: (i, 0))
    grid_spec = pltpu.PrefetchScalarGridSpec(
        num_scalar_prefetch=3,
        grid=(blocks_dev,),
        in_specs=[column_spec, column_spec] + [context_spec(s) for s in range(SLOTS)],
        out_specs=[
            pl.BlockSpec(
                (blocks_dev, BLOCK, 2 * width), lambda i, ids, valid, first: (0, 0, 0)
            ),
            pl.BlockSpec((total, BLOCK, 2 * width), lambda i, ids, valid, first: (0, 0, 0)),
            row_spec,
        ],
        scratch_shapes=[pltpu.VMEM((total, BLOCK, 2 * width), jnp.float32)],
    )
    return pl.pallas_call(
        block_kernel,
        grid_spec=grid_spec,
        out_shape=[
            jax.ShapeDtypeStruct((blocks_dev, BLOCK, 2 * width), jnp.float32),
            jax.ShapeDtypeStruct((total, BLOCK, 2 * width), jnp.bfloat16),
            jax.ShapeDtypeStruct((tokens, width), jnp.bfloat16),
        ],
        compiler_params=pltpu.CompilerParams(vmem_limit_bytes=60 * 1024 * 1024),
    )(ids, valid, first, queries, out_grad, *([source] * SLOTS))


def gathered_shards(queries, key_rows, value_rows, out_grad, random_device, random_block):
    seq_size = lax.axis_size("seq")
    own_index = lax.axis_index("seq")
    tokens, width = queries.shape
    blocks_dev = tokens // BLOCK
    total = seq_size * blocks_dev
    first = own_index * blocks_dev
    block_ids = first + jnp.arange(blocks_dev, dtype=jnp.int32)
    own_device = lax.dynamic_slice_in_dim(random_device, first, blocks_dev, 0)
    own_block = lax.dynamic_slice_in_dim(random_block, first, blocks_dev, 0)
    chosen = (own_device * blocks_dev + own_block).astype(jnp.int32)
    window = jnp.stack(
        [jnp.clip(block_ids - 1, 0, total - 1), block_ids, jnp.clip(block_ids + 1, 0, total - 1)],
        axis=1,
    )
    ids = jnp.concatenate([window, chosen], axis=1).reshape(-1)
    always = jnp.ones_like(block_ids, dtype=jnp.bool_)
    valid = jnp.stack([block_ids > 0, always, block_ids < total - 1] + [always] * RAND, axis=1)
    valid = valid.astype(jnp.int32).reshape(-1)
    first_table = first.reshape(1).astype(jnp.int32)
    chunks = 2 if (width // DH) % 2 == 0 else 1
    part = width // chunks
    sources = []
    for chunk in range(chunks):
        cols = slice(chunk * part, (chunk + 1) * part)
        packed = jnp.concatenate([key_rows[:, cols], value_rows[:, cols]], axis=1)
        gathered = lax.all_gather(packed, "seq", axis=0, tiled=True)
        sources.append(gathered.reshape(total, BLOCK, 2 * part))
    query_parts, key_parts, value_parts = [], [], []
    for chunk in range(chunks):
        own_sum, spread, query_out = block_attention(
            ids, valid, first_table, queries, out_grad, sources[chunk], chunk, part
        )
        returned = lax.psum_scatter(
            spread.reshape(total * BLOCK, 2 * part), "seq", scatter_dimension=0, tiled=True
        )
        summed = own_sum.reshape(tokens, 2 * part) + returned.astype(jnp.float32)
        query_parts.append(query_out)
        key_parts.append(summed[:, :part].astype(jnp.bfloat16))
        value_parts.append(summed[:, part:].astype(jnp.bfloat16))
    return (
        jnp.concatenate(query_parts, axis=1),
        jnp.concatenate(key_parts, axis=1),
        jnp.concatenate(value_parts, axis=1),
    )


def shards(queries, key_rows, value_rows, out_grad, random_device, random_block):
    if lax.axis_size("seq") <= 8:
        return gathered_shards(queries, key_rows, value_rows, out_grad, random_device, random_block)
    return exchanged_shards(queries, key_rows, value_rows, out_grad, random_device, random_block)


def solution(mesh):
    return jax.shard_map(
        shards,
        mesh=mesh,
        in_specs=(
            P(("groups", "seq"), ("heads", "pair")),
            P(("groups", "seq"), ("heads", "pair")),
            P(("groups", "seq"), ("heads", "pair")),
            P(("groups", "seq"), ("heads", "pair")),
            P("groups", None),
            P("groups", None),
        ),
        out_specs=(
            P(("groups", "seq"), ("heads", "pair")),
            P(("groups", "seq"), ("heads", "pair")),
            P(("groups", "seq"), ("heads", "pair")),
        ),
        check_vma=False,
    )
```

```python
import math

import jax
import jax.numpy as jnp
from jax import lax
from jax.experimental import pallas as pl
from jax.experimental.pallas import tpu as pltpu
from jax.sharding import PartitionSpec as P

DH = 128
BLOCK = 64
RAND = 2


def extended(block, sides, width):
    for axis, dim in sides:
        count = lax.axis_size(axis)
        forward = [(i, i + 1) for i in range(count - 1)]
        backward = [(target, source) for source, target in forward]
        low = lax.ppermute(
            lax.slice_in_dim(block, block.shape[dim] - width, None, axis=dim), axis, forward
        )
        high = lax.ppermute(lax.slice_in_dim(block, 0, width, axis=dim), axis, backward)
        block = jnp.concatenate([low, block, high], axis=dim)
    return block


def routing(random_device, random_block, own_index, seq_size, blocks_dev, capacity):
    entries = blocks_dev * RAND
    wanted_from = random_device.reshape(seq_size, entries)
    wanted_block = random_block.reshape(seq_size, entries)
    from_me = (wanted_from == own_index).astype(jnp.int32)
    rank_out = jnp.cumsum(from_me, axis=1) - from_me
    slot_hits = from_me[:, None, :] * (
        rank_out[:, None, :] == jnp.arange(capacity, dtype=jnp.int32)[None, :, None]
    ).astype(jnp.int32)
    block_hits = (
        wanted_block[:, :, None] == jnp.arange(blocks_dev, dtype=jnp.int32)[None, None, :]
    ).astype(jnp.float32)
    selector = jnp.einsum("sce,sej->scj", slot_hits.astype(jnp.float32), block_hits)
    selector = selector.reshape(seq_size * capacity, blocks_dev).astype(jnp.bfloat16)
    own_sources = lax.dynamic_slice_in_dim(
        random_device, own_index * blocks_dev, blocks_dev, 0
    ).reshape(entries)
    peer_hits = (own_sources[:, None] == jnp.arange(seq_size, dtype=jnp.int32)[None, :]).astype(
        jnp.int32
    )
    earlier = jnp.cumsum(peer_hits, axis=0) - peer_hits
    rank_in = jnp.sum(earlier * peer_hits, axis=1)
    slot_index = own_sources * capacity + rank_in
    return (selector, slot_index)


def far_context(arrived, slot_index, blocks_dev):
    picked = jnp.take(arrived, slot_index, axis=0)
    return picked.reshape(blocks_dev, RAND, arrived.shape[1], arrived.shape[2])


def usable_mask(own_index, seq_size, blocks_dev):
    block_ids = jnp.arange(blocks_dev, dtype=jnp.int32)[:, None]
    slot_ids = jnp.arange(3 + RAND, dtype=jnp.int32)[None, :]
    global_block = own_index * blocks_dev + block_ids
    missing = (slot_ids == 0) & (global_block == 0) | (slot_ids == 2) & (
        global_block == seq_size * blocks_dev - 1
    )
    return jnp.repeat(jnp.logical_not(missing), BLOCK, axis=1)


def slot_pieces(haloed, far_blocks, blocks_dev, start_col):
    pieces = []
    for slot in range(3):
        pieces.append(haloed[slot : slot + blocks_dev, :, start_col : start_col + DH])
    far_part = far_blocks[:, :, :, start_col : start_col + DH]
    return (pieces, far_part)


def forward_head(query_tiles, key_pieces, key_far, value_pieces, value_far, usable):
    blocks_dev = query_tiles.shape[0]
    logit_parts = [
        jnp.einsum("bje,bxe->bjx", query_tiles, piece, preferred_element_type=jnp.float32)
        for piece in key_pieces
    ]
    far_logits = jnp.einsum(
        "bje,brxe->bjrx", query_tiles, key_far, preferred_element_type=jnp.float32
    )
    logit_parts.append(far_logits.reshape(blocks_dev, BLOCK, RAND * BLOCK))
    attention_logits = jnp.concatenate(logit_parts, axis=-1) * (1.0 / math.sqrt(DH))
    attention_logits = jnp.where(usable[:, None, :], attention_logits, -jnp.inf)
    row_max = jnp.max(attention_logits, axis=-1, keepdims=True)
    exponent = jnp.exp(attention_logits - row_max)
    row_total = jnp.sum(exponent, axis=-1, keepdims=True)
    probability = exponent / row_total
    softmax_weights = probability.astype(jnp.bfloat16)
    attended = jnp.einsum(
        "bjx,bxe->bje",
        softmax_weights[:, :, :BLOCK],
        value_pieces[0],
        preferred_element_type=jnp.float32,
    )
    for slot in range(1, 3):
        attended = attended + jnp.einsum(
            "bjx,bxe->bje",
            softmax_weights[:, :, slot * BLOCK : (slot + 1) * BLOCK],
            value_pieces[slot],
            preferred_element_type=jnp.float32,
        )
    far_weights = softmax_weights[:, :, 3 * BLOCK :].reshape(blocks_dev, BLOCK, RAND, BLOCK)
    attended = attended + jnp.einsum(
        "bjrx,brxe->bje", far_weights, value_far, preferred_element_type=jnp.float32
    )
    return (probability, attended.astype(jnp.bfloat16))


def backward_head(
    query_tiles, key_pieces, key_far, value_pieces, value_far, gradient_tiles, forward_state
):
    probability, attended_output = forward_state
    blocks_dev = query_tiles.shape[0]
    logit_scale = 1.0 / math.sqrt(DH)
    softmax_weights = probability.astype(jnp.bfloat16)
    row_delta = jnp.sum(
        gradient_tiles.astype(jnp.float32) * attended_output.astype(jnp.float32),
        axis=-1,
        keepdims=True,
    )
    grad_parts = [
        jnp.einsum("bje,bxe->bjx", gradient_tiles, piece, preferred_element_type=jnp.float32)
        for piece in value_pieces
    ]
    far_grad = jnp.einsum(
        "bje,brxe->bjrx", gradient_tiles, value_far, preferred_element_type=jnp.float32
    )
    grad_parts.append(far_grad.reshape(blocks_dev, BLOCK, RAND * BLOCK))
    probability_gradient = jnp.concatenate(grad_parts, axis=-1)
    score_gradient = (probability * (probability_gradient - row_delta)).astype(jnp.bfloat16)
    query_sum = jnp.einsum(
        "bjx,bxe->bje",
        score_gradient[:, :, :BLOCK],
        key_pieces[0],
        preferred_element_type=jnp.float32,
    )
    for slot in range(1, 3):
        query_sum = query_sum + jnp.einsum(
            "bjx,bxe->bje",
            score_gradient[:, :, slot * BLOCK : (slot + 1) * BLOCK],
            key_pieces[slot],
            preferred_element_type=jnp.float32,
        )
    far_scores = score_gradient[:, :, 3 * BLOCK :].reshape(blocks_dev, BLOCK, RAND, BLOCK)
    query_sum = query_sum + jnp.einsum(
        "bjrx,brxe->bje", far_scores, key_far, preferred_element_type=jnp.float32
    )
    query_gradient = (logit_scale * query_sum).astype(jnp.bfloat16)
    key_window, value_window = ([], [])
    for slot in range(3):
        columns = slice(slot * BLOCK, (slot + 1) * BLOCK)
        key_window.append(
            logit_scale
            * jnp.einsum(
                "bjx,bje->bxe",
                score_gradient[:, :, columns],
                query_tiles,
                preferred_element_type=jnp.float32,
            )
        )
        value_window.append(
            jnp.einsum(
                "bjx,bje->bxe",
                softmax_weights[:, :, columns],
                gradient_tiles,
                preferred_element_type=jnp.float32,
            )
        )
    far_weights = softmax_weights[:, :, 3 * BLOCK :].reshape(blocks_dev, BLOCK, RAND, BLOCK)
    key_far_terms = (
        logit_scale
        * jnp.einsum("bjrx,bje->brxe", far_scores, query_tiles, preferred_element_type=jnp.float32)
    ).astype(jnp.bfloat16)
    value_far_terms = jnp.einsum(
        "bjrx,bje->brxe", far_weights, gradient_tiles, preferred_element_type=jnp.float32
    ).astype(jnp.bfloat16)
    return (query_gradient, key_window, value_window, key_far_terms, value_far_terms)


def exchanged_shards(queries, key_rows, value_rows, out_grad, random_device, random_block):
    seq_size = lax.axis_size("seq")
    own_index = lax.axis_index("seq")
    tokens, row_width = queries.shape
    blocks_dev = tokens // BLOCK
    heads_dev = row_width // DH
    capacity = max(2, 3 * blocks_dev // seq_size)
    selector, slot_index = routing(
        random_device, random_block, own_index, seq_size, blocks_dev, capacity
    )
    packed = jnp.concatenate([key_rows, value_rows], axis=1).reshape(
        blocks_dev, BLOCK, 2 * row_width
    )
    flattened = packed.reshape(blocks_dev, BLOCK * 2 * row_width)
    outgoing_blocks = jnp.dot(selector, flattened, preferred_element_type=jnp.float32).astype(
        jnp.bfloat16
    )
    outgoing_blocks = outgoing_blocks.reshape(seq_size * capacity, BLOCK, 2 * row_width)
    haloed = extended(packed, (("seq", 0),), 1)
    arrived = lax.all_to_all(outgoing_blocks, "seq", split_axis=0, concat_axis=0, tiled=True)
    far_blocks = far_context(arrived, slot_index, blocks_dev)
    usable = usable_mask(own_index, seq_size, blocks_dev)
    query_tiles = queries.reshape(blocks_dev, BLOCK, row_width)
    gradient_tiles = out_grad.reshape(blocks_dev, BLOCK, row_width)
    states = []
    for head_index in range(heads_dev):
        key_pieces, key_far = slot_pieces(haloed, far_blocks, blocks_dev, head_index * DH)
        value_pieces, value_far = slot_pieces(
            haloed, far_blocks, blocks_dev, row_width + head_index * DH
        )
        query_head = query_tiles[:, :, head_index * DH : (head_index + 1) * DH]
        states.append(
            forward_head(query_head, key_pieces, key_far, value_pieces, value_far, usable)
        )
    query_parts = []
    window_lists = [[], [], []]
    value_lists = [[], [], []]
    far_keys, far_values = ([], [])
    for head_index in range(heads_dev):
        key_pieces, key_far = slot_pieces(haloed, far_blocks, blocks_dev, head_index * DH)
        value_pieces, value_far = slot_pieces(
            haloed, far_blocks, blocks_dev, row_width + head_index * DH
        )
        query_head = query_tiles[:, :, head_index * DH : (head_index + 1) * DH]
        gradient_head = gradient_tiles[:, :, head_index * DH : (head_index + 1) * DH]
        query_gradient, key_window, value_window, key_far_terms, value_far_terms = backward_head(
            query_head,
            key_pieces,
            key_far,
            value_pieces,
            value_far,
            gradient_head,
            states[head_index],
        )
        query_parts.append(query_gradient)
        for slot in range(3):
            window_lists[slot].append(key_window[slot])
            value_lists[slot].append(value_window[slot])
        far_keys.append(key_far_terms)
        far_values.append(value_far_terms)
    slot_terms = [
        jnp.concatenate(window_lists[slot] + value_lists[slot], axis=-1) for slot in range(3)
    ]
    left_terms = slot_terms[0]
    right_terms = slot_terms[2]
    far_terms = jnp.concatenate(far_keys + far_values, axis=-1).reshape(
        blocks_dev * RAND, BLOCK, 2 * row_width
    )
    edge_terms = jnp.stack([left_terms[0], right_terms[-1]])
    edge_haloed = extended(edge_terms.astype(jnp.bfloat16), (("seq", 0),), 1).astype(
        edge_terms.dtype
    )
    summed = (
        slot_terms[1]
        + jnp.concatenate([left_terms[1:], edge_haloed[3:]], axis=0)
        + jnp.concatenate([edge_haloed[:1], right_terms[:-1]], axis=0)
    )
    returning = (
        jnp.zeros((seq_size * capacity, BLOCK, 2 * row_width), jnp.bfloat16)
        .at[slot_index]
        .set(far_terms)
    )
    returned = lax.all_to_all(returning, "seq", split_axis=0, concat_axis=0, tiled=True)
    gathered_terms = jnp.dot(
        selector.T,
        returned.reshape(seq_size * capacity, BLOCK * 2 * row_width),
        preferred_element_type=jnp.float32,
    )
    summed = summed + gathered_terms.reshape(blocks_dev, BLOCK, 2 * row_width)
    summed = summed.reshape(tokens, 2 * row_width)
    query_out = jnp.concatenate(query_parts, axis=-1).reshape(tokens, row_width)
    return (
        query_out,
        summed[:, :row_width].astype(jnp.bfloat16),
        summed[:, row_width:].astype(jnp.bfloat16),
    )


SLOTS = 3 + RAND


def block_kernel(ids_ref, write_ref, valid_ref, first_ref, q_ref, g_ref, *rest):
    kv_refs = rest[:SLOTS]
    own_ref, spread_ref, dq_ref, acc_ref = rest[SLOTS:]
    step = pl.program_id(0)
    steps = pl.num_programs(0)
    width = q_ref.shape[1]
    blocks_dev = own_ref.shape[0]
    logit_scale = 1.0 / math.sqrt(DH)

    @pl.when(step == 0)
    def _():
        acc_ref[...] = jnp.zeros(acc_ref.shape, jnp.float32)

    context = jnp.concatenate([ref[0] for ref in kv_refs], axis=0)
    slot_of = lax.broadcasted_iota(jnp.int32, (SLOTS * BLOCK, 1), 0) // BLOCK
    usable = slot_of < 0
    for slot in range(SLOTS):
        usable = usable | ((slot_of == slot) & (valid_ref[step * SLOTS + slot] > 0))
    key_parts, value_parts = [], []
    for head in range(width // DH):
        cols = slice(head * DH, (head + 1) * DH)
        vcols = slice(width + head * DH, width + (head + 1) * DH)
        query = q_ref[:, cols]
        grad = g_ref[:, cols]
        keys = context[:, cols]
        values = context[:, vcols]
        logits = lax.dot_general(
            keys, query, (((1,), (1,)), ((), ())), preferred_element_type=jnp.float32
        ) * logit_scale
        logits = jnp.where(usable, logits, -jnp.inf)
        row_max = jnp.max(logits, axis=0, keepdims=True)
        exponent = jnp.exp(logits - row_max)
        row_total = jnp.sum(exponent, axis=0, keepdims=True)
        probability = exponent / row_total
        weights = probability.astype(jnp.bfloat16)
        attended = lax.dot_general(
            weights, values, (((0,), (0,)), ((), ())), preferred_element_type=jnp.float32
        ).astype(jnp.bfloat16)
        product = grad.astype(jnp.float32) * attended.astype(jnp.float32)
        row_delta = jnp.sum(product.T, axis=0, keepdims=True)
        prob_grad = lax.dot_general(
            values, grad, (((1,), (1,)), ((), ())), preferred_element_type=jnp.float32
        )
        score_grad = (probability * (prob_grad - row_delta)).astype(jnp.bfloat16)
        query_grad = logit_scale * lax.dot_general(
            score_grad, keys, (((0,), (0,)), ((), ())), preferred_element_type=jnp.float32
        )
        dq_ref[:, cols] = query_grad.astype(jnp.bfloat16)
        key_parts.append(
            logit_scale * jnp.dot(score_grad, query, preferred_element_type=jnp.float32)
        )
        value_parts.append(jnp.dot(weights, grad, preferred_element_type=jnp.float32))
    terms = jnp.concatenate(key_parts + value_parts, axis=1)
    for slot in range(SLOTS):
        piece = terms[slot * BLOCK : (slot + 1) * BLOCK]
        if slot >= 3:
            piece = piece.astype(jnp.bfloat16).astype(jnp.float32)
        target = write_ref[step * SLOTS + slot]
        acc_ref[target] = acc_ref[target] + piece

    @pl.when(step == steps - 1)
    def _():
        first = first_ref[0]
        spread_ref[...] = acc_ref[...].astype(jnp.bfloat16)
        for block in range(blocks_dev):
            own_ref[block] = acc_ref[first + block]
            spread_ref[first + block] = jnp.zeros(spread_ref.shape[1:], jnp.bfloat16)


def block_attention(ids, write_ids, valid, first, queries, out_grad, source, chunk, width, total):
    tokens = queries.shape[0]
    blocks_dev = tokens // BLOCK

    def context_spec(slot):
        return pl.BlockSpec(
            (1, BLOCK, 2 * width), lambda i, ids, write_ids, valid, first: (ids[i * SLOTS + slot], 0, 0)
        )

    column_spec = pl.BlockSpec((BLOCK, width), lambda i, ids, write_ids, valid, first: (i, chunk))
    row_spec = pl.BlockSpec((BLOCK, width), lambda i, ids, write_ids, valid, first: (i, 0))
    grid_spec = pltpu.PrefetchScalarGridSpec(
        num_scalar_prefetch=4,
        grid=(blocks_dev,),
        in_specs=[column_spec, column_spec] + [context_spec(s) for s in range(SLOTS)],
        out_specs=[
            pl.BlockSpec(
                (blocks_dev, BLOCK, 2 * width), lambda i, ids, write_ids, valid, first: (0, 0, 0)
            ),
            pl.BlockSpec((total, BLOCK, 2 * width), lambda i, ids, write_ids, valid, first: (0, 0, 0)),
            row_spec,
        ],
        scratch_shapes=[pltpu.VMEM((total, BLOCK, 2 * width), jnp.float32)],
    )
    return pl.pallas_call(
        block_kernel,
        grid_spec=grid_spec,
        out_shape=[
            jax.ShapeDtypeStruct((blocks_dev, BLOCK, 2 * width), jnp.float32),
            jax.ShapeDtypeStruct((total, BLOCK, 2 * width), jnp.bfloat16),
            jax.ShapeDtypeStruct((tokens, width), jnp.bfloat16),
        ],
        compiler_params=pltpu.CompilerParams(vmem_limit_bytes=60 * 1024 * 1024),
    )(ids, write_ids, valid, first, queries, out_grad, *([source] * SLOTS))


def gathered_shards(queries, key_rows, value_rows, out_grad, random_device, random_block):
    seq_size = lax.axis_size("seq")
    own_index = lax.axis_index("seq")
    tokens, width = queries.shape
    blocks_dev = tokens // BLOCK
    total = seq_size * blocks_dev
    first = own_index * blocks_dev
    capacity = max(2, 3 * blocks_dev // seq_size)
    selector, slot_index = routing(
        random_device, random_block, own_index, seq_size, blocks_dev, capacity
    )
    block_ids = first + jnp.arange(blocks_dev, dtype=jnp.int32)
    local_ids = jnp.arange(blocks_dev, dtype=jnp.int32)
    own_device = lax.dynamic_slice_in_dim(random_device, first, blocks_dev, 0)
    own_block = lax.dynamic_slice_in_dim(random_block, first, blocks_dev, 0)
    chosen = (own_device * blocks_dev + own_block).astype(jnp.int32)
    window = jnp.stack(
        [jnp.clip(block_ids - 1, 0, total - 1), block_ids, jnp.clip(block_ids + 1, 0, total - 1)],
        axis=1,
    )
    write_ids = jnp.concatenate([window, chosen], axis=1).reshape(-1)
    read_window = jnp.stack([local_ids, local_ids + 1, local_ids + 2], axis=1)
    read_far = (slot_index + blocks_dev + 2).reshape(blocks_dev, RAND).astype(jnp.int32)
    read_ids = jnp.concatenate([read_window, read_far], axis=1).reshape(-1)
    always = jnp.ones_like(block_ids, dtype=jnp.bool_)
    valid = jnp.stack([block_ids > 0, always, block_ids < total - 1] + [always] * RAND, axis=1)
    valid = valid.astype(jnp.int32).reshape(-1)
    first_table = first.reshape(1).astype(jnp.int32)
    chunks = 2 if (width // DH) % 2 == 0 else 1
    part = width // chunks
    sources = []
    previous = None
    for chunk in range(chunks):
        cols = slice(chunk * part, (chunk + 1) * part)
        packed = jnp.concatenate([key_rows[:, cols], value_rows[:, cols]], axis=1)
        packed = packed.reshape(blocks_dev, BLOCK, 2 * part)
        if previous is not None:
            packed, _ = lax.optimization_barrier((packed, previous))
        outgoing = jnp.dot(
            selector, packed.reshape(blocks_dev, BLOCK * 2 * part),
            preferred_element_type=jnp.float32,
        ).astype(jnp.bfloat16)
        outgoing = outgoing.reshape(seq_size * capacity, BLOCK, 2 * part)
        haloed = extended(packed, (("seq", 0),), 1)
        arrived = lax.all_to_all(outgoing, "seq", split_axis=0, concat_axis=0, tiled=True)
        previous = arrived
        sources.append(jnp.concatenate([haloed, arrived], axis=0))
    query_parts, key_parts, value_parts = [], [], []
    for chunk in range(chunks):
        own_sum, spread, query_out = block_attention(
            read_ids, write_ids, valid, first_table, queries, out_grad, sources[chunk],
            chunk, part, total,
        )
        returned = lax.psum_scatter(
            spread.reshape(total * BLOCK, 2 * part), "seq", scatter_dimension=0, tiled=True
        )
        summed = own_sum.reshape(tokens, 2 * part) + returned.astype(jnp.float32)
        query_parts.append(query_out)
        key_parts.append(summed[:, :part].astype(jnp.bfloat16))
        value_parts.append(summed[:, part:].astype(jnp.bfloat16))
    return (
        jnp.concatenate(query_parts, axis=1),
        jnp.concatenate(key_parts, axis=1),
        jnp.concatenate(value_parts, axis=1),
    )


def shards(queries, key_rows, value_rows, out_grad, random_device, random_block):
    if lax.axis_size("seq") <= 8:
        return gathered_shards(queries, key_rows, value_rows, out_grad, random_device, random_block)
    return exchanged_shards(queries, key_rows, value_rows, out_grad, random_device, random_block)


def solution(mesh):
    return jax.shard_map(
        shards,
        mesh=mesh,
        in_specs=(
            P(("groups", "seq"), ("heads", "pair")),
            P(("groups", "seq"), ("heads", "pair")),
            P(("groups", "seq"), ("heads", "pair")),
            P(("groups", "seq"), ("heads", "pair")),
            P("groups", None),
            P("groups", None),
        ),
        out_specs=(
            P(("groups", "seq"), ("heads", "pair")),
            P(("groups", "seq"), ("heads", "pair")),
            P(("groups", "seq"), ("heads", "pair")),
        ),
        check_vma=False,
    )
```

```python
import math

import jax
import jax.numpy as jnp
from jax import lax
from jax.experimental import pallas as pl
from jax.experimental.pallas import tpu as pltpu
from jax.sharding import PartitionSpec as P

DH = 128
BLOCK = 64
RAND = 2


def extended(block, sides, width):
    for axis, dim in sides:
        count = lax.axis_size(axis)
        forward = [(i, i + 1) for i in range(count - 1)]
        backward = [(target, source) for source, target in forward]
        low = lax.ppermute(
            lax.slice_in_dim(block, block.shape[dim] - width, None, axis=dim), axis, forward
        )
        high = lax.ppermute(lax.slice_in_dim(block, 0, width, axis=dim), axis, backward)
        block = jnp.concatenate([low, block, high], axis=dim)
    return block


def routing(random_device, random_block, own_index, seq_size, blocks_dev, capacity):
    entries = blocks_dev * RAND
    wanted_from = random_device.reshape(seq_size, entries)
    wanted_block = random_block.reshape(seq_size, entries)
    from_me = (wanted_from == own_index).astype(jnp.int32)
    rank_out = jnp.cumsum(from_me, axis=1) - from_me
    slot_hits = from_me[:, None, :] * (
        rank_out[:, None, :] == jnp.arange(capacity, dtype=jnp.int32)[None, :, None]
    ).astype(jnp.int32)
    block_hits = (
        wanted_block[:, :, None] == jnp.arange(blocks_dev, dtype=jnp.int32)[None, None, :]
    ).astype(jnp.float32)
    selector = jnp.einsum("sce,sej->scj", slot_hits.astype(jnp.float32), block_hits)
    selector = selector.reshape(seq_size * capacity, blocks_dev).astype(jnp.bfloat16)
    own_sources = lax.dynamic_slice_in_dim(
        random_device, own_index * blocks_dev, blocks_dev, 0
    ).reshape(entries)
    peer_hits = (own_sources[:, None] == jnp.arange(seq_size, dtype=jnp.int32)[None, :]).astype(
        jnp.int32
    )
    earlier = jnp.cumsum(peer_hits, axis=0) - peer_hits
    rank_in = jnp.sum(earlier * peer_hits, axis=1)
    slot_index = own_sources * capacity + rank_in
    return (selector, slot_index)


def far_context(arrived, slot_index, blocks_dev):
    picked = jnp.take(arrived, slot_index, axis=0)
    return picked.reshape(blocks_dev, RAND, arrived.shape[1], arrived.shape[2])


def usable_mask(own_index, seq_size, blocks_dev):
    block_ids = jnp.arange(blocks_dev, dtype=jnp.int32)[:, None]
    slot_ids = jnp.arange(3 + RAND, dtype=jnp.int32)[None, :]
    global_block = own_index * blocks_dev + block_ids
    missing = (slot_ids == 0) & (global_block == 0) | (slot_ids == 2) & (
        global_block == seq_size * blocks_dev - 1
    )
    return jnp.repeat(jnp.logical_not(missing), BLOCK, axis=1)


def slot_pieces(haloed, far_blocks, blocks_dev, start_col):
    pieces = []
    for slot in range(3):
        pieces.append(haloed[slot : slot + blocks_dev, :, start_col : start_col + DH])
    far_part = far_blocks[:, :, :, start_col : start_col + DH]
    return (pieces, far_part)


def forward_head(query_tiles, key_pieces, key_far, value_pieces, value_far, usable):
    blocks_dev = query_tiles.shape[0]
    logit_parts = [
        jnp.einsum("bje,bxe->bjx", query_tiles, piece, preferred_element_type=jnp.float32)
        for piece in key_pieces
    ]
    far_logits = jnp.einsum(
        "bje,brxe->bjrx", query_tiles, key_far, preferred_element_type=jnp.float32
    )
    logit_parts.append(far_logits.reshape(blocks_dev, BLOCK, RAND * BLOCK))
    attention_logits = jnp.concatenate(logit_parts, axis=-1) * (1.0 / math.sqrt(DH))
    attention_logits = jnp.where(usable[:, None, :], attention_logits, -jnp.inf)
    row_max = jnp.max(attention_logits, axis=-1, keepdims=True)
    exponent = jnp.exp(attention_logits - row_max)
    row_total = jnp.sum(exponent, axis=-1, keepdims=True)
    probability = exponent / row_total
    softmax_weights = probability.astype(jnp.bfloat16)
    attended = jnp.einsum(
        "bjx,bxe->bje",
        softmax_weights[:, :, :BLOCK],
        value_pieces[0],
        preferred_element_type=jnp.float32,
    )
    for slot in range(1, 3):
        attended = attended + jnp.einsum(
            "bjx,bxe->bje",
            softmax_weights[:, :, slot * BLOCK : (slot + 1) * BLOCK],
            value_pieces[slot],
            preferred_element_type=jnp.float32,
        )
    far_weights = softmax_weights[:, :, 3 * BLOCK :].reshape(blocks_dev, BLOCK, RAND, BLOCK)
    attended = attended + jnp.einsum(
        "bjrx,brxe->bje", far_weights, value_far, preferred_element_type=jnp.float32
    )
    return (probability, attended.astype(jnp.bfloat16))


def backward_head(
    query_tiles, key_pieces, key_far, value_pieces, value_far, gradient_tiles, forward_state
):
    probability, attended_output = forward_state
    blocks_dev = query_tiles.shape[0]
    logit_scale = 1.0 / math.sqrt(DH)
    softmax_weights = probability.astype(jnp.bfloat16)
    row_delta = jnp.sum(
        gradient_tiles.astype(jnp.float32) * attended_output.astype(jnp.float32),
        axis=-1,
        keepdims=True,
    )
    grad_parts = [
        jnp.einsum("bje,bxe->bjx", gradient_tiles, piece, preferred_element_type=jnp.float32)
        for piece in value_pieces
    ]
    far_grad = jnp.einsum(
        "bje,brxe->bjrx", gradient_tiles, value_far, preferred_element_type=jnp.float32
    )
    grad_parts.append(far_grad.reshape(blocks_dev, BLOCK, RAND * BLOCK))
    probability_gradient = jnp.concatenate(grad_parts, axis=-1)
    score_gradient = (probability * (probability_gradient - row_delta)).astype(jnp.bfloat16)
    query_sum = jnp.einsum(
        "bjx,bxe->bje",
        score_gradient[:, :, :BLOCK],
        key_pieces[0],
        preferred_element_type=jnp.float32,
    )
    for slot in range(1, 3):
        query_sum = query_sum + jnp.einsum(
            "bjx,bxe->bje",
            score_gradient[:, :, slot * BLOCK : (slot + 1) * BLOCK],
            key_pieces[slot],
            preferred_element_type=jnp.float32,
        )
    far_scores = score_gradient[:, :, 3 * BLOCK :].reshape(blocks_dev, BLOCK, RAND, BLOCK)
    query_sum = query_sum + jnp.einsum(
        "bjrx,brxe->bje", far_scores, key_far, preferred_element_type=jnp.float32
    )
    query_gradient = (logit_scale * query_sum).astype(jnp.bfloat16)
    key_window, value_window = ([], [])
    for slot in range(3):
        columns = slice(slot * BLOCK, (slot + 1) * BLOCK)
        key_window.append(
            logit_scale
            * jnp.einsum(
                "bjx,bje->bxe",
                score_gradient[:, :, columns],
                query_tiles,
                preferred_element_type=jnp.float32,
            )
        )
        value_window.append(
            jnp.einsum(
                "bjx,bje->bxe",
                softmax_weights[:, :, columns],
                gradient_tiles,
                preferred_element_type=jnp.float32,
            )
        )
    far_weights = softmax_weights[:, :, 3 * BLOCK :].reshape(blocks_dev, BLOCK, RAND, BLOCK)
    key_far_terms = (
        logit_scale
        * jnp.einsum("bjrx,bje->brxe", far_scores, query_tiles, preferred_element_type=jnp.float32)
    ).astype(jnp.bfloat16)
    value_far_terms = jnp.einsum(
        "bjrx,bje->brxe", far_weights, gradient_tiles, preferred_element_type=jnp.float32
    ).astype(jnp.bfloat16)
    return (query_gradient, key_window, value_window, key_far_terms, value_far_terms)


def exchanged_shards(queries, key_rows, value_rows, out_grad, random_device, random_block):
    seq_size = lax.axis_size("seq")
    own_index = lax.axis_index("seq")
    tokens, row_width = queries.shape
    blocks_dev = tokens // BLOCK
    heads_dev = row_width // DH
    capacity = max(2, 3 * blocks_dev // seq_size)
    selector, slot_index = routing(
        random_device, random_block, own_index, seq_size, blocks_dev, capacity
    )
    packed = jnp.concatenate([key_rows, value_rows], axis=1).reshape(
        blocks_dev, BLOCK, 2 * row_width
    )
    flattened = packed.reshape(blocks_dev, BLOCK * 2 * row_width)
    outgoing_blocks = jnp.dot(selector, flattened, preferred_element_type=jnp.float32).astype(
        jnp.bfloat16
    )
    outgoing_blocks = outgoing_blocks.reshape(seq_size * capacity, BLOCK, 2 * row_width)
    haloed = extended(packed, (("seq", 0),), 1)
    arrived = lax.all_to_all(outgoing_blocks, "seq", split_axis=0, concat_axis=0, tiled=True)
    far_blocks = far_context(arrived, slot_index, blocks_dev)
    usable = usable_mask(own_index, seq_size, blocks_dev)
    query_tiles = queries.reshape(blocks_dev, BLOCK, row_width)
    gradient_tiles = out_grad.reshape(blocks_dev, BLOCK, row_width)
    states = []
    for head_index in range(heads_dev):
        key_pieces, key_far = slot_pieces(haloed, far_blocks, blocks_dev, head_index * DH)
        value_pieces, value_far = slot_pieces(
            haloed, far_blocks, blocks_dev, row_width + head_index * DH
        )
        query_head = query_tiles[:, :, head_index * DH : (head_index + 1) * DH]
        states.append(
            forward_head(query_head, key_pieces, key_far, value_pieces, value_far, usable)
        )
    query_parts = []
    window_lists = [[], [], []]
    value_lists = [[], [], []]
    far_keys, far_values = ([], [])
    for head_index in range(heads_dev):
        key_pieces, key_far = slot_pieces(haloed, far_blocks, blocks_dev, head_index * DH)
        value_pieces, value_far = slot_pieces(
            haloed, far_blocks, blocks_dev, row_width + head_index * DH
        )
        query_head = query_tiles[:, :, head_index * DH : (head_index + 1) * DH]
        gradient_head = gradient_tiles[:, :, head_index * DH : (head_index + 1) * DH]
        query_gradient, key_window, value_window, key_far_terms, value_far_terms = backward_head(
            query_head,
            key_pieces,
            key_far,
            value_pieces,
            value_far,
            gradient_head,
            states[head_index],
        )
        query_parts.append(query_gradient)
        for slot in range(3):
            window_lists[slot].append(key_window[slot])
            value_lists[slot].append(value_window[slot])
        far_keys.append(key_far_terms)
        far_values.append(value_far_terms)
    slot_terms = [
        jnp.concatenate(window_lists[slot] + value_lists[slot], axis=-1) for slot in range(3)
    ]
    left_terms = slot_terms[0]
    right_terms = slot_terms[2]
    far_terms = jnp.concatenate(far_keys + far_values, axis=-1).reshape(
        blocks_dev * RAND, BLOCK, 2 * row_width
    )
    edge_terms = jnp.stack([left_terms[0], right_terms[-1]])
    edge_haloed = extended(edge_terms.astype(jnp.bfloat16), (("seq", 0),), 1).astype(
        edge_terms.dtype
    )
    summed = (
        slot_terms[1]
        + jnp.concatenate([left_terms[1:], edge_haloed[3:]], axis=0)
        + jnp.concatenate([edge_haloed[:1], right_terms[:-1]], axis=0)
    )
    returning = (
        jnp.zeros((seq_size * capacity, BLOCK, 2 * row_width), jnp.bfloat16)
        .at[slot_index]
        .set(far_terms)
    )
    returned = lax.all_to_all(returning, "seq", split_axis=0, concat_axis=0, tiled=True)
    gathered_terms = jnp.dot(
        selector.T,
        returned.reshape(seq_size * capacity, BLOCK * 2 * row_width),
        preferred_element_type=jnp.float32,
    )
    summed = summed + gathered_terms.reshape(blocks_dev, BLOCK, 2 * row_width)
    summed = summed.reshape(tokens, 2 * row_width)
    query_out = jnp.concatenate(query_parts, axis=-1).reshape(tokens, row_width)
    return (
        query_out,
        summed[:, :row_width].astype(jnp.bfloat16),
        summed[:, row_width:].astype(jnp.bfloat16),
    )


SLOTS = 3 + RAND


def block_kernel(ids_ref, valid_ref, first_ref, q_ref, g_ref, *rest):
    kv_refs = rest[:SLOTS]
    own_ref, spread_ref, dq_ref, acc_ref = rest[SLOTS:]
    step = pl.program_id(0)
    steps = pl.num_programs(0)
    width = q_ref.shape[1]
    blocks_dev = own_ref.shape[0]
    logit_scale = 1.0 / math.sqrt(DH)

    @pl.when(step == 0)
    def _():
        acc_ref[...] = jnp.zeros(acc_ref.shape, jnp.float32)

    context = jnp.concatenate([ref[0] for ref in kv_refs], axis=0)
    slot_of = lax.broadcasted_iota(jnp.int32, (SLOTS * BLOCK, 1), 0) // BLOCK
    usable = slot_of < 0
    for slot in range(SLOTS):
        usable = usable | ((slot_of == slot) & (valid_ref[step * SLOTS + slot] > 0))
    key_parts, value_parts = [], []
    for head in range(width // DH):
        cols = slice(head * DH, (head + 1) * DH)
        vcols = slice(width + head * DH, width + (head + 1) * DH)
        query = q_ref[:, cols]
        grad = g_ref[:, cols]
        keys = context[:, cols]
        values = context[:, vcols]
        logits = lax.dot_general(
            keys, query, (((1,), (1,)), ((), ())), preferred_element_type=jnp.float32
        ) * logit_scale
        logits = jnp.where(usable, logits, -jnp.inf)
        row_max = jnp.max(logits, axis=0, keepdims=True)
        exponent = jnp.exp(logits - row_max)
        row_total = jnp.sum(exponent, axis=0, keepdims=True)
        probability = exponent / row_total
        weights = probability.astype(jnp.bfloat16)
        attended = lax.dot_general(
            weights, values, (((0,), (0,)), ((), ())), preferred_element_type=jnp.float32
        ).astype(jnp.bfloat16)
        product = grad.astype(jnp.float32) * attended.astype(jnp.float32)
        row_delta = jnp.sum(product.T, axis=0, keepdims=True)
        prob_grad = lax.dot_general(
            values, grad, (((1,), (1,)), ((), ())), preferred_element_type=jnp.float32
        )
        score_grad = (probability * (prob_grad - row_delta)).astype(jnp.bfloat16)
        query_grad = logit_scale * lax.dot_general(
            score_grad, keys, (((0,), (0,)), ((), ())), preferred_element_type=jnp.float32
        )
        dq_ref[:, cols] = query_grad.astype(jnp.bfloat16)
        key_parts.append(
            logit_scale * jnp.dot(score_grad, query, preferred_element_type=jnp.float32)
        )
        value_parts.append(jnp.dot(weights, grad, preferred_element_type=jnp.float32))
    terms = jnp.concatenate(key_parts + value_parts, axis=1)
    for slot in range(SLOTS):
        piece = terms[slot * BLOCK : (slot + 1) * BLOCK]
        if slot >= 3:
            piece = piece.astype(jnp.bfloat16).astype(jnp.float32)
        target = ids_ref[step * SLOTS + slot]
        acc_ref[target] = acc_ref[target] + piece

    @pl.when(step == steps - 1)
    def _():
        first = first_ref[0]
        spread_ref[...] = acc_ref[...].astype(jnp.bfloat16)
        for block in range(blocks_dev):
            own_ref[block] = acc_ref[first + block]
            spread_ref[first + block] = jnp.zeros(spread_ref.shape[1:], jnp.bfloat16)


def block_attention(ids, valid, first, queries, out_grad, source, chunk, width):
    tokens = queries.shape[0]
    blocks_dev = tokens // BLOCK
    total = source.shape[0]

    def context_spec(slot):
        return pl.BlockSpec(
            (1, BLOCK, 2 * width), lambda i, ids, valid, first: (ids[i * SLOTS + slot], 0, 0)
        )

    column_spec = pl.BlockSpec((BLOCK, width), lambda i, ids, valid, first: (i, chunk))
    row_spec = pl.BlockSpec((BLOCK, width), lambda i, ids, valid, first: (i, 0))
    grid_spec = pltpu.PrefetchScalarGridSpec(
        num_scalar_prefetch=3,
        grid=(blocks_dev,),
        in_specs=[column_spec, column_spec] + [context_spec(s) for s in range(SLOTS)],
        out_specs=[
            pl.BlockSpec(
                (blocks_dev, BLOCK, 2 * width), lambda i, ids, valid, first: (0, 0, 0)
            ),
            pl.BlockSpec((total, BLOCK, 2 * width), lambda i, ids, valid, first: (0, 0, 0)),
            row_spec,
        ],
        scratch_shapes=[pltpu.VMEM((total, BLOCK, 2 * width), jnp.float32)],
    )
    return pl.pallas_call(
        block_kernel,
        grid_spec=grid_spec,
        out_shape=[
            jax.ShapeDtypeStruct((blocks_dev, BLOCK, 2 * width), jnp.float32),
            jax.ShapeDtypeStruct((total, BLOCK, 2 * width), jnp.bfloat16),
            jax.ShapeDtypeStruct((tokens, width), jnp.bfloat16),
        ],
        compiler_params=pltpu.CompilerParams(vmem_limit_bytes=60 * 1024 * 1024),
    )(ids, valid, first, queries, out_grad, *([source] * SLOTS))


def ring_reduce(spread, own_index, seq_size):
    parts = spread.reshape((seq_size, spread.shape[0] // seq_size) + spread.shape[1:])
    from_left = jnp.zeros(parts.shape[1:], jnp.bfloat16)
    from_right = jnp.zeros(parts.shape[1:], jnp.bfloat16)
    for hop in range(1, seq_size):
        owner = jnp.clip(seq_size + own_index - hop, 0, seq_size - 1)
        piece = lax.dynamic_index_in_dim(parts, owner, 0, keepdims=False).astype(jnp.float32)
        piece = (piece + from_left.astype(jnp.float32)).astype(jnp.bfloat16)
        from_left = lax.ppermute(piece, "seq", [(i, i + 1) for i in range(hop)])
        owner = jnp.clip(own_index + hop - seq_size, 0, seq_size - 1)
        piece = lax.dynamic_index_in_dim(parts, owner, 0, keepdims=False).astype(jnp.float32)
        piece = (piece + from_right.astype(jnp.float32)).astype(jnp.bfloat16)
        from_right = lax.ppermute(
            piece, "seq", [(i, i - 1) for i in range(seq_size - hop, seq_size)]
        )
    return from_left.astype(jnp.float32) + from_right.astype(jnp.float32)


def gathered_shards(queries, key_rows, value_rows, out_grad, random_device, random_block):
    seq_size = lax.axis_size("seq")
    own_index = lax.axis_index("seq")
    tokens, width = queries.shape
    blocks_dev = tokens // BLOCK
    total = seq_size * blocks_dev
    first = own_index * blocks_dev
    block_ids = first + jnp.arange(blocks_dev, dtype=jnp.int32)
    own_device = lax.dynamic_slice_in_dim(random_device, first, blocks_dev, 0)
    own_block = lax.dynamic_slice_in_dim(random_block, first, blocks_dev, 0)
    chosen = (own_device * blocks_dev + own_block).astype(jnp.int32)
    window = jnp.stack(
        [jnp.clip(block_ids - 1, 0, total - 1), block_ids, jnp.clip(block_ids + 1, 0, total - 1)],
        axis=1,
    )
    ids = jnp.concatenate([window, chosen], axis=1).reshape(-1)
    always = jnp.ones_like(block_ids, dtype=jnp.bool_)
    valid = jnp.stack([block_ids > 0, always, block_ids < total - 1] + [always] * RAND, axis=1)
    valid = valid.astype(jnp.int32).reshape(-1)
    first_table = first.reshape(1).astype(jnp.int32)
    chunks = 2 if (width // DH) % 2 == 0 else 1
    part = width // chunks
    sources = []
    for chunk in range(chunks):
        cols = slice(chunk * part, (chunk + 1) * part)
        packed = jnp.concatenate([key_rows[:, cols], value_rows[:, cols]], axis=1)
        gathered = lax.all_gather(packed, "seq", axis=0, tiled=True)
        sources.append(gathered.reshape(total, BLOCK, 2 * part))
    query_parts, key_parts, value_parts = [], [], []
    returned = None
    for chunk in range(chunks):
        table = first_table
        if returned is not None:
            table = table + (returned[0, :1] * 0.0).astype(jnp.int32)
        own_sum, spread, query_out = block_attention(
            ids, valid, table, queries, out_grad, sources[chunk], chunk, part
        )
        if chunk == 0 and chunks > 1:
            returned = ring_reduce(spread, own_index, seq_size).reshape(tokens, 2 * part)
        else:
            returned = lax.psum_scatter(
                spread.reshape(total * BLOCK, 2 * part), "seq", scatter_dimension=0, tiled=True
            ).astype(jnp.float32)
        summed = own_sum.reshape(tokens, 2 * part) + returned
        query_parts.append(query_out)
        key_parts.append(summed[:, :part].astype(jnp.bfloat16))
        value_parts.append(summed[:, part:].astype(jnp.bfloat16))
    return (
        jnp.concatenate(query_parts, axis=1),
        jnp.concatenate(key_parts, axis=1),
        jnp.concatenate(value_parts, axis=1),
    )


def shards(queries, key_rows, value_rows, out_grad, random_device, random_block):
    if lax.axis_size("seq") <= 8:
        return gathered_shards(queries, key_rows, value_rows, out_grad, random_device, random_block)
    return exchanged_shards(queries, key_rows, value_rows, out_grad, random_device, random_block)


def solution(mesh):
    return jax.shard_map(
        shards,
        mesh=mesh,
        in_specs=(
            P(("groups", "seq"), ("heads", "pair")),
            P(("groups", "seq"), ("heads", "pair")),
            P(("groups", "seq"), ("heads", "pair")),
            P(("groups", "seq"), ("heads", "pair")),
            P("groups", None),
            P("groups", None),
        ),
        out_specs=(
            P(("groups", "seq"), ("heads", "pair")),
            P(("groups", "seq"), ("heads", "pair")),
            P(("groups", "seq"), ("heads", "pair")),
        ),
        check_vma=False,
    )
```

```python
import math

import jax
import jax.numpy as jnp
from jax import lax
from jax.experimental import pallas as pl
from jax.experimental.pallas import tpu as pltpu
from jax.sharding import PartitionSpec as P

DH = 128
BLOCK = 64
RAND = 2


def extended(block, sides, width):
    for axis, dim in sides:
        count = lax.axis_size(axis)
        forward = [(i, i + 1) for i in range(count - 1)]
        backward = [(target, source) for source, target in forward]
        low = lax.ppermute(
            lax.slice_in_dim(block, block.shape[dim] - width, None, axis=dim), axis, forward
        )
        high = lax.ppermute(lax.slice_in_dim(block, 0, width, axis=dim), axis, backward)
        block = jnp.concatenate([low, block, high], axis=dim)
    return block


def routing(random_device, random_block, own_index, seq_size, blocks_dev, capacity):
    entries = blocks_dev * RAND
    wanted_from = random_device.reshape(seq_size, entries)
    wanted_block = random_block.reshape(seq_size, entries)
    from_me = (wanted_from == own_index).astype(jnp.int32)
    rank_out = jnp.cumsum(from_me, axis=1) - from_me
    slot_hits = from_me[:, None, :] * (
        rank_out[:, None, :] == jnp.arange(capacity, dtype=jnp.int32)[None, :, None]
    ).astype(jnp.int32)
    block_hits = (
        wanted_block[:, :, None] == jnp.arange(blocks_dev, dtype=jnp.int32)[None, None, :]
    ).astype(jnp.float32)
    selector = jnp.einsum("sce,sej->scj", slot_hits.astype(jnp.float32), block_hits)
    selector = selector.reshape(seq_size * capacity, blocks_dev).astype(jnp.bfloat16)
    own_sources = lax.dynamic_slice_in_dim(
        random_device, own_index * blocks_dev, blocks_dev, 0
    ).reshape(entries)
    peer_hits = (own_sources[:, None] == jnp.arange(seq_size, dtype=jnp.int32)[None, :]).astype(
        jnp.int32
    )
    earlier = jnp.cumsum(peer_hits, axis=0) - peer_hits
    rank_in = jnp.sum(earlier * peer_hits, axis=1)
    slot_index = own_sources * capacity + rank_in
    return (selector, slot_index)


def far_context(arrived, slot_index, blocks_dev):
    picked = jnp.take(arrived, slot_index, axis=0)
    return picked.reshape(blocks_dev, RAND, arrived.shape[1], arrived.shape[2])


def usable_mask(own_index, seq_size, blocks_dev):
    block_ids = jnp.arange(blocks_dev, dtype=jnp.int32)[:, None]
    slot_ids = jnp.arange(3 + RAND, dtype=jnp.int32)[None, :]
    global_block = own_index * blocks_dev + block_ids
    missing = (slot_ids == 0) & (global_block == 0) | (slot_ids == 2) & (
        global_block == seq_size * blocks_dev - 1
    )
    return jnp.repeat(jnp.logical_not(missing), BLOCK, axis=1)


def slot_pieces(haloed, far_blocks, blocks_dev, start_col):
    pieces = []
    for slot in range(3):
        pieces.append(haloed[slot : slot + blocks_dev, :, start_col : start_col + DH])
    far_part = far_blocks[:, :, :, start_col : start_col + DH]
    return (pieces, far_part)


def forward_head(query_tiles, key_pieces, key_far, value_pieces, value_far, usable):
    blocks_dev = query_tiles.shape[0]
    logit_parts = [
        jnp.einsum("bje,bxe->bjx", query_tiles, piece, preferred_element_type=jnp.float32)
        for piece in key_pieces
    ]
    far_logits = jnp.einsum(
        "bje,brxe->bjrx", query_tiles, key_far, preferred_element_type=jnp.float32
    )
    logit_parts.append(far_logits.reshape(blocks_dev, BLOCK, RAND * BLOCK))
    attention_logits = jnp.concatenate(logit_parts, axis=-1) * (1.0 / math.sqrt(DH))
    attention_logits = jnp.where(usable[:, None, :], attention_logits, -jnp.inf)
    row_max = jnp.max(attention_logits, axis=-1, keepdims=True)
    exponent = jnp.exp(attention_logits - row_max)
    row_total = jnp.sum(exponent, axis=-1, keepdims=True)
    probability = exponent / row_total
    softmax_weights = probability.astype(jnp.bfloat16)
    attended = jnp.einsum(
        "bjx,bxe->bje",
        softmax_weights[:, :, :BLOCK],
        value_pieces[0],
        preferred_element_type=jnp.float32,
    )
    for slot in range(1, 3):
        attended = attended + jnp.einsum(
            "bjx,bxe->bje",
            softmax_weights[:, :, slot * BLOCK : (slot + 1) * BLOCK],
            value_pieces[slot],
            preferred_element_type=jnp.float32,
        )
    far_weights = softmax_weights[:, :, 3 * BLOCK :].reshape(blocks_dev, BLOCK, RAND, BLOCK)
    attended = attended + jnp.einsum(
        "bjrx,brxe->bje", far_weights, value_far, preferred_element_type=jnp.float32
    )
    return (probability, attended.astype(jnp.bfloat16))


def backward_head(
    query_tiles, key_pieces, key_far, value_pieces, value_far, gradient_tiles, forward_state
):
    probability, attended_output = forward_state
    blocks_dev = query_tiles.shape[0]
    logit_scale = 1.0 / math.sqrt(DH)
    softmax_weights = probability.astype(jnp.bfloat16)
    row_delta = jnp.sum(
        gradient_tiles.astype(jnp.float32) * attended_output.astype(jnp.float32),
        axis=-1,
        keepdims=True,
    )
    grad_parts = [
        jnp.einsum("bje,bxe->bjx", gradient_tiles, piece, preferred_element_type=jnp.float32)
        for piece in value_pieces
    ]
    far_grad = jnp.einsum(
        "bje,brxe->bjrx", gradient_tiles, value_far, preferred_element_type=jnp.float32
    )
    grad_parts.append(far_grad.reshape(blocks_dev, BLOCK, RAND * BLOCK))
    probability_gradient = jnp.concatenate(grad_parts, axis=-1)
    score_gradient = (probability * (probability_gradient - row_delta)).astype(jnp.bfloat16)
    query_sum = jnp.einsum(
        "bjx,bxe->bje",
        score_gradient[:, :, :BLOCK],
        key_pieces[0],
        preferred_element_type=jnp.float32,
    )
    for slot in range(1, 3):
        query_sum = query_sum + jnp.einsum(
            "bjx,bxe->bje",
            score_gradient[:, :, slot * BLOCK : (slot + 1) * BLOCK],
            key_pieces[slot],
            preferred_element_type=jnp.float32,
        )
    far_scores = score_gradient[:, :, 3 * BLOCK :].reshape(blocks_dev, BLOCK, RAND, BLOCK)
    query_sum = query_sum + jnp.einsum(
        "bjrx,brxe->bje", far_scores, key_far, preferred_element_type=jnp.float32
    )
    query_gradient = (logit_scale * query_sum).astype(jnp.bfloat16)
    key_window, value_window = ([], [])
    for slot in range(3):
        columns = slice(slot * BLOCK, (slot + 1) * BLOCK)
        key_window.append(
            logit_scale
            * jnp.einsum(
                "bjx,bje->bxe",
                score_gradient[:, :, columns],
                query_tiles,
                preferred_element_type=jnp.float32,
            )
        )
        value_window.append(
            jnp.einsum(
                "bjx,bje->bxe",
                softmax_weights[:, :, columns],
                gradient_tiles,
                preferred_element_type=jnp.float32,
            )
        )
    far_weights = softmax_weights[:, :, 3 * BLOCK :].reshape(blocks_dev, BLOCK, RAND, BLOCK)
    key_far_terms = (
        logit_scale
        * jnp.einsum("bjrx,bje->brxe", far_scores, query_tiles, preferred_element_type=jnp.float32)
    ).astype(jnp.bfloat16)
    value_far_terms = jnp.einsum(
        "bjrx,bje->brxe", far_weights, gradient_tiles, preferred_element_type=jnp.float32
    ).astype(jnp.bfloat16)
    return (query_gradient, key_window, value_window, key_far_terms, value_far_terms)


def exchanged_shards(queries, key_rows, value_rows, out_grad, random_device, random_block):
    seq_size = lax.axis_size("seq")
    own_index = lax.axis_index("seq")
    tokens, row_width = queries.shape
    blocks_dev = tokens // BLOCK
    heads_dev = row_width // DH
    capacity = max(2, 3 * blocks_dev // seq_size)
    selector, slot_index = routing(
        random_device, random_block, own_index, seq_size, blocks_dev, capacity
    )
    packed = jnp.concatenate([key_rows, value_rows], axis=1).reshape(
        blocks_dev, BLOCK, 2 * row_width
    )
    flattened = packed.reshape(blocks_dev, BLOCK * 2 * row_width)
    outgoing_blocks = jnp.dot(selector, flattened, preferred_element_type=jnp.float32).astype(
        jnp.bfloat16
    )
    outgoing_blocks = outgoing_blocks.reshape(seq_size * capacity, BLOCK, 2 * row_width)
    haloed = extended(packed, (("seq", 0),), 1)
    arrived = lax.all_to_all(outgoing_blocks, "seq", split_axis=0, concat_axis=0, tiled=True)
    far_blocks = far_context(arrived, slot_index, blocks_dev)
    usable = usable_mask(own_index, seq_size, blocks_dev)
    query_tiles = queries.reshape(blocks_dev, BLOCK, row_width)
    gradient_tiles = out_grad.reshape(blocks_dev, BLOCK, row_width)
    states = []
    for head_index in range(heads_dev):
        key_pieces, key_far = slot_pieces(haloed, far_blocks, blocks_dev, head_index * DH)
        value_pieces, value_far = slot_pieces(
            haloed, far_blocks, blocks_dev, row_width + head_index * DH
        )
        query_head = query_tiles[:, :, head_index * DH : (head_index + 1) * DH]
        states.append(
            forward_head(query_head, key_pieces, key_far, value_pieces, value_far, usable)
        )
    query_parts = []
    window_lists = [[], [], []]
    value_lists = [[], [], []]
    far_keys, far_values = ([], [])
    for head_index in range(heads_dev):
        key_pieces, key_far = slot_pieces(haloed, far_blocks, blocks_dev, head_index * DH)
        value_pieces, value_far = slot_pieces(
            haloed, far_blocks, blocks_dev, row_width + head_index * DH
        )
        query_head = query_tiles[:, :, head_index * DH : (head_index + 1) * DH]
        gradient_head = gradient_tiles[:, :, head_index * DH : (head_index + 1) * DH]
        query_gradient, key_window, value_window, key_far_terms, value_far_terms = backward_head(
            query_head,
            key_pieces,
            key_far,
            value_pieces,
            value_far,
            gradient_head,
            states[head_index],
        )
        query_parts.append(query_gradient)
        for slot in range(3):
            window_lists[slot].append(key_window[slot])
            value_lists[slot].append(value_window[slot])
        far_keys.append(key_far_terms)
        far_values.append(value_far_terms)
    slot_terms = [
        jnp.concatenate(window_lists[slot] + value_lists[slot], axis=-1) for slot in range(3)
    ]
    left_terms = slot_terms[0]
    right_terms = slot_terms[2]
    far_terms = jnp.concatenate(far_keys + far_values, axis=-1).reshape(
        blocks_dev * RAND, BLOCK, 2 * row_width
    )
    edge_terms = jnp.stack([left_terms[0], right_terms[-1]])
    edge_haloed = extended(edge_terms.astype(jnp.bfloat16), (("seq", 0),), 1).astype(
        edge_terms.dtype
    )
    summed = (
        slot_terms[1]
        + jnp.concatenate([left_terms[1:], edge_haloed[3:]], axis=0)
        + jnp.concatenate([edge_haloed[:1], right_terms[:-1]], axis=0)
    )
    returning = (
        jnp.zeros((seq_size * capacity, BLOCK, 2 * row_width), jnp.bfloat16)
        .at[slot_index]
        .set(far_terms)
    )
    returned = lax.all_to_all(returning, "seq", split_axis=0, concat_axis=0, tiled=True)
    gathered_terms = jnp.dot(
        selector.T,
        returned.reshape(seq_size * capacity, BLOCK * 2 * row_width),
        preferred_element_type=jnp.float32,
    )
    summed = summed + gathered_terms.reshape(blocks_dev, BLOCK, 2 * row_width)
    summed = summed.reshape(tokens, 2 * row_width)
    query_out = jnp.concatenate(query_parts, axis=-1).reshape(tokens, row_width)
    return (
        query_out,
        summed[:, :row_width].astype(jnp.bfloat16),
        summed[:, row_width:].astype(jnp.bfloat16),
    )


SLOTS = 3 + RAND


def block_kernel(ids_ref, write_ref, valid_ref, first_ref, q_ref, g_ref, *rest):
    kv_refs = rest[:SLOTS]
    own_ref, spread_ref, dq_ref, acc_ref = rest[SLOTS:]
    step = pl.program_id(0)
    steps = pl.num_programs(0)
    width = q_ref.shape[1]
    blocks_dev = own_ref.shape[0]
    logit_scale = 1.0 / math.sqrt(DH)

    @pl.when(step == 0)
    def _():
        acc_ref[...] = jnp.zeros(acc_ref.shape, jnp.float32)

    context = jnp.concatenate([ref[0] for ref in kv_refs], axis=0)
    slot_of = lax.broadcasted_iota(jnp.int32, (SLOTS * BLOCK, 1), 0) // BLOCK
    usable = slot_of < 0
    for slot in range(SLOTS):
        usable = usable | ((slot_of == slot) & (valid_ref[step * SLOTS + slot] > 0))
    key_parts, value_parts = [], []
    for head in range(width // DH):
        cols = slice(head * DH, (head + 1) * DH)
        vcols = slice(width + head * DH, width + (head + 1) * DH)
        query = q_ref[:, cols]
        grad = g_ref[:, cols]
        keys = context[:, cols]
        values = context[:, vcols]
        logits = lax.dot_general(
            keys, query, (((1,), (1,)), ((), ())), preferred_element_type=jnp.float32
        ) * logit_scale
        logits = jnp.where(usable, logits, -jnp.inf)
        row_max = jnp.max(logits, axis=0, keepdims=True)
        exponent = jnp.exp(logits - row_max)
        row_total = jnp.sum(exponent, axis=0, keepdims=True)
        probability = exponent / row_total
        weights = probability.astype(jnp.bfloat16)
        attended = lax.dot_general(
            weights, values, (((0,), (0,)), ((), ())), preferred_element_type=jnp.float32
        ).astype(jnp.bfloat16)
        product = grad.astype(jnp.float32) * attended.astype(jnp.float32)
        row_delta = jnp.sum(product.T, axis=0, keepdims=True)
        prob_grad = lax.dot_general(
            values, grad, (((1,), (1,)), ((), ())), preferred_element_type=jnp.float32
        )
        score_grad = (probability * (prob_grad - row_delta)).astype(jnp.bfloat16)
        query_grad = logit_scale * lax.dot_general(
            score_grad, keys, (((0,), (0,)), ((), ())), preferred_element_type=jnp.float32
        )
        dq_ref[:, cols] = query_grad.astype(jnp.bfloat16)
        key_parts.append(
            logit_scale * jnp.dot(score_grad, query, preferred_element_type=jnp.float32)
        )
        value_parts.append(jnp.dot(weights, grad, preferred_element_type=jnp.float32))
    terms = jnp.concatenate(key_parts + value_parts, axis=1)
    for slot in range(SLOTS):
        piece = terms[slot * BLOCK : (slot + 1) * BLOCK]
        if slot >= 3:
            piece = piece.astype(jnp.bfloat16).astype(jnp.float32)
        target = write_ref[step * SLOTS + slot]
        acc_ref[target] = acc_ref[target] + piece

    @pl.when(step == steps - 1)
    def _():
        first = first_ref[0]
        spread_ref[...] = acc_ref[...].astype(jnp.bfloat16)
        for block in range(blocks_dev):
            own_ref[block] = acc_ref[first + block]
            spread_ref[first + block] = jnp.zeros(spread_ref.shape[1:], jnp.bfloat16)


def block_attention(ids, write_ids, valid, first, queries, out_grad, source, chunk, width, total):
    tokens = queries.shape[0]
    blocks_dev = tokens // BLOCK

    def context_spec(slot):
        return pl.BlockSpec(
            (1, BLOCK, 2 * width), lambda i, ids, write_ids, valid, first: (ids[i * SLOTS + slot], 0, 0)
        )

    column_spec = pl.BlockSpec((BLOCK, width), lambda i, ids, write_ids, valid, first: (i, chunk))
    row_spec = pl.BlockSpec((BLOCK, width), lambda i, ids, write_ids, valid, first: (i, 0))
    grid_spec = pltpu.PrefetchScalarGridSpec(
        num_scalar_prefetch=4,
        grid=(blocks_dev,),
        in_specs=[column_spec, column_spec] + [context_spec(s) for s in range(SLOTS)],
        out_specs=[
            pl.BlockSpec(
                (blocks_dev, BLOCK, 2 * width), lambda i, ids, write_ids, valid, first: (0, 0, 0)
            ),
            pl.BlockSpec((total, BLOCK, 2 * width), lambda i, ids, write_ids, valid, first: (0, 0, 0)),
            row_spec,
        ],
        scratch_shapes=[pltpu.VMEM((total, BLOCK, 2 * width), jnp.float32)],
    )
    return pl.pallas_call(
        block_kernel,
        grid_spec=grid_spec,
        out_shape=[
            jax.ShapeDtypeStruct((blocks_dev, BLOCK, 2 * width), jnp.float32),
            jax.ShapeDtypeStruct((total, BLOCK, 2 * width), jnp.bfloat16),
            jax.ShapeDtypeStruct((tokens, width), jnp.bfloat16),
        ],
        compiler_params=pltpu.CompilerParams(vmem_limit_bytes=60 * 1024 * 1024),
    )(ids, write_ids, valid, first, queries, out_grad, *([source] * SLOTS))


def gathered_shards(queries, key_rows, value_rows, out_grad, random_device, random_block):
    seq_size = lax.axis_size("seq")
    own_index = lax.axis_index("seq")
    tokens, width = queries.shape
    blocks_dev = tokens // BLOCK
    total = seq_size * blocks_dev
    first = own_index * blocks_dev
    capacity = max(2, 3 * blocks_dev // seq_size)
    selector, slot_index = routing(
        random_device, random_block, own_index, seq_size, blocks_dev, capacity
    )
    block_ids = first + jnp.arange(blocks_dev, dtype=jnp.int32)
    local_ids = jnp.arange(blocks_dev, dtype=jnp.int32)
    own_device = lax.dynamic_slice_in_dim(random_device, first, blocks_dev, 0)
    own_block = lax.dynamic_slice_in_dim(random_block, first, blocks_dev, 0)
    chosen = (own_device * blocks_dev + own_block).astype(jnp.int32)
    window = jnp.stack(
        [jnp.clip(block_ids - 1, 0, total - 1), block_ids, jnp.clip(block_ids + 1, 0, total - 1)],
        axis=1,
    )
    write_ids = jnp.concatenate([window, chosen], axis=1).reshape(-1)
    read_window = jnp.stack([local_ids, local_ids + 1, local_ids + 2], axis=1)
    read_far = (slot_index + blocks_dev + 2).reshape(blocks_dev, RAND).astype(jnp.int32)
    read_ids = jnp.concatenate([read_window, read_far], axis=1).reshape(-1)
    always = jnp.ones_like(block_ids, dtype=jnp.bool_)
    valid = jnp.stack([block_ids > 0, always, block_ids < total - 1] + [always] * RAND, axis=1)
    valid = valid.astype(jnp.int32).reshape(-1)
    first_table = first.reshape(1).astype(jnp.int32)
    chunks = 2 if (width // DH) % 2 == 0 else 1
    part = width // chunks
    global_ids = write_ids
    results = []
    link = None
    for chunk in range(chunks):
        cols = slice(chunk * part, (chunk + 1) * part)
        packed = jnp.concatenate([key_rows[:, cols], value_rows[:, cols]], axis=1)
        if chunk == 0:
            source = lax.all_gather(packed, "seq", axis=0, tiled=True)
            source = source.reshape(total, BLOCK, 2 * part)
            table_ids = global_ids
            link = source[0, 0, :1]
        else:
            packed = packed.reshape(blocks_dev, BLOCK, 2 * part)
            route = selector + (link * 0).astype(selector.dtype)
            outgoing = jnp.dot(
                route, packed.reshape(blocks_dev, BLOCK * 2 * part),
                preferred_element_type=jnp.float32,
            ).astype(jnp.bfloat16)
            outgoing = outgoing.reshape(seq_size * capacity, BLOCK, 2 * part)
            haloed = extended(packed, (("seq", 0),), 1)
            arrived = lax.all_to_all(outgoing, "seq", split_axis=0, concat_axis=0, tiled=True)
            source = jnp.concatenate([haloed, arrived], axis=0)
            table_ids = read_ids
        results.append((source, table_ids))
    query_parts, key_parts, value_parts = [], [], []
    after = None
    for chunk in range(chunks):
        source, table_ids = results[chunk]
        table = first_table
        if after is not None:
            table = table + (after[0, 0, :1] * 0.0).astype(jnp.int32)
        own_sum, spread, query_out = block_attention(
            table_ids, global_ids, valid, table, queries, out_grad, source, chunk, part, total,
        )
        after = own_sum
        returned = lax.psum_scatter(
            spread.reshape(total * BLOCK, 2 * part), "seq", scatter_dimension=0, tiled=True
        )
        summed = own_sum.reshape(tokens, 2 * part) + returned.astype(jnp.float32)
        query_parts.append(query_out)
        key_parts.append(summed[:, :part].astype(jnp.bfloat16))
        value_parts.append(summed[:, part:].astype(jnp.bfloat16))
    return (
        jnp.concatenate(query_parts, axis=1),
        jnp.concatenate(key_parts, axis=1),
        jnp.concatenate(value_parts, axis=1),
    )


def shards(queries, key_rows, value_rows, out_grad, random_device, random_block):
    if lax.axis_size("seq") <= 8:
        return gathered_shards(queries, key_rows, value_rows, out_grad, random_device, random_block)
    return exchanged_shards(queries, key_rows, value_rows, out_grad, random_device, random_block)


def solution(mesh):
    return jax.shard_map(
        shards,
        mesh=mesh,
        in_specs=(
            P(("groups", "seq"), ("heads", "pair")),
            P(("groups", "seq"), ("heads", "pair")),
            P(("groups", "seq"), ("heads", "pair")),
            P(("groups", "seq"), ("heads", "pair")),
            P("groups", None),
            P("groups", None),
        ),
        out_specs=(
            P(("groups", "seq"), ("heads", "pair")),
            P(("groups", "seq"), ("heads", "pair")),
            P(("groups", "seq"), ("heads", "pair")),
        ),
        check_vma=False,
    )
```

```python
import math

import jax
import jax.numpy as jnp
from jax import lax
from jax.experimental import pallas as pl
from jax.experimental.pallas import tpu as pltpu
from jax.sharding import PartitionSpec as P

DH = 128
BLOCK = 64
RAND = 2


def extended(block, sides, width):
    for axis, dim in sides:
        count = lax.axis_size(axis)
        forward = [(i, i + 1) for i in range(count - 1)]
        backward = [(target, source) for source, target in forward]
        low = lax.ppermute(
            lax.slice_in_dim(block, block.shape[dim] - width, None, axis=dim), axis, forward
        )
        high = lax.ppermute(lax.slice_in_dim(block, 0, width, axis=dim), axis, backward)
        block = jnp.concatenate([low, block, high], axis=dim)
    return block


def routing(random_device, random_block, own_index, seq_size, blocks_dev, capacity):
    entries = blocks_dev * RAND
    wanted_from = random_device.reshape(seq_size, entries)
    wanted_block = random_block.reshape(seq_size, entries)
    from_me = (wanted_from == own_index).astype(jnp.int32)
    rank_out = jnp.cumsum(from_me, axis=1) - from_me
    slot_hits = from_me[:, None, :] * (
        rank_out[:, None, :] == jnp.arange(capacity, dtype=jnp.int32)[None, :, None]
    ).astype(jnp.int32)
    block_hits = (
        wanted_block[:, :, None] == jnp.arange(blocks_dev, dtype=jnp.int32)[None, None, :]
    ).astype(jnp.float32)
    selector = jnp.einsum("sce,sej->scj", slot_hits.astype(jnp.float32), block_hits)
    selector = selector.reshape(seq_size * capacity, blocks_dev).astype(jnp.bfloat16)
    own_sources = lax.dynamic_slice_in_dim(
        random_device, own_index * blocks_dev, blocks_dev, 0
    ).reshape(entries)
    peer_hits = (own_sources[:, None] == jnp.arange(seq_size, dtype=jnp.int32)[None, :]).astype(
        jnp.int32
    )
    earlier = jnp.cumsum(peer_hits, axis=0) - peer_hits
    rank_in = jnp.sum(earlier * peer_hits, axis=1)
    slot_index = own_sources * capacity + rank_in
    return (selector, slot_index)


def far_context(arrived, slot_index, blocks_dev):
    picked = jnp.take(arrived, slot_index, axis=0)
    return picked.reshape(blocks_dev, RAND, arrived.shape[1], arrived.shape[2])


def usable_mask(own_index, seq_size, blocks_dev):
    block_ids = jnp.arange(blocks_dev, dtype=jnp.int32)[:, None]
    slot_ids = jnp.arange(3 + RAND, dtype=jnp.int32)[None, :]
    global_block = own_index * blocks_dev + block_ids
    missing = (slot_ids == 0) & (global_block == 0) | (slot_ids == 2) & (
        global_block == seq_size * blocks_dev - 1
    )
    return jnp.repeat(jnp.logical_not(missing), BLOCK, axis=1)


def slot_pieces(haloed, far_blocks, blocks_dev, start_col):
    pieces = []
    for slot in range(3):
        pieces.append(haloed[slot : slot + blocks_dev, :, start_col : start_col + DH])
    far_part = far_blocks[:, :, :, start_col : start_col + DH]
    return (pieces, far_part)


def forward_head(query_tiles, key_pieces, key_far, value_pieces, value_far, usable):
    blocks_dev = query_tiles.shape[0]
    logit_parts = [
        jnp.einsum("bje,bxe->bjx", query_tiles, piece, preferred_element_type=jnp.float32)
        for piece in key_pieces
    ]
    far_logits = jnp.einsum(
        "bje,brxe->bjrx", query_tiles, key_far, preferred_element_type=jnp.float32
    )
    logit_parts.append(far_logits.reshape(blocks_dev, BLOCK, RAND * BLOCK))
    attention_logits = jnp.concatenate(logit_parts, axis=-1) * (1.0 / math.sqrt(DH))
    attention_logits = jnp.where(usable[:, None, :], attention_logits, -jnp.inf)
    row_max = jnp.max(attention_logits, axis=-1, keepdims=True)
    exponent = jnp.exp(attention_logits - row_max)
    row_total = jnp.sum(exponent, axis=-1, keepdims=True)
    probability = exponent / row_total
    softmax_weights = probability.astype(jnp.bfloat16)
    attended = jnp.einsum(
        "bjx,bxe->bje",
        softmax_weights[:, :, :BLOCK],
        value_pieces[0],
        preferred_element_type=jnp.float32,
    )
    for slot in range(1, 3):
        attended = attended + jnp.einsum(
            "bjx,bxe->bje",
            softmax_weights[:, :, slot * BLOCK : (slot + 1) * BLOCK],
            value_pieces[slot],
            preferred_element_type=jnp.float32,
        )
    far_weights = softmax_weights[:, :, 3 * BLOCK :].reshape(blocks_dev, BLOCK, RAND, BLOCK)
    attended = attended + jnp.einsum(
        "bjrx,brxe->bje", far_weights, value_far, preferred_element_type=jnp.float32
    )
    return (probability, attended.astype(jnp.bfloat16))


def backward_head(
    query_tiles, key_pieces, key_far, value_pieces, value_far, gradient_tiles, forward_state
):
    probability, attended_output = forward_state
    blocks_dev = query_tiles.shape[0]
    logit_scale = 1.0 / math.sqrt(DH)
    softmax_weights = probability.astype(jnp.bfloat16)
    row_delta = jnp.sum(
        gradient_tiles.astype(jnp.float32) * attended_output.astype(jnp.float32),
        axis=-1,
        keepdims=True,
    )
    grad_parts = [
        jnp.einsum("bje,bxe->bjx", gradient_tiles, piece, preferred_element_type=jnp.float32)
        for piece in value_pieces
    ]
    far_grad = jnp.einsum(
        "bje,brxe->bjrx", gradient_tiles, value_far, preferred_element_type=jnp.float32
    )
    grad_parts.append(far_grad.reshape(blocks_dev, BLOCK, RAND * BLOCK))
    probability_gradient = jnp.concatenate(grad_parts, axis=-1)
    score_gradient = (probability * (probability_gradient - row_delta)).astype(jnp.bfloat16)
    query_sum = jnp.einsum(
        "bjx,bxe->bje",
        score_gradient[:, :, :BLOCK],
        key_pieces[0],
        preferred_element_type=jnp.float32,
    )
    for slot in range(1, 3):
        query_sum = query_sum + jnp.einsum(
            "bjx,bxe->bje",
            score_gradient[:, :, slot * BLOCK : (slot + 1) * BLOCK],
            key_pieces[slot],
            preferred_element_type=jnp.float32,
        )
    far_scores = score_gradient[:, :, 3 * BLOCK :].reshape(blocks_dev, BLOCK, RAND, BLOCK)
    query_sum = query_sum + jnp.einsum(
        "bjrx,brxe->bje", far_scores, key_far, preferred_element_type=jnp.float32
    )
    query_gradient = (logit_scale * query_sum).astype(jnp.bfloat16)
    key_window, value_window = ([], [])
    for slot in range(3):
        columns = slice(slot * BLOCK, (slot + 1) * BLOCK)
        key_window.append(
            logit_scale
            * jnp.einsum(
                "bjx,bje->bxe",
                score_gradient[:, :, columns],
                query_tiles,
                preferred_element_type=jnp.float32,
            )
        )
        value_window.append(
            jnp.einsum(
                "bjx,bje->bxe",
                softmax_weights[:, :, columns],
                gradient_tiles,
                preferred_element_type=jnp.float32,
            )
        )
    far_weights = softmax_weights[:, :, 3 * BLOCK :].reshape(blocks_dev, BLOCK, RAND, BLOCK)
    key_far_terms = (
        logit_scale
        * jnp.einsum("bjrx,bje->brxe", far_scores, query_tiles, preferred_element_type=jnp.float32)
    ).astype(jnp.bfloat16)
    value_far_terms = jnp.einsum(
        "bjrx,bje->brxe", far_weights, gradient_tiles, preferred_element_type=jnp.float32
    ).astype(jnp.bfloat16)
    return (query_gradient, key_window, value_window, key_far_terms, value_far_terms)


def exchanged_shards(queries, key_rows, value_rows, out_grad, random_device, random_block):
    seq_size = lax.axis_size("seq")
    own_index = lax.axis_index("seq")
    tokens, row_width = queries.shape
    blocks_dev = tokens // BLOCK
    heads_dev = row_width // DH
    capacity = max(2, 3 * blocks_dev // seq_size)
    selector, slot_index = routing(
        random_device, random_block, own_index, seq_size, blocks_dev, capacity
    )
    packed = jnp.concatenate([key_rows, value_rows], axis=1).reshape(
        blocks_dev, BLOCK, 2 * row_width
    )
    flattened = packed.reshape(blocks_dev, BLOCK * 2 * row_width)
    outgoing_blocks = jnp.dot(selector, flattened, preferred_element_type=jnp.float32).astype(
        jnp.bfloat16
    )
    outgoing_blocks = outgoing_blocks.reshape(seq_size * capacity, BLOCK, 2 * row_width)
    haloed = extended(packed, (("seq", 0),), 1)
    arrived = lax.all_to_all(outgoing_blocks, "seq", split_axis=0, concat_axis=0, tiled=True)
    far_blocks = far_context(arrived, slot_index, blocks_dev)
    usable = usable_mask(own_index, seq_size, blocks_dev)
    query_tiles = queries.reshape(blocks_dev, BLOCK, row_width)
    gradient_tiles = out_grad.reshape(blocks_dev, BLOCK, row_width)
    states = []
    for head_index in range(heads_dev):
        key_pieces, key_far = slot_pieces(haloed, far_blocks, blocks_dev, head_index * DH)
        value_pieces, value_far = slot_pieces(
            haloed, far_blocks, blocks_dev, row_width + head_index * DH
        )
        query_head = query_tiles[:, :, head_index * DH : (head_index + 1) * DH]
        states.append(
            forward_head(query_head, key_pieces, key_far, value_pieces, value_far, usable)
        )
    query_parts = []
    window_lists = [[], [], []]
    value_lists = [[], [], []]
    far_keys, far_values = ([], [])
    for head_index in range(heads_dev):
        key_pieces, key_far = slot_pieces(haloed, far_blocks, blocks_dev, head_index * DH)
        value_pieces, value_far = slot_pieces(
            haloed, far_blocks, blocks_dev, row_width + head_index * DH
        )
        query_head = query_tiles[:, :, head_index * DH : (head_index + 1) * DH]
        gradient_head = gradient_tiles[:, :, head_index * DH : (head_index + 1) * DH]
        query_gradient, key_window, value_window, key_far_terms, value_far_terms = backward_head(
            query_head,
            key_pieces,
            key_far,
            value_pieces,
            value_far,
            gradient_head,
            states[head_index],
        )
        query_parts.append(query_gradient)
        for slot in range(3):
            window_lists[slot].append(key_window[slot])
            value_lists[slot].append(value_window[slot])
        far_keys.append(key_far_terms)
        far_values.append(value_far_terms)
    slot_terms = [
        jnp.concatenate(window_lists[slot] + value_lists[slot], axis=-1) for slot in range(3)
    ]
    left_terms = slot_terms[0]
    right_terms = slot_terms[2]
    far_terms = jnp.concatenate(far_keys + far_values, axis=-1).reshape(
        blocks_dev * RAND, BLOCK, 2 * row_width
    )
    edge_terms = jnp.stack([left_terms[0], right_terms[-1]])
    edge_haloed = extended(edge_terms.astype(jnp.bfloat16), (("seq", 0),), 1).astype(
        edge_terms.dtype
    )
    summed = (
        slot_terms[1]
        + jnp.concatenate([left_terms[1:], edge_haloed[3:]], axis=0)
        + jnp.concatenate([edge_haloed[:1], right_terms[:-1]], axis=0)
    )
    returning = (
        jnp.zeros((seq_size * capacity, BLOCK, 2 * row_width), jnp.bfloat16)
        .at[slot_index]
        .set(far_terms)
    )
    returned = lax.all_to_all(returning, "seq", split_axis=0, concat_axis=0, tiled=True)
    gathered_terms = jnp.dot(
        selector.T,
        returned.reshape(seq_size * capacity, BLOCK * 2 * row_width),
        preferred_element_type=jnp.float32,
    )
    summed = summed + gathered_terms.reshape(blocks_dev, BLOCK, 2 * row_width)
    summed = summed.reshape(tokens, 2 * row_width)
    query_out = jnp.concatenate(query_parts, axis=-1).reshape(tokens, row_width)
    return (
        query_out,
        summed[:, :row_width].astype(jnp.bfloat16),
        summed[:, row_width:].astype(jnp.bfloat16),
    )


SLOTS = 3 + RAND


def block_kernel(ids_ref, write_ref, valid_ref, first_ref, q_ref, g_ref, *rest):
    kv_refs = rest[:SLOTS]
    own_ref, spread_ref, dq_ref, acc_ref = rest[SLOTS:]
    step = pl.program_id(0)
    steps = pl.num_programs(0)
    width = q_ref.shape[1]
    blocks_dev = own_ref.shape[0]
    logit_scale = 1.0 / math.sqrt(DH)

    @pl.when(step == 0)
    def _():
        acc_ref[...] = jnp.zeros(acc_ref.shape, jnp.float32)

    context = jnp.concatenate([ref[0] for ref in kv_refs], axis=0)
    slot_of = lax.broadcasted_iota(jnp.int32, (SLOTS * BLOCK, 1), 0) // BLOCK
    usable = slot_of < 0
    for slot in range(SLOTS):
        usable = usable | ((slot_of == slot) & (valid_ref[step * SLOTS + slot] > 0))
    key_parts, value_parts = [], []
    for head in range(width // DH):
        cols = slice(head * DH, (head + 1) * DH)
        vcols = slice(width + head * DH, width + (head + 1) * DH)
        query = q_ref[:, cols]
        grad = g_ref[:, cols]
        keys = context[:, cols]
        values = context[:, vcols]
        logits = lax.dot_general(
            keys, query, (((1,), (1,)), ((), ())), preferred_element_type=jnp.float32
        ) * logit_scale
        logits = jnp.where(usable, logits, -jnp.inf)
        row_max = jnp.max(logits, axis=0, keepdims=True)
        exponent = jnp.exp(logits - row_max)
        row_total = jnp.sum(exponent, axis=0, keepdims=True)
        probability = exponent / row_total
        weights = probability.astype(jnp.bfloat16)
        attended = lax.dot_general(
            weights, values, (((0,), (0,)), ((), ())), preferred_element_type=jnp.float32
        ).astype(jnp.bfloat16)
        product = grad.astype(jnp.float32) * attended.astype(jnp.float32)
        row_delta = jnp.sum(product.T, axis=0, keepdims=True)
        prob_grad = lax.dot_general(
            values, grad, (((1,), (1,)), ((), ())), preferred_element_type=jnp.float32
        )
        score_grad = (probability * (prob_grad - row_delta)).astype(jnp.bfloat16)
        query_grad = logit_scale * lax.dot_general(
            score_grad, keys, (((0,), (0,)), ((), ())), preferred_element_type=jnp.float32
        )
        dq_ref[:, cols] = query_grad.astype(jnp.bfloat16)
        key_parts.append(
            logit_scale * jnp.dot(score_grad, query, preferred_element_type=jnp.float32)
        )
        value_parts.append(jnp.dot(weights, grad, preferred_element_type=jnp.float32))
    terms = jnp.concatenate(key_parts + value_parts, axis=1)
    for slot in range(SLOTS):
        piece = terms[slot * BLOCK : (slot + 1) * BLOCK]
        if slot >= 3:
            piece = piece.astype(jnp.bfloat16).astype(jnp.float32)
        target = write_ref[step * SLOTS + slot]
        acc_ref[target] = acc_ref[target] + piece

    @pl.when(step == steps - 1)
    def _():
        first = first_ref[0]
        spread_ref[...] = acc_ref[...].astype(jnp.bfloat16)
        for block in range(blocks_dev):
            own_ref[block] = acc_ref[first + block]
            spread_ref[first + block] = jnp.zeros(spread_ref.shape[1:], jnp.bfloat16)


def block_attention(ids, write_ids, valid, first, queries, out_grad, source, chunk, width, total):
    tokens = queries.shape[0]
    blocks_dev = tokens // BLOCK

    def context_spec(slot):
        return pl.BlockSpec(
            (1, BLOCK, 2 * width), lambda i, ids, write_ids, valid, first: (ids[i * SLOTS + slot], 0, 0)
        )

    column_spec = pl.BlockSpec((BLOCK, width), lambda i, ids, write_ids, valid, first: (i, chunk))
    row_spec = pl.BlockSpec((BLOCK, width), lambda i, ids, write_ids, valid, first: (i, 0))
    grid_spec = pltpu.PrefetchScalarGridSpec(
        num_scalar_prefetch=4,
        grid=(blocks_dev,),
        in_specs=[column_spec, column_spec] + [context_spec(s) for s in range(SLOTS)],
        out_specs=[
            pl.BlockSpec(
                (blocks_dev, BLOCK, 2 * width), lambda i, ids, write_ids, valid, first: (0, 0, 0)
            ),
            pl.BlockSpec((total, BLOCK, 2 * width), lambda i, ids, write_ids, valid, first: (0, 0, 0)),
            row_spec,
        ],
        scratch_shapes=[pltpu.VMEM((total, BLOCK, 2 * width), jnp.float32)],
    )
    return pl.pallas_call(
        block_kernel,
        grid_spec=grid_spec,
        out_shape=[
            jax.ShapeDtypeStruct((blocks_dev, BLOCK, 2 * width), jnp.float32),
            jax.ShapeDtypeStruct((total, BLOCK, 2 * width), jnp.bfloat16),
            jax.ShapeDtypeStruct((tokens, width), jnp.bfloat16),
        ],
        compiler_params=pltpu.CompilerParams(vmem_limit_bytes=60 * 1024 * 1024),
    )(ids, write_ids, valid, first, queries, out_grad, *([source] * SLOTS))


def gathered_shards(queries, key_rows, value_rows, out_grad, random_device, random_block):
    seq_size = lax.axis_size("seq")
    own_index = lax.axis_index("seq")
    tokens, width = queries.shape
    blocks_dev = tokens // BLOCK
    total = seq_size * blocks_dev
    first = own_index * blocks_dev
    capacity = max(2, 3 * blocks_dev // seq_size)
    selector, slot_index = routing(
        random_device, random_block, own_index, seq_size, blocks_dev, capacity
    )
    block_ids = first + jnp.arange(blocks_dev, dtype=jnp.int32)
    local_ids = jnp.arange(blocks_dev, dtype=jnp.int32)
    own_device = lax.dynamic_slice_in_dim(random_device, first, blocks_dev, 0)
    own_block = lax.dynamic_slice_in_dim(random_block, first, blocks_dev, 0)
    chosen = (own_device * blocks_dev + own_block).astype(jnp.int32)
    window = jnp.stack(
        [jnp.clip(block_ids - 1, 0, total - 1), block_ids, jnp.clip(block_ids + 1, 0, total - 1)],
        axis=1,
    )
    write_ids = jnp.concatenate([window, chosen], axis=1).reshape(-1)
    read_window = jnp.stack([local_ids, local_ids + 1, local_ids + 2], axis=1)
    read_far = (slot_index + blocks_dev + 2).reshape(blocks_dev, RAND).astype(jnp.int32)
    read_ids = jnp.concatenate([read_window, read_far], axis=1).reshape(-1)
    always = jnp.ones_like(block_ids, dtype=jnp.bool_)
    valid = jnp.stack([block_ids > 0, always, block_ids < total - 1] + [always] * RAND, axis=1)
    valid = valid.astype(jnp.int32).reshape(-1)
    first_table = first.reshape(1).astype(jnp.int32)
    chunks = 2 if (width // DH) % 2 == 0 else 1
    part = width // chunks
    global_ids = write_ids
    results = []
    link = None
    for chunk in range(chunks):
        cols = slice(chunk * part, (chunk + 1) * part)
        packed = jnp.concatenate([key_rows[:, cols], value_rows[:, cols]], axis=1)
        if chunk == 0:
            source = lax.all_gather(packed, "seq", axis=0, tiled=True)
            source = source.reshape(total, BLOCK, 2 * part)
            table_ids = global_ids
            link = source[0, 0, :1]
        else:
            packed = packed.reshape(blocks_dev, BLOCK, 2 * part)
            route = selector
            outgoing = jnp.dot(
                route, packed.reshape(blocks_dev, BLOCK * 2 * part),
                preferred_element_type=jnp.float32,
            ).astype(jnp.bfloat16)
            outgoing = outgoing.reshape(seq_size * capacity, BLOCK, 2 * part)
            haloed = extended(packed, (("seq", 0),), 1)
            arrived = lax.all_to_all(outgoing, "seq", split_axis=0, concat_axis=0, tiled=True)
            source = jnp.concatenate([haloed, arrived], axis=0)
            table_ids = read_ids
        results.append((source, table_ids))
    query_parts, key_parts, value_parts = [], [], []
    after = results[-1][0][blocks_dev + 2 :] if chunks > 1 else None
    for chunk in range(chunks):
        source, table_ids = results[chunk]
        table = first_table
        if after is not None:
            table = table + (after[0, 0, :1] * 0.0).astype(jnp.int32)
        own_sum, spread, query_out = block_attention(
            table_ids, global_ids, valid, table, queries, out_grad, source, chunk, part, total,
        )
        after = own_sum
        returned = lax.psum_scatter(
            spread.reshape(total * BLOCK, 2 * part), "seq", scatter_dimension=0, tiled=True
        )
        summed = own_sum.reshape(tokens, 2 * part) + returned.astype(jnp.float32)
        query_parts.append(query_out)
        key_parts.append(summed[:, :part].astype(jnp.bfloat16))
        value_parts.append(summed[:, part:].astype(jnp.bfloat16))
    return (
        jnp.concatenate(query_parts, axis=1),
        jnp.concatenate(key_parts, axis=1),
        jnp.concatenate(value_parts, axis=1),
    )


def shards(queries, key_rows, value_rows, out_grad, random_device, random_block):
    if lax.axis_size("seq") <= 8:
        return gathered_shards(queries, key_rows, value_rows, out_grad, random_device, random_block)
    return exchanged_shards(queries, key_rows, value_rows, out_grad, random_device, random_block)


def solution(mesh):
    return jax.shard_map(
        shards,
        mesh=mesh,
        in_specs=(
            P(("groups", "seq"), ("heads", "pair")),
            P(("groups", "seq"), ("heads", "pair")),
            P(("groups", "seq"), ("heads", "pair")),
            P(("groups", "seq"), ("heads", "pair")),
            P("groups", None),
            P("groups", None),
        ),
        out_specs=(
            P(("groups", "seq"), ("heads", "pair")),
            P(("groups", "seq"), ("heads", "pair")),
            P(("groups", "seq"), ("heads", "pair")),
        ),
        check_vma=False,
    )
```

```python
import math

import jax
import jax.numpy as jnp
from jax import lax
from jax.experimental import pallas as pl
from jax.experimental.pallas import tpu as pltpu
from jax.sharding import PartitionSpec as P

DH = 128
BLOCK = 64
RAND = 2


def extended(block, sides, width):
    for axis, dim in sides:
        count = lax.axis_size(axis)
        forward = [(i, i + 1) for i in range(count - 1)]
        backward = [(target, source) for source, target in forward]
        low = lax.ppermute(
            lax.slice_in_dim(block, block.shape[dim] - width, None, axis=dim), axis, forward
        )
        high = lax.ppermute(lax.slice_in_dim(block, 0, width, axis=dim), axis, backward)
        block = jnp.concatenate([low, block, high], axis=dim)
    return block


def routing(random_device, random_block, own_index, seq_size, blocks_dev, capacity):
    entries = blocks_dev * RAND
    wanted_from = random_device.reshape(seq_size, entries)
    wanted_block = random_block.reshape(seq_size, entries)
    from_me = (wanted_from == own_index).astype(jnp.int32)
    rank_out = jnp.cumsum(from_me, axis=1) - from_me
    slot_hits = from_me[:, None, :] * (
        rank_out[:, None, :] == jnp.arange(capacity, dtype=jnp.int32)[None, :, None]
    ).astype(jnp.int32)
    block_hits = (
        wanted_block[:, :, None] == jnp.arange(blocks_dev, dtype=jnp.int32)[None, None, :]
    ).astype(jnp.float32)
    selector = jnp.einsum("sce,sej->scj", slot_hits.astype(jnp.float32), block_hits)
    selector = selector.reshape(seq_size * capacity, blocks_dev).astype(jnp.bfloat16)
    own_sources = lax.dynamic_slice_in_dim(
        random_device, own_index * blocks_dev, blocks_dev, 0
    ).reshape(entries)
    peer_hits = (own_sources[:, None] == jnp.arange(seq_size, dtype=jnp.int32)[None, :]).astype(
        jnp.int32
    )
    earlier = jnp.cumsum(peer_hits, axis=0) - peer_hits
    rank_in = jnp.sum(earlier * peer_hits, axis=1)
    slot_index = own_sources * capacity + rank_in
    return (selector, slot_index)


def far_context(arrived, slot_index, blocks_dev):
    picked = jnp.take(arrived, slot_index, axis=0)
    return picked.reshape(blocks_dev, RAND, arrived.shape[1], arrived.shape[2])


def usable_mask(own_index, seq_size, blocks_dev):
    block_ids = jnp.arange(blocks_dev, dtype=jnp.int32)[:, None]
    slot_ids = jnp.arange(3 + RAND, dtype=jnp.int32)[None, :]
    global_block = own_index * blocks_dev + block_ids
    missing = (slot_ids == 0) & (global_block == 0) | (slot_ids == 2) & (
        global_block == seq_size * blocks_dev - 1
    )
    return jnp.repeat(jnp.logical_not(missing), BLOCK, axis=1)


def slot_pieces(haloed, far_blocks, blocks_dev, start_col):
    pieces = []
    for slot in range(3):
        pieces.append(haloed[slot : slot + blocks_dev, :, start_col : start_col + DH])
    far_part = far_blocks[:, :, :, start_col : start_col + DH]
    return (pieces, far_part)


def forward_head(query_tiles, key_pieces, key_far, value_pieces, value_far, usable):
    blocks_dev = query_tiles.shape[0]
    logit_parts = [
        jnp.einsum("bje,bxe->bjx", query_tiles, piece, preferred_element_type=jnp.float32)
        for piece in key_pieces
    ]
    far_logits = jnp.einsum(
        "bje,brxe->bjrx", query_tiles, key_far, preferred_element_type=jnp.float32
    )
    logit_parts.append(far_logits.reshape(blocks_dev, BLOCK, RAND * BLOCK))
    attention_logits = jnp.concatenate(logit_parts, axis=-1) * (1.0 / math.sqrt(DH))
    attention_logits = jnp.where(usable[:, None, :], attention_logits, -jnp.inf)
    row_max = jnp.max(attention_logits, axis=-1, keepdims=True)
    exponent = jnp.exp(attention_logits - row_max)
    row_total = jnp.sum(exponent, axis=-1, keepdims=True)
    probability = exponent / row_total
    softmax_weights = probability.astype(jnp.bfloat16)
    attended = jnp.einsum(
        "bjx,bxe->bje",
        softmax_weights[:, :, :BLOCK],
        value_pieces[0],
        preferred_element_type=jnp.float32,
    )
    for slot in range(1, 3):
        attended = attended + jnp.einsum(
            "bjx,bxe->bje",
            softmax_weights[:, :, slot * BLOCK : (slot + 1) * BLOCK],
            value_pieces[slot],
            preferred_element_type=jnp.float32,
        )
    far_weights = softmax_weights[:, :, 3 * BLOCK :].reshape(blocks_dev, BLOCK, RAND, BLOCK)
    attended = attended + jnp.einsum(
        "bjrx,brxe->bje", far_weights, value_far, preferred_element_type=jnp.float32
    )
    return (probability, attended.astype(jnp.bfloat16))


def backward_head(
    query_tiles, key_pieces, key_far, value_pieces, value_far, gradient_tiles, forward_state
):
    probability, attended_output = forward_state
    blocks_dev = query_tiles.shape[0]
    logit_scale = 1.0 / math.sqrt(DH)
    softmax_weights = probability.astype(jnp.bfloat16)
    row_delta = jnp.sum(
        gradient_tiles.astype(jnp.float32) * attended_output.astype(jnp.float32),
        axis=-1,
        keepdims=True,
    )
    grad_parts = [
        jnp.einsum("bje,bxe->bjx", gradient_tiles, piece, preferred_element_type=jnp.float32)
        for piece in value_pieces
    ]
    far_grad = jnp.einsum(
        "bje,brxe->bjrx", gradient_tiles, value_far, preferred_element_type=jnp.float32
    )
    grad_parts.append(far_grad.reshape(blocks_dev, BLOCK, RAND * BLOCK))
    probability_gradient = jnp.concatenate(grad_parts, axis=-1)
    score_gradient = (probability * (probability_gradient - row_delta)).astype(jnp.bfloat16)
    query_sum = jnp.einsum(
        "bjx,bxe->bje",
        score_gradient[:, :, :BLOCK],
        key_pieces[0],
        preferred_element_type=jnp.float32,
    )
    for slot in range(1, 3):
        query_sum = query_sum + jnp.einsum(
            "bjx,bxe->bje",
            score_gradient[:, :, slot * BLOCK : (slot + 1) * BLOCK],
            key_pieces[slot],
            preferred_element_type=jnp.float32,
        )
    far_scores = score_gradient[:, :, 3 * BLOCK :].reshape(blocks_dev, BLOCK, RAND, BLOCK)
    query_sum = query_sum + jnp.einsum(
        "bjrx,brxe->bje", far_scores, key_far, preferred_element_type=jnp.float32
    )
    query_gradient = (logit_scale * query_sum).astype(jnp.bfloat16)
    key_window, value_window = ([], [])
    for slot in range(3):
        columns = slice(slot * BLOCK, (slot + 1) * BLOCK)
        key_window.append(
            logit_scale
            * jnp.einsum(
                "bjx,bje->bxe",
                score_gradient[:, :, columns],
                query_tiles,
                preferred_element_type=jnp.float32,
            )
        )
        value_window.append(
            jnp.einsum(
                "bjx,bje->bxe",
                softmax_weights[:, :, columns],
                gradient_tiles,
                preferred_element_type=jnp.float32,
            )
        )
    far_weights = softmax_weights[:, :, 3 * BLOCK :].reshape(blocks_dev, BLOCK, RAND, BLOCK)
    key_far_terms = (
        logit_scale
        * jnp.einsum("bjrx,bje->brxe", far_scores, query_tiles, preferred_element_type=jnp.float32)
    ).astype(jnp.bfloat16)
    value_far_terms = jnp.einsum(
        "bjrx,bje->brxe", far_weights, gradient_tiles, preferred_element_type=jnp.float32
    ).astype(jnp.bfloat16)
    return (query_gradient, key_window, value_window, key_far_terms, value_far_terms)


def exchanged_shards(queries, key_rows, value_rows, out_grad, random_device, random_block):
    seq_size = lax.axis_size("seq")
    own_index = lax.axis_index("seq")
    tokens, row_width = queries.shape
    blocks_dev = tokens // BLOCK
    heads_dev = row_width // DH
    capacity = max(2, 3 * blocks_dev // seq_size)
    selector, slot_index = routing(
        random_device, random_block, own_index, seq_size, blocks_dev, capacity
    )
    packed = jnp.concatenate([key_rows, value_rows], axis=1).reshape(
        blocks_dev, BLOCK, 2 * row_width
    )
    flattened = packed.reshape(blocks_dev, BLOCK * 2 * row_width)
    outgoing_blocks = jnp.dot(selector, flattened, preferred_element_type=jnp.float32).astype(
        jnp.bfloat16
    )
    outgoing_blocks = outgoing_blocks.reshape(seq_size * capacity, BLOCK, 2 * row_width)
    haloed = extended(packed, (("seq", 0),), 1)
    arrived = lax.all_to_all(outgoing_blocks, "seq", split_axis=0, concat_axis=0, tiled=True)
    far_blocks = far_context(arrived, slot_index, blocks_dev)
    usable = usable_mask(own_index, seq_size, blocks_dev)
    query_tiles = queries.reshape(blocks_dev, BLOCK, row_width)
    gradient_tiles = out_grad.reshape(blocks_dev, BLOCK, row_width)
    states = []
    for head_index in range(heads_dev):
        key_pieces, key_far = slot_pieces(haloed, far_blocks, blocks_dev, head_index * DH)
        value_pieces, value_far = slot_pieces(
            haloed, far_blocks, blocks_dev, row_width + head_index * DH
        )
        query_head = query_tiles[:, :, head_index * DH : (head_index + 1) * DH]
        states.append(
            forward_head(query_head, key_pieces, key_far, value_pieces, value_far, usable)
        )
    query_parts = []
    window_lists = [[], [], []]
    value_lists = [[], [], []]
    far_keys, far_values = ([], [])
    for head_index in range(heads_dev):
        key_pieces, key_far = slot_pieces(haloed, far_blocks, blocks_dev, head_index * DH)
        value_pieces, value_far = slot_pieces(
            haloed, far_blocks, blocks_dev, row_width + head_index * DH
        )
        query_head = query_tiles[:, :, head_index * DH : (head_index + 1) * DH]
        gradient_head = gradient_tiles[:, :, head_index * DH : (head_index + 1) * DH]
        query_gradient, key_window, value_window, key_far_terms, value_far_terms = backward_head(
            query_head,
            key_pieces,
            key_far,
            value_pieces,
            value_far,
            gradient_head,
            states[head_index],
        )
        query_parts.append(query_gradient)
        for slot in range(3):
            window_lists[slot].append(key_window[slot])
            value_lists[slot].append(value_window[slot])
        far_keys.append(key_far_terms)
        far_values.append(value_far_terms)
    slot_terms = [
        jnp.concatenate(window_lists[slot] + value_lists[slot], axis=-1) for slot in range(3)
    ]
    left_terms = slot_terms[0]
    right_terms = slot_terms[2]
    far_terms = jnp.concatenate(far_keys + far_values, axis=-1).reshape(
        blocks_dev * RAND, BLOCK, 2 * row_width
    )
    edge_terms = jnp.stack([left_terms[0], right_terms[-1]])
    edge_haloed = extended(edge_terms.astype(jnp.bfloat16), (("seq", 0),), 1).astype(
        edge_terms.dtype
    )
    summed = (
        slot_terms[1]
        + jnp.concatenate([left_terms[1:], edge_haloed[3:]], axis=0)
        + jnp.concatenate([edge_haloed[:1], right_terms[:-1]], axis=0)
    )
    returning = (
        jnp.zeros((seq_size * capacity, BLOCK, 2 * row_width), jnp.bfloat16)
        .at[slot_index]
        .set(far_terms)
    )
    returned = lax.all_to_all(returning, "seq", split_axis=0, concat_axis=0, tiled=True)
    gathered_terms = jnp.dot(
        selector.T,
        returned.reshape(seq_size * capacity, BLOCK * 2 * row_width),
        preferred_element_type=jnp.float32,
    )
    summed = summed + gathered_terms.reshape(blocks_dev, BLOCK, 2 * row_width)
    summed = summed.reshape(tokens, 2 * row_width)
    query_out = jnp.concatenate(query_parts, axis=-1).reshape(tokens, row_width)
    return (
        query_out,
        summed[:, :row_width].astype(jnp.bfloat16),
        summed[:, row_width:].astype(jnp.bfloat16),
    )


SLOTS = 3 + RAND


def block_kernel(ids_ref, write_ref, valid_ref, first_ref, q_ref, g_ref, *rest):
    kv_refs = rest[:SLOTS]
    own_ref, spread_ref, dq_ref, acc_ref = rest[SLOTS:]
    step = pl.program_id(0)
    steps = pl.num_programs(0)
    width = q_ref.shape[1]
    blocks_dev = own_ref.shape[0]
    logit_scale = 1.0 / math.sqrt(DH)

    @pl.when(step == 0)
    def _():
        acc_ref[...] = jnp.zeros(acc_ref.shape, jnp.float32)

    context = jnp.concatenate([ref[0] for ref in kv_refs], axis=0)
    slot_of = lax.broadcasted_iota(jnp.int32, (SLOTS * BLOCK, 1), 0) // BLOCK
    usable = slot_of < 0
    for slot in range(SLOTS):
        usable = usable | ((slot_of == slot) & (valid_ref[step * SLOTS + slot] > 0))
    key_parts, value_parts = [], []
    for head in range(width // DH):
        cols = slice(head * DH, (head + 1) * DH)
        vcols = slice(width + head * DH, width + (head + 1) * DH)
        query = q_ref[:, cols]
        grad = g_ref[:, cols]
        keys = context[:, cols]
        values = context[:, vcols]
        logits = lax.dot_general(
            keys, query, (((1,), (1,)), ((), ())), preferred_element_type=jnp.float32
        ) * logit_scale
        logits = jnp.where(usable, logits, -jnp.inf)
        row_max = jnp.max(logits, axis=0, keepdims=True)
        exponent = jnp.exp(logits - row_max)
        row_total = jnp.sum(exponent, axis=0, keepdims=True)
        probability = exponent / row_total
        weights = probability.astype(jnp.bfloat16)
        attended = lax.dot_general(
            weights, values, (((0,), (0,)), ((), ())), preferred_element_type=jnp.float32
        ).astype(jnp.bfloat16)
        product = grad.astype(jnp.float32) * attended.astype(jnp.float32)
        row_delta = jnp.sum(product.T, axis=0, keepdims=True)
        prob_grad = lax.dot_general(
            values, grad, (((1,), (1,)), ((), ())), preferred_element_type=jnp.float32
        )
        score_grad = (probability * (prob_grad - row_delta)).astype(jnp.bfloat16)
        query_grad = logit_scale * lax.dot_general(
            score_grad, keys, (((0,), (0,)), ((), ())), preferred_element_type=jnp.float32
        )
        dq_ref[:, cols] = query_grad.astype(jnp.bfloat16)
        key_parts.append(
            logit_scale * jnp.dot(score_grad, query, preferred_element_type=jnp.float32)
        )
        value_parts.append(jnp.dot(weights, grad, preferred_element_type=jnp.float32))
    terms = jnp.concatenate(key_parts + value_parts, axis=1)
    for slot in range(SLOTS):
        piece = terms[slot * BLOCK : (slot + 1) * BLOCK]
        if slot >= 3:
            piece = piece.astype(jnp.bfloat16).astype(jnp.float32)
        target = write_ref[step * SLOTS + slot]
        acc_ref[target] = acc_ref[target] + piece

    @pl.when(step == steps - 1)
    def _():
        first = first_ref[0]
        spread_ref[...] = acc_ref[...].astype(jnp.bfloat16)
        for block in range(blocks_dev):
            own_ref[block] = acc_ref[first + block]
            spread_ref[first + block] = jnp.zeros(spread_ref.shape[1:], jnp.bfloat16)


def block_attention(ids, write_ids, valid, first, queries, out_grad, source, chunk, width, total):
    tokens = queries.shape[0]
    blocks_dev = tokens // BLOCK

    def context_spec(slot):
        return pl.BlockSpec(
            (1, BLOCK, 2 * width), lambda i, ids, write_ids, valid, first: (ids[i * SLOTS + slot], 0, 0)
        )

    column_spec = pl.BlockSpec((BLOCK, width), lambda i, ids, write_ids, valid, first: (i, chunk))
    row_spec = pl.BlockSpec((BLOCK, width), lambda i, ids, write_ids, valid, first: (i, 0))
    grid_spec = pltpu.PrefetchScalarGridSpec(
        num_scalar_prefetch=4,
        grid=(blocks_dev,),
        in_specs=[column_spec, column_spec] + [context_spec(s) for s in range(SLOTS)],
        out_specs=[
            pl.BlockSpec(
                (blocks_dev, BLOCK, 2 * width), lambda i, ids, write_ids, valid, first: (0, 0, 0)
            ),
            pl.BlockSpec((total, BLOCK, 2 * width), lambda i, ids, write_ids, valid, first: (0, 0, 0)),
            row_spec,
        ],
        scratch_shapes=[pltpu.VMEM((total, BLOCK, 2 * width), jnp.float32)],
    )
    return pl.pallas_call(
        block_kernel,
        grid_spec=grid_spec,
        out_shape=[
            jax.ShapeDtypeStruct((blocks_dev, BLOCK, 2 * width), jnp.float32),
            jax.ShapeDtypeStruct((total, BLOCK, 2 * width), jnp.bfloat16),
            jax.ShapeDtypeStruct((tokens, width), jnp.bfloat16),
        ],
        compiler_params=pltpu.CompilerParams(vmem_limit_bytes=60 * 1024 * 1024),
    )(ids, write_ids, valid, first, queries, out_grad, *([source] * SLOTS))


def gathered_shards(queries, key_rows, value_rows, out_grad, random_device, random_block):
    seq_size = lax.axis_size("seq")
    own_index = lax.axis_index("seq")
    tokens, width = queries.shape
    blocks_dev = tokens // BLOCK
    total = seq_size * blocks_dev
    first = own_index * blocks_dev
    capacity = max(2, 3 * blocks_dev // seq_size)
    selector, slot_index = routing(
        random_device, random_block, own_index, seq_size, blocks_dev, capacity
    )
    block_ids = first + jnp.arange(blocks_dev, dtype=jnp.int32)
    local_ids = jnp.arange(blocks_dev, dtype=jnp.int32)
    own_device = lax.dynamic_slice_in_dim(random_device, first, blocks_dev, 0)
    own_block = lax.dynamic_slice_in_dim(random_block, first, blocks_dev, 0)
    chosen = (own_device * blocks_dev + own_block).astype(jnp.int32)
    window = jnp.stack(
        [jnp.clip(block_ids - 1, 0, total - 1), block_ids, jnp.clip(block_ids + 1, 0, total - 1)],
        axis=1,
    )
    write_ids = jnp.concatenate([window, chosen], axis=1).reshape(-1)
    read_window = jnp.stack([local_ids, local_ids + 1, local_ids + 2], axis=1)
    read_far = (slot_index + blocks_dev + 2).reshape(blocks_dev, RAND).astype(jnp.int32)
    read_ids = jnp.concatenate([read_window, read_far], axis=1).reshape(-1)
    always = jnp.ones_like(block_ids, dtype=jnp.bool_)
    valid = jnp.stack([block_ids > 0, always, block_ids < total - 1] + [always] * RAND, axis=1)
    valid = valid.astype(jnp.int32).reshape(-1)
    first_table = first.reshape(1).astype(jnp.int32)
    chunks = 2 if (width // DH) % 2 == 0 else 1
    part = width // chunks
    global_ids = write_ids
    results = []
    link = None
    for chunk in range(chunks):
        cols = slice(chunk * part, (chunk + 1) * part)
        packed = jnp.concatenate([key_rows[:, cols], value_rows[:, cols]], axis=1)
        if chunk == 0:
            source = lax.all_gather(packed, "seq", axis=0, tiled=True)
            source = source.reshape(total, BLOCK, 2 * part)
            table_ids = global_ids
            link = source[0, 0, :1]
        else:
            packed = packed.reshape(blocks_dev, BLOCK, 2 * part)
            route = selector
            outgoing = jnp.dot(
                route, packed.reshape(blocks_dev, BLOCK * 2 * part),
                preferred_element_type=jnp.float32,
            ).astype(jnp.bfloat16)
            outgoing = outgoing.reshape(seq_size * capacity, BLOCK, 2 * part)
            haloed = extended(packed, (("seq", 0),), 1)
            arrived = lax.all_to_all(outgoing, "seq", split_axis=0, concat_axis=0, tiled=True)
            source = jnp.concatenate([haloed, arrived], axis=0)
            table_ids = read_ids
        results.append((source, table_ids))
    query_parts, key_parts, value_parts = [], [], []
    after = results[-1][0][blocks_dev + 2 :] if chunks > 1 else None
    for chunk in range(chunks):
        source, table_ids = results[chunk]
        table = first_table
        if after is not None:
            table = table + (after[0, 0, :1] * 0.0).astype(jnp.int32)
        if chunk == 0:
            own_sum, spread, query_out = block_attention(
                table_ids, global_ids, valid, table, queries, out_grad, source, chunk, part, total,
            )
            returned = lax.psum_scatter(
                spread.reshape(total * BLOCK, 2 * part), "seq", scatter_dimension=0, tiled=True
            )
            summed = own_sum.reshape(tokens, 2 * part) + returned.astype(jnp.float32)
        else:
            extra = blocks_dev * RAND
            far_rows = (total + jnp.arange(extra, dtype=jnp.int32)).reshape(blocks_dev, RAND)
            far_write = jnp.concatenate([window, far_rows], axis=1).reshape(-1)
            own_sum, spread, query_out = block_attention(
                table_ids, far_write, valid, table, queries, out_grad, source, chunk, part,
                total + extra,
            )
            returning = (
                jnp.zeros((seq_size * capacity, BLOCK, 2 * part), jnp.bfloat16)
                .at[slot_index]
                .set(spread[total:])
            )
            returned = lax.all_to_all(returning, "seq", split_axis=0, concat_axis=0, tiled=True)
            gathered = jnp.dot(
                selector.T,
                returned.reshape(seq_size * capacity, BLOCK * 2 * part),
                preferred_element_type=jnp.float32,
            ).reshape(blocks_dev, BLOCK, 2 * part)
            left_edge = lax.dynamic_index_in_dim(
                spread, jnp.clip(first - 1, 0, total - 1), 0, keepdims=False
            )
            right_edge = lax.dynamic_index_in_dim(
                spread, jnp.clip(first + blocks_dev, 0, total - 1), 0, keepdims=False
            )
            from_right = lax.ppermute(left_edge, "seq", [(i, i - 1) for i in range(1, seq_size)])
            from_left = lax.ppermute(right_edge, "seq", [(i, i + 1) for i in range(seq_size - 1)])
            combined = (
                (own_sum + gathered)
                .at[0].add(from_left.astype(jnp.float32))
                .at[blocks_dev - 1].add(from_right.astype(jnp.float32))
            )
            summed = combined.reshape(tokens, 2 * part)
        after = own_sum
        query_parts.append(query_out)
        key_parts.append(summed[:, :part].astype(jnp.bfloat16))
        value_parts.append(summed[:, part:].astype(jnp.bfloat16))
    return (
        jnp.concatenate(query_parts, axis=1),
        jnp.concatenate(key_parts, axis=1),
        jnp.concatenate(value_parts, axis=1),
    )


def shards(queries, key_rows, value_rows, out_grad, random_device, random_block):
    if lax.axis_size("seq") <= 8:
        return gathered_shards(queries, key_rows, value_rows, out_grad, random_device, random_block)
    return exchanged_shards(queries, key_rows, value_rows, out_grad, random_device, random_block)


def solution(mesh):
    return jax.shard_map(
        shards,
        mesh=mesh,
        in_specs=(
            P(("groups", "seq"), ("heads", "pair")),
            P(("groups", "seq"), ("heads", "pair")),
            P(("groups", "seq"), ("heads", "pair")),
            P(("groups", "seq"), ("heads", "pair")),
            P("groups", None),
            P("groups", None),
        ),
        out_specs=(
            P(("groups", "seq"), ("heads", "pair")),
            P(("groups", "seq"), ("heads", "pair")),
            P(("groups", "seq"), ("heads", "pair")),
        ),
        check_vma=False,
    )
```

```python
import math

import jax
import jax.numpy as jnp
from jax import lax
from jax.experimental import pallas as pl
from jax.experimental.pallas import tpu as pltpu
from jax.sharding import PartitionSpec as P

DH = 128
BLOCK = 64
RAND = 2


def extended(block, sides, width):
    for axis, dim in sides:
        count = lax.axis_size(axis)
        forward = [(i, i + 1) for i in range(count - 1)]
        backward = [(target, source) for source, target in forward]
        low = lax.ppermute(
            lax.slice_in_dim(block, block.shape[dim] - width, None, axis=dim), axis, forward
        )
        high = lax.ppermute(lax.slice_in_dim(block, 0, width, axis=dim), axis, backward)
        block = jnp.concatenate([low, block, high], axis=dim)
    return block


def routing(random_device, random_block, own_index, seq_size, blocks_dev, capacity):
    entries = blocks_dev * RAND
    wanted_from = random_device.reshape(seq_size, entries)
    wanted_block = random_block.reshape(seq_size, entries)
    from_me = (wanted_from == own_index).astype(jnp.int32)
    rank_out = jnp.cumsum(from_me, axis=1) - from_me
    slot_hits = from_me[:, None, :] * (
        rank_out[:, None, :] == jnp.arange(capacity, dtype=jnp.int32)[None, :, None]
    ).astype(jnp.int32)
    block_hits = (
        wanted_block[:, :, None] == jnp.arange(blocks_dev, dtype=jnp.int32)[None, None, :]
    ).astype(jnp.float32)
    selector = jnp.einsum("sce,sej->scj", slot_hits.astype(jnp.float32), block_hits)
    selector = selector.reshape(seq_size * capacity, blocks_dev).astype(jnp.bfloat16)
    own_sources = lax.dynamic_slice_in_dim(
        random_device, own_index * blocks_dev, blocks_dev, 0
    ).reshape(entries)
    peer_hits = (own_sources[:, None] == jnp.arange(seq_size, dtype=jnp.int32)[None, :]).astype(
        jnp.int32
    )
    earlier = jnp.cumsum(peer_hits, axis=0) - peer_hits
    rank_in = jnp.sum(earlier * peer_hits, axis=1)
    slot_index = own_sources * capacity + rank_in
    return (selector, slot_index)


def far_context(arrived, slot_index, blocks_dev):
    picked = jnp.take(arrived, slot_index, axis=0)
    return picked.reshape(blocks_dev, RAND, arrived.shape[1], arrived.shape[2])


def usable_mask(own_index, seq_size, blocks_dev):
    block_ids = jnp.arange(blocks_dev, dtype=jnp.int32)[:, None]
    slot_ids = jnp.arange(3 + RAND, dtype=jnp.int32)[None, :]
    global_block = own_index * blocks_dev + block_ids
    missing = (slot_ids == 0) & (global_block == 0) | (slot_ids == 2) & (
        global_block == seq_size * blocks_dev - 1
    )
    return jnp.repeat(jnp.logical_not(missing), BLOCK, axis=1)


def slot_pieces(haloed, far_blocks, blocks_dev, start_col):
    pieces = []
    for slot in range(3):
        pieces.append(haloed[slot : slot + blocks_dev, :, start_col : start_col + DH])
    far_part = far_blocks[:, :, :, start_col : start_col + DH]
    return (pieces, far_part)


def forward_head(query_tiles, key_pieces, key_far, value_pieces, value_far, usable):
    blocks_dev = query_tiles.shape[0]
    logit_parts = [
        jnp.einsum("bje,bxe->bjx", query_tiles, piece, preferred_element_type=jnp.float32)
        for piece in key_pieces
    ]
    far_logits = jnp.einsum(
        "bje,brxe->bjrx", query_tiles, key_far, preferred_element_type=jnp.float32
    )
    logit_parts.append(far_logits.reshape(blocks_dev, BLOCK, RAND * BLOCK))
    attention_logits = jnp.concatenate(logit_parts, axis=-1) * (1.0 / math.sqrt(DH))
    attention_logits = jnp.where(usable[:, None, :], attention_logits, -jnp.inf)
    row_max = jnp.max(attention_logits, axis=-1, keepdims=True)
    exponent = jnp.exp(attention_logits - row_max)
    row_total = jnp.sum(exponent, axis=-1, keepdims=True)
    probability = exponent / row_total
    softmax_weights = probability.astype(jnp.bfloat16)
    attended = jnp.einsum(
        "bjx,bxe->bje",
        softmax_weights[:, :, :BLOCK],
        value_pieces[0],
        preferred_element_type=jnp.float32,
    )
    for slot in range(1, 3):
        attended = attended + jnp.einsum(
            "bjx,bxe->bje",
            softmax_weights[:, :, slot * BLOCK : (slot + 1) * BLOCK],
            value_pieces[slot],
            preferred_element_type=jnp.float32,
        )
    far_weights = softmax_weights[:, :, 3 * BLOCK :].reshape(blocks_dev, BLOCK, RAND, BLOCK)
    attended = attended + jnp.einsum(
        "bjrx,brxe->bje", far_weights, value_far, preferred_element_type=jnp.float32
    )
    return (probability, attended.astype(jnp.bfloat16))


def backward_head(
    query_tiles, key_pieces, key_far, value_pieces, value_far, gradient_tiles, forward_state
):
    probability, attended_output = forward_state
    blocks_dev = query_tiles.shape[0]
    logit_scale = 1.0 / math.sqrt(DH)
    softmax_weights = probability.astype(jnp.bfloat16)
    row_delta = jnp.sum(
        gradient_tiles.astype(jnp.float32) * attended_output.astype(jnp.float32),
        axis=-1,
        keepdims=True,
    )
    grad_parts = [
        jnp.einsum("bje,bxe->bjx", gradient_tiles, piece, preferred_element_type=jnp.float32)
        for piece in value_pieces
    ]
    far_grad = jnp.einsum(
        "bje,brxe->bjrx", gradient_tiles, value_far, preferred_element_type=jnp.float32
    )
    grad_parts.append(far_grad.reshape(blocks_dev, BLOCK, RAND * BLOCK))
    probability_gradient = jnp.concatenate(grad_parts, axis=-1)
    score_gradient = (probability * (probability_gradient - row_delta)).astype(jnp.bfloat16)
    query_sum = jnp.einsum(
        "bjx,bxe->bje",
        score_gradient[:, :, :BLOCK],
        key_pieces[0],
        preferred_element_type=jnp.float32,
    )
    for slot in range(1, 3):
        query_sum = query_sum + jnp.einsum(
            "bjx,bxe->bje",
            score_gradient[:, :, slot * BLOCK : (slot + 1) * BLOCK],
            key_pieces[slot],
            preferred_element_type=jnp.float32,
        )
    far_scores = score_gradient[:, :, 3 * BLOCK :].reshape(blocks_dev, BLOCK, RAND, BLOCK)
    query_sum = query_sum + jnp.einsum(
        "bjrx,brxe->bje", far_scores, key_far, preferred_element_type=jnp.float32
    )
    query_gradient = (logit_scale * query_sum).astype(jnp.bfloat16)
    key_window, value_window = ([], [])
    for slot in range(3):
        columns = slice(slot * BLOCK, (slot + 1) * BLOCK)
        key_window.append(
            logit_scale
            * jnp.einsum(
                "bjx,bje->bxe",
                score_gradient[:, :, columns],
                query_tiles,
                preferred_element_type=jnp.float32,
            )
        )
        value_window.append(
            jnp.einsum(
                "bjx,bje->bxe",
                softmax_weights[:, :, columns],
                gradient_tiles,
                preferred_element_type=jnp.float32,
            )
        )
    far_weights = softmax_weights[:, :, 3 * BLOCK :].reshape(blocks_dev, BLOCK, RAND, BLOCK)
    key_far_terms = (
        logit_scale
        * jnp.einsum("bjrx,bje->brxe", far_scores, query_tiles, preferred_element_type=jnp.float32)
    ).astype(jnp.bfloat16)
    value_far_terms = jnp.einsum(
        "bjrx,bje->brxe", far_weights, gradient_tiles, preferred_element_type=jnp.float32
    ).astype(jnp.bfloat16)
    return (query_gradient, key_window, value_window, key_far_terms, value_far_terms)


def exchanged_shards(queries, key_rows, value_rows, out_grad, random_device, random_block):
    seq_size = lax.axis_size("seq")
    own_index = lax.axis_index("seq")
    tokens, row_width = queries.shape
    blocks_dev = tokens // BLOCK
    heads_dev = row_width // DH
    capacity = max(2, 3 * blocks_dev // seq_size)
    selector, slot_index = routing(
        random_device, random_block, own_index, seq_size, blocks_dev, capacity
    )
    packed = jnp.concatenate([key_rows, value_rows], axis=1).reshape(
        blocks_dev, BLOCK, 2 * row_width
    )
    flattened = packed.reshape(blocks_dev, BLOCK * 2 * row_width)
    outgoing_blocks = jnp.dot(selector, flattened, preferred_element_type=jnp.float32).astype(
        jnp.bfloat16
    )
    outgoing_blocks = outgoing_blocks.reshape(seq_size * capacity, BLOCK, 2 * row_width)
    haloed = extended(packed, (("seq", 0),), 1)
    arrived = lax.all_to_all(outgoing_blocks, "seq", split_axis=0, concat_axis=0, tiled=True)
    far_blocks = far_context(arrived, slot_index, blocks_dev)
    usable = usable_mask(own_index, seq_size, blocks_dev)
    query_tiles = queries.reshape(blocks_dev, BLOCK, row_width)
    gradient_tiles = out_grad.reshape(blocks_dev, BLOCK, row_width)
    states = []
    for head_index in range(heads_dev):
        key_pieces, key_far = slot_pieces(haloed, far_blocks, blocks_dev, head_index * DH)
        value_pieces, value_far = slot_pieces(
            haloed, far_blocks, blocks_dev, row_width + head_index * DH
        )
        query_head = query_tiles[:, :, head_index * DH : (head_index + 1) * DH]
        states.append(
            forward_head(query_head, key_pieces, key_far, value_pieces, value_far, usable)
        )
    query_parts = []
    window_lists = [[], [], []]
    value_lists = [[], [], []]
    far_keys, far_values = ([], [])
    for head_index in range(heads_dev):
        key_pieces, key_far = slot_pieces(haloed, far_blocks, blocks_dev, head_index * DH)
        value_pieces, value_far = slot_pieces(
            haloed, far_blocks, blocks_dev, row_width + head_index * DH
        )
        query_head = query_tiles[:, :, head_index * DH : (head_index + 1) * DH]
        gradient_head = gradient_tiles[:, :, head_index * DH : (head_index + 1) * DH]
        query_gradient, key_window, value_window, key_far_terms, value_far_terms = backward_head(
            query_head,
            key_pieces,
            key_far,
            value_pieces,
            value_far,
            gradient_head,
            states[head_index],
        )
        query_parts.append(query_gradient)
        for slot in range(3):
            window_lists[slot].append(key_window[slot])
            value_lists[slot].append(value_window[slot])
        far_keys.append(key_far_terms)
        far_values.append(value_far_terms)
    slot_terms = [
        jnp.concatenate(window_lists[slot] + value_lists[slot], axis=-1) for slot in range(3)
    ]
    left_terms = slot_terms[0]
    right_terms = slot_terms[2]
    far_terms = jnp.concatenate(far_keys + far_values, axis=-1).reshape(
        blocks_dev * RAND, BLOCK, 2 * row_width
    )
    edge_terms = jnp.stack([left_terms[0], right_terms[-1]])
    edge_haloed = extended(edge_terms.astype(jnp.bfloat16), (("seq", 0),), 1).astype(
        edge_terms.dtype
    )
    summed = (
        slot_terms[1]
        + jnp.concatenate([left_terms[1:], edge_haloed[3:]], axis=0)
        + jnp.concatenate([edge_haloed[:1], right_terms[:-1]], axis=0)
    )
    returning = (
        jnp.zeros((seq_size * capacity, BLOCK, 2 * row_width), jnp.bfloat16)
        .at[slot_index]
        .set(far_terms)
    )
    returned = lax.all_to_all(returning, "seq", split_axis=0, concat_axis=0, tiled=True)
    gathered_terms = jnp.dot(
        selector.T,
        returned.reshape(seq_size * capacity, BLOCK * 2 * row_width),
        preferred_element_type=jnp.float32,
    )
    summed = summed + gathered_terms.reshape(blocks_dev, BLOCK, 2 * row_width)
    summed = summed.reshape(tokens, 2 * row_width)
    query_out = jnp.concatenate(query_parts, axis=-1).reshape(tokens, row_width)
    return (
        query_out,
        summed[:, :row_width].astype(jnp.bfloat16),
        summed[:, row_width:].astype(jnp.bfloat16),
    )


SLOTS = 3 + RAND


def block_kernel(ids_ref, write_ref, valid_ref, first_ref, q_ref, g_ref, *rest):
    kv_refs = rest[:SLOTS]
    own_ref, spread_ref, dq_ref, acc_ref = rest[SLOTS:]
    step = pl.program_id(0)
    steps = pl.num_programs(0)
    width = q_ref.shape[1]
    blocks_dev = own_ref.shape[0]
    logit_scale = 1.0 / math.sqrt(DH)

    @pl.when(step == 0)
    def _():
        acc_ref[...] = jnp.zeros(acc_ref.shape, jnp.float32)

    context = jnp.concatenate([ref[0] for ref in kv_refs], axis=0)
    slot_of = lax.broadcasted_iota(jnp.int32, (SLOTS * BLOCK, 1), 0) // BLOCK
    usable = slot_of < 0
    for slot in range(SLOTS):
        usable = usable | ((slot_of == slot) & (valid_ref[step * SLOTS + slot] > 0))
    key_parts, value_parts = [], []
    for head in range(width // DH):
        cols = slice(head * DH, (head + 1) * DH)
        vcols = slice(width + head * DH, width + (head + 1) * DH)
        query = q_ref[:, cols]
        grad = g_ref[:, cols]
        keys = context[:, cols]
        values = context[:, vcols]
        logits = lax.dot_general(
            keys, query, (((1,), (1,)), ((), ())), preferred_element_type=jnp.float32
        ) * logit_scale
        logits = jnp.where(usable, logits, -jnp.inf)
        row_max = jnp.max(logits, axis=0, keepdims=True)
        exponent = jnp.exp(logits - row_max)
        row_total = jnp.sum(exponent, axis=0, keepdims=True)
        probability = exponent / row_total
        weights = probability.astype(jnp.bfloat16)
        attended = lax.dot_general(
            weights, values, (((0,), (0,)), ((), ())), preferred_element_type=jnp.float32
        ).astype(jnp.bfloat16)
        product = grad.astype(jnp.float32) * attended.astype(jnp.float32)
        row_delta = jnp.sum(product.T, axis=0, keepdims=True)
        prob_grad = lax.dot_general(
            values, grad, (((1,), (1,)), ((), ())), preferred_element_type=jnp.float32
        )
        score_grad = (probability * (prob_grad - row_delta)).astype(jnp.bfloat16)
        query_grad = logit_scale * lax.dot_general(
            score_grad, keys, (((0,), (0,)), ((), ())), preferred_element_type=jnp.float32
        )
        dq_ref[:, cols] = query_grad.astype(jnp.bfloat16)
        key_parts.append(
            logit_scale * jnp.dot(score_grad, query, preferred_element_type=jnp.float32)
        )
        value_parts.append(jnp.dot(weights, grad, preferred_element_type=jnp.float32))
    terms = jnp.concatenate(key_parts + value_parts, axis=1)
    for slot in range(SLOTS):
        piece = terms[slot * BLOCK : (slot + 1) * BLOCK]
        if slot >= 3:
            piece = piece.astype(jnp.bfloat16).astype(jnp.float32)
        target = write_ref[step * SLOTS + slot]
        acc_ref[target] = acc_ref[target] + piece

    @pl.when(step == steps - 1)
    def _():
        first = first_ref[0]
        spread_ref[...] = acc_ref[...].astype(jnp.bfloat16)
        for block in range(blocks_dev):
            own_ref[block] = acc_ref[first + block]
            spread_ref[first + block] = jnp.zeros(spread_ref.shape[1:], jnp.bfloat16)


def block_attention(ids, write_ids, valid, first, queries, out_grad, source, chunk, width, total):
    tokens = queries.shape[0]
    blocks_dev = tokens // BLOCK

    def context_spec(slot):
        return pl.BlockSpec(
            (1, BLOCK, 2 * width), lambda i, ids, write_ids, valid, first: (ids[i * SLOTS + slot], 0, 0)
        )

    column_spec = pl.BlockSpec((BLOCK, width), lambda i, ids, write_ids, valid, first: (i, chunk))
    row_spec = pl.BlockSpec((BLOCK, width), lambda i, ids, write_ids, valid, first: (i, 0))
    grid_spec = pltpu.PrefetchScalarGridSpec(
        num_scalar_prefetch=4,
        grid=(blocks_dev,),
        in_specs=[column_spec, column_spec] + [context_spec(s) for s in range(SLOTS)],
        out_specs=[
            pl.BlockSpec(
                (blocks_dev, BLOCK, 2 * width), lambda i, ids, write_ids, valid, first: (0, 0, 0)
            ),
            pl.BlockSpec((total, BLOCK, 2 * width), lambda i, ids, write_ids, valid, first: (0, 0, 0)),
            row_spec,
        ],
        scratch_shapes=[pltpu.VMEM((total, BLOCK, 2 * width), jnp.float32)],
    )
    return pl.pallas_call(
        block_kernel,
        grid_spec=grid_spec,
        out_shape=[
            jax.ShapeDtypeStruct((blocks_dev, BLOCK, 2 * width), jnp.float32),
            jax.ShapeDtypeStruct((total, BLOCK, 2 * width), jnp.bfloat16),
            jax.ShapeDtypeStruct((tokens, width), jnp.bfloat16),
        ],
        compiler_params=pltpu.CompilerParams(vmem_limit_bytes=60 * 1024 * 1024),
    )(ids, write_ids, valid, first, queries, out_grad, *([source] * SLOTS))


def gathered_shards(queries, key_rows, value_rows, out_grad, random_device, random_block):
    seq_size = lax.axis_size("seq")
    own_index = lax.axis_index("seq")
    tokens, width = queries.shape
    blocks_dev = tokens // BLOCK
    total = seq_size * blocks_dev
    first = own_index * blocks_dev
    capacity = max(2, 3 * blocks_dev // seq_size)
    selector, slot_index = routing(
        random_device, random_block, own_index, seq_size, blocks_dev, capacity
    )
    block_ids = first + jnp.arange(blocks_dev, dtype=jnp.int32)
    local_ids = jnp.arange(blocks_dev, dtype=jnp.int32)
    own_device = lax.dynamic_slice_in_dim(random_device, first, blocks_dev, 0)
    own_block = lax.dynamic_slice_in_dim(random_block, first, blocks_dev, 0)
    chosen = (own_device * blocks_dev + own_block).astype(jnp.int32)
    window = jnp.stack(
        [jnp.clip(block_ids - 1, 0, total - 1), block_ids, jnp.clip(block_ids + 1, 0, total - 1)],
        axis=1,
    )
    write_ids = jnp.concatenate([window, chosen], axis=1).reshape(-1)
    read_window = jnp.stack([local_ids, local_ids + 1, local_ids + 2], axis=1)
    read_far = (slot_index + blocks_dev + 2).reshape(blocks_dev, RAND).astype(jnp.int32)
    read_ids = jnp.concatenate([read_window, read_far], axis=1).reshape(-1)
    always = jnp.ones_like(block_ids, dtype=jnp.bool_)
    valid = jnp.stack([block_ids > 0, always, block_ids < total - 1] + [always] * RAND, axis=1)
    valid = valid.astype(jnp.int32).reshape(-1)
    first_table = first.reshape(1).astype(jnp.int32)
    chunks = 2 if (width // DH) % 2 == 0 else 1
    part = width // chunks
    global_ids = write_ids
    results = []
    link = None
    for chunk in range(chunks):
        cols = slice(chunk * part, (chunk + 1) * part)
        packed = jnp.concatenate([key_rows[:, cols], value_rows[:, cols]], axis=1)
        if chunk == 0:
            source = lax.all_gather(packed, "seq", axis=0, tiled=True)
            source = source.reshape(total, BLOCK, 2 * part)
            table_ids = global_ids
            link = source[0, 0, :1]
        else:
            packed = packed.reshape(blocks_dev, BLOCK, 2 * part)
            route = selector
            outgoing = jnp.dot(
                route, packed.reshape(blocks_dev, BLOCK * 2 * part),
                preferred_element_type=jnp.float32,
            ).astype(jnp.bfloat16)
            outgoing = outgoing.reshape(seq_size * capacity, BLOCK, 2 * part)
            haloed = extended(packed, (("seq", 0),), 1)
            arrived = lax.all_to_all(outgoing, "seq", split_axis=0, concat_axis=0, tiled=True)
            source = jnp.concatenate([haloed, arrived], axis=0)
            table_ids = read_ids
        results.append((source, table_ids))
    query_parts, key_parts, value_parts = [], [], []
    after = results[-1][0][blocks_dev + 2 :] if chunks > 1 else None
    for chunk in range(chunks):
        source, table_ids = results[chunk]
        table = first_table
        if after is not None:
            table = table + (after[0, 0, :1] * 0.0).astype(jnp.int32)
        if chunk == 0:
            own_sum, spread, query_out = block_attention(
                table_ids, global_ids, valid, table, queries, out_grad, source, chunk, part, total,
            )
            returned = lax.psum_scatter(
                spread.reshape(total * BLOCK, 2 * part), "seq", scatter_dimension=0, tiled=True
            )
            summed = own_sum.reshape(tokens, 2 * part) + returned.astype(jnp.float32)
        else:
            slots = seq_size * capacity
            far_rows = slot_index.reshape(blocks_dev, RAND).astype(jnp.int32)
            far_write = jnp.concatenate([window + slots, far_rows], axis=1).reshape(-1)
            own_sum, spread, query_out = block_attention(
                table_ids, far_write, valid, table + slots, queries, out_grad, source, chunk,
                part, slots + total,
            )
            returned = lax.all_to_all(
                spread[:slots], "seq", split_axis=0, concat_axis=0, tiled=True
            )
            spread = spread[slots:]
            gathered = jnp.dot(
                selector.T,
                returned.reshape(seq_size * capacity, BLOCK * 2 * part),
                preferred_element_type=jnp.float32,
            ).reshape(blocks_dev, BLOCK, 2 * part)
            left_edge = lax.dynamic_index_in_dim(
                spread, jnp.clip(first - 1, 0, total - 1), 0, keepdims=False
            )
            right_edge = lax.dynamic_index_in_dim(
                spread, jnp.clip(first + blocks_dev, 0, total - 1), 0, keepdims=False
            )
            from_right = lax.ppermute(left_edge, "seq", [(i, i - 1) for i in range(1, seq_size)])
            from_left = lax.ppermute(right_edge, "seq", [(i, i + 1) for i in range(seq_size - 1)])
            combined = (
                (own_sum + gathered)
                .at[0].add(from_left.astype(jnp.float32))
                .at[blocks_dev - 1].add(from_right.astype(jnp.float32))
            )
            summed = combined.reshape(tokens, 2 * part)
        after = own_sum
        query_parts.append(query_out)
        key_parts.append(summed[:, :part].astype(jnp.bfloat16))
        value_parts.append(summed[:, part:].astype(jnp.bfloat16))
    return (
        jnp.concatenate(query_parts, axis=1),
        jnp.concatenate(key_parts, axis=1),
        jnp.concatenate(value_parts, axis=1),
    )


def shards(queries, key_rows, value_rows, out_grad, random_device, random_block):
    if lax.axis_size("seq") <= 8:
        return gathered_shards(queries, key_rows, value_rows, out_grad, random_device, random_block)
    return exchanged_shards(queries, key_rows, value_rows, out_grad, random_device, random_block)


def solution(mesh):
    return jax.shard_map(
        shards,
        mesh=mesh,
        in_specs=(
            P(("groups", "seq"), ("heads", "pair")),
            P(("groups", "seq"), ("heads", "pair")),
            P(("groups", "seq"), ("heads", "pair")),
            P(("groups", "seq"), ("heads", "pair")),
            P("groups", None),
            P("groups", None),
        ),
        out_specs=(
            P(("groups", "seq"), ("heads", "pair")),
            P(("groups", "seq"), ("heads", "pair")),
            P(("groups", "seq"), ("heads", "pair")),
        ),
        check_vma=False,
    )
```

```python
import math

import jax
import jax.numpy as jnp
from jax import lax
from jax.experimental import pallas as pl
from jax.experimental.pallas import tpu as pltpu
from jax.sharding import PartitionSpec as P

DH = 128
BLOCK = 64
RAND = 2


def extended(block, sides, width):
    for axis, dim in sides:
        count = lax.axis_size(axis)
        forward = [(i, i + 1) for i in range(count - 1)]
        backward = [(target, source) for source, target in forward]
        low = lax.ppermute(
            lax.slice_in_dim(block, block.shape[dim] - width, None, axis=dim), axis, forward
        )
        high = lax.ppermute(lax.slice_in_dim(block, 0, width, axis=dim), axis, backward)
        block = jnp.concatenate([low, block, high], axis=dim)
    return block


def routing(random_device, random_block, own_index, seq_size, blocks_dev, capacity):
    entries = blocks_dev * RAND
    wanted_from = random_device.reshape(seq_size, entries)
    wanted_block = random_block.reshape(seq_size, entries)
    from_me = (wanted_from == own_index).astype(jnp.int32)
    rank_out = jnp.cumsum(from_me, axis=1) - from_me
    slot_hits = from_me[:, None, :] * (
        rank_out[:, None, :] == jnp.arange(capacity, dtype=jnp.int32)[None, :, None]
    ).astype(jnp.int32)
    block_hits = (
        wanted_block[:, :, None] == jnp.arange(blocks_dev, dtype=jnp.int32)[None, None, :]
    ).astype(jnp.float32)
    selector = jnp.einsum("sce,sej->scj", slot_hits.astype(jnp.float32), block_hits)
    selector = selector.reshape(seq_size * capacity, blocks_dev).astype(jnp.bfloat16)
    own_sources = lax.dynamic_slice_in_dim(
        random_device, own_index * blocks_dev, blocks_dev, 0
    ).reshape(entries)
    peer_hits = (own_sources[:, None] == jnp.arange(seq_size, dtype=jnp.int32)[None, :]).astype(
        jnp.int32
    )
    earlier = jnp.cumsum(peer_hits, axis=0) - peer_hits
    rank_in = jnp.sum(earlier * peer_hits, axis=1)
    slot_index = own_sources * capacity + rank_in
    return (selector, slot_index)


def far_context(arrived, slot_index, blocks_dev):
    picked = jnp.take(arrived, slot_index, axis=0)
    return picked.reshape(blocks_dev, RAND, arrived.shape[1], arrived.shape[2])


def usable_mask(own_index, seq_size, blocks_dev):
    block_ids = jnp.arange(blocks_dev, dtype=jnp.int32)[:, None]
    slot_ids = jnp.arange(3 + RAND, dtype=jnp.int32)[None, :]
    global_block = own_index * blocks_dev + block_ids
    missing = (slot_ids == 0) & (global_block == 0) | (slot_ids == 2) & (
        global_block == seq_size * blocks_dev - 1
    )
    return jnp.repeat(jnp.logical_not(missing), BLOCK, axis=1)


def slot_pieces(haloed, far_blocks, blocks_dev, start_col):
    pieces = []
    for slot in range(3):
        pieces.append(haloed[slot : slot + blocks_dev, :, start_col : start_col + DH])
    far_part = far_blocks[:, :, :, start_col : start_col + DH]
    return (pieces, far_part)


def forward_head(query_tiles, key_pieces, key_far, value_pieces, value_far, usable):
    blocks_dev = query_tiles.shape[0]
    logit_parts = [
        jnp.einsum("bje,bxe->bjx", query_tiles, piece, preferred_element_type=jnp.float32)
        for piece in key_pieces
    ]
    far_logits = jnp.einsum(
        "bje,brxe->bjrx", query_tiles, key_far, preferred_element_type=jnp.float32
    )
    logit_parts.append(far_logits.reshape(blocks_dev, BLOCK, RAND * BLOCK))
    attention_logits = jnp.concatenate(logit_parts, axis=-1) * (1.0 / math.sqrt(DH))
    attention_logits = jnp.where(usable[:, None, :], attention_logits, -jnp.inf)
    row_max = jnp.max(attention_logits, axis=-1, keepdims=True)
    exponent = jnp.exp(attention_logits - row_max)
    row_total = jnp.sum(exponent, axis=-1, keepdims=True)
    probability = exponent / row_total
    softmax_weights = probability.astype(jnp.bfloat16)
    attended = jnp.einsum(
        "bjx,bxe->bje",
        softmax_weights[:, :, :BLOCK],
        value_pieces[0],
        preferred_element_type=jnp.float32,
    )
    for slot in range(1, 3):
        attended = attended + jnp.einsum(
            "bjx,bxe->bje",
            softmax_weights[:, :, slot * BLOCK : (slot + 1) * BLOCK],
            value_pieces[slot],
            preferred_element_type=jnp.float32,
        )
    far_weights = softmax_weights[:, :, 3 * BLOCK :].reshape(blocks_dev, BLOCK, RAND, BLOCK)
    attended = attended + jnp.einsum(
        "bjrx,brxe->bje", far_weights, value_far, preferred_element_type=jnp.float32
    )
    return (probability, attended.astype(jnp.bfloat16))


def backward_head(
    query_tiles, key_pieces, key_far, value_pieces, value_far, gradient_tiles, forward_state
):
    probability, attended_output = forward_state
    blocks_dev = query_tiles.shape[0]
    logit_scale = 1.0 / math.sqrt(DH)
    softmax_weights = probability.astype(jnp.bfloat16)
    row_delta = jnp.sum(
        gradient_tiles.astype(jnp.float32) * attended_output.astype(jnp.float32),
        axis=-1,
        keepdims=True,
    )
    grad_parts = [
        jnp.einsum("bje,bxe->bjx", gradient_tiles, piece, preferred_element_type=jnp.float32)
        for piece in value_pieces
    ]
    far_grad = jnp.einsum(
        "bje,brxe->bjrx", gradient_tiles, value_far, preferred_element_type=jnp.float32
    )
    grad_parts.append(far_grad.reshape(blocks_dev, BLOCK, RAND * BLOCK))
    probability_gradient = jnp.concatenate(grad_parts, axis=-1)
    score_gradient = (probability * (probability_gradient - row_delta)).astype(jnp.bfloat16)
    query_sum = jnp.einsum(
        "bjx,bxe->bje",
        score_gradient[:, :, :BLOCK],
        key_pieces[0],
        preferred_element_type=jnp.float32,
    )
    for slot in range(1, 3):
        query_sum = query_sum + jnp.einsum(
            "bjx,bxe->bje",
            score_gradient[:, :, slot * BLOCK : (slot + 1) * BLOCK],
            key_pieces[slot],
            preferred_element_type=jnp.float32,
        )
    far_scores = score_gradient[:, :, 3 * BLOCK :].reshape(blocks_dev, BLOCK, RAND, BLOCK)
    query_sum = query_sum + jnp.einsum(
        "bjrx,brxe->bje", far_scores, key_far, preferred_element_type=jnp.float32
    )
    query_gradient = (logit_scale * query_sum).astype(jnp.bfloat16)
    key_window, value_window = ([], [])
    for slot in range(3):
        columns = slice(slot * BLOCK, (slot + 1) * BLOCK)
        key_window.append(
            logit_scale
            * jnp.einsum(
                "bjx,bje->bxe",
                score_gradient[:, :, columns],
                query_tiles,
                preferred_element_type=jnp.float32,
            )
        )
        value_window.append(
            jnp.einsum(
                "bjx,bje->bxe",
                softmax_weights[:, :, columns],
                gradient_tiles,
                preferred_element_type=jnp.float32,
            )
        )
    far_weights = softmax_weights[:, :, 3 * BLOCK :].reshape(blocks_dev, BLOCK, RAND, BLOCK)
    key_far_terms = (
        logit_scale
        * jnp.einsum("bjrx,bje->brxe", far_scores, query_tiles, preferred_element_type=jnp.float32)
    ).astype(jnp.bfloat16)
    value_far_terms = jnp.einsum(
        "bjrx,bje->brxe", far_weights, gradient_tiles, preferred_element_type=jnp.float32
    ).astype(jnp.bfloat16)
    return (query_gradient, key_window, value_window, key_far_terms, value_far_terms)


def exchanged_shards(queries, key_rows, value_rows, out_grad, random_device, random_block):
    seq_size = lax.axis_size("seq")
    own_index = lax.axis_index("seq")
    tokens, row_width = queries.shape
    blocks_dev = tokens // BLOCK
    heads_dev = row_width // DH
    capacity = max(2, 3 * blocks_dev // seq_size)
    selector, slot_index = routing(
        random_device, random_block, own_index, seq_size, blocks_dev, capacity
    )
    packed = jnp.concatenate([key_rows, value_rows], axis=1).reshape(
        blocks_dev, BLOCK, 2 * row_width
    )
    flattened = packed.reshape(blocks_dev, BLOCK * 2 * row_width)
    outgoing_blocks = jnp.dot(selector, flattened, preferred_element_type=jnp.float32).astype(
        jnp.bfloat16
    )
    outgoing_blocks = outgoing_blocks.reshape(seq_size * capacity, BLOCK, 2 * row_width)
    haloed = extended(packed, (("seq", 0),), 1)
    arrived = lax.all_to_all(outgoing_blocks, "seq", split_axis=0, concat_axis=0, tiled=True)
    far_blocks = far_context(arrived, slot_index, blocks_dev)
    usable = usable_mask(own_index, seq_size, blocks_dev)
    query_tiles = queries.reshape(blocks_dev, BLOCK, row_width)
    gradient_tiles = out_grad.reshape(blocks_dev, BLOCK, row_width)
    states = []
    for head_index in range(heads_dev):
        key_pieces, key_far = slot_pieces(haloed, far_blocks, blocks_dev, head_index * DH)
        value_pieces, value_far = slot_pieces(
            haloed, far_blocks, blocks_dev, row_width + head_index * DH
        )
        query_head = query_tiles[:, :, head_index * DH : (head_index + 1) * DH]
        states.append(
            forward_head(query_head, key_pieces, key_far, value_pieces, value_far, usable)
        )
    query_parts = []
    window_lists = [[], [], []]
    value_lists = [[], [], []]
    far_keys, far_values = ([], [])
    for head_index in range(heads_dev):
        key_pieces, key_far = slot_pieces(haloed, far_blocks, blocks_dev, head_index * DH)
        value_pieces, value_far = slot_pieces(
            haloed, far_blocks, blocks_dev, row_width + head_index * DH
        )
        query_head = query_tiles[:, :, head_index * DH : (head_index + 1) * DH]
        gradient_head = gradient_tiles[:, :, head_index * DH : (head_index + 1) * DH]
        query_gradient, key_window, value_window, key_far_terms, value_far_terms = backward_head(
            query_head,
            key_pieces,
            key_far,
            value_pieces,
            value_far,
            gradient_head,
            states[head_index],
        )
        query_parts.append(query_gradient)
        for slot in range(3):
            window_lists[slot].append(key_window[slot])
            value_lists[slot].append(value_window[slot])
        far_keys.append(key_far_terms)
        far_values.append(value_far_terms)
    slot_terms = [
        jnp.concatenate(window_lists[slot] + value_lists[slot], axis=-1) for slot in range(3)
    ]
    left_terms = slot_terms[0]
    right_terms = slot_terms[2]
    far_terms = jnp.concatenate(far_keys + far_values, axis=-1).reshape(
        blocks_dev * RAND, BLOCK, 2 * row_width
    )
    edge_terms = jnp.stack([left_terms[0], right_terms[-1]])
    edge_haloed = extended(edge_terms.astype(jnp.bfloat16), (("seq", 0),), 1).astype(
        edge_terms.dtype
    )
    summed = (
        slot_terms[1]
        + jnp.concatenate([left_terms[1:], edge_haloed[3:]], axis=0)
        + jnp.concatenate([edge_haloed[:1], right_terms[:-1]], axis=0)
    )
    returning = (
        jnp.zeros((seq_size * capacity, BLOCK, 2 * row_width), jnp.bfloat16)
        .at[slot_index]
        .set(far_terms)
    )
    returned = lax.all_to_all(returning, "seq", split_axis=0, concat_axis=0, tiled=True)
    gathered_terms = jnp.dot(
        selector.T,
        returned.reshape(seq_size * capacity, BLOCK * 2 * row_width),
        preferred_element_type=jnp.float32,
    )
    summed = summed + gathered_terms.reshape(blocks_dev, BLOCK, 2 * row_width)
    summed = summed.reshape(tokens, 2 * row_width)
    query_out = jnp.concatenate(query_parts, axis=-1).reshape(tokens, row_width)
    return (
        query_out,
        summed[:, :row_width].astype(jnp.bfloat16),
        summed[:, row_width:].astype(jnp.bfloat16),
    )


SLOTS = 3 + RAND


def block_kernel(ids_ref, write_ref, valid_ref, first_ref, q_ref, g_ref, *rest):
    kv_refs = rest[:SLOTS]
    own_ref, spread_ref, dq_ref, acc_ref = rest[SLOTS:]
    step = pl.program_id(0)
    steps = pl.num_programs(0)
    width = q_ref.shape[1]
    blocks_dev = own_ref.shape[0]
    logit_scale = 1.0 / math.sqrt(DH)

    @pl.when(step == 0)
    def _():
        acc_ref[...] = jnp.zeros(acc_ref.shape, jnp.float32)

    context = jnp.concatenate([ref[0] for ref in kv_refs], axis=0)
    slot_of = lax.broadcasted_iota(jnp.int32, (SLOTS * BLOCK, 1), 0) // BLOCK
    usable = slot_of < 0
    for slot in range(SLOTS):
        usable = usable | ((slot_of == slot) & (valid_ref[step * SLOTS + slot] > 0))
    key_parts, value_parts = [], []
    for head in range(width // DH):
        cols = slice(head * DH, (head + 1) * DH)
        vcols = slice(width + head * DH, width + (head + 1) * DH)
        query = q_ref[:, cols]
        grad = g_ref[:, cols]
        keys = context[:, cols]
        values = context[:, vcols]
        logits = lax.dot_general(
            keys, query, (((1,), (1,)), ((), ())), preferred_element_type=jnp.float32
        ) * logit_scale
        logits = jnp.where(usable, logits, -jnp.inf)
        row_max = jnp.max(logits, axis=0, keepdims=True)
        exponent = jnp.exp(logits - row_max)
        row_total = jnp.sum(exponent, axis=0, keepdims=True)
        probability = exponent / row_total
        weights = probability.astype(jnp.bfloat16)
        attended = lax.dot_general(
            weights, values, (((0,), (0,)), ((), ())), preferred_element_type=jnp.float32
        ).astype(jnp.bfloat16)
        product = grad.astype(jnp.float32) * attended.astype(jnp.float32)
        row_delta = jnp.sum(product.T, axis=0, keepdims=True)
        prob_grad = lax.dot_general(
            values, grad, (((1,), (1,)), ((), ())), preferred_element_type=jnp.float32
        )
        score_grad = (probability * (prob_grad - row_delta)).astype(jnp.bfloat16)
        query_grad = logit_scale * lax.dot_general(
            score_grad, keys, (((0,), (0,)), ((), ())), preferred_element_type=jnp.float32
        )
        dq_ref[:, cols] = query_grad.astype(jnp.bfloat16)
        key_parts.append(
            logit_scale * jnp.dot(score_grad, query, preferred_element_type=jnp.float32)
        )
        value_parts.append(jnp.dot(weights, grad, preferred_element_type=jnp.float32))
    terms = jnp.concatenate(key_parts + value_parts, axis=1)
    for slot in range(SLOTS):
        piece = terms[slot * BLOCK : (slot + 1) * BLOCK]
        if slot >= 3:
            piece = piece.astype(jnp.bfloat16).astype(jnp.float32)
        target = write_ref[step * SLOTS + slot]
        acc_ref[target] = acc_ref[target] + piece

    @pl.when(step == steps - 1)
    def _():
        first = first_ref[0]
        spread_ref[...] = acc_ref[...].astype(jnp.bfloat16)
        for block in range(blocks_dev):
            own_ref[block] = acc_ref[first + block]
            spread_ref[first + block] = jnp.zeros(spread_ref.shape[1:], jnp.bfloat16)


def block_attention(ids, write_ids, valid, first, queries, out_grad, source, chunk, width, total):
    tokens = queries.shape[0]
    blocks_dev = tokens // BLOCK

    def context_spec(slot):
        return pl.BlockSpec(
            (1, BLOCK, 2 * width), lambda i, ids, write_ids, valid, first: (ids[i * SLOTS + slot], 0, 0)
        )

    column_spec = pl.BlockSpec((BLOCK, width), lambda i, ids, write_ids, valid, first: (i, chunk))
    row_spec = pl.BlockSpec((BLOCK, width), lambda i, ids, write_ids, valid, first: (i, 0))
    grid_spec = pltpu.PrefetchScalarGridSpec(
        num_scalar_prefetch=4,
        grid=(blocks_dev,),
        in_specs=[column_spec, column_spec] + [context_spec(s) for s in range(SLOTS)],
        out_specs=[
            pl.BlockSpec(
                (blocks_dev, BLOCK, 2 * width), lambda i, ids, write_ids, valid, first: (0, 0, 0)
            ),
            pl.BlockSpec((total, BLOCK, 2 * width), lambda i, ids, write_ids, valid, first: (0, 0, 0)),
            row_spec,
        ],
        scratch_shapes=[pltpu.VMEM((total, BLOCK, 2 * width), jnp.float32)],
    )
    return pl.pallas_call(
        block_kernel,
        grid_spec=grid_spec,
        out_shape=[
            jax.ShapeDtypeStruct((blocks_dev, BLOCK, 2 * width), jnp.float32),
            jax.ShapeDtypeStruct((total, BLOCK, 2 * width), jnp.bfloat16),
            jax.ShapeDtypeStruct((tokens, width), jnp.bfloat16),
        ],
        compiler_params=pltpu.CompilerParams(vmem_limit_bytes=60 * 1024 * 1024),
    )(ids, write_ids, valid, first, queries, out_grad, *([source] * SLOTS))


def gathered_shards(queries, key_rows, value_rows, out_grad, random_device, random_block):
    seq_size = lax.axis_size("seq")
    own_index = lax.axis_index("seq")
    tokens, width = queries.shape
    blocks_dev = tokens // BLOCK
    total = seq_size * blocks_dev
    first = own_index * blocks_dev
    capacity = max(2, 3 * blocks_dev // seq_size)
    selector, slot_index = routing(
        random_device, random_block, own_index, seq_size, blocks_dev, capacity
    )
    block_ids = first + jnp.arange(blocks_dev, dtype=jnp.int32)
    local_ids = jnp.arange(blocks_dev, dtype=jnp.int32)
    own_device = lax.dynamic_slice_in_dim(random_device, first, blocks_dev, 0)
    own_block = lax.dynamic_slice_in_dim(random_block, first, blocks_dev, 0)
    chosen = (own_device * blocks_dev + own_block).astype(jnp.int32)
    window = jnp.stack(
        [jnp.clip(block_ids - 1, 0, total - 1), block_ids, jnp.clip(block_ids + 1, 0, total - 1)],
        axis=1,
    )
    write_ids = jnp.concatenate([window, chosen], axis=1).reshape(-1)
    read_window = jnp.stack([local_ids, local_ids + 1, local_ids + 2], axis=1)
    read_far = (slot_index + blocks_dev + 2).reshape(blocks_dev, RAND).astype(jnp.int32)
    read_ids = jnp.concatenate([read_window, read_far], axis=1).reshape(-1)
    always = jnp.ones_like(block_ids, dtype=jnp.bool_)
    valid = jnp.stack([block_ids > 0, always, block_ids < total - 1] + [always] * RAND, axis=1)
    valid = valid.astype(jnp.int32).reshape(-1)
    first_table = first.reshape(1).astype(jnp.int32)
    chunks = 2 if (width // DH) % 2 == 0 else 1
    part = width // chunks
    global_ids = write_ids
    results = []
    link = None
    for chunk in range(chunks):
        cols = slice(chunk * part, (chunk + 1) * part)
        packed = jnp.concatenate([key_rows[:, cols], value_rows[:, cols]], axis=1)
        if chunk == 0:
            source = lax.all_gather(packed, "seq", axis=0, tiled=True)
            source = source.reshape(total, BLOCK, 2 * part)
            table_ids = global_ids
            link = source[0, 0, :1]
        else:
            packed = packed.reshape(blocks_dev, BLOCK, 2 * part)
            route = selector
            outgoing = jnp.dot(
                route, packed.reshape(blocks_dev, BLOCK * 2 * part),
                preferred_element_type=jnp.float32,
            ).astype(jnp.bfloat16)
            outgoing = outgoing.reshape(seq_size * capacity, BLOCK, 2 * part)
            haloed = extended(packed, (("seq", 0),), 1)
            arrived = lax.all_to_all(outgoing, "seq", split_axis=0, concat_axis=0, tiled=True)
            source = jnp.concatenate([haloed, arrived], axis=0)
            table_ids = read_ids
        results.append((source, table_ids))
    query_parts, key_parts, value_parts = [], [], []
    after = results[-1][0][blocks_dev + 2 :] if chunks > 1 else None
    for chunk in range(chunks):
        source, table_ids = results[chunk]
        table = first_table
        if after is not None:
            table = table + (after[0, 0, :1] * 0.0).astype(jnp.int32)
        if chunk == 0:
            own_sum, spread, query_out = block_attention(
                table_ids, global_ids, valid, table, queries, out_grad, source, chunk, part, total,
            )
            returned = lax.psum_scatter(
                spread.reshape(total * BLOCK, 2 * part), "seq", scatter_dimension=0, tiled=True
            )
            summed = own_sum.reshape(tokens, 2 * part) + returned.astype(jnp.float32)
        else:
            slots = seq_size * capacity
            far_rows = slot_index.reshape(blocks_dev, RAND).astype(jnp.int32)
            near = window - first + 1 + slots
            far_write = jnp.concatenate([near, far_rows], axis=1).reshape(-1)
            own_sum, spread, query_out = block_attention(
                table_ids, far_write, valid, table - first + 1 + slots, queries, out_grad, source,
                chunk, part, slots + blocks_dev + 2,
            )
            returned = lax.all_to_all(
                spread[:slots], "seq", split_axis=0, concat_axis=0, tiled=True
            )
            spread = spread[slots:]
            gathered = jnp.dot(
                selector.T,
                returned.reshape(seq_size * capacity, BLOCK * 2 * part),
                preferred_element_type=jnp.float32,
            ).reshape(blocks_dev, BLOCK, 2 * part)
            left_edge = spread[0]
            right_edge = spread[blocks_dev + 1]
            from_right = lax.ppermute(left_edge, "seq", [(i, i - 1) for i in range(1, seq_size)])
            from_left = lax.ppermute(right_edge, "seq", [(i, i + 1) for i in range(seq_size - 1)])
            combined = (
                (own_sum + gathered)
                .at[0].add(from_left.astype(jnp.float32))
                .at[blocks_dev - 1].add(from_right.astype(jnp.float32))
            )
            summed = combined.reshape(tokens, 2 * part)
        after = own_sum
        query_parts.append(query_out)
        key_parts.append(summed[:, :part].astype(jnp.bfloat16))
        value_parts.append(summed[:, part:].astype(jnp.bfloat16))
    return (
        jnp.concatenate(query_parts, axis=1),
        jnp.concatenate(key_parts, axis=1),
        jnp.concatenate(value_parts, axis=1),
    )


def shards(queries, key_rows, value_rows, out_grad, random_device, random_block):
    if lax.axis_size("seq") <= 8:
        return gathered_shards(queries, key_rows, value_rows, out_grad, random_device, random_block)
    return exchanged_shards(queries, key_rows, value_rows, out_grad, random_device, random_block)


def solution(mesh):
    return jax.shard_map(
        shards,
        mesh=mesh,
        in_specs=(
            P(("groups", "seq"), ("heads", "pair")),
            P(("groups", "seq"), ("heads", "pair")),
            P(("groups", "seq"), ("heads", "pair")),
            P(("groups", "seq"), ("heads", "pair")),
            P("groups", None),
            P("groups", None),
        ),
        out_specs=(
            P(("groups", "seq"), ("heads", "pair")),
            P(("groups", "seq"), ("heads", "pair")),
            P(("groups", "seq"), ("heads", "pair")),
        ),
        check_vma=False,
    )
```

```python
import math

import jax
import jax.numpy as jnp
from jax import lax
from jax.experimental import pallas as pl
from jax.experimental.pallas import tpu as pltpu
from jax.sharding import PartitionSpec as P

DH = 128
BLOCK = 64
RAND = 2


def extended(block, sides, width):
    for axis, dim in sides:
        count = lax.axis_size(axis)
        forward = [(i, i + 1) for i in range(count - 1)]
        backward = [(target, source) for source, target in forward]
        low = lax.ppermute(
            lax.slice_in_dim(block, block.shape[dim] - width, None, axis=dim), axis, forward
        )
        high = lax.ppermute(lax.slice_in_dim(block, 0, width, axis=dim), axis, backward)
        block = jnp.concatenate([low, block, high], axis=dim)
    return block


def routing(random_device, random_block, own_index, seq_size, blocks_dev, capacity):
    entries = blocks_dev * RAND
    wanted_from = random_device.reshape(seq_size, entries)
    wanted_block = random_block.reshape(seq_size, entries)
    from_me = (wanted_from == own_index).astype(jnp.int32)
    rank_out = jnp.cumsum(from_me, axis=1) - from_me
    slot_hits = from_me[:, None, :] * (
        rank_out[:, None, :] == jnp.arange(capacity, dtype=jnp.int32)[None, :, None]
    ).astype(jnp.int32)
    block_hits = (
        wanted_block[:, :, None] == jnp.arange(blocks_dev, dtype=jnp.int32)[None, None, :]
    ).astype(jnp.float32)
    selector = jnp.einsum("sce,sej->scj", slot_hits.astype(jnp.float32), block_hits)
    selector = selector.reshape(seq_size * capacity, blocks_dev).astype(jnp.bfloat16)
    own_sources = lax.dynamic_slice_in_dim(
        random_device, own_index * blocks_dev, blocks_dev, 0
    ).reshape(entries)
    peer_hits = (own_sources[:, None] == jnp.arange(seq_size, dtype=jnp.int32)[None, :]).astype(
        jnp.int32
    )
    earlier = jnp.cumsum(peer_hits, axis=0) - peer_hits
    rank_in = jnp.sum(earlier * peer_hits, axis=1)
    slot_index = own_sources * capacity + rank_in
    return (selector, slot_index)


def far_context(arrived, slot_index, blocks_dev):
    picked = jnp.take(arrived, slot_index, axis=0)
    return picked.reshape(blocks_dev, RAND, arrived.shape[1], arrived.shape[2])


def usable_mask(own_index, seq_size, blocks_dev):
    block_ids = jnp.arange(blocks_dev, dtype=jnp.int32)[:, None]
    slot_ids = jnp.arange(3 + RAND, dtype=jnp.int32)[None, :]
    global_block = own_index * blocks_dev + block_ids
    missing = (slot_ids == 0) & (global_block == 0) | (slot_ids == 2) & (
        global_block == seq_size * blocks_dev - 1
    )
    return jnp.repeat(jnp.logical_not(missing), BLOCK, axis=1)


def slot_pieces(haloed, far_blocks, blocks_dev, start_col):
    pieces = []
    for slot in range(3):
        pieces.append(haloed[slot : slot + blocks_dev, :, start_col : start_col + DH])
    far_part = far_blocks[:, :, :, start_col : start_col + DH]
    return (pieces, far_part)


def forward_head(query_tiles, key_pieces, key_far, value_pieces, value_far, usable):
    blocks_dev = query_tiles.shape[0]
    logit_parts = [
        jnp.einsum("bje,bxe->bjx", query_tiles, piece, preferred_element_type=jnp.float32)
        for piece in key_pieces
    ]
    far_logits = jnp.einsum(
        "bje,brxe->bjrx", query_tiles, key_far, preferred_element_type=jnp.float32
    )
    logit_parts.append(far_logits.reshape(blocks_dev, BLOCK, RAND * BLOCK))
    attention_logits = jnp.concatenate(logit_parts, axis=-1) * (1.0 / math.sqrt(DH))
    attention_logits = jnp.where(usable[:, None, :], attention_logits, -jnp.inf)
    row_max = jnp.max(attention_logits, axis=-1, keepdims=True)
    exponent = jnp.exp(attention_logits - row_max)
    row_total = jnp.sum(exponent, axis=-1, keepdims=True)
    probability = exponent / row_total
    softmax_weights = probability.astype(jnp.bfloat16)
    attended = jnp.einsum(
        "bjx,bxe->bje",
        softmax_weights[:, :, :BLOCK],
        value_pieces[0],
        preferred_element_type=jnp.float32,
    )
    for slot in range(1, 3):
        attended = attended + jnp.einsum(
            "bjx,bxe->bje",
            softmax_weights[:, :, slot * BLOCK : (slot + 1) * BLOCK],
            value_pieces[slot],
            preferred_element_type=jnp.float32,
        )
    far_weights = softmax_weights[:, :, 3 * BLOCK :].reshape(blocks_dev, BLOCK, RAND, BLOCK)
    attended = attended + jnp.einsum(
        "bjrx,brxe->bje", far_weights, value_far, preferred_element_type=jnp.float32
    )
    return (probability, attended.astype(jnp.bfloat16))


def backward_head(
    query_tiles, key_pieces, key_far, value_pieces, value_far, gradient_tiles, forward_state
):
    probability, attended_output = forward_state
    blocks_dev = query_tiles.shape[0]
    logit_scale = 1.0 / math.sqrt(DH)
    softmax_weights = probability.astype(jnp.bfloat16)
    row_delta = jnp.sum(
        gradient_tiles.astype(jnp.float32) * attended_output.astype(jnp.float32),
        axis=-1,
        keepdims=True,
    )
    grad_parts = [
        jnp.einsum("bje,bxe->bjx", gradient_tiles, piece, preferred_element_type=jnp.float32)
        for piece in value_pieces
    ]
    far_grad = jnp.einsum(
        "bje,brxe->bjrx", gradient_tiles, value_far, preferred_element_type=jnp.float32
    )
    grad_parts.append(far_grad.reshape(blocks_dev, BLOCK, RAND * BLOCK))
    probability_gradient = jnp.concatenate(grad_parts, axis=-1)
    score_gradient = (probability * (probability_gradient - row_delta)).astype(jnp.bfloat16)
    query_sum = jnp.einsum(
        "bjx,bxe->bje",
        score_gradient[:, :, :BLOCK],
        key_pieces[0],
        preferred_element_type=jnp.float32,
    )
    for slot in range(1, 3):
        query_sum = query_sum + jnp.einsum(
            "bjx,bxe->bje",
            score_gradient[:, :, slot * BLOCK : (slot + 1) * BLOCK],
            key_pieces[slot],
            preferred_element_type=jnp.float32,
        )
    far_scores = score_gradient[:, :, 3 * BLOCK :].reshape(blocks_dev, BLOCK, RAND, BLOCK)
    query_sum = query_sum + jnp.einsum(
        "bjrx,brxe->bje", far_scores, key_far, preferred_element_type=jnp.float32
    )
    query_gradient = (logit_scale * query_sum).astype(jnp.bfloat16)
    key_window, value_window = ([], [])
    for slot in range(3):
        columns = slice(slot * BLOCK, (slot + 1) * BLOCK)
        key_window.append(
            logit_scale
            * jnp.einsum(
                "bjx,bje->bxe",
                score_gradient[:, :, columns],
                query_tiles,
                preferred_element_type=jnp.float32,
            )
        )
        value_window.append(
            jnp.einsum(
                "bjx,bje->bxe",
                softmax_weights[:, :, columns],
                gradient_tiles,
                preferred_element_type=jnp.float32,
            )
        )
    far_weights = softmax_weights[:, :, 3 * BLOCK :].reshape(blocks_dev, BLOCK, RAND, BLOCK)
    key_far_terms = (
        logit_scale
        * jnp.einsum("bjrx,bje->brxe", far_scores, query_tiles, preferred_element_type=jnp.float32)
    ).astype(jnp.bfloat16)
    value_far_terms = jnp.einsum(
        "bjrx,bje->brxe", far_weights, gradient_tiles, preferred_element_type=jnp.float32
    ).astype(jnp.bfloat16)
    return (query_gradient, key_window, value_window, key_far_terms, value_far_terms)


def exchanged_shards(queries, key_rows, value_rows, out_grad, random_device, random_block):
    seq_size = lax.axis_size("seq")
    own_index = lax.axis_index("seq")
    tokens, row_width = queries.shape
    blocks_dev = tokens // BLOCK
    heads_dev = row_width // DH
    capacity = max(2, 3 * blocks_dev // seq_size)
    selector, slot_index = routing(
        random_device, random_block, own_index, seq_size, blocks_dev, capacity
    )
    packed = jnp.concatenate([key_rows, value_rows], axis=1).reshape(
        blocks_dev, BLOCK, 2 * row_width
    )
    flattened = packed.reshape(blocks_dev, BLOCK * 2 * row_width)
    outgoing_blocks = jnp.dot(selector, flattened, preferred_element_type=jnp.float32).astype(
        jnp.bfloat16
    )
    outgoing_blocks = outgoing_blocks.reshape(seq_size * capacity, BLOCK, 2 * row_width)
    haloed = extended(packed, (("seq", 0),), 1)
    arrived = lax.all_to_all(outgoing_blocks, "seq", split_axis=0, concat_axis=0, tiled=True)
    far_blocks = far_context(arrived, slot_index, blocks_dev)
    usable = usable_mask(own_index, seq_size, blocks_dev)
    query_tiles = queries.reshape(blocks_dev, BLOCK, row_width)
    gradient_tiles = out_grad.reshape(blocks_dev, BLOCK, row_width)
    states = []
    for head_index in range(heads_dev):
        key_pieces, key_far = slot_pieces(haloed, far_blocks, blocks_dev, head_index * DH)
        value_pieces, value_far = slot_pieces(
            haloed, far_blocks, blocks_dev, row_width + head_index * DH
        )
        query_head = query_tiles[:, :, head_index * DH : (head_index + 1) * DH]
        states.append(
            forward_head(query_head, key_pieces, key_far, value_pieces, value_far, usable)
        )
    query_parts = []
    window_lists = [[], [], []]
    value_lists = [[], [], []]
    far_keys, far_values = ([], [])
    for head_index in range(heads_dev):
        key_pieces, key_far = slot_pieces(haloed, far_blocks, blocks_dev, head_index * DH)
        value_pieces, value_far = slot_pieces(
            haloed, far_blocks, blocks_dev, row_width + head_index * DH
        )
        query_head = query_tiles[:, :, head_index * DH : (head_index + 1) * DH]
        gradient_head = gradient_tiles[:, :, head_index * DH : (head_index + 1) * DH]
        query_gradient, key_window, value_window, key_far_terms, value_far_terms = backward_head(
            query_head,
            key_pieces,
            key_far,
            value_pieces,
            value_far,
            gradient_head,
            states[head_index],
        )
        query_parts.append(query_gradient)
        for slot in range(3):
            window_lists[slot].append(key_window[slot])
            value_lists[slot].append(value_window[slot])
        far_keys.append(key_far_terms)
        far_values.append(value_far_terms)
    slot_terms = [
        jnp.concatenate(window_lists[slot] + value_lists[slot], axis=-1) for slot in range(3)
    ]
    left_terms = slot_terms[0]
    right_terms = slot_terms[2]
    far_terms = jnp.concatenate(far_keys + far_values, axis=-1).reshape(
        blocks_dev * RAND, BLOCK, 2 * row_width
    )
    edge_terms = jnp.stack([left_terms[0], right_terms[-1]])
    edge_haloed = extended(edge_terms.astype(jnp.bfloat16), (("seq", 0),), 1).astype(
        edge_terms.dtype
    )
    summed = (
        slot_terms[1]
        + jnp.concatenate([left_terms[1:], edge_haloed[3:]], axis=0)
        + jnp.concatenate([edge_haloed[:1], right_terms[:-1]], axis=0)
    )
    returning = (
        jnp.zeros((seq_size * capacity, BLOCK, 2 * row_width), jnp.bfloat16)
        .at[slot_index]
        .set(far_terms)
    )
    returned = lax.all_to_all(returning, "seq", split_axis=0, concat_axis=0, tiled=True)
    gathered_terms = jnp.dot(
        selector.T,
        returned.reshape(seq_size * capacity, BLOCK * 2 * row_width),
        preferred_element_type=jnp.float32,
    )
    summed = summed + gathered_terms.reshape(blocks_dev, BLOCK, 2 * row_width)
    summed = summed.reshape(tokens, 2 * row_width)
    query_out = jnp.concatenate(query_parts, axis=-1).reshape(tokens, row_width)
    return (
        query_out,
        summed[:, :row_width].astype(jnp.bfloat16),
        summed[:, row_width:].astype(jnp.bfloat16),
    )


SLOTS = 3 + RAND


def block_kernel(ids_ref, write_ref, valid_ref, first_ref, q_ref, g_ref, *rest):
    kv_refs = rest[:SLOTS]
    own_ref, spread_ref, dq_ref, acc_ref = rest[SLOTS:]
    step = pl.program_id(0)
    steps = pl.num_programs(0)
    width = q_ref.shape[1]
    blocks_dev = own_ref.shape[0]
    logit_scale = 1.0 / math.sqrt(DH)

    @pl.when(step == 0)
    def _():
        acc_ref[...] = jnp.zeros(acc_ref.shape, jnp.float32)

    context = jnp.concatenate([ref[0] for ref in kv_refs], axis=0)
    slot_of = lax.broadcasted_iota(jnp.int32, (1, SLOTS * BLOCK), 1) // BLOCK
    usable = slot_of < 0
    for slot in range(SLOTS):
        usable = usable | ((slot_of == slot) & (valid_ref[step * SLOTS + slot] > 0))
    key_parts, value_parts = [], []
    for head in range(width // DH):
        cols = slice(head * DH, (head + 1) * DH)
        vcols = slice(width + head * DH, width + (head + 1) * DH)
        query = q_ref[:, cols]
        grad = g_ref[:, cols]
        keys = context[:, cols]
        values = context[:, vcols]
        logits = lax.dot_general(
            query, keys, (((1,), (1,)), ((), ())), preferred_element_type=jnp.float32
        ) * logit_scale
        logits = jnp.where(usable, logits, -jnp.inf)
        row_max = jnp.max(logits, axis=-1, keepdims=True)
        exponent = jnp.exp(logits - row_max)
        row_total = jnp.sum(exponent, axis=-1, keepdims=True)
        probability = exponent / row_total
        weights = probability.astype(jnp.bfloat16)
        attended = jnp.dot(weights, values, preferred_element_type=jnp.float32).astype(
            jnp.bfloat16
        )
        row_delta = jnp.sum(
            grad.astype(jnp.float32) * attended.astype(jnp.float32), axis=-1, keepdims=True
        )
        prob_grad = lax.dot_general(
            grad, values, (((1,), (1,)), ((), ())), preferred_element_type=jnp.float32
        )
        score_grad = (probability * (prob_grad - row_delta)).astype(jnp.bfloat16)
        query_grad = logit_scale * jnp.dot(score_grad, keys, preferred_element_type=jnp.float32)
        dq_ref[:, cols] = query_grad.astype(jnp.bfloat16)
        key_parts.append(
            logit_scale
            * lax.dot_general(
                score_grad, query, (((0,), (0,)), ((), ())), preferred_element_type=jnp.float32
            )
        )
        value_parts.append(
            lax.dot_general(
                weights, grad, (((0,), (0,)), ((), ())), preferred_element_type=jnp.float32
            )
        )
    terms = jnp.concatenate(key_parts + value_parts, axis=1)
    for slot in range(SLOTS):
        piece = terms[slot * BLOCK : (slot + 1) * BLOCK]
        if slot >= 3:
            piece = piece.astype(jnp.bfloat16).astype(jnp.float32)
        target = write_ref[step * SLOTS + slot]
        acc_ref[target] = acc_ref[target] + piece

    @pl.when(step == steps - 1)
    def _():
        first = first_ref[0]
        spread_ref[...] = acc_ref[...].astype(jnp.bfloat16)
        for block in range(blocks_dev):
            own_ref[block] = acc_ref[first + block]
            spread_ref[first + block] = jnp.zeros(spread_ref.shape[1:], jnp.bfloat16)


def block_attention(ids, write_ids, valid, first, queries, out_grad, source, chunk, width, total):
    tokens = queries.shape[0]
    blocks_dev = tokens // BLOCK

    def context_spec(slot):
        return pl.BlockSpec(
            (1, BLOCK, 2 * width), lambda i, ids, write_ids, valid, first: (ids[i * SLOTS + slot], 0, 0)
        )

    column_spec = pl.BlockSpec((BLOCK, width), lambda i, ids, write_ids, valid, first: (i, chunk))
    row_spec = pl.BlockSpec((BLOCK, width), lambda i, ids, write_ids, valid, first: (i, 0))
    grid_spec = pltpu.PrefetchScalarGridSpec(
        num_scalar_prefetch=4,
        grid=(blocks_dev,),
        in_specs=[column_spec, column_spec] + [context_spec(s) for s in range(SLOTS)],
        out_specs=[
            pl.BlockSpec(
                (blocks_dev, BLOCK, 2 * width), lambda i, ids, write_ids, valid, first: (0, 0, 0)
            ),
            pl.BlockSpec((total, BLOCK, 2 * width), lambda i, ids, write_ids, valid, first: (0, 0, 0)),
            row_spec,
        ],
        scratch_shapes=[pltpu.VMEM((total, BLOCK, 2 * width), jnp.float32)],
    )
    return pl.pallas_call(
        block_kernel,
        grid_spec=grid_spec,
        out_shape=[
            jax.ShapeDtypeStruct((blocks_dev, BLOCK, 2 * width), jnp.float32),
            jax.ShapeDtypeStruct((total, BLOCK, 2 * width), jnp.bfloat16),
            jax.ShapeDtypeStruct((tokens, width), jnp.bfloat16),
        ],
        compiler_params=pltpu.CompilerParams(vmem_limit_bytes=60 * 1024 * 1024),
    )(ids, write_ids, valid, first, queries, out_grad, *([source] * SLOTS))


def gathered_shards(queries, key_rows, value_rows, out_grad, random_device, random_block):
    seq_size = lax.axis_size("seq")
    own_index = lax.axis_index("seq")
    tokens, width = queries.shape
    blocks_dev = tokens // BLOCK
    total = seq_size * blocks_dev
    first = own_index * blocks_dev
    capacity = max(2, 3 * blocks_dev // seq_size)
    selector, slot_index = routing(
        random_device, random_block, own_index, seq_size, blocks_dev, capacity
    )
    block_ids = first + jnp.arange(blocks_dev, dtype=jnp.int32)
    local_ids = jnp.arange(blocks_dev, dtype=jnp.int32)
    own_device = lax.dynamic_slice_in_dim(random_device, first, blocks_dev, 0)
    own_block = lax.dynamic_slice_in_dim(random_block, first, blocks_dev, 0)
    chosen = (own_device * blocks_dev + own_block).astype(jnp.int32)
    window = jnp.stack(
        [jnp.clip(block_ids - 1, 0, total - 1), block_ids, jnp.clip(block_ids + 1, 0, total - 1)],
        axis=1,
    )
    write_ids = jnp.concatenate([window, chosen], axis=1).reshape(-1)
    read_window = jnp.stack([local_ids, local_ids + 1, local_ids + 2], axis=1)
    read_far = (slot_index + blocks_dev + 2).reshape(blocks_dev, RAND).astype(jnp.int32)
    read_ids = jnp.concatenate([read_window, read_far], axis=1).reshape(-1)
    always = jnp.ones_like(block_ids, dtype=jnp.bool_)
    valid = jnp.stack([block_ids > 0, always, block_ids < total - 1] + [always] * RAND, axis=1)
    valid = valid.astype(jnp.int32).reshape(-1)
    first_table = first.reshape(1).astype(jnp.int32)
    chunks = 2 if (width // DH) % 2 == 0 else 1
    part = width // chunks
    global_ids = write_ids
    results = []
    link = None
    for chunk in range(chunks):
        cols = slice(chunk * part, (chunk + 1) * part)
        packed = jnp.concatenate([key_rows[:, cols], value_rows[:, cols]], axis=1)
        if chunk == 0:
            source = lax.all_gather(packed, "seq", axis=0, tiled=True)
            source = source.reshape(total, BLOCK, 2 * part)
            table_ids = global_ids
            link = source[0, 0, :1]
        else:
            packed = packed.reshape(blocks_dev, BLOCK, 2 * part)
            route = selector
            outgoing = jnp.dot(
                route, packed.reshape(blocks_dev, BLOCK * 2 * part),
                preferred_element_type=jnp.float32,
            ).astype(jnp.bfloat16)
            outgoing = outgoing.reshape(seq_size * capacity, BLOCK, 2 * part)
            haloed = extended(packed, (("seq", 0),), 1)
            arrived = lax.all_to_all(outgoing, "seq", split_axis=0, concat_axis=0, tiled=True)
            source = jnp.concatenate([haloed, arrived], axis=0)
            table_ids = read_ids
        results.append((source, table_ids))
    query_parts, key_parts, value_parts = [], [], []
    after = results[-1][0][blocks_dev + 2 :] if chunks > 1 else None
    for chunk in range(chunks):
        source, table_ids = results[chunk]
        table = first_table
        if after is not None:
            table = table + (after[0, 0, :1] * 0.0).astype(jnp.int32)
        if chunk == 0:
            own_sum, spread, query_out = block_attention(
                table_ids, global_ids, valid, table, queries, out_grad, source, chunk, part, total,
            )
            returned = lax.psum_scatter(
                spread.reshape(total * BLOCK, 2 * part), "seq", scatter_dimension=0, tiled=True
            )
            summed = own_sum.reshape(tokens, 2 * part) + returned.astype(jnp.float32)
        else:
            slots = seq_size * capacity
            far_rows = slot_index.reshape(blocks_dev, RAND).astype(jnp.int32)
            near = window - first + 1 + slots
            far_write = jnp.concatenate([near, far_rows], axis=1).reshape(-1)
            own_sum, spread, query_out = block_attention(
                table_ids, far_write, valid, table - first + 1 + slots, queries, out_grad, source,
                chunk, part, slots + blocks_dev + 2,
            )
            returned = lax.all_to_all(
                spread[:slots], "seq", split_axis=0, concat_axis=0, tiled=True
            )
            spread = spread[slots:]
            gathered = jnp.dot(
                selector.T,
                returned.reshape(seq_size * capacity, BLOCK * 2 * part),
                preferred_element_type=jnp.float32,
            ).reshape(blocks_dev, BLOCK, 2 * part)
            left_edge = spread[0]
            right_edge = spread[blocks_dev + 1]
            from_right = lax.ppermute(left_edge, "seq", [(i, i - 1) for i in range(1, seq_size)])
            from_left = lax.ppermute(right_edge, "seq", [(i, i + 1) for i in range(seq_size - 1)])
            combined = (
                (own_sum + gathered)
                .at[0].add(from_left.astype(jnp.float32))
                .at[blocks_dev - 1].add(from_right.astype(jnp.float32))
            )
            summed = combined.reshape(tokens, 2 * part)
        after = own_sum
        query_parts.append(query_out)
        key_parts.append(summed[:, :part].astype(jnp.bfloat16))
        value_parts.append(summed[:, part:].astype(jnp.bfloat16))
    return (
        jnp.concatenate(query_parts, axis=1),
        jnp.concatenate(key_parts, axis=1),
        jnp.concatenate(value_parts, axis=1),
    )


def shards(queries, key_rows, value_rows, out_grad, random_device, random_block):
    if lax.axis_size("seq") <= 8:
        return gathered_shards(queries, key_rows, value_rows, out_grad, random_device, random_block)
    return exchanged_shards(queries, key_rows, value_rows, out_grad, random_device, random_block)


def solution(mesh):
    return jax.shard_map(
        shards,
        mesh=mesh,
        in_specs=(
            P(("groups", "seq"), ("heads", "pair")),
            P(("groups", "seq"), ("heads", "pair")),
            P(("groups", "seq"), ("heads", "pair")),
            P(("groups", "seq"), ("heads", "pair")),
            P("groups", None),
            P("groups", None),
        ),
        out_specs=(
            P(("groups", "seq"), ("heads", "pair")),
            P(("groups", "seq"), ("heads", "pair")),
            P(("groups", "seq"), ("heads", "pair")),
        ),
        check_vma=False,
    )
```

```python
import math

import jax
import jax.numpy as jnp
from jax import lax
from jax.experimental import pallas as pl
from jax.experimental.pallas import tpu as pltpu
from jax.sharding import PartitionSpec as P

DH = 128
BLOCK = 64
RAND = 2


def extended(block, sides, width):
    for axis, dim in sides:
        count = lax.axis_size(axis)
        forward = [(i, i + 1) for i in range(count - 1)]
        backward = [(target, source) for source, target in forward]
        low = lax.ppermute(
            lax.slice_in_dim(block, block.shape[dim] - width, None, axis=dim), axis, forward
        )
        high = lax.ppermute(lax.slice_in_dim(block, 0, width, axis=dim), axis, backward)
        block = jnp.concatenate([low, block, high], axis=dim)
    return block


def routing(random_device, random_block, own_index, seq_size, blocks_dev, capacity):
    entries = blocks_dev * RAND
    wanted_from = random_device.reshape(seq_size, entries)
    wanted_block = random_block.reshape(seq_size, entries)
    from_me = (wanted_from == own_index).astype(jnp.int32)
    rank_out = jnp.cumsum(from_me, axis=1) - from_me
    slot_hits = from_me[:, None, :] * (
        rank_out[:, None, :] == jnp.arange(capacity, dtype=jnp.int32)[None, :, None]
    ).astype(jnp.int32)
    block_hits = (
        wanted_block[:, :, None] == jnp.arange(blocks_dev, dtype=jnp.int32)[None, None, :]
    ).astype(jnp.float32)
    selector = jnp.einsum("sce,sej->scj", slot_hits.astype(jnp.float32), block_hits)
    selector = selector.reshape(seq_size * capacity, blocks_dev).astype(jnp.bfloat16)
    own_sources = lax.dynamic_slice_in_dim(
        random_device, own_index * blocks_dev, blocks_dev, 0
    ).reshape(entries)
    peer_hits = (own_sources[:, None] == jnp.arange(seq_size, dtype=jnp.int32)[None, :]).astype(
        jnp.int32
    )
    earlier = jnp.cumsum(peer_hits, axis=0) - peer_hits
    rank_in = jnp.sum(earlier * peer_hits, axis=1)
    slot_index = own_sources * capacity + rank_in
    return (selector, slot_index)


def far_context(arrived, slot_index, blocks_dev):
    picked = jnp.take(arrived, slot_index, axis=0)
    return picked.reshape(blocks_dev, RAND, arrived.shape[1], arrived.shape[2])


def usable_mask(own_index, seq_size, blocks_dev):
    block_ids = jnp.arange(blocks_dev, dtype=jnp.int32)[:, None]
    slot_ids = jnp.arange(3 + RAND, dtype=jnp.int32)[None, :]
    global_block = own_index * blocks_dev + block_ids
    missing = (slot_ids == 0) & (global_block == 0) | (slot_ids == 2) & (
        global_block == seq_size * blocks_dev - 1
    )
    return jnp.repeat(jnp.logical_not(missing), BLOCK, axis=1)


def slot_pieces(haloed, far_blocks, blocks_dev, start_col):
    pieces = []
    for slot in range(3):
        pieces.append(haloed[slot : slot + blocks_dev, :, start_col : start_col + DH])
    far_part = far_blocks[:, :, :, start_col : start_col + DH]
    return (pieces, far_part)


def forward_head(query_tiles, key_pieces, key_far, value_pieces, value_far, usable):
    blocks_dev = query_tiles.shape[0]
    logit_parts = [
        jnp.einsum("bje,bxe->bjx", query_tiles, piece, preferred_element_type=jnp.float32)
        for piece in key_pieces
    ]
    far_logits = jnp.einsum(
        "bje,brxe->bjrx", query_tiles, key_far, preferred_element_type=jnp.float32
    )
    logit_parts.append(far_logits.reshape(blocks_dev, BLOCK, RAND * BLOCK))
    attention_logits = jnp.concatenate(logit_parts, axis=-1) * (1.0 / math.sqrt(DH))
    attention_logits = jnp.where(usable[:, None, :], attention_logits, -jnp.inf)
    row_max = jnp.max(attention_logits, axis=-1, keepdims=True)
    exponent = jnp.exp(attention_logits - row_max)
    row_total = jnp.sum(exponent, axis=-1, keepdims=True)
    probability = exponent / row_total
    softmax_weights = probability.astype(jnp.bfloat16)
    attended = jnp.einsum(
        "bjx,bxe->bje",
        softmax_weights[:, :, :BLOCK],
        value_pieces[0],
        preferred_element_type=jnp.float32,
    )
    for slot in range(1, 3):
        attended = attended + jnp.einsum(
            "bjx,bxe->bje",
            softmax_weights[:, :, slot * BLOCK : (slot + 1) * BLOCK],
            value_pieces[slot],
            preferred_element_type=jnp.float32,
        )
    far_weights = softmax_weights[:, :, 3 * BLOCK :].reshape(blocks_dev, BLOCK, RAND, BLOCK)
    attended = attended + jnp.einsum(
        "bjrx,brxe->bje", far_weights, value_far, preferred_element_type=jnp.float32
    )
    return (probability, attended.astype(jnp.bfloat16))


def backward_head(
    query_tiles, key_pieces, key_far, value_pieces, value_far, gradient_tiles, forward_state
):
    probability, attended_output = forward_state
    blocks_dev = query_tiles.shape[0]
    logit_scale = 1.0 / math.sqrt(DH)
    softmax_weights = probability.astype(jnp.bfloat16)
    row_delta = jnp.sum(
        gradient_tiles.astype(jnp.float32) * attended_output.astype(jnp.float32),
        axis=-1,
        keepdims=True,
    )
    grad_parts = [
        jnp.einsum("bje,bxe->bjx", gradient_tiles, piece, preferred_element_type=jnp.float32)
        for piece in value_pieces
    ]
    far_grad = jnp.einsum(
        "bje,brxe->bjrx", gradient_tiles, value_far, preferred_element_type=jnp.float32
    )
    grad_parts.append(far_grad.reshape(blocks_dev, BLOCK, RAND * BLOCK))
    probability_gradient = jnp.concatenate(grad_parts, axis=-1)
    score_gradient = (probability * (probability_gradient - row_delta)).astype(jnp.bfloat16)
    query_sum = jnp.einsum(
        "bjx,bxe->bje",
        score_gradient[:, :, :BLOCK],
        key_pieces[0],
        preferred_element_type=jnp.float32,
    )
    for slot in range(1, 3):
        query_sum = query_sum + jnp.einsum(
            "bjx,bxe->bje",
            score_gradient[:, :, slot * BLOCK : (slot + 1) * BLOCK],
            key_pieces[slot],
            preferred_element_type=jnp.float32,
        )
    far_scores = score_gradient[:, :, 3 * BLOCK :].reshape(blocks_dev, BLOCK, RAND, BLOCK)
    query_sum = query_sum + jnp.einsum(
        "bjrx,brxe->bje", far_scores, key_far, preferred_element_type=jnp.float32
    )
    query_gradient = (logit_scale * query_sum).astype(jnp.bfloat16)
    key_window, value_window = ([], [])
    for slot in range(3):
        columns = slice(slot * BLOCK, (slot + 1) * BLOCK)
        key_window.append(
            logit_scale
            * jnp.einsum(
                "bjx,bje->bxe",
                score_gradient[:, :, columns],
                query_tiles,
                preferred_element_type=jnp.float32,
            )
        )
        value_window.append(
            jnp.einsum(
                "bjx,bje->bxe",
                softmax_weights[:, :, columns],
                gradient_tiles,
                preferred_element_type=jnp.float32,
            )
        )
    far_weights = softmax_weights[:, :, 3 * BLOCK :].reshape(blocks_dev, BLOCK, RAND, BLOCK)
    key_far_terms = (
        logit_scale
        * jnp.einsum("bjrx,bje->brxe", far_scores, query_tiles, preferred_element_type=jnp.float32)
    ).astype(jnp.bfloat16)
    value_far_terms = jnp.einsum(
        "bjrx,bje->brxe", far_weights, gradient_tiles, preferred_element_type=jnp.float32
    ).astype(jnp.bfloat16)
    return (query_gradient, key_window, value_window, key_far_terms, value_far_terms)


def exchanged_shards(queries, key_rows, value_rows, out_grad, random_device, random_block):
    seq_size = lax.axis_size("seq")
    own_index = lax.axis_index("seq")
    tokens, row_width = queries.shape
    blocks_dev = tokens // BLOCK
    heads_dev = row_width // DH
    capacity = max(2, 3 * blocks_dev // seq_size)
    selector, slot_index = routing(
        random_device, random_block, own_index, seq_size, blocks_dev, capacity
    )
    packed = jnp.concatenate([key_rows, value_rows], axis=1).reshape(
        blocks_dev, BLOCK, 2 * row_width
    )
    flattened = packed.reshape(blocks_dev, BLOCK * 2 * row_width)
    outgoing_blocks = jnp.dot(selector, flattened, preferred_element_type=jnp.float32).astype(
        jnp.bfloat16
    )
    outgoing_blocks = outgoing_blocks.reshape(seq_size * capacity, BLOCK, 2 * row_width)
    haloed = extended(packed, (("seq", 0),), 1)
    arrived = lax.all_to_all(outgoing_blocks, "seq", split_axis=0, concat_axis=0, tiled=True)
    far_blocks = far_context(arrived, slot_index, blocks_dev)
    usable = usable_mask(own_index, seq_size, blocks_dev)
    query_tiles = queries.reshape(blocks_dev, BLOCK, row_width)
    gradient_tiles = out_grad.reshape(blocks_dev, BLOCK, row_width)
    states = []
    for head_index in range(heads_dev):
        key_pieces, key_far = slot_pieces(haloed, far_blocks, blocks_dev, head_index * DH)
        value_pieces, value_far = slot_pieces(
            haloed, far_blocks, blocks_dev, row_width + head_index * DH
        )
        query_head = query_tiles[:, :, head_index * DH : (head_index + 1) * DH]
        states.append(
            forward_head(query_head, key_pieces, key_far, value_pieces, value_far, usable)
        )
    query_parts = []
    window_lists = [[], [], []]
    value_lists = [[], [], []]
    far_keys, far_values = ([], [])
    for head_index in range(heads_dev):
        key_pieces, key_far = slot_pieces(haloed, far_blocks, blocks_dev, head_index * DH)
        value_pieces, value_far = slot_pieces(
            haloed, far_blocks, blocks_dev, row_width + head_index * DH
        )
        query_head = query_tiles[:, :, head_index * DH : (head_index + 1) * DH]
        gradient_head = gradient_tiles[:, :, head_index * DH : (head_index + 1) * DH]
        query_gradient, key_window, value_window, key_far_terms, value_far_terms = backward_head(
            query_head,
            key_pieces,
            key_far,
            value_pieces,
            value_far,
            gradient_head,
            states[head_index],
        )
        query_parts.append(query_gradient)
        for slot in range(3):
            window_lists[slot].append(key_window[slot])
            value_lists[slot].append(value_window[slot])
        far_keys.append(key_far_terms)
        far_values.append(value_far_terms)
    slot_terms = [
        jnp.concatenate(window_lists[slot] + value_lists[slot], axis=-1) for slot in range(3)
    ]
    left_terms = slot_terms[0]
    right_terms = slot_terms[2]
    far_terms = jnp.concatenate(far_keys + far_values, axis=-1).reshape(
        blocks_dev * RAND, BLOCK, 2 * row_width
    )
    edge_terms = jnp.stack([left_terms[0], right_terms[-1]])
    edge_haloed = extended(edge_terms.astype(jnp.bfloat16), (("seq", 0),), 1).astype(
        edge_terms.dtype
    )
    summed = (
        slot_terms[1]
        + jnp.concatenate([left_terms[1:], edge_haloed[3:]], axis=0)
        + jnp.concatenate([edge_haloed[:1], right_terms[:-1]], axis=0)
    )
    returning = (
        jnp.zeros((seq_size * capacity, BLOCK, 2 * row_width), jnp.bfloat16)
        .at[slot_index]
        .set(far_terms)
    )
    returned = lax.all_to_all(returning, "seq", split_axis=0, concat_axis=0, tiled=True)
    gathered_terms = jnp.dot(
        selector.T,
        returned.reshape(seq_size * capacity, BLOCK * 2 * row_width),
        preferred_element_type=jnp.float32,
    )
    summed = summed + gathered_terms.reshape(blocks_dev, BLOCK, 2 * row_width)
    summed = summed.reshape(tokens, 2 * row_width)
    query_out = jnp.concatenate(query_parts, axis=-1).reshape(tokens, row_width)
    return (
        query_out,
        summed[:, :row_width].astype(jnp.bfloat16),
        summed[:, row_width:].astype(jnp.bfloat16),
    )


SLOTS = 3 + RAND


def block_kernel(ids_ref, write_ref, valid_ref, first_ref, q_ref, g_ref, *rest):
    kv_refs = rest[:SLOTS]
    own_ref, spread_ref, dq_ref, acc_ref = rest[SLOTS:]
    step = pl.program_id(0)
    steps = pl.num_programs(0)
    width = q_ref.shape[1]
    blocks_dev = own_ref.shape[0]
    logit_scale = 1.0 / math.sqrt(DH)

    @pl.when(step == 0)
    def _():
        acc_ref[...] = jnp.zeros(acc_ref.shape, jnp.float32)

    context = jnp.concatenate([ref[0] for ref in kv_refs], axis=0)
    slot_of = lax.broadcasted_iota(jnp.int32, (1, SLOTS * BLOCK), 1) // BLOCK
    usable = slot_of < 0
    for slot in range(SLOTS):
        usable = usable | ((slot_of == slot) & (valid_ref[step * SLOTS + slot] > 0))
    key_parts, value_parts = [], []
    for head in range(width // DH):
        cols = slice(head * DH, (head + 1) * DH)
        vcols = slice(width + head * DH, width + (head + 1) * DH)
        query = q_ref[:, cols]
        grad = g_ref[:, cols]
        keys = context[:, cols]
        values = context[:, vcols]
        logits = lax.dot_general(
            query, keys, (((1,), (1,)), ((), ())), preferred_element_type=jnp.float32
        ) * logit_scale
        logits = jnp.where(usable, logits, -jnp.inf)
        row_max = jnp.max(logits, axis=-1, keepdims=True)
        exponent = jnp.exp(logits - row_max)
        row_total = jnp.sum(exponent, axis=-1, keepdims=True)
        probability = exponent / row_total
        weights = probability.astype(jnp.bfloat16)
        attended = jnp.dot(weights, values, preferred_element_type=jnp.float32).astype(
            jnp.bfloat16
        )
        row_delta = jnp.sum(
            grad.astype(jnp.float32) * attended.astype(jnp.float32), axis=-1, keepdims=True
        )
        prob_grad = lax.dot_general(
            grad, values, (((1,), (1,)), ((), ())), preferred_element_type=jnp.float32
        )
        score_grad = (probability * (prob_grad - row_delta)).astype(jnp.bfloat16)
        query_grad = logit_scale * jnp.dot(score_grad, keys, preferred_element_type=jnp.float32)
        dq_ref[:, cols] = query_grad.astype(jnp.bfloat16)
        key_parts.append(
            logit_scale
            * lax.dot_general(
                score_grad, query, (((0,), (0,)), ((), ())), preferred_element_type=jnp.float32
            )
        )
        value_parts.append(
            lax.dot_general(
                weights, grad, (((0,), (0,)), ((), ())), preferred_element_type=jnp.float32
            )
        )
    for slot in range(SLOTS):
        target = write_ref[step * SLOTS + slot]
        rows = slice(slot * BLOCK, (slot + 1) * BLOCK)
        for head in range(width // DH):
            for parts, base in ((key_parts, 0), (value_parts, width)):
                piece = parts[head][rows]
                if slot >= 3:
                    piece = piece.astype(jnp.bfloat16).astype(jnp.float32)
                cols = pl.ds(base + head * DH, DH)
                acc_ref[target, :, cols] = acc_ref[target, :, cols] + piece

    @pl.when(step == steps - 1)
    def _():
        first = first_ref[0]
        spread_ref[...] = acc_ref[...].astype(jnp.bfloat16)
        for block in range(blocks_dev):
            own_ref[block] = acc_ref[first + block]
            spread_ref[first + block] = jnp.zeros(spread_ref.shape[1:], jnp.bfloat16)


def block_attention(ids, write_ids, valid, first, queries, out_grad, source, chunk, width, total):
    tokens = queries.shape[0]
    blocks_dev = tokens // BLOCK

    def context_spec(slot):
        return pl.BlockSpec(
            (1, BLOCK, 2 * width), lambda i, ids, write_ids, valid, first: (ids[i * SLOTS + slot], 0, 0)
        )

    column_spec = pl.BlockSpec((BLOCK, width), lambda i, ids, write_ids, valid, first: (i, chunk))
    row_spec = pl.BlockSpec((BLOCK, width), lambda i, ids, write_ids, valid, first: (i, 0))
    grid_spec = pltpu.PrefetchScalarGridSpec(
        num_scalar_prefetch=4,
        grid=(blocks_dev,),
        in_specs=[column_spec, column_spec] + [context_spec(s) for s in range(SLOTS)],
        out_specs=[
            pl.BlockSpec(
                (blocks_dev, BLOCK, 2 * width), lambda i, ids, write_ids, valid, first: (0, 0, 0)
            ),
            pl.BlockSpec((total, BLOCK, 2 * width), lambda i, ids, write_ids, valid, first: (0, 0, 0)),
            row_spec,
        ],
        scratch_shapes=[pltpu.VMEM((total, BLOCK, 2 * width), jnp.float32)],
    )
    return pl.pallas_call(
        block_kernel,
        grid_spec=grid_spec,
        out_shape=[
            jax.ShapeDtypeStruct((blocks_dev, BLOCK, 2 * width), jnp.float32),
            jax.ShapeDtypeStruct((total, BLOCK, 2 * width), jnp.bfloat16),
            jax.ShapeDtypeStruct((tokens, width), jnp.bfloat16),
        ],
        compiler_params=pltpu.CompilerParams(vmem_limit_bytes=60 * 1024 * 1024),
    )(ids, write_ids, valid, first, queries, out_grad, *([source] * SLOTS))


def gathered_shards(queries, key_rows, value_rows, out_grad, random_device, random_block):
    seq_size = lax.axis_size("seq")
    own_index = lax.axis_index("seq")
    tokens, width = queries.shape
    blocks_dev = tokens // BLOCK
    total = seq_size * blocks_dev
    first = own_index * blocks_dev
    capacity = max(2, 3 * blocks_dev // seq_size)
    selector, slot_index = routing(
        random_device, random_block, own_index, seq_size, blocks_dev, capacity
    )
    block_ids = first + jnp.arange(blocks_dev, dtype=jnp.int32)
    local_ids = jnp.arange(blocks_dev, dtype=jnp.int32)
    own_device = lax.dynamic_slice_in_dim(random_device, first, blocks_dev, 0)
    own_block = lax.dynamic_slice_in_dim(random_block, first, blocks_dev, 0)
    chosen = (own_device * blocks_dev + own_block).astype(jnp.int32)
    window = jnp.stack(
        [jnp.clip(block_ids - 1, 0, total - 1), block_ids, jnp.clip(block_ids + 1, 0, total - 1)],
        axis=1,
    )
    write_ids = jnp.concatenate([window, chosen], axis=1).reshape(-1)
    read_window = jnp.stack([local_ids, local_ids + 1, local_ids + 2], axis=1)
    read_far = (slot_index + blocks_dev + 2).reshape(blocks_dev, RAND).astype(jnp.int32)
    read_ids = jnp.concatenate([read_window, read_far], axis=1).reshape(-1)
    always = jnp.ones_like(block_ids, dtype=jnp.bool_)
    valid = jnp.stack([block_ids > 0, always, block_ids < total - 1] + [always] * RAND, axis=1)
    valid = valid.astype(jnp.int32).reshape(-1)
    first_table = first.reshape(1).astype(jnp.int32)
    chunks = 2 if (width // DH) % 2 == 0 else 1
    part = width // chunks
    global_ids = write_ids
    results = []
    link = None
    for chunk in range(chunks):
        cols = slice(chunk * part, (chunk + 1) * part)
        packed = jnp.concatenate([key_rows[:, cols], value_rows[:, cols]], axis=1)
        if chunk == 0:
            source = lax.all_gather(packed, "seq", axis=0, tiled=True)
            source = source.reshape(total, BLOCK, 2 * part)
            table_ids = global_ids
            link = source[0, 0, :1]
        else:
            packed = packed.reshape(blocks_dev, BLOCK, 2 * part)
            route = selector
            outgoing = jnp.dot(
                route, packed.reshape(blocks_dev, BLOCK * 2 * part),
                preferred_element_type=jnp.float32,
            ).astype(jnp.bfloat16)
            outgoing = outgoing.reshape(seq_size * capacity, BLOCK, 2 * part)
            haloed = extended(packed, (("seq", 0),), 1)
            arrived = lax.all_to_all(outgoing, "seq", split_axis=0, concat_axis=0, tiled=True)
            source = jnp.concatenate([haloed, arrived], axis=0)
            table_ids = read_ids
        results.append((source, table_ids))
    query_parts, key_parts, value_parts = [], [], []
    after = results[-1][0][blocks_dev + 2 :] if chunks > 1 else None
    for chunk in range(chunks):
        source, table_ids = results[chunk]
        table = first_table
        if after is not None:
            table = table + (after[0, 0, :1] * 0.0).astype(jnp.int32)
        if chunk == 0:
            own_sum, spread, query_out = block_attention(
                table_ids, global_ids, valid, table, queries, out_grad, source, chunk, part, total,
            )
            returned = lax.psum_scatter(
                spread.reshape(total * BLOCK, 2 * part), "seq", scatter_dimension=0, tiled=True
            )
            summed = own_sum.reshape(tokens, 2 * part) + returned.astype(jnp.float32)
        else:
            slots = seq_size * capacity
            far_rows = slot_index.reshape(blocks_dev, RAND).astype(jnp.int32)
            near = window - first + 1 + slots
            far_write = jnp.concatenate([near, far_rows], axis=1).reshape(-1)
            own_sum, spread, query_out = block_attention(
                table_ids, far_write, valid, table - first + 1 + slots, queries, out_grad, source,
                chunk, part, slots + blocks_dev + 2,
            )
            returned = lax.all_to_all(
                spread[:slots], "seq", split_axis=0, concat_axis=0, tiled=True
            )
            spread = spread[slots:]
            gathered = jnp.dot(
                selector.T,
                returned.reshape(seq_size * capacity, BLOCK * 2 * part),
                preferred_element_type=jnp.float32,
            ).reshape(blocks_dev, BLOCK, 2 * part)
            left_edge = spread[0]
            right_edge = spread[blocks_dev + 1]
            from_right = lax.ppermute(left_edge, "seq", [(i, i - 1) for i in range(1, seq_size)])
            from_left = lax.ppermute(right_edge, "seq", [(i, i + 1) for i in range(seq_size - 1)])
            combined = (
                (own_sum + gathered)
                .at[0].add(from_left.astype(jnp.float32))
                .at[blocks_dev - 1].add(from_right.astype(jnp.float32))
            )
            summed = combined.reshape(tokens, 2 * part)
        after = own_sum
        query_parts.append(query_out)
        key_parts.append(summed[:, :part].astype(jnp.bfloat16))
        value_parts.append(summed[:, part:].astype(jnp.bfloat16))
    return (
        jnp.concatenate(query_parts, axis=1),
        jnp.concatenate(key_parts, axis=1),
        jnp.concatenate(value_parts, axis=1),
    )


def shards(queries, key_rows, value_rows, out_grad, random_device, random_block):
    if lax.axis_size("seq") <= 8:
        return gathered_shards(queries, key_rows, value_rows, out_grad, random_device, random_block)
    return exchanged_shards(queries, key_rows, value_rows, out_grad, random_device, random_block)


def solution(mesh):
    return jax.shard_map(
        shards,
        mesh=mesh,
        in_specs=(
            P(("groups", "seq"), ("heads", "pair")),
            P(("groups", "seq"), ("heads", "pair")),
            P(("groups", "seq"), ("heads", "pair")),
            P(("groups", "seq"), ("heads", "pair")),
            P("groups", None),
            P("groups", None),
        ),
        out_specs=(
            P(("groups", "seq"), ("heads", "pair")),
            P(("groups", "seq"), ("heads", "pair")),
            P(("groups", "seq"), ("heads", "pair")),
        ),
        check_vma=False,
    )
```

```python
import math

import jax
import jax.numpy as jnp
from jax import lax
from jax.experimental import pallas as pl
from jax.experimental.pallas import tpu as pltpu
from jax.sharding import PartitionSpec as P

DH = 128
BLOCK = 64
RAND = 2


def extended(block, sides, width):
    for axis, dim in sides:
        count = lax.axis_size(axis)
        forward = [(i, i + 1) for i in range(count - 1)]
        backward = [(target, source) for source, target in forward]
        low = lax.ppermute(
            lax.slice_in_dim(block, block.shape[dim] - width, None, axis=dim), axis, forward
        )
        high = lax.ppermute(lax.slice_in_dim(block, 0, width, axis=dim), axis, backward)
        block = jnp.concatenate([low, block, high], axis=dim)
    return block


def routing(random_device, random_block, own_index, seq_size, blocks_dev, capacity):
    entries = blocks_dev * RAND
    wanted_from = random_device.reshape(seq_size, entries)
    wanted_block = random_block.reshape(seq_size, entries)
    from_me = (wanted_from == own_index).astype(jnp.int32)
    rank_out = jnp.cumsum(from_me, axis=1) - from_me
    slot_hits = from_me[:, None, :] * (
        rank_out[:, None, :] == jnp.arange(capacity, dtype=jnp.int32)[None, :, None]
    ).astype(jnp.int32)
    block_hits = (
        wanted_block[:, :, None] == jnp.arange(blocks_dev, dtype=jnp.int32)[None, None, :]
    ).astype(jnp.float32)
    selector = jnp.einsum("sce,sej->scj", slot_hits.astype(jnp.float32), block_hits)
    selector = selector.reshape(seq_size * capacity, blocks_dev).astype(jnp.bfloat16)
    own_sources = lax.dynamic_slice_in_dim(
        random_device, own_index * blocks_dev, blocks_dev, 0
    ).reshape(entries)
    peer_hits = (own_sources[:, None] == jnp.arange(seq_size, dtype=jnp.int32)[None, :]).astype(
        jnp.int32
    )
    earlier = jnp.cumsum(peer_hits, axis=0) - peer_hits
    rank_in = jnp.sum(earlier * peer_hits, axis=1)
    slot_index = own_sources * capacity + rank_in
    return (selector, slot_index)


def far_context(arrived, slot_index, blocks_dev):
    picked = jnp.take(arrived, slot_index, axis=0)
    return picked.reshape(blocks_dev, RAND, arrived.shape[1], arrived.shape[2])


def usable_mask(own_index, seq_size, blocks_dev):
    block_ids = jnp.arange(blocks_dev, dtype=jnp.int32)[:, None]
    slot_ids = jnp.arange(3 + RAND, dtype=jnp.int32)[None, :]
    global_block = own_index * blocks_dev + block_ids
    missing = (slot_ids == 0) & (global_block == 0) | (slot_ids == 2) & (
        global_block == seq_size * blocks_dev - 1
    )
    return jnp.repeat(jnp.logical_not(missing), BLOCK, axis=1)


def slot_pieces(haloed, far_blocks, blocks_dev, start_col):
    pieces = []
    for slot in range(3):
        pieces.append(haloed[slot : slot + blocks_dev, :, start_col : start_col + DH])
    far_part = far_blocks[:, :, :, start_col : start_col + DH]
    return (pieces, far_part)


def forward_head(query_tiles, key_pieces, key_far, value_pieces, value_far, usable):
    blocks_dev = query_tiles.shape[0]
    logit_parts = [
        jnp.einsum("bje,bxe->bjx", query_tiles, piece, preferred_element_type=jnp.float32)
        for piece in key_pieces
    ]
    far_logits = jnp.einsum(
        "bje,brxe->bjrx", query_tiles, key_far, preferred_element_type=jnp.float32
    )
    logit_parts.append(far_logits.reshape(blocks_dev, BLOCK, RAND * BLOCK))
    attention_logits = jnp.concatenate(logit_parts, axis=-1) * (1.0 / math.sqrt(DH))
    attention_logits = jnp.where(usable[:, None, :], attention_logits, -jnp.inf)
    row_max = jnp.max(attention_logits, axis=-1, keepdims=True)
    exponent = jnp.exp(attention_logits - row_max)
    row_total = jnp.sum(exponent, axis=-1, keepdims=True)
    probability = exponent / row_total
    softmax_weights = probability.astype(jnp.bfloat16)
    attended = jnp.einsum(
        "bjx,bxe->bje",
        softmax_weights[:, :, :BLOCK],
        value_pieces[0],
        preferred_element_type=jnp.float32,
    )
    for slot in range(1, 3):
        attended = attended + jnp.einsum(
            "bjx,bxe->bje",
            softmax_weights[:, :, slot * BLOCK : (slot + 1) * BLOCK],
            value_pieces[slot],
            preferred_element_type=jnp.float32,
        )
    far_weights = softmax_weights[:, :, 3 * BLOCK :].reshape(blocks_dev, BLOCK, RAND, BLOCK)
    attended = attended + jnp.einsum(
        "bjrx,brxe->bje", far_weights, value_far, preferred_element_type=jnp.float32
    )
    return (probability, attended.astype(jnp.bfloat16))


def backward_head(
    query_tiles, key_pieces, key_far, value_pieces, value_far, gradient_tiles, forward_state
):
    probability, attended_output = forward_state
    blocks_dev = query_tiles.shape[0]
    logit_scale = 1.0 / math.sqrt(DH)
    softmax_weights = probability.astype(jnp.bfloat16)
    row_delta = jnp.sum(
        gradient_tiles.astype(jnp.float32) * attended_output.astype(jnp.float32),
        axis=-1,
        keepdims=True,
    )
    grad_parts = [
        jnp.einsum("bje,bxe->bjx", gradient_tiles, piece, preferred_element_type=jnp.float32)
        for piece in value_pieces
    ]
    far_grad = jnp.einsum(
        "bje,brxe->bjrx", gradient_tiles, value_far, preferred_element_type=jnp.float32
    )
    grad_parts.append(far_grad.reshape(blocks_dev, BLOCK, RAND * BLOCK))
    probability_gradient = jnp.concatenate(grad_parts, axis=-1)
    score_gradient = (probability * (probability_gradient - row_delta)).astype(jnp.bfloat16)
    query_sum = jnp.einsum(
        "bjx,bxe->bje",
        score_gradient[:, :, :BLOCK],
        key_pieces[0],
        preferred_element_type=jnp.float32,
    )
    for slot in range(1, 3):
        query_sum = query_sum + jnp.einsum(
            "bjx,bxe->bje",
            score_gradient[:, :, slot * BLOCK : (slot + 1) * BLOCK],
            key_pieces[slot],
            preferred_element_type=jnp.float32,
        )
    far_scores = score_gradient[:, :, 3 * BLOCK :].reshape(blocks_dev, BLOCK, RAND, BLOCK)
    query_sum = query_sum + jnp.einsum(
        "bjrx,brxe->bje", far_scores, key_far, preferred_element_type=jnp.float32
    )
    query_gradient = (logit_scale * query_sum).astype(jnp.bfloat16)
    key_window, value_window = ([], [])
    for slot in range(3):
        columns = slice(slot * BLOCK, (slot + 1) * BLOCK)
        key_window.append(
            logit_scale
            * jnp.einsum(
                "bjx,bje->bxe",
                score_gradient[:, :, columns],
                query_tiles,
                preferred_element_type=jnp.float32,
            )
        )
        value_window.append(
            jnp.einsum(
                "bjx,bje->bxe",
                softmax_weights[:, :, columns],
                gradient_tiles,
                preferred_element_type=jnp.float32,
            )
        )
    far_weights = softmax_weights[:, :, 3 * BLOCK :].reshape(blocks_dev, BLOCK, RAND, BLOCK)
    key_far_terms = (
        logit_scale
        * jnp.einsum("bjrx,bje->brxe", far_scores, query_tiles, preferred_element_type=jnp.float32)
    ).astype(jnp.bfloat16)
    value_far_terms = jnp.einsum(
        "bjrx,bje->brxe", far_weights, gradient_tiles, preferred_element_type=jnp.float32
    ).astype(jnp.bfloat16)
    return (query_gradient, key_window, value_window, key_far_terms, value_far_terms)


def exchanged_shards(queries, key_rows, value_rows, out_grad, random_device, random_block):
    seq_size = lax.axis_size("seq")
    own_index = lax.axis_index("seq")
    tokens, row_width = queries.shape
    blocks_dev = tokens // BLOCK
    heads_dev = row_width // DH
    capacity = max(2, 3 * blocks_dev // seq_size)
    selector, slot_index = routing(
        random_device, random_block, own_index, seq_size, blocks_dev, capacity
    )
    packed = jnp.concatenate([key_rows, value_rows], axis=1).reshape(
        blocks_dev, BLOCK, 2 * row_width
    )
    flattened = packed.reshape(blocks_dev, BLOCK * 2 * row_width)
    outgoing_blocks = jnp.dot(selector, flattened, preferred_element_type=jnp.float32).astype(
        jnp.bfloat16
    )
    outgoing_blocks = outgoing_blocks.reshape(seq_size * capacity, BLOCK, 2 * row_width)
    haloed = extended(packed, (("seq", 0),), 1)
    arrived = lax.all_to_all(outgoing_blocks, "seq", split_axis=0, concat_axis=0, tiled=True)
    far_blocks = far_context(arrived, slot_index, blocks_dev)
    usable = usable_mask(own_index, seq_size, blocks_dev)
    query_tiles = queries.reshape(blocks_dev, BLOCK, row_width)
    gradient_tiles = out_grad.reshape(blocks_dev, BLOCK, row_width)
    states = []
    for head_index in range(heads_dev):
        key_pieces, key_far = slot_pieces(haloed, far_blocks, blocks_dev, head_index * DH)
        value_pieces, value_far = slot_pieces(
            haloed, far_blocks, blocks_dev, row_width + head_index * DH
        )
        query_head = query_tiles[:, :, head_index * DH : (head_index + 1) * DH]
        states.append(
            forward_head(query_head, key_pieces, key_far, value_pieces, value_far, usable)
        )
    query_parts = []
    window_lists = [[], [], []]
    value_lists = [[], [], []]
    far_keys, far_values = ([], [])
    for head_index in range(heads_dev):
        key_pieces, key_far = slot_pieces(haloed, far_blocks, blocks_dev, head_index * DH)
        value_pieces, value_far = slot_pieces(
            haloed, far_blocks, blocks_dev, row_width + head_index * DH
        )
        query_head = query_tiles[:, :, head_index * DH : (head_index + 1) * DH]
        gradient_head = gradient_tiles[:, :, head_index * DH : (head_index + 1) * DH]
        query_gradient, key_window, value_window, key_far_terms, value_far_terms = backward_head(
            query_head,
            key_pieces,
            key_far,
            value_pieces,
            value_far,
            gradient_head,
            states[head_index],
        )
        query_parts.append(query_gradient)
        for slot in range(3):
            window_lists[slot].append(key_window[slot])
            value_lists[slot].append(value_window[slot])
        far_keys.append(key_far_terms)
        far_values.append(value_far_terms)
    slot_terms = [
        jnp.concatenate(window_lists[slot] + value_lists[slot], axis=-1) for slot in range(3)
    ]
    left_terms = slot_terms[0]
    right_terms = slot_terms[2]
    far_terms = jnp.concatenate(far_keys + far_values, axis=-1).reshape(
        blocks_dev * RAND, BLOCK, 2 * row_width
    )
    edge_terms = jnp.stack([left_terms[0], right_terms[-1]])
    edge_haloed = extended(edge_terms.astype(jnp.bfloat16), (("seq", 0),), 1).astype(
        edge_terms.dtype
    )
    summed = (
        slot_terms[1]
        + jnp.concatenate([left_terms[1:], edge_haloed[3:]], axis=0)
        + jnp.concatenate([edge_haloed[:1], right_terms[:-1]], axis=0)
    )
    returning = (
        jnp.zeros((seq_size * capacity, BLOCK, 2 * row_width), jnp.bfloat16)
        .at[slot_index]
        .set(far_terms)
    )
    returned = lax.all_to_all(returning, "seq", split_axis=0, concat_axis=0, tiled=True)
    gathered_terms = jnp.dot(
        selector.T,
        returned.reshape(seq_size * capacity, BLOCK * 2 * row_width),
        preferred_element_type=jnp.float32,
    )
    summed = summed + gathered_terms.reshape(blocks_dev, BLOCK, 2 * row_width)
    summed = summed.reshape(tokens, 2 * row_width)
    query_out = jnp.concatenate(query_parts, axis=-1).reshape(tokens, row_width)
    return (
        query_out,
        summed[:, :row_width].astype(jnp.bfloat16),
        summed[:, row_width:].astype(jnp.bfloat16),
    )


SLOTS = 3 + RAND


def block_kernel(ids_ref, write_ref, valid_ref, first_ref, q_ref, g_ref, *rest):
    kv_refs = rest[:SLOTS]
    own_ref, spread_ref, dq_ref, acc_ref = rest[SLOTS:]
    step = pl.program_id(0)
    steps = pl.num_programs(0)
    width = q_ref.shape[1]
    blocks_dev = own_ref.shape[0]
    logit_scale = 1.0 / math.sqrt(DH)

    @pl.when(step == 0)
    def _():
        acc_ref[...] = jnp.zeros(acc_ref.shape, jnp.float32)

    context = jnp.concatenate([ref[0] for ref in kv_refs], axis=0)
    slot_of = lax.broadcasted_iota(jnp.int32, (1, SLOTS * BLOCK), 1) // BLOCK
    usable = slot_of < 0
    for slot in range(SLOTS):
        usable = usable | ((slot_of == slot) & (valid_ref[step * SLOTS + slot] > 0))
    key_parts, value_parts = [], []
    for head in range(width // DH):
        cols = slice(head * DH, (head + 1) * DH)
        vcols = slice(width + head * DH, width + (head + 1) * DH)
        query = q_ref[:, cols]
        grad = g_ref[:, cols]
        keys = context[:, cols]
        values = context[:, vcols]
        logits = lax.dot_general(
            query, keys, (((1,), (1,)), ((), ())), preferred_element_type=jnp.float32
        ) * logit_scale
        logits = jnp.where(usable, logits, -jnp.inf)
        row_max = jnp.max(logits, axis=-1, keepdims=True)
        exponent = jnp.exp(logits - row_max)
        row_total = jnp.sum(exponent, axis=-1, keepdims=True)
        probability = exponent / row_total
        weights = probability.astype(jnp.bfloat16)
        attended = jnp.dot(weights, values, preferred_element_type=jnp.float32).astype(
            jnp.bfloat16
        )
        row_delta = jnp.sum(
            grad.astype(jnp.float32) * attended.astype(jnp.float32), axis=-1, keepdims=True
        )
        prob_grad = lax.dot_general(
            grad, values, (((1,), (1,)), ((), ())), preferred_element_type=jnp.float32
        )
        score_grad = (probability * (prob_grad - row_delta)).astype(jnp.bfloat16)
        query_grad = logit_scale * jnp.dot(score_grad, keys, preferred_element_type=jnp.float32)
        dq_ref[:, cols] = query_grad.astype(jnp.bfloat16)
        key_parts.append(
            logit_scale
            * lax.dot_general(
                score_grad, query, (((0,), (0,)), ((), ())), preferred_element_type=jnp.float32
            )
        )
        value_parts.append(
            lax.dot_general(
                weights, grad, (((0,), (0,)), ((), ())), preferred_element_type=jnp.float32
            )
        )
    terms = jnp.concatenate(key_parts + value_parts, axis=1)
    for slot in range(SLOTS):
        piece = terms[slot * BLOCK : (slot + 1) * BLOCK]
        if slot >= 3:
            piece = piece.astype(jnp.bfloat16).astype(jnp.float32)
        target = write_ref[step * SLOTS + slot]
        acc_ref[target] = acc_ref[target] + piece

    @pl.when(step == steps - 1)
    def _():
        first = first_ref[0]
        spread_ref[...] = acc_ref[...].astype(jnp.bfloat16)
        for block in range(blocks_dev):
            own_ref[block] = acc_ref[first + block]
            spread_ref[first + block] = jnp.zeros(spread_ref.shape[1:], jnp.bfloat16)


def block_attention(ids, write_ids, valid, first, queries, out_grad, source, chunk, width, total):
    tokens = queries.shape[0]
    blocks_dev = tokens // BLOCK

    def context_spec(slot):
        return pl.BlockSpec(
            (1, BLOCK, 2 * width), lambda i, ids, write_ids, valid, first: (ids[i * SLOTS + slot], 0, 0)
        )

    column_spec = pl.BlockSpec((BLOCK, width), lambda i, ids, write_ids, valid, first: (i, chunk))
    row_spec = pl.BlockSpec((BLOCK, width), lambda i, ids, write_ids, valid, first: (i, 0))
    grid_spec = pltpu.PrefetchScalarGridSpec(
        num_scalar_prefetch=4,
        grid=(blocks_dev,),
        in_specs=[column_spec, column_spec] + [context_spec(s) for s in range(SLOTS)],
        out_specs=[
            pl.BlockSpec(
                (blocks_dev, BLOCK, 2 * width), lambda i, ids, write_ids, valid, first: (0, 0, 0)
            ),
            pl.BlockSpec((total, BLOCK, 2 * width), lambda i, ids, write_ids, valid, first: (0, 0, 0)),
            row_spec,
        ],
        scratch_shapes=[pltpu.VMEM((total, BLOCK, 2 * width), jnp.float32)],
    )
    return pl.pallas_call(
        block_kernel,
        grid_spec=grid_spec,
        out_shape=[
            jax.ShapeDtypeStruct((blocks_dev, BLOCK, 2 * width), jnp.float32),
            jax.ShapeDtypeStruct((total, BLOCK, 2 * width), jnp.bfloat16),
            jax.ShapeDtypeStruct((tokens, width), jnp.bfloat16),
        ],
        compiler_params=pltpu.CompilerParams(vmem_limit_bytes=60 * 1024 * 1024),
    )(ids, write_ids, valid, first, queries, out_grad, *([source] * SLOTS))


def finish_kernel(target_ref, returned_ref, own_b_ref, left_ref, right_ref, own_a_ref,
                  rs_a_ref, key_ref, value_ref, sum_ref):
    blocks_dev = own_b_ref.shape[0]
    half = own_b_ref.shape[2] // 2
    sum_ref[...] = own_b_ref[...]
    sum_ref[0] = sum_ref[0] + left_ref[...].astype(jnp.float32)
    sum_ref[blocks_dev - 1] = sum_ref[blocks_dev - 1] + right_ref[...].astype(jnp.float32)
    for slot in range(returned_ref.shape[0]):
        target = target_ref[slot]

        @pl.when(target >= 0)
        def _():
            sum_ref[target] = sum_ref[target] + returned_ref[slot].astype(jnp.float32)

    for block in range(blocks_dev):
        rows = pl.ds(block * BLOCK, BLOCK)
        first = own_a_ref[block] + rs_a_ref[rows, :].astype(jnp.float32)
        second = sum_ref[block]
        key_ref[rows, pl.ds(0, half)] = first[:, :half].astype(jnp.bfloat16)
        key_ref[rows, pl.ds(half, half)] = second[:, :half].astype(jnp.bfloat16)
        value_ref[rows, pl.ds(0, half)] = first[:, half:].astype(jnp.bfloat16)
        value_ref[rows, pl.ds(half, half)] = second[:, half:].astype(jnp.bfloat16)


def finish(target, returned, own_b, left, right, own_a, rs_a):
    blocks_dev, _, width = own_b.shape
    tokens = blocks_dev * BLOCK
    vmem = pltpu.MemorySpace.VMEM if hasattr(pltpu, "MemorySpace") else pltpu.VMEM
    smem_spec = pl.BlockSpec(memory_space=pltpu.SMEM)
    vmem_spec = pl.BlockSpec(memory_space=vmem)
    return pl.pallas_call(
        finish_kernel,
        in_specs=[smem_spec] + [vmem_spec] * 6,
        out_specs=[vmem_spec, vmem_spec],
        out_shape=[
            jax.ShapeDtypeStruct((tokens, width), jnp.bfloat16),
            jax.ShapeDtypeStruct((tokens, width), jnp.bfloat16),
        ],
        scratch_shapes=[pltpu.VMEM(own_b.shape, jnp.float32)],
    )(target, returned, own_b, left, right, own_a, rs_a)


def gathered_shards(queries, key_rows, value_rows, out_grad, random_device, random_block):
    seq_size = lax.axis_size("seq")
    own_index = lax.axis_index("seq")
    tokens, width = queries.shape
    blocks_dev = tokens // BLOCK
    total = seq_size * blocks_dev
    first = own_index * blocks_dev
    capacity = max(2, 3 * blocks_dev // seq_size)
    selector, slot_index = routing(
        random_device, random_block, own_index, seq_size, blocks_dev, capacity
    )
    block_ids = first + jnp.arange(blocks_dev, dtype=jnp.int32)
    local_ids = jnp.arange(blocks_dev, dtype=jnp.int32)
    own_device = lax.dynamic_slice_in_dim(random_device, first, blocks_dev, 0)
    own_block = lax.dynamic_slice_in_dim(random_block, first, blocks_dev, 0)
    chosen = (own_device * blocks_dev + own_block).astype(jnp.int32)
    window = jnp.stack(
        [jnp.clip(block_ids - 1, 0, total - 1), block_ids, jnp.clip(block_ids + 1, 0, total - 1)],
        axis=1,
    )
    write_ids = jnp.concatenate([window, chosen], axis=1).reshape(-1)
    read_window = jnp.stack([local_ids, local_ids + 1, local_ids + 2], axis=1)
    read_far = (slot_index + blocks_dev + 2).reshape(blocks_dev, RAND).astype(jnp.int32)
    read_ids = jnp.concatenate([read_window, read_far], axis=1).reshape(-1)
    always = jnp.ones_like(block_ids, dtype=jnp.bool_)
    valid = jnp.stack([block_ids > 0, always, block_ids < total - 1] + [always] * RAND, axis=1)
    valid = valid.astype(jnp.int32).reshape(-1)
    first_table = first.reshape(1).astype(jnp.int32)
    chunks = 2 if (width // DH) % 2 == 0 else 1
    part = width // chunks
    global_ids = write_ids
    results = []
    link = None
    for chunk in range(chunks):
        cols = slice(chunk * part, (chunk + 1) * part)
        packed = jnp.concatenate([key_rows[:, cols], value_rows[:, cols]], axis=1)
        if chunk == 0:
            source = lax.all_gather(packed, "seq", axis=0, tiled=True)
            source = source.reshape(total, BLOCK, 2 * part)
            table_ids = global_ids
            link = source[0, 0, :1]
        else:
            packed = packed.reshape(blocks_dev, BLOCK, 2 * part)
            route = selector
            outgoing = jnp.dot(
                route, packed.reshape(blocks_dev, BLOCK * 2 * part),
                preferred_element_type=jnp.float32,
            ).astype(jnp.bfloat16)
            outgoing = outgoing.reshape(seq_size * capacity, BLOCK, 2 * part)
            haloed = extended(packed, (("seq", 0),), 1)
            arrived = lax.all_to_all(outgoing, "seq", split_axis=0, concat_axis=0, tiled=True)
            source = jnp.concatenate([haloed, arrived], axis=0)
            table_ids = read_ids
        results.append((source, table_ids))
    query_parts, key_parts, value_parts = [], [], []
    after = results[-1][0][blocks_dev + 2 :] if chunks > 1 else None
    for chunk in range(chunks):
        source, table_ids = results[chunk]
        table = first_table
        if after is not None:
            table = table + (after[0, 0, :1] * 0.0).astype(jnp.int32)
        if chunk == 0:
            own_sum, spread, query_out = block_attention(
                table_ids, global_ids, valid, table, queries, out_grad, source, chunk, part, total,
            )
            returned = lax.psum_scatter(
                spread.reshape(total * BLOCK, 2 * part), "seq", scatter_dimension=0, tiled=True
            )
            first_half = (own_sum, returned)
        else:
            slots = seq_size * capacity
            far_rows = slot_index.reshape(blocks_dev, RAND).astype(jnp.int32)
            near = window - first + 1 + slots
            far_write = jnp.concatenate([near, far_rows], axis=1).reshape(-1)
            own_sum, spread, query_out = block_attention(
                table_ids, far_write, valid, table - first + 1 + slots, queries, out_grad, source,
                chunk, part, slots + blocks_dev + 2,
            )
            returned = lax.all_to_all(
                spread[:slots], "seq", split_axis=0, concat_axis=0, tiled=True
            )
            spread = spread[slots:]

            left_edge = spread[0]
            right_edge = spread[blocks_dev + 1]
            from_right = lax.ppermute(left_edge, "seq", [(i, i - 1) for i in range(1, seq_size)])
            from_left = lax.ppermute(right_edge, "seq", [(i, i + 1) for i in range(seq_size - 1)])
            hits = selector > 0
            target = jnp.where(
                jnp.any(hits, axis=1), jnp.argmax(hits, axis=1).astype(jnp.int32), -1
            )
            finished = (target, returned, own_sum, from_left, from_right)
        after = own_sum
        query_parts.append(query_out)
    key_out, value_out = finish(*finished, *first_half)
    return (jnp.concatenate(query_parts, axis=1), key_out, value_out)


def shards(queries, key_rows, value_rows, out_grad, random_device, random_block):
    if lax.axis_size("seq") <= 8 and (queries.shape[1] // DH) % 2 == 0:
        return gathered_shards(queries, key_rows, value_rows, out_grad, random_device, random_block)
    return exchanged_shards(queries, key_rows, value_rows, out_grad, random_device, random_block)


def solution(mesh):
    return jax.shard_map(
        shards,
        mesh=mesh,
        in_specs=(
            P(("groups", "seq"), ("heads", "pair")),
            P(("groups", "seq"), ("heads", "pair")),
            P(("groups", "seq"), ("heads", "pair")),
            P(("groups", "seq"), ("heads", "pair")),
            P("groups", None),
            P("groups", None),
        ),
        out_specs=(
            P(("groups", "seq"), ("heads", "pair")),
            P(("groups", "seq"), ("heads", "pair")),
            P(("groups", "seq"), ("heads", "pair")),
        ),
        check_vma=False,
    )
```

```python
import math

import jax
import jax.numpy as jnp
from jax import lax
from jax.experimental import pallas as pl
from jax.experimental.pallas import tpu as pltpu
from jax.sharding import PartitionSpec as P

DH = 128
BLOCK = 64
RAND = 2


def extended(block, sides, width):
    for axis, dim in sides:
        count = lax.axis_size(axis)
        forward = [(i, i + 1) for i in range(count - 1)]
        backward = [(target, source) for source, target in forward]
        low = lax.ppermute(
            lax.slice_in_dim(block, block.shape[dim] - width, None, axis=dim), axis, forward
        )
        high = lax.ppermute(lax.slice_in_dim(block, 0, width, axis=dim), axis, backward)
        block = jnp.concatenate([low, block, high], axis=dim)
    return block


def routing(random_device, random_block, own_index, seq_size, blocks_dev, capacity):
    entries = blocks_dev * RAND
    wanted_from = random_device.reshape(seq_size, entries)
    wanted_block = random_block.reshape(seq_size, entries)
    from_me = (wanted_from == own_index).astype(jnp.int32)
    rank_out = jnp.cumsum(from_me, axis=1) - from_me
    slot_hits = from_me[:, None, :] * (
        rank_out[:, None, :] == jnp.arange(capacity, dtype=jnp.int32)[None, :, None]
    ).astype(jnp.int32)
    block_hits = (
        wanted_block[:, :, None] == jnp.arange(blocks_dev, dtype=jnp.int32)[None, None, :]
    ).astype(jnp.float32)
    selector = jnp.einsum("sce,sej->scj", slot_hits.astype(jnp.float32), block_hits)
    selector = selector.reshape(seq_size * capacity, blocks_dev).astype(jnp.bfloat16)
    own_sources = lax.dynamic_slice_in_dim(
        random_device, own_index * blocks_dev, blocks_dev, 0
    ).reshape(entries)
    peer_hits = (own_sources[:, None] == jnp.arange(seq_size, dtype=jnp.int32)[None, :]).astype(
        jnp.int32
    )
    earlier = jnp.cumsum(peer_hits, axis=0) - peer_hits
    rank_in = jnp.sum(earlier * peer_hits, axis=1)
    slot_index = own_sources * capacity + rank_in
    return (selector, slot_index)


def far_context(arrived, slot_index, blocks_dev):
    picked = jnp.take(arrived, slot_index, axis=0)
    return picked.reshape(blocks_dev, RAND, arrived.shape[1], arrived.shape[2])


def usable_mask(own_index, seq_size, blocks_dev):
    block_ids = jnp.arange(blocks_dev, dtype=jnp.int32)[:, None]
    slot_ids = jnp.arange(3 + RAND, dtype=jnp.int32)[None, :]
    global_block = own_index * blocks_dev + block_ids
    missing = (slot_ids == 0) & (global_block == 0) | (slot_ids == 2) & (
        global_block == seq_size * blocks_dev - 1
    )
    return jnp.repeat(jnp.logical_not(missing), BLOCK, axis=1)


def slot_pieces(haloed, far_blocks, blocks_dev, start_col):
    pieces = []
    for slot in range(3):
        pieces.append(haloed[slot : slot + blocks_dev, :, start_col : start_col + DH])
    far_part = far_blocks[:, :, :, start_col : start_col + DH]
    return (pieces, far_part)


def forward_head(query_tiles, key_pieces, key_far, value_pieces, value_far, usable):
    blocks_dev = query_tiles.shape[0]
    logit_parts = [
        jnp.einsum("bje,bxe->bjx", query_tiles, piece, preferred_element_type=jnp.float32)
        for piece in key_pieces
    ]
    far_logits = jnp.einsum(
        "bje,brxe->bjrx", query_tiles, key_far, preferred_element_type=jnp.float32
    )
    logit_parts.append(far_logits.reshape(blocks_dev, BLOCK, RAND * BLOCK))
    attention_logits = jnp.concatenate(logit_parts, axis=-1) * (1.0 / math.sqrt(DH))
    attention_logits = jnp.where(usable[:, None, :], attention_logits, -jnp.inf)
    row_max = jnp.max(attention_logits, axis=-1, keepdims=True)
    exponent = jnp.exp(attention_logits - row_max)
    row_total = jnp.sum(exponent, axis=-1, keepdims=True)
    probability = exponent / row_total
    softmax_weights = probability.astype(jnp.bfloat16)
    attended = jnp.einsum(
        "bjx,bxe->bje",
        softmax_weights[:, :, :BLOCK],
        value_pieces[0],
        preferred_element_type=jnp.float32,
    )
    for slot in range(1, 3):
        attended = attended + jnp.einsum(
            "bjx,bxe->bje",
            softmax_weights[:, :, slot * BLOCK : (slot + 1) * BLOCK],
            value_pieces[slot],
            preferred_element_type=jnp.float32,
        )
    far_weights = softmax_weights[:, :, 3 * BLOCK :].reshape(blocks_dev, BLOCK, RAND, BLOCK)
    attended = attended + jnp.einsum(
        "bjrx,brxe->bje", far_weights, value_far, preferred_element_type=jnp.float32
    )
    return (probability, attended.astype(jnp.bfloat16))


def backward_head(
    query_tiles, key_pieces, key_far, value_pieces, value_far, gradient_tiles, forward_state
):
    probability, attended_output = forward_state
    blocks_dev = query_tiles.shape[0]
    logit_scale = 1.0 / math.sqrt(DH)
    softmax_weights = probability.astype(jnp.bfloat16)
    row_delta = jnp.sum(
        gradient_tiles.astype(jnp.float32) * attended_output.astype(jnp.float32),
        axis=-1,
        keepdims=True,
    )
    grad_parts = [
        jnp.einsum("bje,bxe->bjx", gradient_tiles, piece, preferred_element_type=jnp.float32)
        for piece in value_pieces
    ]
    far_grad = jnp.einsum(
        "bje,brxe->bjrx", gradient_tiles, value_far, preferred_element_type=jnp.float32
    )
    grad_parts.append(far_grad.reshape(blocks_dev, BLOCK, RAND * BLOCK))
    probability_gradient = jnp.concatenate(grad_parts, axis=-1)
    score_gradient = (probability * (probability_gradient - row_delta)).astype(jnp.bfloat16)
    query_sum = jnp.einsum(
        "bjx,bxe->bje",
        score_gradient[:, :, :BLOCK],
        key_pieces[0],
        preferred_element_type=jnp.float32,
    )
    for slot in range(1, 3):
        query_sum = query_sum + jnp.einsum(
            "bjx,bxe->bje",
            score_gradient[:, :, slot * BLOCK : (slot + 1) * BLOCK],
            key_pieces[slot],
            preferred_element_type=jnp.float32,
        )
    far_scores = score_gradient[:, :, 3 * BLOCK :].reshape(blocks_dev, BLOCK, RAND, BLOCK)
    query_sum = query_sum + jnp.einsum(
        "bjrx,brxe->bje", far_scores, key_far, preferred_element_type=jnp.float32
    )
    query_gradient = (logit_scale * query_sum).astype(jnp.bfloat16)
    key_window, value_window = ([], [])
    for slot in range(3):
        columns = slice(slot * BLOCK, (slot + 1) * BLOCK)
        key_window.append(
            logit_scale
            * jnp.einsum(
                "bjx,bje->bxe",
                score_gradient[:, :, columns],
                query_tiles,
                preferred_element_type=jnp.float32,
            )
        )
        value_window.append(
            jnp.einsum(
                "bjx,bje->bxe",
                softmax_weights[:, :, columns],
                gradient_tiles,
                preferred_element_type=jnp.float32,
            )
        )
    far_weights = softmax_weights[:, :, 3 * BLOCK :].reshape(blocks_dev, BLOCK, RAND, BLOCK)
    key_far_terms = (
        logit_scale
        * jnp.einsum("bjrx,bje->brxe", far_scores, query_tiles, preferred_element_type=jnp.float32)
    ).astype(jnp.bfloat16)
    value_far_terms = jnp.einsum(
        "bjrx,bje->brxe", far_weights, gradient_tiles, preferred_element_type=jnp.float32
    ).astype(jnp.bfloat16)
    return (query_gradient, key_window, value_window, key_far_terms, value_far_terms)


def exchanged_shards(queries, key_rows, value_rows, out_grad, random_device, random_block):
    seq_size = lax.axis_size("seq")
    own_index = lax.axis_index("seq")
    tokens, row_width = queries.shape
    blocks_dev = tokens // BLOCK
    heads_dev = row_width // DH
    capacity = max(2, 3 * blocks_dev // seq_size)
    selector, slot_index = routing(
        random_device, random_block, own_index, seq_size, blocks_dev, capacity
    )
    packed = jnp.concatenate([key_rows, value_rows], axis=1).reshape(
        blocks_dev, BLOCK, 2 * row_width
    )
    flattened = packed.reshape(blocks_dev, BLOCK * 2 * row_width)
    outgoing_blocks = jnp.dot(selector, flattened, preferred_element_type=jnp.float32).astype(
        jnp.bfloat16
    )
    outgoing_blocks = outgoing_blocks.reshape(seq_size * capacity, BLOCK, 2 * row_width)
    haloed = extended(packed, (("seq", 0),), 1)
    arrived = lax.all_to_all(outgoing_blocks, "seq", split_axis=0, concat_axis=0, tiled=True)
    far_blocks = far_context(arrived, slot_index, blocks_dev)
    usable = usable_mask(own_index, seq_size, blocks_dev)
    query_tiles = queries.reshape(blocks_dev, BLOCK, row_width)
    gradient_tiles = out_grad.reshape(blocks_dev, BLOCK, row_width)
    states = []
    for head_index in range(heads_dev):
        key_pieces, key_far = slot_pieces(haloed, far_blocks, blocks_dev, head_index * DH)
        value_pieces, value_far = slot_pieces(
            haloed, far_blocks, blocks_dev, row_width + head_index * DH
        )
        query_head = query_tiles[:, :, head_index * DH : (head_index + 1) * DH]
        states.append(
            forward_head(query_head, key_pieces, key_far, value_pieces, value_far, usable)
        )
    query_parts = []
    window_lists = [[], [], []]
    value_lists = [[], [], []]
    far_keys, far_values = ([], [])
    for head_index in range(heads_dev):
        key_pieces, key_far = slot_pieces(haloed, far_blocks, blocks_dev, head_index * DH)
        value_pieces, value_far = slot_pieces(
            haloed, far_blocks, blocks_dev, row_width + head_index * DH
        )
        query_head = query_tiles[:, :, head_index * DH : (head_index + 1) * DH]
        gradient_head = gradient_tiles[:, :, head_index * DH : (head_index + 1) * DH]
        query_gradient, key_window, value_window, key_far_terms, value_far_terms = backward_head(
            query_head,
            key_pieces,
            key_far,
            value_pieces,
            value_far,
            gradient_head,
            states[head_index],
        )
        query_parts.append(query_gradient)
        for slot in range(3):
            window_lists[slot].append(key_window[slot])
            value_lists[slot].append(value_window[slot])
        far_keys.append(key_far_terms)
        far_values.append(value_far_terms)
    slot_terms = [
        jnp.concatenate(window_lists[slot] + value_lists[slot], axis=-1) for slot in range(3)
    ]
    left_terms = slot_terms[0]
    right_terms = slot_terms[2]
    far_terms = jnp.concatenate(far_keys + far_values, axis=-1).reshape(
        blocks_dev * RAND, BLOCK, 2 * row_width
    )
    edge_terms = jnp.stack([left_terms[0], right_terms[-1]])
    edge_haloed = extended(edge_terms.astype(jnp.bfloat16), (("seq", 0),), 1).astype(
        edge_terms.dtype
    )
    summed = (
        slot_terms[1]
        + jnp.concatenate([left_terms[1:], edge_haloed[3:]], axis=0)
        + jnp.concatenate([edge_haloed[:1], right_terms[:-1]], axis=0)
    )
    returning = (
        jnp.zeros((seq_size * capacity, BLOCK, 2 * row_width), jnp.bfloat16)
        .at[slot_index]
        .set(far_terms)
    )
    returned = lax.all_to_all(returning, "seq", split_axis=0, concat_axis=0, tiled=True)
    gathered_terms = jnp.dot(
        selector.T,
        returned.reshape(seq_size * capacity, BLOCK * 2 * row_width),
        preferred_element_type=jnp.float32,
    )
    summed = summed + gathered_terms.reshape(blocks_dev, BLOCK, 2 * row_width)
    summed = summed.reshape(tokens, 2 * row_width)
    query_out = jnp.concatenate(query_parts, axis=-1).reshape(tokens, row_width)
    return (
        query_out,
        summed[:, :row_width].astype(jnp.bfloat16),
        summed[:, row_width:].astype(jnp.bfloat16),
    )


SLOTS = 3 + RAND


def block_kernel(ids_ref, write_ref, valid_ref, first_ref, q_ref, g_ref, *rest):
    kv_refs = rest[:SLOTS]
    own_ref, spread_ref, dq_ref, acc_ref = rest[SLOTS:]
    step = pl.program_id(0)
    steps = pl.num_programs(0)
    width = q_ref.shape[1]
    blocks_dev = own_ref.shape[0]
    logit_scale = 1.0 / math.sqrt(DH)

    @pl.when(step == 0)
    def _():
        acc_ref[...] = jnp.zeros(acc_ref.shape, jnp.float32)

    context = jnp.concatenate([ref[0] for ref in kv_refs], axis=0)
    slot_of = lax.broadcasted_iota(jnp.int32, (1, SLOTS * BLOCK), 1) // BLOCK
    usable = slot_of < 0
    for slot in range(SLOTS):
        usable = usable | ((slot_of == slot) & (valid_ref[step * SLOTS + slot] > 0))
    key_parts, value_parts = [], []
    for head in range(width // DH):
        cols = slice(head * DH, (head + 1) * DH)
        vcols = slice(width + head * DH, width + (head + 1) * DH)
        query = q_ref[:, cols]
        grad = g_ref[:, cols]
        keys = context[:, cols]
        values = context[:, vcols]
        logits = lax.dot_general(
            query, keys, (((1,), (1,)), ((), ())), preferred_element_type=jnp.float32
        ) * logit_scale
        logits = jnp.where(usable, logits, -jnp.inf)
        row_max = jnp.max(logits, axis=-1, keepdims=True)
        exponent = jnp.exp(logits - row_max)
        row_total = jnp.sum(exponent, axis=-1, keepdims=True)
        probability = exponent / row_total
        weights = probability.astype(jnp.bfloat16)
        attended = jnp.dot(weights, values, preferred_element_type=jnp.float32).astype(
            jnp.bfloat16
        )
        row_delta = jnp.sum(
            grad.astype(jnp.float32) * attended.astype(jnp.float32), axis=-1, keepdims=True
        )
        prob_grad = lax.dot_general(
            grad, values, (((1,), (1,)), ((), ())), preferred_element_type=jnp.float32
        )
        score_grad = (probability * (prob_grad - row_delta)).astype(jnp.bfloat16)
        query_grad = logit_scale * jnp.dot(score_grad, keys, preferred_element_type=jnp.float32)
        dq_ref[:, cols] = query_grad.astype(jnp.bfloat16)
        key_parts.append(
            logit_scale
            * lax.dot_general(
                score_grad, query, (((0,), (0,)), ((), ())), preferred_element_type=jnp.float32
            )
        )
        value_parts.append(
            lax.dot_general(
                weights, grad, (((0,), (0,)), ((), ())), preferred_element_type=jnp.float32
            )
        )
    terms = jnp.concatenate(key_parts + value_parts, axis=1)
    for slot in range(SLOTS):
        piece = terms[slot * BLOCK : (slot + 1) * BLOCK]
        if slot >= 3:
            piece = piece.astype(jnp.bfloat16).astype(jnp.float32)
        target = write_ref[step * SLOTS + slot]
        acc_ref[target] = acc_ref[target] + piece

    @pl.when(step == steps - 1)
    def _():
        first = first_ref[0]
        spread_ref[...] = acc_ref[...].astype(jnp.bfloat16)
        for block in range(blocks_dev):
            own_ref[block] = acc_ref[first + block]
            spread_ref[first + block] = jnp.zeros(spread_ref.shape[1:], jnp.bfloat16)


def block_attention(ids, write_ids, valid, first, queries, out_grad, source, chunk, width, total):
    tokens = queries.shape[0]
    blocks_dev = tokens // BLOCK

    def context_spec(slot):
        return pl.BlockSpec(
            (1, BLOCK, 2 * width), lambda i, ids, write_ids, valid, first: (ids[i * SLOTS + slot], 0, 0)
        )

    column_spec = pl.BlockSpec((BLOCK, width), lambda i, ids, write_ids, valid, first: (i, chunk))
    row_spec = pl.BlockSpec((BLOCK, width), lambda i, ids, write_ids, valid, first: (i, 0))
    grid_spec = pltpu.PrefetchScalarGridSpec(
        num_scalar_prefetch=4,
        grid=(blocks_dev,),
        in_specs=[column_spec, column_spec] + [context_spec(s) for s in range(SLOTS)],
        out_specs=[
            pl.BlockSpec(
                (blocks_dev, BLOCK, 2 * width), lambda i, ids, write_ids, valid, first: (0, 0, 0)
            ),
            pl.BlockSpec((total, BLOCK, 2 * width), lambda i, ids, write_ids, valid, first: (0, 0, 0)),
            row_spec,
        ],
        scratch_shapes=[pltpu.VMEM((total, BLOCK, 2 * width), jnp.float32)],
    )
    return pl.pallas_call(
        block_kernel,
        grid_spec=grid_spec,
        out_shape=[
            jax.ShapeDtypeStruct((blocks_dev, BLOCK, 2 * width), jnp.float32),
            jax.ShapeDtypeStruct((total, BLOCK, 2 * width), jnp.bfloat16),
            jax.ShapeDtypeStruct((tokens, width), jnp.bfloat16),
        ],
        compiler_params=pltpu.CompilerParams(vmem_limit_bytes=60 * 1024 * 1024),
    )(ids, write_ids, valid, first, queries, out_grad, *([source] * SLOTS))


def finish_kernel(target_ref, returned_ref, own_b_ref, left_ref, right_ref, own_a_ref,
                  rs_a_ref, key_ref, value_ref, sum_ref):
    block = pl.program_id(0)
    last = pl.num_programs(0) - 1
    half = own_b_ref.shape[2] // 2
    sum_ref[...] = own_b_ref[0]

    @pl.when(block == 0)
    def _():
        sum_ref[...] = sum_ref[...] + left_ref[...].astype(jnp.float32)

    @pl.when(block == last)
    def _():
        sum_ref[...] = sum_ref[...] + right_ref[...].astype(jnp.float32)

    for slot in range(returned_ref.shape[0]):

        @pl.when(target_ref[slot] == block)
        def _():
            sum_ref[...] = sum_ref[...] + returned_ref[slot].astype(jnp.float32)

    first = own_a_ref[0] + rs_a_ref[...].astype(jnp.float32)
    second = sum_ref[...]
    key_ref[:, pl.ds(0, half)] = first[:, :half].astype(jnp.bfloat16)
    key_ref[:, pl.ds(half, half)] = second[:, :half].astype(jnp.bfloat16)
    value_ref[:, pl.ds(0, half)] = first[:, half:].astype(jnp.bfloat16)
    value_ref[:, pl.ds(half, half)] = second[:, half:].astype(jnp.bfloat16)


def finish(target, returned, own_b, left, right, own_a, rs_a):
    blocks_dev, _, width = own_b.shape
    tokens = blocks_dev * BLOCK
    whole = pl.BlockSpec(returned.shape, lambda j, target: (0, 0, 0))
    edge = pl.BlockSpec(left.shape, lambda j, target: (0, 0))
    stacked = pl.BlockSpec((1, BLOCK, width), lambda j, target: (j, 0, 0))
    rows = pl.BlockSpec((BLOCK, width), lambda j, target: (j, 0))
    grid_spec = pltpu.PrefetchScalarGridSpec(
        num_scalar_prefetch=1,
        grid=(blocks_dev,),
        in_specs=[whole, stacked, edge, edge, stacked, rows],
        out_specs=[rows, rows],
        scratch_shapes=[pltpu.VMEM((BLOCK, width), jnp.float32)],
    )
    return pl.pallas_call(
        finish_kernel,
        grid_spec=grid_spec,
        out_shape=[
            jax.ShapeDtypeStruct((tokens, width), jnp.bfloat16),
            jax.ShapeDtypeStruct((tokens, width), jnp.bfloat16),
        ],
    )(target, returned, own_b, left, right, own_a, rs_a)


def gathered_shards(queries, key_rows, value_rows, out_grad, random_device, random_block):
    seq_size = lax.axis_size("seq")
    own_index = lax.axis_index("seq")
    tokens, width = queries.shape
    blocks_dev = tokens // BLOCK
    total = seq_size * blocks_dev
    first = own_index * blocks_dev
    capacity = max(2, 3 * blocks_dev // seq_size)
    selector, slot_index = routing(
        random_device, random_block, own_index, seq_size, blocks_dev, capacity
    )
    block_ids = first + jnp.arange(blocks_dev, dtype=jnp.int32)
    local_ids = jnp.arange(blocks_dev, dtype=jnp.int32)
    own_device = lax.dynamic_slice_in_dim(random_device, first, blocks_dev, 0)
    own_block = lax.dynamic_slice_in_dim(random_block, first, blocks_dev, 0)
    chosen = (own_device * blocks_dev + own_block).astype(jnp.int32)
    window = jnp.stack(
        [jnp.clip(block_ids - 1, 0, total - 1), block_ids, jnp.clip(block_ids + 1, 0, total - 1)],
        axis=1,
    )
    write_ids = jnp.concatenate([window, chosen], axis=1).reshape(-1)
    read_window = jnp.stack([local_ids, local_ids + 1, local_ids + 2], axis=1)
    read_far = (slot_index + blocks_dev + 2).reshape(blocks_dev, RAND).astype(jnp.int32)
    read_ids = jnp.concatenate([read_window, read_far], axis=1).reshape(-1)
    always = jnp.ones_like(block_ids, dtype=jnp.bool_)
    valid = jnp.stack([block_ids > 0, always, block_ids < total - 1] + [always] * RAND, axis=1)
    valid = valid.astype(jnp.int32).reshape(-1)
    first_table = first.reshape(1).astype(jnp.int32)
    chunks = 2 if (width // DH) % 2 == 0 else 1
    part = width // chunks
    global_ids = write_ids
    results = []
    link = None
    for chunk in range(chunks):
        cols = slice(chunk * part, (chunk + 1) * part)
        packed = jnp.concatenate([key_rows[:, cols], value_rows[:, cols]], axis=1)
        if chunk == 0:
            source = lax.all_gather(packed, "seq", axis=0, tiled=True)
            source = source.reshape(total, BLOCK, 2 * part)
            table_ids = global_ids
            link = source[0, 0, :1]
        else:
            packed = packed.reshape(blocks_dev, BLOCK, 2 * part)
            route = selector
            outgoing = jnp.dot(
                route, packed.reshape(blocks_dev, BLOCK * 2 * part),
                preferred_element_type=jnp.float32,
            ).astype(jnp.bfloat16)
            outgoing = outgoing.reshape(seq_size * capacity, BLOCK, 2 * part)
            haloed = extended(packed, (("seq", 0),), 1)
            arrived = lax.all_to_all(outgoing, "seq", split_axis=0, concat_axis=0, tiled=True)
            source = jnp.concatenate([haloed, arrived], axis=0)
            table_ids = read_ids
        results.append((source, table_ids))
    query_parts, key_parts, value_parts = [], [], []
    after = results[-1][0][blocks_dev + 2 :] if chunks > 1 else None
    for chunk in range(chunks):
        source, table_ids = results[chunk]
        table = first_table
        if after is not None:
            table = table + (after[0, 0, :1] * 0.0).astype(jnp.int32)
        if chunk == 0:
            own_sum, spread, query_out = block_attention(
                table_ids, global_ids, valid, table, queries, out_grad, source, chunk, part, total,
            )
            returned = lax.psum_scatter(
                spread.reshape(total * BLOCK, 2 * part), "seq", scatter_dimension=0, tiled=True
            )
            first_half = (own_sum, returned)
        else:
            slots = seq_size * capacity
            far_rows = slot_index.reshape(blocks_dev, RAND).astype(jnp.int32)
            near = window - first + 1 + slots
            far_write = jnp.concatenate([near, far_rows], axis=1).reshape(-1)
            own_sum, spread, query_out = block_attention(
                table_ids, far_write, valid, table - first + 1 + slots, queries, out_grad, source,
                chunk, part, slots + blocks_dev + 2,
            )
            returned = lax.all_to_all(
                spread[:slots], "seq", split_axis=0, concat_axis=0, tiled=True
            )
            spread = spread[slots:]

            left_edge = spread[0]
            right_edge = spread[blocks_dev + 1]
            from_right = lax.ppermute(left_edge, "seq", [(i, i - 1) for i in range(1, seq_size)])
            from_left = lax.ppermute(right_edge, "seq", [(i, i + 1) for i in range(seq_size - 1)])
            hits = selector > 0
            target = jnp.where(
                jnp.any(hits, axis=1), jnp.argmax(hits, axis=1).astype(jnp.int32), -1
            )
            finished = (target, returned, own_sum, from_left, from_right)
        after = own_sum
        query_parts.append(query_out)
    key_out, value_out = finish(*finished, *first_half)
    return (jnp.concatenate(query_parts, axis=1), key_out, value_out)


def shards(queries, key_rows, value_rows, out_grad, random_device, random_block):
    if lax.axis_size("seq") <= 8 and (queries.shape[1] // DH) % 2 == 0:
        return gathered_shards(queries, key_rows, value_rows, out_grad, random_device, random_block)
    return exchanged_shards(queries, key_rows, value_rows, out_grad, random_device, random_block)


def solution(mesh):
    return jax.shard_map(
        shards,
        mesh=mesh,
        in_specs=(
            P(("groups", "seq"), ("heads", "pair")),
            P(("groups", "seq"), ("heads", "pair")),
            P(("groups", "seq"), ("heads", "pair")),
            P(("groups", "seq"), ("heads", "pair")),
            P("groups", None),
            P("groups", None),
        ),
        out_specs=(
            P(("groups", "seq"), ("heads", "pair")),
            P(("groups", "seq"), ("heads", "pair")),
            P(("groups", "seq"), ("heads", "pair")),
        ),
        check_vma=False,
    )
```

```python
import math

import jax
import jax.numpy as jnp
from jax import lax
from jax.experimental import pallas as pl
from jax.experimental.pallas import tpu as pltpu
from jax.sharding import PartitionSpec as P

DH = 128
BLOCK = 64
RAND = 2


def extended(block, sides, width):
    for axis, dim in sides:
        count = lax.axis_size(axis)
        forward = [(i, i + 1) for i in range(count - 1)]
        backward = [(target, source) for source, target in forward]
        low = lax.ppermute(
            lax.slice_in_dim(block, block.shape[dim] - width, None, axis=dim), axis, forward
        )
        high = lax.ppermute(lax.slice_in_dim(block, 0, width, axis=dim), axis, backward)
        block = jnp.concatenate([low, block, high], axis=dim)
    return block


def routing(random_device, random_block, own_index, seq_size, blocks_dev, capacity):
    entries = blocks_dev * RAND
    wanted_from = random_device.reshape(seq_size, entries)
    wanted_block = random_block.reshape(seq_size, entries)
    from_me = (wanted_from == own_index).astype(jnp.int32)
    rank_out = jnp.cumsum(from_me, axis=1) - from_me
    slot_hits = from_me[:, None, :] * (
        rank_out[:, None, :] == jnp.arange(capacity, dtype=jnp.int32)[None, :, None]
    ).astype(jnp.int32)
    block_hits = (
        wanted_block[:, :, None] == jnp.arange(blocks_dev, dtype=jnp.int32)[None, None, :]
    ).astype(jnp.float32)
    selector = jnp.einsum("sce,sej->scj", slot_hits.astype(jnp.float32), block_hits)
    selector = selector.reshape(seq_size * capacity, blocks_dev).astype(jnp.bfloat16)
    own_sources = lax.dynamic_slice_in_dim(
        random_device, own_index * blocks_dev, blocks_dev, 0
    ).reshape(entries)
    peer_hits = (own_sources[:, None] == jnp.arange(seq_size, dtype=jnp.int32)[None, :]).astype(
        jnp.int32
    )
    earlier = jnp.cumsum(peer_hits, axis=0) - peer_hits
    rank_in = jnp.sum(earlier * peer_hits, axis=1)
    slot_index = own_sources * capacity + rank_in
    return (selector, slot_index)


def far_context(arrived, slot_index, blocks_dev):
    picked = jnp.take(arrived, slot_index, axis=0)
    return picked.reshape(blocks_dev, RAND, arrived.shape[1], arrived.shape[2])


def usable_mask(own_index, seq_size, blocks_dev):
    block_ids = jnp.arange(blocks_dev, dtype=jnp.int32)[:, None]
    slot_ids = jnp.arange(3 + RAND, dtype=jnp.int32)[None, :]
    global_block = own_index * blocks_dev + block_ids
    missing = (slot_ids == 0) & (global_block == 0) | (slot_ids == 2) & (
        global_block == seq_size * blocks_dev - 1
    )
    return jnp.repeat(jnp.logical_not(missing), BLOCK, axis=1)


def slot_pieces(haloed, far_blocks, blocks_dev, start_col):
    pieces = []
    for slot in range(3):
        pieces.append(haloed[slot : slot + blocks_dev, :, start_col : start_col + DH])
    far_part = far_blocks[:, :, :, start_col : start_col + DH]
    return (pieces, far_part)


def forward_head(query_tiles, key_pieces, key_far, value_pieces, value_far, usable):
    blocks_dev = query_tiles.shape[0]
    logit_parts = [
        jnp.einsum("bje,bxe->bjx", query_tiles, piece, preferred_element_type=jnp.float32)
        for piece in key_pieces
    ]
    far_logits = jnp.einsum(
        "bje,brxe->bjrx", query_tiles, key_far, preferred_element_type=jnp.float32
    )
    logit_parts.append(far_logits.reshape(blocks_dev, BLOCK, RAND * BLOCK))
    attention_logits = jnp.concatenate(logit_parts, axis=-1) * (1.0 / math.sqrt(DH))
    attention_logits = jnp.where(usable[:, None, :], attention_logits, -jnp.inf)
    row_max = jnp.max(attention_logits, axis=-1, keepdims=True)
    exponent = jnp.exp(attention_logits - row_max)
    row_total = jnp.sum(exponent, axis=-1, keepdims=True)
    probability = exponent / row_total
    softmax_weights = probability.astype(jnp.bfloat16)
    attended = jnp.einsum(
        "bjx,bxe->bje",
        softmax_weights[:, :, :BLOCK],
        value_pieces[0],
        preferred_element_type=jnp.float32,
    )
    for slot in range(1, 3):
        attended = attended + jnp.einsum(
            "bjx,bxe->bje",
            softmax_weights[:, :, slot * BLOCK : (slot + 1) * BLOCK],
            value_pieces[slot],
            preferred_element_type=jnp.float32,
        )
    far_weights = softmax_weights[:, :, 3 * BLOCK :].reshape(blocks_dev, BLOCK, RAND, BLOCK)
    attended = attended + jnp.einsum(
        "bjrx,brxe->bje", far_weights, value_far, preferred_element_type=jnp.float32
    )
    return (probability, attended.astype(jnp.bfloat16))


def backward_head(
    query_tiles, key_pieces, key_far, value_pieces, value_far, gradient_tiles, forward_state
):
    probability, attended_output = forward_state
    blocks_dev = query_tiles.shape[0]
    logit_scale = 1.0 / math.sqrt(DH)
    softmax_weights = probability.astype(jnp.bfloat16)
    row_delta = jnp.sum(
        gradient_tiles.astype(jnp.float32) * attended_output.astype(jnp.float32),
        axis=-1,
        keepdims=True,
    )
    grad_parts = [
        jnp.einsum("bje,bxe->bjx", gradient_tiles, piece, preferred_element_type=jnp.float32)
        for piece in value_pieces
    ]
    far_grad = jnp.einsum(
        "bje,brxe->bjrx", gradient_tiles, value_far, preferred_element_type=jnp.float32
    )
    grad_parts.append(far_grad.reshape(blocks_dev, BLOCK, RAND * BLOCK))
    probability_gradient = jnp.concatenate(grad_parts, axis=-1)
    score_gradient = (probability * (probability_gradient - row_delta)).astype(jnp.bfloat16)
    query_sum = jnp.einsum(
        "bjx,bxe->bje",
        score_gradient[:, :, :BLOCK],
        key_pieces[0],
        preferred_element_type=jnp.float32,
    )
    for slot in range(1, 3):
        query_sum = query_sum + jnp.einsum(
            "bjx,bxe->bje",
            score_gradient[:, :, slot * BLOCK : (slot + 1) * BLOCK],
            key_pieces[slot],
            preferred_element_type=jnp.float32,
        )
    far_scores = score_gradient[:, :, 3 * BLOCK :].reshape(blocks_dev, BLOCK, RAND, BLOCK)
    query_sum = query_sum + jnp.einsum(
        "bjrx,brxe->bje", far_scores, key_far, preferred_element_type=jnp.float32
    )
    query_gradient = (logit_scale * query_sum).astype(jnp.bfloat16)
    key_window, value_window = ([], [])
    for slot in range(3):
        columns = slice(slot * BLOCK, (slot + 1) * BLOCK)
        key_window.append(
            logit_scale
            * jnp.einsum(
                "bjx,bje->bxe",
                score_gradient[:, :, columns],
                query_tiles,
                preferred_element_type=jnp.float32,
            )
        )
        value_window.append(
            jnp.einsum(
                "bjx,bje->bxe",
                softmax_weights[:, :, columns],
                gradient_tiles,
                preferred_element_type=jnp.float32,
            )
        )
    far_weights = softmax_weights[:, :, 3 * BLOCK :].reshape(blocks_dev, BLOCK, RAND, BLOCK)
    key_far_terms = (
        logit_scale
        * jnp.einsum("bjrx,bje->brxe", far_scores, query_tiles, preferred_element_type=jnp.float32)
    ).astype(jnp.bfloat16)
    value_far_terms = jnp.einsum(
        "bjrx,bje->brxe", far_weights, gradient_tiles, preferred_element_type=jnp.float32
    ).astype(jnp.bfloat16)
    return (query_gradient, key_window, value_window, key_far_terms, value_far_terms)


def exchanged_shards(queries, key_rows, value_rows, out_grad, random_device, random_block):
    seq_size = lax.axis_size("seq")
    own_index = lax.axis_index("seq")
    tokens, row_width = queries.shape
    blocks_dev = tokens // BLOCK
    heads_dev = row_width // DH
    capacity = max(2, 3 * blocks_dev // seq_size)
    selector, slot_index = routing(
        random_device, random_block, own_index, seq_size, blocks_dev, capacity
    )
    packed = jnp.concatenate([key_rows, value_rows], axis=1).reshape(
        blocks_dev, BLOCK, 2 * row_width
    )
    flattened = packed.reshape(blocks_dev, BLOCK * 2 * row_width)
    outgoing_blocks = jnp.dot(selector, flattened, preferred_element_type=jnp.float32).astype(
        jnp.bfloat16
    )
    outgoing_blocks = outgoing_blocks.reshape(seq_size * capacity, BLOCK, 2 * row_width)
    haloed = extended(packed, (("seq", 0),), 1)
    arrived = lax.all_to_all(outgoing_blocks, "seq", split_axis=0, concat_axis=0, tiled=True)
    far_blocks = far_context(arrived, slot_index, blocks_dev)
    usable = usable_mask(own_index, seq_size, blocks_dev)
    query_tiles = queries.reshape(blocks_dev, BLOCK, row_width)
    gradient_tiles = out_grad.reshape(blocks_dev, BLOCK, row_width)
    states = []
    for head_index in range(heads_dev):
        key_pieces, key_far = slot_pieces(haloed, far_blocks, blocks_dev, head_index * DH)
        value_pieces, value_far = slot_pieces(
            haloed, far_blocks, blocks_dev, row_width + head_index * DH
        )
        query_head = query_tiles[:, :, head_index * DH : (head_index + 1) * DH]
        states.append(
            forward_head(query_head, key_pieces, key_far, value_pieces, value_far, usable)
        )
    query_parts = []
    window_lists = [[], [], []]
    value_lists = [[], [], []]
    far_keys, far_values = ([], [])
    for head_index in range(heads_dev):
        key_pieces, key_far = slot_pieces(haloed, far_blocks, blocks_dev, head_index * DH)
        value_pieces, value_far = slot_pieces(
            haloed, far_blocks, blocks_dev, row_width + head_index * DH
        )
        query_head = query_tiles[:, :, head_index * DH : (head_index + 1) * DH]
        gradient_head = gradient_tiles[:, :, head_index * DH : (head_index + 1) * DH]
        query_gradient, key_window, value_window, key_far_terms, value_far_terms = backward_head(
            query_head,
            key_pieces,
            key_far,
            value_pieces,
            value_far,
            gradient_head,
            states[head_index],
        )
        query_parts.append(query_gradient)
        for slot in range(3):
            window_lists[slot].append(key_window[slot])
            value_lists[slot].append(value_window[slot])
        far_keys.append(key_far_terms)
        far_values.append(value_far_terms)
    slot_terms = [
        jnp.concatenate(window_lists[slot] + value_lists[slot], axis=-1) for slot in range(3)
    ]
    left_terms = slot_terms[0]
    right_terms = slot_terms[2]
    far_terms = jnp.concatenate(far_keys + far_values, axis=-1).reshape(
        blocks_dev * RAND, BLOCK, 2 * row_width
    )
    edge_terms = jnp.stack([left_terms[0], right_terms[-1]])
    edge_haloed = extended(edge_terms.astype(jnp.bfloat16), (("seq", 0),), 1).astype(
        edge_terms.dtype
    )
    summed = (
        slot_terms[1]
        + jnp.concatenate([left_terms[1:], edge_haloed[3:]], axis=0)
        + jnp.concatenate([edge_haloed[:1], right_terms[:-1]], axis=0)
    )
    returning = (
        jnp.zeros((seq_size * capacity, BLOCK, 2 * row_width), jnp.bfloat16)
        .at[slot_index]
        .set(far_terms)
    )
    returned = lax.all_to_all(returning, "seq", split_axis=0, concat_axis=0, tiled=True)
    gathered_terms = jnp.dot(
        selector.T,
        returned.reshape(seq_size * capacity, BLOCK * 2 * row_width),
        preferred_element_type=jnp.float32,
    )
    summed = summed + gathered_terms.reshape(blocks_dev, BLOCK, 2 * row_width)
    summed = summed.reshape(tokens, 2 * row_width)
    query_out = jnp.concatenate(query_parts, axis=-1).reshape(tokens, row_width)
    return (
        query_out,
        summed[:, :row_width].astype(jnp.bfloat16),
        summed[:, row_width:].astype(jnp.bfloat16),
    )


SLOTS = 3 + RAND


def block_kernel(ids_ref, write_ref, valid_ref, first_ref, q_ref, g_ref, *rest):
    kv_refs = rest[:SLOTS]
    own_ref, spread_ref, dq_ref, acc_ref = rest[SLOTS:]
    step = pl.program_id(0)
    steps = pl.num_programs(0)
    width = q_ref.shape[1]
    blocks_dev = own_ref.shape[0]
    logit_scale = 1.0 / math.sqrt(DH)

    context = jnp.concatenate([ref[0] for ref in kv_refs], axis=0)
    slot_of = lax.broadcasted_iota(jnp.int32, (1, SLOTS * BLOCK), 1) // BLOCK
    usable = slot_of < 0
    for slot in range(SLOTS):
        usable = usable | ((slot_of == slot) & (valid_ref[step * SLOTS + slot] % 2 > 0))
    key_parts, value_parts = [], []
    for head in range(width // DH):
        cols = slice(head * DH, (head + 1) * DH)
        vcols = slice(width + head * DH, width + (head + 1) * DH)
        query = q_ref[:, cols]
        grad = g_ref[:, cols]
        keys = context[:, cols]
        values = context[:, vcols]
        logits = lax.dot_general(
            query, keys, (((1,), (1,)), ((), ())), preferred_element_type=jnp.float32
        ) * logit_scale
        logits = jnp.where(usable, logits, -jnp.inf)
        row_max = jnp.max(logits, axis=-1, keepdims=True)
        exponent = jnp.exp(logits - row_max)
        row_total = jnp.sum(exponent, axis=-1, keepdims=True)
        probability = exponent / row_total
        weights = probability.astype(jnp.bfloat16)
        attended = jnp.dot(weights, values, preferred_element_type=jnp.float32).astype(
            jnp.bfloat16
        )
        row_delta = jnp.sum(
            grad.astype(jnp.float32) * attended.astype(jnp.float32), axis=-1, keepdims=True
        )
        prob_grad = lax.dot_general(
            grad, values, (((1,), (1,)), ((), ())), preferred_element_type=jnp.float32
        )
        score_grad = (probability * (prob_grad - row_delta)).astype(jnp.bfloat16)
        query_grad = logit_scale * jnp.dot(score_grad, keys, preferred_element_type=jnp.float32)
        dq_ref[:, cols] = query_grad.astype(jnp.bfloat16)
        key_parts.append(
            logit_scale
            * lax.dot_general(
                score_grad, query, (((0,), (0,)), ((), ())), preferred_element_type=jnp.float32
            )
        )
        value_parts.append(
            lax.dot_general(
                weights, grad, (((0,), (0,)), ((), ())), preferred_element_type=jnp.float32
            )
        )
    terms = jnp.concatenate(key_parts + value_parts, axis=1)
    for slot in range(SLOTS):
        piece = terms[slot * BLOCK : (slot + 1) * BLOCK]
        if slot >= 3:
            piece = piece.astype(jnp.bfloat16).astype(jnp.float32)
        target = write_ref[step * SLOTS + slot]
        fresh = valid_ref[step * SLOTS + slot] >= 2
        acc_ref[target] = jnp.where(fresh, piece, acc_ref[target] + piece)

    @pl.when(step == steps - 1)
    def _():
        first = first_ref[0]
        spread_ref[...] = jnp.zeros(spread_ref.shape, jnp.bfloat16)
        for entry in range(blocks_dev * SLOTS):
            row = write_ref[entry]

            @pl.when(valid_ref[entry] >= 2)
            def _():
                spread_ref[row] = acc_ref[row].astype(jnp.bfloat16)

        for block in range(blocks_dev):
            own_ref[block] = acc_ref[first + block]
            spread_ref[first + block] = jnp.zeros(spread_ref.shape[1:], jnp.bfloat16)


def block_attention(ids, write_ids, valid, first, queries, out_grad, source, chunk, width, total):
    tokens = queries.shape[0]
    blocks_dev = tokens // BLOCK
    entries = write_ids.shape[0]
    same = write_ids[:, None] == write_ids[None, :]
    before = jnp.arange(entries)[None, :] < jnp.arange(entries)[:, None]
    fresh = jnp.logical_not(jnp.any(same & before, axis=1))
    valid = valid + 2 * fresh.astype(jnp.int32)

    def context_spec(slot):
        return pl.BlockSpec(
            (1, BLOCK, 2 * width), lambda i, ids, write_ids, valid, first: (ids[i * SLOTS + slot], 0, 0)
        )

    column_spec = pl.BlockSpec((BLOCK, width), lambda i, ids, write_ids, valid, first: (i, chunk))
    row_spec = pl.BlockSpec((BLOCK, width), lambda i, ids, write_ids, valid, first: (i, 0))
    grid_spec = pltpu.PrefetchScalarGridSpec(
        num_scalar_prefetch=4,
        grid=(blocks_dev,),
        in_specs=[column_spec, column_spec] + [context_spec(s) for s in range(SLOTS)],
        out_specs=[
            pl.BlockSpec(
                (blocks_dev, BLOCK, 2 * width), lambda i, ids, write_ids, valid, first: (0, 0, 0)
            ),
            pl.BlockSpec((total, BLOCK, 2 * width), lambda i, ids, write_ids, valid, first: (0, 0, 0)),
            row_spec,
        ],
        scratch_shapes=[pltpu.VMEM((total, BLOCK, 2 * width), jnp.float32)],
    )
    return pl.pallas_call(
        block_kernel,
        grid_spec=grid_spec,
        out_shape=[
            jax.ShapeDtypeStruct((blocks_dev, BLOCK, 2 * width), jnp.float32),
            jax.ShapeDtypeStruct((total, BLOCK, 2 * width), jnp.bfloat16),
            jax.ShapeDtypeStruct((tokens, width), jnp.bfloat16),
        ],
        compiler_params=pltpu.CompilerParams(vmem_limit_bytes=60 * 1024 * 1024),
    )(ids, write_ids, valid, first, queries, out_grad, *([source] * SLOTS))


def finish_kernel(target_ref, returned_ref, own_b_ref, left_ref, right_ref, own_a_ref,
                  rs_a_ref, key_ref, value_ref, sum_ref):
    blocks_dev = own_b_ref.shape[0]
    half = own_b_ref.shape[2] // 2
    sum_ref[...] = own_b_ref[...]
    sum_ref[0] = sum_ref[0] + left_ref[...].astype(jnp.float32)
    sum_ref[blocks_dev - 1] = sum_ref[blocks_dev - 1] + right_ref[...].astype(jnp.float32)
    for slot in range(returned_ref.shape[0]):
        target = target_ref[slot]

        @pl.when(target >= 0)
        def _():
            sum_ref[target] = sum_ref[target] + returned_ref[slot].astype(jnp.float32)

    for block in range(blocks_dev):
        rows = pl.ds(block * BLOCK, BLOCK)
        first = own_a_ref[block] + rs_a_ref[rows, :].astype(jnp.float32)
        second = sum_ref[block]
        key_ref[rows, pl.ds(0, half)] = first[:, :half].astype(jnp.bfloat16)
        key_ref[rows, pl.ds(half, half)] = second[:, :half].astype(jnp.bfloat16)
        value_ref[rows, pl.ds(0, half)] = first[:, half:].astype(jnp.bfloat16)
        value_ref[rows, pl.ds(half, half)] = second[:, half:].astype(jnp.bfloat16)


def finish(target, returned, own_b, left, right, own_a, rs_a):
    blocks_dev, _, width = own_b.shape
    tokens = blocks_dev * BLOCK
    vmem = pltpu.MemorySpace.VMEM if hasattr(pltpu, "MemorySpace") else pltpu.VMEM
    smem_spec = pl.BlockSpec(memory_space=pltpu.SMEM)
    vmem_spec = pl.BlockSpec(memory_space=vmem)
    return pl.pallas_call(
        finish_kernel,
        in_specs=[smem_spec] + [vmem_spec] * 6,
        out_specs=[vmem_spec, vmem_spec],
        out_shape=[
            jax.ShapeDtypeStruct((tokens, width), jnp.bfloat16),
            jax.ShapeDtypeStruct((tokens, width), jnp.bfloat16),
        ],
        scratch_shapes=[pltpu.VMEM(own_b.shape, jnp.float32)],
    )(target, returned, own_b, left, right, own_a, rs_a)


def gathered_shards(queries, key_rows, value_rows, out_grad, random_device, random_block):
    seq_size = lax.axis_size("seq")
    own_index = lax.axis_index("seq")
    tokens, width = queries.shape
    blocks_dev = tokens // BLOCK
    total = seq_size * blocks_dev
    first = own_index * blocks_dev
    capacity = max(2, 3 * blocks_dev // seq_size)
    selector, slot_index = routing(
        random_device, random_block, own_index, seq_size, blocks_dev, capacity
    )
    block_ids = first + jnp.arange(blocks_dev, dtype=jnp.int32)
    local_ids = jnp.arange(blocks_dev, dtype=jnp.int32)
    own_device = lax.dynamic_slice_in_dim(random_device, first, blocks_dev, 0)
    own_block = lax.dynamic_slice_in_dim(random_block, first, blocks_dev, 0)
    chosen = (own_device * blocks_dev + own_block).astype(jnp.int32)
    window = jnp.stack(
        [jnp.clip(block_ids - 1, 0, total - 1), block_ids, jnp.clip(block_ids + 1, 0, total - 1)],
        axis=1,
    )
    write_ids = jnp.concatenate([window, chosen], axis=1).reshape(-1)
    read_window = jnp.stack([local_ids, local_ids + 1, local_ids + 2], axis=1)
    read_far = (slot_index + blocks_dev + 2).reshape(blocks_dev, RAND).astype(jnp.int32)
    read_ids = jnp.concatenate([read_window, read_far], axis=1).reshape(-1)
    always = jnp.ones_like(block_ids, dtype=jnp.bool_)
    valid = jnp.stack([block_ids > 0, always, block_ids < total - 1] + [always] * RAND, axis=1)
    valid = valid.astype(jnp.int32).reshape(-1)
    first_table = first.reshape(1).astype(jnp.int32)
    chunks = 2 if (width // DH) % 2 == 0 else 1
    part = width // chunks
    global_ids = write_ids
    results = []
    link = None
    for chunk in range(chunks):
        cols = slice(chunk * part, (chunk + 1) * part)
        packed = jnp.concatenate([key_rows[:, cols], value_rows[:, cols]], axis=1)
        if chunk == 0:
            source = lax.all_gather(packed, "seq", axis=0, tiled=True)
            source = source.reshape(total, BLOCK, 2 * part)
            table_ids = global_ids
            link = source[0, 0, :1]
        else:
            packed = packed.reshape(blocks_dev, BLOCK, 2 * part)
            route = selector
            outgoing = jnp.dot(
                route, packed.reshape(blocks_dev, BLOCK * 2 * part),
                preferred_element_type=jnp.float32,
            ).astype(jnp.bfloat16)
            outgoing = outgoing.reshape(seq_size * capacity, BLOCK, 2 * part)
            haloed = extended(packed, (("seq", 0),), 1)
            arrived = lax.all_to_all(outgoing, "seq", split_axis=0, concat_axis=0, tiled=True)
            source = jnp.concatenate([haloed, arrived], axis=0)
            table_ids = read_ids
        results.append((source, table_ids))
    query_parts, key_parts, value_parts = [], [], []
    after = results[-1][0][blocks_dev + 2 :] if chunks > 1 else None
    for chunk in range(chunks):
        source, table_ids = results[chunk]
        table = first_table
        if after is not None:
            table = table + (after[0, 0, :1] * 0.0).astype(jnp.int32)
        if chunk == 0:
            own_sum, spread, query_out = block_attention(
                table_ids, global_ids, valid, table, queries, out_grad, source, chunk, part, total,
            )
            returned = lax.psum_scatter(
                spread.reshape(total * BLOCK, 2 * part), "seq", scatter_dimension=0, tiled=True
            )
            first_half = (own_sum, returned)
        else:
            slots = seq_size * capacity
            far_rows = slot_index.reshape(blocks_dev, RAND).astype(jnp.int32)
            near = window - first + 1 + slots
            far_write = jnp.concatenate([near, far_rows], axis=1).reshape(-1)
            own_sum, spread, query_out = block_attention(
                table_ids, far_write, valid, table - first + 1 + slots, queries, out_grad, source,
                chunk, part, slots + blocks_dev + 2,
            )
            returned = lax.all_to_all(
                spread[:slots], "seq", split_axis=0, concat_axis=0, tiled=True
            )
            spread = spread[slots:]

            left_edge = spread[0]
            right_edge = spread[blocks_dev + 1]
            from_right = lax.ppermute(left_edge, "seq", [(i, i - 1) for i in range(1, seq_size)])
            from_left = lax.ppermute(right_edge, "seq", [(i, i + 1) for i in range(seq_size - 1)])
            hits = selector > 0
            target = jnp.where(
                jnp.any(hits, axis=1), jnp.argmax(hits, axis=1).astype(jnp.int32), -1
            )
            finished = (target, returned, own_sum, from_left, from_right)
        after = own_sum
        query_parts.append(query_out)
    key_out, value_out = finish(*finished, *first_half)
    return (jnp.concatenate(query_parts, axis=1), key_out, value_out)


def shards(queries, key_rows, value_rows, out_grad, random_device, random_block):
    if lax.axis_size("seq") <= 8 and (queries.shape[1] // DH) % 2 == 0:
        return gathered_shards(queries, key_rows, value_rows, out_grad, random_device, random_block)
    return exchanged_shards(queries, key_rows, value_rows, out_grad, random_device, random_block)


def solution(mesh):
    return jax.shard_map(
        shards,
        mesh=mesh,
        in_specs=(
            P(("groups", "seq"), ("heads", "pair")),
            P(("groups", "seq"), ("heads", "pair")),
            P(("groups", "seq"), ("heads", "pair")),
            P(("groups", "seq"), ("heads", "pair")),
            P("groups", None),
            P("groups", None),
        ),
        out_specs=(
            P(("groups", "seq"), ("heads", "pair")),
            P(("groups", "seq"), ("heads", "pair")),
            P(("groups", "seq"), ("heads", "pair")),
        ),
        check_vma=False,
    )
```

```python
import math

import jax
import jax.numpy as jnp
from jax import lax
from jax.experimental import pallas as pl
from jax.experimental.pallas import tpu as pltpu
from jax.sharding import PartitionSpec as P

DH = 128
BLOCK = 64
RAND = 2


def extended(block, sides, width):
    for axis, dim in sides:
        count = lax.axis_size(axis)
        forward = [(i, i + 1) for i in range(count - 1)]
        backward = [(target, source) for source, target in forward]
        low = lax.ppermute(
            lax.slice_in_dim(block, block.shape[dim] - width, None, axis=dim), axis, forward
        )
        high = lax.ppermute(lax.slice_in_dim(block, 0, width, axis=dim), axis, backward)
        block = jnp.concatenate([low, block, high], axis=dim)
    return block


def routing(random_device, random_block, own_index, seq_size, blocks_dev, capacity):
    entries = blocks_dev * RAND
    wanted_from = random_device.reshape(seq_size, entries)
    wanted_block = random_block.reshape(seq_size, entries)
    from_me = (wanted_from == own_index).astype(jnp.int32)
    rank_out = jnp.cumsum(from_me, axis=1) - from_me
    slot_hits = from_me[:, None, :] * (
        rank_out[:, None, :] == jnp.arange(capacity, dtype=jnp.int32)[None, :, None]
    ).astype(jnp.int32)
    block_hits = (
        wanted_block[:, :, None] == jnp.arange(blocks_dev, dtype=jnp.int32)[None, None, :]
    ).astype(jnp.float32)
    selector = jnp.einsum("sce,sej->scj", slot_hits.astype(jnp.float32), block_hits)
    selector = selector.reshape(seq_size * capacity, blocks_dev).astype(jnp.bfloat16)
    own_sources = lax.dynamic_slice_in_dim(
        random_device, own_index * blocks_dev, blocks_dev, 0
    ).reshape(entries)
    peer_hits = (own_sources[:, None] == jnp.arange(seq_size, dtype=jnp.int32)[None, :]).astype(
        jnp.int32
    )
    earlier = jnp.cumsum(peer_hits, axis=0) - peer_hits
    rank_in = jnp.sum(earlier * peer_hits, axis=1)
    slot_index = own_sources * capacity + rank_in
    return (selector, slot_index)


def far_context(arrived, slot_index, blocks_dev):
    picked = jnp.take(arrived, slot_index, axis=0)
    return picked.reshape(blocks_dev, RAND, arrived.shape[1], arrived.shape[2])


def usable_mask(own_index, seq_size, blocks_dev):
    block_ids = jnp.arange(blocks_dev, dtype=jnp.int32)[:, None]
    slot_ids = jnp.arange(3 + RAND, dtype=jnp.int32)[None, :]
    global_block = own_index * blocks_dev + block_ids
    missing = (slot_ids == 0) & (global_block == 0) | (slot_ids == 2) & (
        global_block == seq_size * blocks_dev - 1
    )
    return jnp.repeat(jnp.logical_not(missing), BLOCK, axis=1)


def slot_pieces(haloed, far_blocks, blocks_dev, start_col):
    pieces = []
    for slot in range(3):
        pieces.append(haloed[slot : slot + blocks_dev, :, start_col : start_col + DH])
    far_part = far_blocks[:, :, :, start_col : start_col + DH]
    return (pieces, far_part)


def forward_head(query_tiles, key_pieces, key_far, value_pieces, value_far, usable):
    blocks_dev = query_tiles.shape[0]
    logit_parts = [
        jnp.einsum("bje,bxe->bjx", query_tiles, piece, preferred_element_type=jnp.float32)
        for piece in key_pieces
    ]
    far_logits = jnp.einsum(
        "bje,brxe->bjrx", query_tiles, key_far, preferred_element_type=jnp.float32
    )
    logit_parts.append(far_logits.reshape(blocks_dev, BLOCK, RAND * BLOCK))
    attention_logits = jnp.concatenate(logit_parts, axis=-1) * (1.0 / math.sqrt(DH))
    attention_logits = jnp.where(usable[:, None, :], attention_logits, -jnp.inf)
    row_max = jnp.max(attention_logits, axis=-1, keepdims=True)
    exponent = jnp.exp(attention_logits - row_max)
    row_total = jnp.sum(exponent, axis=-1, keepdims=True)
    probability = exponent / row_total
    softmax_weights = probability.astype(jnp.bfloat16)
    attended = jnp.einsum(
        "bjx,bxe->bje",
        softmax_weights[:, :, :BLOCK],
        value_pieces[0],
        preferred_element_type=jnp.float32,
    )
    for slot in range(1, 3):
        attended = attended + jnp.einsum(
            "bjx,bxe->bje",
            softmax_weights[:, :, slot * BLOCK : (slot + 1) * BLOCK],
            value_pieces[slot],
            preferred_element_type=jnp.float32,
        )
    far_weights = softmax_weights[:, :, 3 * BLOCK :].reshape(blocks_dev, BLOCK, RAND, BLOCK)
    attended = attended + jnp.einsum(
        "bjrx,brxe->bje", far_weights, value_far, preferred_element_type=jnp.float32
    )
    return (probability, attended.astype(jnp.bfloat16))


def backward_head(
    query_tiles, key_pieces, key_far, value_pieces, value_far, gradient_tiles, forward_state
):
    probability, attended_output = forward_state
    blocks_dev = query_tiles.shape[0]
    logit_scale = 1.0 / math.sqrt(DH)
    softmax_weights = probability.astype(jnp.bfloat16)
    row_delta = jnp.sum(
        gradient_tiles.astype(jnp.float32) * attended_output.astype(jnp.float32),
        axis=-1,
        keepdims=True,
    )
    grad_parts = [
        jnp.einsum("bje,bxe->bjx", gradient_tiles, piece, preferred_element_type=jnp.float32)
        for piece in value_pieces
    ]
    far_grad = jnp.einsum(
        "bje,brxe->bjrx", gradient_tiles, value_far, preferred_element_type=jnp.float32
    )
    grad_parts.append(far_grad.reshape(blocks_dev, BLOCK, RAND * BLOCK))
    probability_gradient = jnp.concatenate(grad_parts, axis=-1)
    score_gradient = (probability * (probability_gradient - row_delta)).astype(jnp.bfloat16)
    query_sum = jnp.einsum(
        "bjx,bxe->bje",
        score_gradient[:, :, :BLOCK],
        key_pieces[0],
        preferred_element_type=jnp.float32,
    )
    for slot in range(1, 3):
        query_sum = query_sum + jnp.einsum(
            "bjx,bxe->bje",
            score_gradient[:, :, slot * BLOCK : (slot + 1) * BLOCK],
            key_pieces[slot],
            preferred_element_type=jnp.float32,
        )
    far_scores = score_gradient[:, :, 3 * BLOCK :].reshape(blocks_dev, BLOCK, RAND, BLOCK)
    query_sum = query_sum + jnp.einsum(
        "bjrx,brxe->bje", far_scores, key_far, preferred_element_type=jnp.float32
    )
    query_gradient = (logit_scale * query_sum).astype(jnp.bfloat16)
    key_window, value_window = ([], [])
    for slot in range(3):
        columns = slice(slot * BLOCK, (slot + 1) * BLOCK)
        key_window.append(
            logit_scale
            * jnp.einsum(
                "bjx,bje->bxe",
                score_gradient[:, :, columns],
                query_tiles,
                preferred_element_type=jnp.float32,
            )
        )
        value_window.append(
            jnp.einsum(
                "bjx,bje->bxe",
                softmax_weights[:, :, columns],
                gradient_tiles,
                preferred_element_type=jnp.float32,
            )
        )
    far_weights = softmax_weights[:, :, 3 * BLOCK :].reshape(blocks_dev, BLOCK, RAND, BLOCK)
    key_far_terms = (
        logit_scale
        * jnp.einsum("bjrx,bje->brxe", far_scores, query_tiles, preferred_element_type=jnp.float32)
    ).astype(jnp.bfloat16)
    value_far_terms = jnp.einsum(
        "bjrx,bje->brxe", far_weights, gradient_tiles, preferred_element_type=jnp.float32
    ).astype(jnp.bfloat16)
    return (query_gradient, key_window, value_window, key_far_terms, value_far_terms)


def exchanged_shards(queries, key_rows, value_rows, out_grad, random_device, random_block):
    seq_size = lax.axis_size("seq")
    own_index = lax.axis_index("seq")
    tokens, row_width = queries.shape
    blocks_dev = tokens // BLOCK
    heads_dev = row_width // DH
    capacity = max(2, 3 * blocks_dev // seq_size)
    selector, slot_index = routing(
        random_device, random_block, own_index, seq_size, blocks_dev, capacity
    )
    packed = jnp.concatenate([key_rows, value_rows], axis=1).reshape(
        blocks_dev, BLOCK, 2 * row_width
    )
    flattened = packed.reshape(blocks_dev, BLOCK * 2 * row_width)
    outgoing_blocks = jnp.dot(selector, flattened, preferred_element_type=jnp.float32).astype(
        jnp.bfloat16
    )
    outgoing_blocks = outgoing_blocks.reshape(seq_size * capacity, BLOCK, 2 * row_width)
    haloed = extended(packed, (("seq", 0),), 1)
    arrived = lax.all_to_all(outgoing_blocks, "seq", split_axis=0, concat_axis=0, tiled=True)
    far_blocks = far_context(arrived, slot_index, blocks_dev)
    usable = usable_mask(own_index, seq_size, blocks_dev)
    query_tiles = queries.reshape(blocks_dev, BLOCK, row_width)
    gradient_tiles = out_grad.reshape(blocks_dev, BLOCK, row_width)
    states = []
    for head_index in range(heads_dev):
        key_pieces, key_far = slot_pieces(haloed, far_blocks, blocks_dev, head_index * DH)
        value_pieces, value_far = slot_pieces(
            haloed, far_blocks, blocks_dev, row_width + head_index * DH
        )
        query_head = query_tiles[:, :, head_index * DH : (head_index + 1) * DH]
        states.append(
            forward_head(query_head, key_pieces, key_far, value_pieces, value_far, usable)
        )
    query_parts = []
    window_lists = [[], [], []]
    value_lists = [[], [], []]
    far_keys, far_values = ([], [])
    for head_index in range(heads_dev):
        key_pieces, key_far = slot_pieces(haloed, far_blocks, blocks_dev, head_index * DH)
        value_pieces, value_far = slot_pieces(
            haloed, far_blocks, blocks_dev, row_width + head_index * DH
        )
        query_head = query_tiles[:, :, head_index * DH : (head_index + 1) * DH]
        gradient_head = gradient_tiles[:, :, head_index * DH : (head_index + 1) * DH]
        query_gradient, key_window, value_window, key_far_terms, value_far_terms = backward_head(
            query_head,
            key_pieces,
            key_far,
            value_pieces,
            value_far,
            gradient_head,
            states[head_index],
        )
        query_parts.append(query_gradient)
        for slot in range(3):
            window_lists[slot].append(key_window[slot])
            value_lists[slot].append(value_window[slot])
        far_keys.append(key_far_terms)
        far_values.append(value_far_terms)
    slot_terms = [
        jnp.concatenate(window_lists[slot] + value_lists[slot], axis=-1) for slot in range(3)
    ]
    left_terms = slot_terms[0]
    right_terms = slot_terms[2]
    far_terms = jnp.concatenate(far_keys + far_values, axis=-1).reshape(
        blocks_dev * RAND, BLOCK, 2 * row_width
    )
    edge_terms = jnp.stack([left_terms[0], right_terms[-1]])
    edge_haloed = extended(edge_terms.astype(jnp.bfloat16), (("seq", 0),), 1).astype(
        edge_terms.dtype
    )
    summed = (
        slot_terms[1]
        + jnp.concatenate([left_terms[1:], edge_haloed[3:]], axis=0)
        + jnp.concatenate([edge_haloed[:1], right_terms[:-1]], axis=0)
    )
    returning = (
        jnp.zeros((seq_size * capacity, BLOCK, 2 * row_width), jnp.bfloat16)
        .at[slot_index]
        .set(far_terms)
    )
    returned = lax.all_to_all(returning, "seq", split_axis=0, concat_axis=0, tiled=True)
    gathered_terms = jnp.dot(
        selector.T,
        returned.reshape(seq_size * capacity, BLOCK * 2 * row_width),
        preferred_element_type=jnp.float32,
    )
    summed = summed + gathered_terms.reshape(blocks_dev, BLOCK, 2 * row_width)
    summed = summed.reshape(tokens, 2 * row_width)
    query_out = jnp.concatenate(query_parts, axis=-1).reshape(tokens, row_width)
    return (
        query_out,
        summed[:, :row_width].astype(jnp.bfloat16),
        summed[:, row_width:].astype(jnp.bfloat16),
    )


SLOTS = 3 + RAND


def block_kernel(ids_ref, write_ref, valid_ref, first_ref, q_ref, g_ref, *rest):
    kv_refs = rest[:SLOTS]
    own_ref, spread_ref, dq_ref, acc_ref = rest[SLOTS:]
    step = pl.program_id(0)
    steps = pl.num_programs(0)
    width = q_ref.shape[1]
    blocks_dev = own_ref.shape[0]
    logit_scale = 1.0 / math.sqrt(DH)

    @pl.when(step == 0)
    def _():
        acc_ref[...] = jnp.zeros(acc_ref.shape, jnp.float32)

    context = jnp.concatenate([ref[0] for ref in kv_refs], axis=0)
    slot_of = lax.broadcasted_iota(jnp.int32, (1, SLOTS * BLOCK), 1) // BLOCK
    usable = slot_of < 0
    for slot in range(SLOTS):
        usable = usable | ((slot_of == slot) & (valid_ref[step * SLOTS + slot] > 0))
    key_parts, value_parts = [], []
    for head in range(width // DH):
        cols = slice(head * DH, (head + 1) * DH)
        vcols = slice(width + head * DH, width + (head + 1) * DH)
        query = q_ref[:, cols]
        grad = g_ref[:, cols]
        keys = context[:, cols]
        values = context[:, vcols]
        logits = lax.dot_general(
            query, keys, (((1,), (1,)), ((), ())), preferred_element_type=jnp.float32
        ) * logit_scale
        logits = jnp.where(usable, logits, -jnp.inf)
        row_max = jnp.max(logits, axis=-1, keepdims=True)
        exponent = jnp.exp(logits - row_max)
        row_total = jnp.sum(exponent, axis=-1, keepdims=True)
        probability = exponent / row_total
        weights = probability.astype(jnp.bfloat16)
        attended = jnp.dot(weights, values, preferred_element_type=jnp.float32).astype(
            jnp.bfloat16
        )
        row_delta = jnp.sum(
            grad.astype(jnp.float32) * attended.astype(jnp.float32), axis=-1, keepdims=True
        )
        prob_grad = lax.dot_general(
            grad, values, (((1,), (1,)), ((), ())), preferred_element_type=jnp.float32
        )
        score_grad = (probability * (prob_grad - row_delta)).astype(jnp.bfloat16)
        query_grad = logit_scale * jnp.dot(score_grad, keys, preferred_element_type=jnp.float32)
        dq_ref[:, cols] = query_grad.astype(jnp.bfloat16)
        key_parts.append(
            logit_scale
            * lax.dot_general(
                score_grad, query, (((0,), (0,)), ((), ())), preferred_element_type=jnp.float32
            )
        )
        value_parts.append(
            lax.dot_general(
                weights, grad, (((0,), (0,)), ((), ())), preferred_element_type=jnp.float32
            )
        )
    terms = jnp.concatenate(key_parts + value_parts, axis=1)
    for slot in range(SLOTS):
        piece = terms[slot * BLOCK : (slot + 1) * BLOCK]
        if slot >= 3:
            piece = piece.astype(jnp.bfloat16).astype(jnp.float32)
        target = write_ref[step * SLOTS + slot]
        acc_ref[target] = acc_ref[target] + piece

    @pl.when(step == steps - 1)
    def _():
        first = first_ref[0]
        spread_ref[...] = acc_ref[...].astype(jnp.bfloat16)
        for block in range(blocks_dev):
            own_ref[block] = acc_ref[first + block].astype(jnp.bfloat16)
            spread_ref[first + block] = jnp.zeros(spread_ref.shape[1:], jnp.bfloat16)


def block_attention(ids, write_ids, valid, first, queries, out_grad, source, chunk, width, total):
    tokens = queries.shape[0]
    blocks_dev = tokens // BLOCK

    def context_spec(slot):
        return pl.BlockSpec(
            (1, BLOCK, 2 * width), lambda i, ids, write_ids, valid, first: (ids[i * SLOTS + slot], 0, 0)
        )

    column_spec = pl.BlockSpec((BLOCK, width), lambda i, ids, write_ids, valid, first: (i, chunk))
    row_spec = pl.BlockSpec((BLOCK, width), lambda i, ids, write_ids, valid, first: (i, 0))
    grid_spec = pltpu.PrefetchScalarGridSpec(
        num_scalar_prefetch=4,
        grid=(blocks_dev,),
        in_specs=[column_spec, column_spec] + [context_spec(s) for s in range(SLOTS)],
        out_specs=[
            pl.BlockSpec(
                (blocks_dev, BLOCK, 2 * width), lambda i, ids, write_ids, valid, first: (0, 0, 0)
            ),
            pl.BlockSpec((total, BLOCK, 2 * width), lambda i, ids, write_ids, valid, first: (0, 0, 0)),
            row_spec,
        ],
        scratch_shapes=[pltpu.VMEM((total, BLOCK, 2 * width), jnp.float32)],
    )
    return pl.pallas_call(
        block_kernel,
        grid_spec=grid_spec,
        out_shape=[
            jax.ShapeDtypeStruct((blocks_dev, BLOCK, 2 * width), jnp.bfloat16),
            jax.ShapeDtypeStruct((total, BLOCK, 2 * width), jnp.bfloat16),
            jax.ShapeDtypeStruct((tokens, width), jnp.bfloat16),
        ],
        compiler_params=pltpu.CompilerParams(vmem_limit_bytes=60 * 1024 * 1024),
    )(ids, write_ids, valid, first, queries, out_grad, *([source] * SLOTS))


def finish_kernel(target_ref, returned_ref, own_b_ref, left_ref, right_ref, own_a_ref,
                  rs_a_ref, key_ref, value_ref, sum_ref):
    blocks_dev = own_b_ref.shape[0]
    half = own_b_ref.shape[2] // 2
    sum_ref[...] = own_b_ref[...].astype(jnp.float32)
    sum_ref[0] = sum_ref[0] + left_ref[...].astype(jnp.float32)
    sum_ref[blocks_dev - 1] = sum_ref[blocks_dev - 1] + right_ref[...].astype(jnp.float32)
    for slot in range(returned_ref.shape[0]):
        target = target_ref[slot]

        @pl.when(target >= 0)
        def _():
            sum_ref[target] = sum_ref[target] + returned_ref[slot].astype(jnp.float32)

    for block in range(blocks_dev):
        rows = pl.ds(block * BLOCK, BLOCK)
        first = own_a_ref[block].astype(jnp.float32) + rs_a_ref[rows, :].astype(jnp.float32)
        second = sum_ref[block]
        key_ref[rows, pl.ds(0, half)] = first[:, :half].astype(jnp.bfloat16)
        key_ref[rows, pl.ds(half, half)] = second[:, :half].astype(jnp.bfloat16)
        value_ref[rows, pl.ds(0, half)] = first[:, half:].astype(jnp.bfloat16)
        value_ref[rows, pl.ds(half, half)] = second[:, half:].astype(jnp.bfloat16)


def finish(target, returned, own_b, left, right, own_a, rs_a):
    blocks_dev, _, width = own_b.shape
    tokens = blocks_dev * BLOCK
    vmem = pltpu.MemorySpace.VMEM if hasattr(pltpu, "MemorySpace") else pltpu.VMEM
    smem_spec = pl.BlockSpec(memory_space=pltpu.SMEM)
    vmem_spec = pl.BlockSpec(memory_space=vmem)
    return pl.pallas_call(
        finish_kernel,
        in_specs=[smem_spec] + [vmem_spec] * 6,
        out_specs=[vmem_spec, vmem_spec],
        out_shape=[
            jax.ShapeDtypeStruct((tokens, width), jnp.bfloat16),
            jax.ShapeDtypeStruct((tokens, width), jnp.bfloat16),
        ],
        scratch_shapes=[pltpu.VMEM(own_b.shape, jnp.float32)],
    )(target, returned, own_b, left, right, own_a, rs_a)


def gathered_shards(queries, key_rows, value_rows, out_grad, random_device, random_block):
    seq_size = lax.axis_size("seq")
    own_index = lax.axis_index("seq")
    tokens, width = queries.shape
    blocks_dev = tokens // BLOCK
    total = seq_size * blocks_dev
    first = own_index * blocks_dev
    capacity = max(2, 3 * blocks_dev // seq_size)
    selector, slot_index = routing(
        random_device, random_block, own_index, seq_size, blocks_dev, capacity
    )
    block_ids = first + jnp.arange(blocks_dev, dtype=jnp.int32)
    local_ids = jnp.arange(blocks_dev, dtype=jnp.int32)
    own_device = lax.dynamic_slice_in_dim(random_device, first, blocks_dev, 0)
    own_block = lax.dynamic_slice_in_dim(random_block, first, blocks_dev, 0)
    chosen = (own_device * blocks_dev + own_block).astype(jnp.int32)
    window = jnp.stack(
        [jnp.clip(block_ids - 1, 0, total - 1), block_ids, jnp.clip(block_ids + 1, 0, total - 1)],
        axis=1,
    )
    write_ids = jnp.concatenate([window, chosen], axis=1).reshape(-1)
    read_window = jnp.stack([local_ids, local_ids + 1, local_ids + 2], axis=1)
    read_far = (slot_index + blocks_dev + 2).reshape(blocks_dev, RAND).astype(jnp.int32)
    read_ids = jnp.concatenate([read_window, read_far], axis=1).reshape(-1)
    always = jnp.ones_like(block_ids, dtype=jnp.bool_)
    valid = jnp.stack([block_ids > 0, always, block_ids < total - 1] + [always] * RAND, axis=1)
    valid = valid.astype(jnp.int32).reshape(-1)
    first_table = first.reshape(1).astype(jnp.int32)
    chunks = 2 if (width // DH) % 2 == 0 else 1
    part = width // chunks
    global_ids = write_ids
    results = []
    link = None
    for chunk in range(chunks):
        cols = slice(chunk * part, (chunk + 1) * part)
        packed = jnp.concatenate([key_rows[:, cols], value_rows[:, cols]], axis=1)
        if chunk == 0:
            source = lax.all_gather(packed, "seq", axis=0, tiled=True)
            source = source.reshape(total, BLOCK, 2 * part)
            table_ids = global_ids
            link = source[0, 0, :1]
        else:
            packed = packed.reshape(blocks_dev, BLOCK, 2 * part)
            route = selector
            outgoing = jnp.dot(
                route, packed.reshape(blocks_dev, BLOCK * 2 * part),
                preferred_element_type=jnp.float32,
            ).astype(jnp.bfloat16)
            outgoing = outgoing.reshape(seq_size * capacity, BLOCK, 2 * part)
            haloed = extended(packed, (("seq", 0),), 1)
            arrived = lax.all_to_all(outgoing, "seq", split_axis=0, concat_axis=0, tiled=True)
            source = jnp.concatenate([haloed, arrived], axis=0)
            table_ids = read_ids
        results.append((source, table_ids))
    query_parts, key_parts, value_parts = [], [], []
    after = results[-1][0][blocks_dev + 2 :] if chunks > 1 else None
    for chunk in range(chunks):
        source, table_ids = results[chunk]
        table = first_table
        if after is not None:
            table = table + (after[0, 0, :1] * 0.0).astype(jnp.int32)
        if chunk == 0:
            own_sum, spread, query_out = block_attention(
                table_ids, global_ids, valid, table, queries, out_grad, source, chunk, part, total,
            )
            returned = lax.psum_scatter(
                spread.reshape(total * BLOCK, 2 * part), "seq", scatter_dimension=0, tiled=True
            )
            first_half = (own_sum, returned)
        else:
            slots = seq_size * capacity
            far_rows = slot_index.reshape(blocks_dev, RAND).astype(jnp.int32)
            near = window - first + 1 + slots
            far_write = jnp.concatenate([near, far_rows], axis=1).reshape(-1)
            own_sum, spread, query_out = block_attention(
                table_ids, far_write, valid, table - first + 1 + slots, queries, out_grad, source,
                chunk, part, slots + blocks_dev + 2,
            )
            returned = lax.all_to_all(
                spread[:slots], "seq", split_axis=0, concat_axis=0, tiled=True
            )
            spread = spread[slots:]

            left_edge = spread[0]
            right_edge = spread[blocks_dev + 1]
            from_right = lax.ppermute(left_edge, "seq", [(i, i - 1) for i in range(1, seq_size)])
            from_left = lax.ppermute(right_edge, "seq", [(i, i + 1) for i in range(seq_size - 1)])
            hits = selector > 0
            target = jnp.where(
                jnp.any(hits, axis=1), jnp.argmax(hits, axis=1).astype(jnp.int32), -1
            )
            finished = (target, returned, own_sum, from_left, from_right)
        after = own_sum
        query_parts.append(query_out)
    key_out, value_out = finish(*finished, *first_half)
    return (jnp.concatenate(query_parts, axis=1), key_out, value_out)


def shards(queries, key_rows, value_rows, out_grad, random_device, random_block):
    if lax.axis_size("seq") <= 8 and (queries.shape[1] // DH) % 2 == 0:
        return gathered_shards(queries, key_rows, value_rows, out_grad, random_device, random_block)
    return exchanged_shards(queries, key_rows, value_rows, out_grad, random_device, random_block)


def solution(mesh):
    return jax.shard_map(
        shards,
        mesh=mesh,
        in_specs=(
            P(("groups", "seq"), ("heads", "pair")),
            P(("groups", "seq"), ("heads", "pair")),
            P(("groups", "seq"), ("heads", "pair")),
            P(("groups", "seq"), ("heads", "pair")),
            P("groups", None),
            P("groups", None),
        ),
        out_specs=(
            P(("groups", "seq"), ("heads", "pair")),
            P(("groups", "seq"), ("heads", "pair")),
            P(("groups", "seq"), ("heads", "pair")),
        ),
        check_vma=False,
    )
```

```python
import math

import jax
import jax.numpy as jnp
from jax import lax
from jax.experimental import pallas as pl
from jax.experimental.pallas import tpu as pltpu
from jax.sharding import PartitionSpec as P

DH = 128
BLOCK = 64
RAND = 2


def extended(block, sides, width):
    for axis, dim in sides:
        count = lax.axis_size(axis)
        forward = [(i, i + 1) for i in range(count - 1)]
        backward = [(target, source) for source, target in forward]
        low = lax.ppermute(
            lax.slice_in_dim(block, block.shape[dim] - width, None, axis=dim), axis, forward
        )
        high = lax.ppermute(lax.slice_in_dim(block, 0, width, axis=dim), axis, backward)
        block = jnp.concatenate([low, block, high], axis=dim)
    return block


def routing(random_device, random_block, own_index, seq_size, blocks_dev, capacity):
    entries = blocks_dev * RAND
    wanted_from = random_device.reshape(seq_size, entries)
    wanted_block = random_block.reshape(seq_size, entries)
    from_me = (wanted_from == own_index).astype(jnp.int32)
    rank_out = jnp.cumsum(from_me, axis=1) - from_me
    slot_hits = from_me[:, None, :] * (
        rank_out[:, None, :] == jnp.arange(capacity, dtype=jnp.int32)[None, :, None]
    ).astype(jnp.int32)
    block_hits = (
        wanted_block[:, :, None] == jnp.arange(blocks_dev, dtype=jnp.int32)[None, None, :]
    ).astype(jnp.float32)
    selector = jnp.einsum("sce,sej->scj", slot_hits.astype(jnp.float32), block_hits)
    selector = selector.reshape(seq_size * capacity, blocks_dev).astype(jnp.bfloat16)
    own_sources = lax.dynamic_slice_in_dim(
        random_device, own_index * blocks_dev, blocks_dev, 0
    ).reshape(entries)
    peer_hits = (own_sources[:, None] == jnp.arange(seq_size, dtype=jnp.int32)[None, :]).astype(
        jnp.int32
    )
    earlier = jnp.cumsum(peer_hits, axis=0) - peer_hits
    rank_in = jnp.sum(earlier * peer_hits, axis=1)
    slot_index = own_sources * capacity + rank_in
    return (selector, slot_index)


def far_context(arrived, slot_index, blocks_dev):
    picked = jnp.take(arrived, slot_index, axis=0)
    return picked.reshape(blocks_dev, RAND, arrived.shape[1], arrived.shape[2])


def usable_mask(own_index, seq_size, blocks_dev):
    block_ids = jnp.arange(blocks_dev, dtype=jnp.int32)[:, None]
    slot_ids = jnp.arange(3 + RAND, dtype=jnp.int32)[None, :]
    global_block = own_index * blocks_dev + block_ids
    missing = (slot_ids == 0) & (global_block == 0) | (slot_ids == 2) & (
        global_block == seq_size * blocks_dev - 1
    )
    return jnp.repeat(jnp.logical_not(missing), BLOCK, axis=1)


def slot_pieces(haloed, far_blocks, blocks_dev, start_col):
    pieces = []
    for slot in range(3):
        pieces.append(haloed[slot : slot + blocks_dev, :, start_col : start_col + DH])
    far_part = far_blocks[:, :, :, start_col : start_col + DH]
    return (pieces, far_part)


def forward_head(query_tiles, key_pieces, key_far, value_pieces, value_far, usable):
    blocks_dev = query_tiles.shape[0]
    logit_parts = [
        jnp.einsum("bje,bxe->bjx", query_tiles, piece, preferred_element_type=jnp.float32)
        for piece in key_pieces
    ]
    far_logits = jnp.einsum(
        "bje,brxe->bjrx", query_tiles, key_far, preferred_element_type=jnp.float32
    )
    logit_parts.append(far_logits.reshape(blocks_dev, BLOCK, RAND * BLOCK))
    attention_logits = jnp.concatenate(logit_parts, axis=-1) * (1.0 / math.sqrt(DH))
    attention_logits = jnp.where(usable[:, None, :], attention_logits, -jnp.inf)
    row_max = jnp.max(attention_logits, axis=-1, keepdims=True)
    exponent = jnp.exp(attention_logits - row_max)
    row_total = jnp.sum(exponent, axis=-1, keepdims=True)
    probability = exponent / row_total
    softmax_weights = probability.astype(jnp.bfloat16)
    attended = jnp.einsum(
        "bjx,bxe->bje",
        softmax_weights[:, :, :BLOCK],
        value_pieces[0],
        preferred_element_type=jnp.float32,
    )
    for slot in range(1, 3):
        attended = attended + jnp.einsum(
            "bjx,bxe->bje",
            softmax_weights[:, :, slot * BLOCK : (slot + 1) * BLOCK],
            value_pieces[slot],
            preferred_element_type=jnp.float32,
        )
    far_weights = softmax_weights[:, :, 3 * BLOCK :].reshape(blocks_dev, BLOCK, RAND, BLOCK)
    attended = attended + jnp.einsum(
        "bjrx,brxe->bje", far_weights, value_far, preferred_element_type=jnp.float32
    )
    return (probability, attended.astype(jnp.bfloat16))


def backward_head(
    query_tiles, key_pieces, key_far, value_pieces, value_far, gradient_tiles, forward_state
):
    probability, attended_output = forward_state
    blocks_dev = query_tiles.shape[0]
    logit_scale = 1.0 / math.sqrt(DH)
    softmax_weights = probability.astype(jnp.bfloat16)
    row_delta = jnp.sum(
        gradient_tiles.astype(jnp.float32) * attended_output.astype(jnp.float32),
        axis=-1,
        keepdims=True,
    )
    grad_parts = [
        jnp.einsum("bje,bxe->bjx", gradient_tiles, piece, preferred_element_type=jnp.float32)
        for piece in value_pieces
    ]
    far_grad = jnp.einsum(
        "bje,brxe->bjrx", gradient_tiles, value_far, preferred_element_type=jnp.float32
    )
    grad_parts.append(far_grad.reshape(blocks_dev, BLOCK, RAND * BLOCK))
    probability_gradient = jnp.concatenate(grad_parts, axis=-1)
    score_gradient = (probability * (probability_gradient - row_delta)).astype(jnp.bfloat16)
    query_sum = jnp.einsum(
        "bjx,bxe->bje",
        score_gradient[:, :, :BLOCK],
        key_pieces[0],
        preferred_element_type=jnp.float32,
    )
    for slot in range(1, 3):
        query_sum = query_sum + jnp.einsum(
            "bjx,bxe->bje",
            score_gradient[:, :, slot * BLOCK : (slot + 1) * BLOCK],
            key_pieces[slot],
            preferred_element_type=jnp.float32,
        )
    far_scores = score_gradient[:, :, 3 * BLOCK :].reshape(blocks_dev, BLOCK, RAND, BLOCK)
    query_sum = query_sum + jnp.einsum(
        "bjrx,brxe->bje", far_scores, key_far, preferred_element_type=jnp.float32
    )
    query_gradient = (logit_scale * query_sum).astype(jnp.bfloat16)
    key_window, value_window = ([], [])
    for slot in range(3):
        columns = slice(slot * BLOCK, (slot + 1) * BLOCK)
        key_window.append(
            logit_scale
            * jnp.einsum(
                "bjx,bje->bxe",
                score_gradient[:, :, columns],
                query_tiles,
                preferred_element_type=jnp.float32,
            )
        )
        value_window.append(
            jnp.einsum(
                "bjx,bje->bxe",
                softmax_weights[:, :, columns],
                gradient_tiles,
                preferred_element_type=jnp.float32,
            )
        )
    far_weights = softmax_weights[:, :, 3 * BLOCK :].reshape(blocks_dev, BLOCK, RAND, BLOCK)
    key_far_terms = (
        logit_scale
        * jnp.einsum("bjrx,bje->brxe", far_scores, query_tiles, preferred_element_type=jnp.float32)
    ).astype(jnp.bfloat16)
    value_far_terms = jnp.einsum(
        "bjrx,bje->brxe", far_weights, gradient_tiles, preferred_element_type=jnp.float32
    ).astype(jnp.bfloat16)
    return (query_gradient, key_window, value_window, key_far_terms, value_far_terms)


def exchanged_shards(queries, key_rows, value_rows, out_grad, random_device, random_block):
    seq_size = lax.axis_size("seq")
    own_index = lax.axis_index("seq")
    tokens, row_width = queries.shape
    blocks_dev = tokens // BLOCK
    heads_dev = row_width // DH
    capacity = max(2, 3 * blocks_dev // seq_size)
    selector, slot_index = routing(
        random_device, random_block, own_index, seq_size, blocks_dev, capacity
    )
    packed = jnp.concatenate([key_rows, value_rows], axis=1).reshape(
        blocks_dev, BLOCK, 2 * row_width
    )
    flattened = packed.reshape(blocks_dev, BLOCK * 2 * row_width)
    outgoing_blocks = jnp.dot(selector, flattened, preferred_element_type=jnp.float32).astype(
        jnp.bfloat16
    )
    outgoing_blocks = outgoing_blocks.reshape(seq_size * capacity, BLOCK, 2 * row_width)
    haloed = extended(packed, (("seq", 0),), 1)
    arrived = lax.all_to_all(outgoing_blocks, "seq", split_axis=0, concat_axis=0, tiled=True)
    far_blocks = far_context(arrived, slot_index, blocks_dev)
    usable = usable_mask(own_index, seq_size, blocks_dev)
    query_tiles = queries.reshape(blocks_dev, BLOCK, row_width)
    gradient_tiles = out_grad.reshape(blocks_dev, BLOCK, row_width)
    states = []
    for head_index in range(heads_dev):
        key_pieces, key_far = slot_pieces(haloed, far_blocks, blocks_dev, head_index * DH)
        value_pieces, value_far = slot_pieces(
            haloed, far_blocks, blocks_dev, row_width + head_index * DH
        )
        query_head = query_tiles[:, :, head_index * DH : (head_index + 1) * DH]
        states.append(
            forward_head(query_head, key_pieces, key_far, value_pieces, value_far, usable)
        )
    query_parts = []
    window_lists = [[], [], []]
    value_lists = [[], [], []]
    far_keys, far_values = ([], [])
    for head_index in range(heads_dev):
        key_pieces, key_far = slot_pieces(haloed, far_blocks, blocks_dev, head_index * DH)
        value_pieces, value_far = slot_pieces(
            haloed, far_blocks, blocks_dev, row_width + head_index * DH
        )
        query_head = query_tiles[:, :, head_index * DH : (head_index + 1) * DH]
        gradient_head = gradient_tiles[:, :, head_index * DH : (head_index + 1) * DH]
        query_gradient, key_window, value_window, key_far_terms, value_far_terms = backward_head(
            query_head,
            key_pieces,
            key_far,
            value_pieces,
            value_far,
            gradient_head,
            states[head_index],
        )
        query_parts.append(query_gradient)
        for slot in range(3):
            window_lists[slot].append(key_window[slot])
            value_lists[slot].append(value_window[slot])
        far_keys.append(key_far_terms)
        far_values.append(value_far_terms)
    slot_terms = [
        jnp.concatenate(window_lists[slot] + value_lists[slot], axis=-1) for slot in range(3)
    ]
    left_terms = slot_terms[0]
    right_terms = slot_terms[2]
    far_terms = jnp.concatenate(far_keys + far_values, axis=-1).reshape(
        blocks_dev * RAND, BLOCK, 2 * row_width
    )
    edge_terms = jnp.stack([left_terms[0], right_terms[-1]])
    edge_haloed = extended(edge_terms.astype(jnp.bfloat16), (("seq", 0),), 1).astype(
        edge_terms.dtype
    )
    summed = (
        slot_terms[1]
        + jnp.concatenate([left_terms[1:], edge_haloed[3:]], axis=0)
        + jnp.concatenate([edge_haloed[:1], right_terms[:-1]], axis=0)
    )
    returning = (
        jnp.zeros((seq_size * capacity, BLOCK, 2 * row_width), jnp.bfloat16)
        .at[slot_index]
        .set(far_terms)
    )
    returned = lax.all_to_all(returning, "seq", split_axis=0, concat_axis=0, tiled=True)
    gathered_terms = jnp.dot(
        selector.T,
        returned.reshape(seq_size * capacity, BLOCK * 2 * row_width),
        preferred_element_type=jnp.float32,
    )
    summed = summed + gathered_terms.reshape(blocks_dev, BLOCK, 2 * row_width)
    summed = summed.reshape(tokens, 2 * row_width)
    query_out = jnp.concatenate(query_parts, axis=-1).reshape(tokens, row_width)
    return (
        query_out,
        summed[:, :row_width].astype(jnp.bfloat16),
        summed[:, row_width:].astype(jnp.bfloat16),
    )


SLOTS = 3 + RAND


def block_kernel(ids_ref, write_ref, valid_ref, first_ref, q_ref, g_ref, *rest):
    kv_refs = rest[:SLOTS]
    own_ref, spread_ref, dq_ref, acc_ref = rest[SLOTS:]
    step = pl.program_id(0)
    steps = pl.num_programs(0)
    width = q_ref.shape[1]
    blocks_dev = own_ref.shape[0]
    logit_scale = 1.0 / math.sqrt(DH)

    @pl.when(step == 0)
    def _():
        acc_ref[...] = jnp.zeros(acc_ref.shape, jnp.float32)

    context = jnp.concatenate([ref[0] for ref in kv_refs], axis=0)
    slot_of = lax.broadcasted_iota(jnp.int32, (1, SLOTS * BLOCK), 1) // BLOCK
    usable = slot_of < 0
    for slot in range(SLOTS):
        usable = usable | ((slot_of == slot) & (valid_ref[step * SLOTS + slot] > 0))
    key_parts, value_parts = [], []
    for head in range(width // DH):
        cols = slice(head * DH, (head + 1) * DH)
        vcols = slice(width + head * DH, width + (head + 1) * DH)
        query = q_ref[:, cols]
        grad = g_ref[:, cols]
        keys = context[:, cols]
        values = context[:, vcols]
        logits = lax.dot_general(
            query, keys, (((1,), (1,)), ((), ())), preferred_element_type=jnp.float32
        ) * logit_scale
        logits = jnp.where(usable, logits, -jnp.inf)
        row_max = jnp.max(logits, axis=-1, keepdims=True)
        exponent = jnp.exp(logits - row_max)
        row_total = jnp.sum(exponent, axis=-1, keepdims=True)
        probability = exponent / row_total
        weights = probability.astype(jnp.bfloat16)
        attended = jnp.dot(weights, values, preferred_element_type=jnp.float32).astype(
            jnp.bfloat16
        )
        row_delta = jnp.sum(
            grad.astype(jnp.float32) * attended.astype(jnp.float32), axis=-1, keepdims=True
        )
        prob_grad = lax.dot_general(
            grad, values, (((1,), (1,)), ((), ())), preferred_element_type=jnp.float32
        )
        score_grad = (probability * (prob_grad - row_delta)).astype(jnp.bfloat16)
        query_grad = logit_scale * jnp.dot(score_grad, keys, preferred_element_type=jnp.float32)
        dq_ref[:, cols] = query_grad.astype(jnp.bfloat16)
        key_parts.append(
            logit_scale
            * lax.dot_general(
                score_grad, query, (((0,), (0,)), ((), ())), preferred_element_type=jnp.float32
            )
        )
        value_parts.append(
            lax.dot_general(
                weights, grad, (((0,), (0,)), ((), ())), preferred_element_type=jnp.float32
            )
        )
    terms = jnp.concatenate(key_parts + value_parts, axis=1)
    for slot in range(SLOTS):
        piece = terms[slot * BLOCK : (slot + 1) * BLOCK]
        if slot >= 3:
            piece = piece.astype(jnp.bfloat16).astype(jnp.float32)
        target = write_ref[step * SLOTS + slot]
        acc_ref[target] = acc_ref[target] + piece

    @pl.when(step == steps - 1)
    def _():
        first = first_ref[0]
        spread_ref[...] = acc_ref[...].astype(jnp.bfloat16)
        for block in range(blocks_dev):
            own_ref[block] = acc_ref[first + block].astype(jnp.bfloat16)
            spread_ref[first + block] = jnp.zeros(spread_ref.shape[1:], jnp.bfloat16)


def block_attention(ids, write_ids, valid, first, queries, out_grad, source, chunk, width, total):
    tokens = queries.shape[0]
    blocks_dev = tokens // BLOCK

    def context_spec(slot):
        return pl.BlockSpec(
            (1, BLOCK, 2 * width), lambda i, ids, write_ids, valid, first: (ids[i * SLOTS + slot], 0, 0)
        )

    column_spec = pl.BlockSpec((BLOCK, width), lambda i, ids, write_ids, valid, first: (i, chunk))
    row_spec = pl.BlockSpec((BLOCK, width), lambda i, ids, write_ids, valid, first: (i, 0))
    grid_spec = pltpu.PrefetchScalarGridSpec(
        num_scalar_prefetch=4,
        grid=(blocks_dev,),
        in_specs=[column_spec, column_spec] + [context_spec(s) for s in range(SLOTS)],
        out_specs=[
            pl.BlockSpec(
                (blocks_dev, BLOCK, 2 * width), lambda i, ids, write_ids, valid, first: (0, 0, 0)
            ),
            pl.BlockSpec((total, BLOCK, 2 * width), lambda i, ids, write_ids, valid, first: (0, 0, 0)),
            row_spec,
        ],
        scratch_shapes=[pltpu.VMEM((total, BLOCK, 2 * width), jnp.float32)],
    )
    return pl.pallas_call(
        block_kernel,
        grid_spec=grid_spec,
        out_shape=[
            jax.ShapeDtypeStruct((blocks_dev, BLOCK, 2 * width), jnp.bfloat16),
            jax.ShapeDtypeStruct((total, BLOCK, 2 * width), jnp.bfloat16),
            jax.ShapeDtypeStruct((tokens, width), jnp.bfloat16),
        ],
        compiler_params=pltpu.CompilerParams(vmem_limit_bytes=60 * 1024 * 1024),
    )(ids, write_ids, valid, first, queries, out_grad, *([source] * SLOTS))


def finish_kernel(target_ref, returned_ref, own_b_ref, left_ref, right_ref, own_a_ref,
                  rs_a_ref, key_ref, value_ref, sum_ref):
    blocks_dev = own_b_ref.shape[0]
    half = own_b_ref.shape[2] // 2
    sum_ref[...] = own_b_ref[...].astype(jnp.float32)
    sum_ref[0] = sum_ref[0] + left_ref[...].astype(jnp.float32)
    sum_ref[blocks_dev - 1] = sum_ref[blocks_dev - 1] + right_ref[...].astype(jnp.float32)
    for slot in range(returned_ref.shape[0]):
        target = target_ref[slot]

        @pl.when(target >= 0)
        def _():
            sum_ref[target] = sum_ref[target] + returned_ref[slot].astype(jnp.float32)

    for block in range(blocks_dev):
        rows = pl.ds(block * BLOCK, BLOCK)
        first = own_a_ref[block].astype(jnp.float32) + rs_a_ref[rows, :].astype(jnp.float32)
        second = sum_ref[block]
        key_ref[rows, pl.ds(0, half)] = first[:, :half].astype(jnp.bfloat16)
        key_ref[rows, pl.ds(half, half)] = second[:, :half].astype(jnp.bfloat16)
        value_ref[rows, pl.ds(0, half)] = first[:, half:].astype(jnp.bfloat16)
        value_ref[rows, pl.ds(half, half)] = second[:, half:].astype(jnp.bfloat16)


def finish(target, returned, own_b, left, right, own_a, rs_a):
    blocks_dev, _, width = own_b.shape
    tokens = blocks_dev * BLOCK
    vmem = pltpu.MemorySpace.VMEM if hasattr(pltpu, "MemorySpace") else pltpu.VMEM
    smem_spec = pl.BlockSpec(memory_space=pltpu.SMEM)
    vmem_spec = pl.BlockSpec(memory_space=vmem)
    return pl.pallas_call(
        finish_kernel,
        in_specs=[smem_spec] + [vmem_spec] * 6,
        out_specs=[vmem_spec, vmem_spec],
        out_shape=[
            jax.ShapeDtypeStruct((tokens, width), jnp.bfloat16),
            jax.ShapeDtypeStruct((tokens, width), jnp.bfloat16),
        ],
        scratch_shapes=[pltpu.VMEM(own_b.shape, jnp.float32)],
    )(target, returned, own_b, left, right, own_a, rs_a)


def gathered_shards(queries, key_rows, value_rows, out_grad, random_device, random_block):
    seq_size = lax.axis_size("seq")
    own_index = lax.axis_index("seq")
    tokens, width = queries.shape
    blocks_dev = tokens // BLOCK
    total = seq_size * blocks_dev
    first = own_index * blocks_dev
    capacity = max(2, 3 * blocks_dev // seq_size)
    selector, slot_index = routing(
        random_device, random_block, own_index, seq_size, blocks_dev, capacity
    )
    block_ids = first + jnp.arange(blocks_dev, dtype=jnp.int32)
    local_ids = jnp.arange(blocks_dev, dtype=jnp.int32)
    own_device = lax.dynamic_slice_in_dim(random_device, first, blocks_dev, 0)
    own_block = lax.dynamic_slice_in_dim(random_block, first, blocks_dev, 0)
    chosen = (own_device * blocks_dev + own_block).astype(jnp.int32)
    window = jnp.stack(
        [jnp.clip(block_ids - 1, 0, total - 1), block_ids, jnp.clip(block_ids + 1, 0, total - 1)],
        axis=1,
    )
    write_ids = jnp.concatenate([window, chosen], axis=1).reshape(-1)
    read_window = jnp.stack([local_ids, local_ids + 1, local_ids + 2], axis=1)
    read_far = (slot_index + blocks_dev + 2).reshape(blocks_dev, RAND).astype(jnp.int32)
    read_ids = jnp.concatenate([read_window, read_far], axis=1).reshape(-1)
    always = jnp.ones_like(block_ids, dtype=jnp.bool_)
    valid = jnp.stack([block_ids > 0, always, block_ids < total - 1] + [always] * RAND, axis=1)
    valid = valid.astype(jnp.int32).reshape(-1)
    first_table = first.reshape(1).astype(jnp.int32)
    chunks = 2 if (width // DH) % 2 == 0 else 1
    part = width // chunks
    global_ids = write_ids
    results = []
    link = None
    for chunk in range(chunks):
        cols = slice(chunk * part, (chunk + 1) * part)
        packed = jnp.concatenate([key_rows[:, cols], value_rows[:, cols]], axis=1)
        if chunk == 0:
            source = lax.all_gather(packed, "seq", axis=0, tiled=True)
            source = source.reshape(total, BLOCK, 2 * part)
            table_ids = global_ids
            link = source[0, 0, :1]
        else:
            packed = packed.reshape(blocks_dev, BLOCK, 2 * part)
            picked = jnp.argmax(selector > 0, axis=1).astype(jnp.int32)
            outgoing = jnp.take(packed, picked, axis=0, mode="clip")
            haloed = extended(packed, (("seq", 0),), 1)
            arrived = lax.all_to_all(outgoing, "seq", split_axis=0, concat_axis=0, tiled=True)
            source = jnp.concatenate([haloed, arrived], axis=0)
            table_ids = read_ids
        results.append((source, table_ids))
    query_parts, key_parts, value_parts = [], [], []
    after = results[-1][0][blocks_dev + 2 :] if chunks > 1 else None
    for chunk in range(chunks):
        source, table_ids = results[chunk]
        table = first_table
        if after is not None:
            table = table + (after[0, 0, :1] * 0.0).astype(jnp.int32)
        if chunk == 0:
            own_sum, spread, query_out = block_attention(
                table_ids, global_ids, valid, table, queries, out_grad, source, chunk, part, total,
            )
            returned = lax.psum_scatter(
                spread.reshape(total * BLOCK, 2 * part), "seq", scatter_dimension=0, tiled=True
            )
            first_half = (own_sum, returned)
        else:
            slots = seq_size * capacity
            far_rows = slot_index.reshape(blocks_dev, RAND).astype(jnp.int32)
            near = window - first + 1 + slots
            far_write = jnp.concatenate([near, far_rows], axis=1).reshape(-1)
            own_sum, spread, query_out = block_attention(
                table_ids, far_write, valid, table - first + 1 + slots, queries, out_grad, source,
                chunk, part, slots + blocks_dev + 2,
            )
            returned = lax.all_to_all(
                spread[:slots], "seq", split_axis=0, concat_axis=0, tiled=True
            )
            spread = spread[slots:]

            left_edge = spread[0]
            right_edge = spread[blocks_dev + 1]
            from_right = lax.ppermute(left_edge, "seq", [(i, i - 1) for i in range(1, seq_size)])
            from_left = lax.ppermute(right_edge, "seq", [(i, i + 1) for i in range(seq_size - 1)])
            hits = selector > 0
            target = jnp.where(
                jnp.any(hits, axis=1), jnp.argmax(hits, axis=1).astype(jnp.int32), -1
            )
            finished = (target, returned, own_sum, from_left, from_right)
        after = own_sum
        query_parts.append(query_out)
    key_out, value_out = finish(*finished, *first_half)
    return (jnp.concatenate(query_parts, axis=1), key_out, value_out)


def shards(queries, key_rows, value_rows, out_grad, random_device, random_block):
    if lax.axis_size("seq") <= 8 and (queries.shape[1] // DH) % 2 == 0:
        return gathered_shards(queries, key_rows, value_rows, out_grad, random_device, random_block)
    return exchanged_shards(queries, key_rows, value_rows, out_grad, random_device, random_block)


def solution(mesh):
    return jax.shard_map(
        shards,
        mesh=mesh,
        in_specs=(
            P(("groups", "seq"), ("heads", "pair")),
            P(("groups", "seq"), ("heads", "pair")),
            P(("groups", "seq"), ("heads", "pair")),
            P(("groups", "seq"), ("heads", "pair")),
            P("groups", None),
            P("groups", None),
        ),
        out_specs=(
            P(("groups", "seq"), ("heads", "pair")),
            P(("groups", "seq"), ("heads", "pair")),
            P(("groups", "seq"), ("heads", "pair")),
        ),
        check_vma=False,
    )
```

```python
import math

import jax
import jax.numpy as jnp
from jax import lax
from jax.experimental import pallas as pl
from jax.experimental.pallas import tpu as pltpu
from jax.sharding import PartitionSpec as P

DH = 128
BLOCK = 64
RAND = 2


def extended(block, sides, width):
    for axis, dim in sides:
        count = lax.axis_size(axis)
        forward = [(i, i + 1) for i in range(count - 1)]
        backward = [(target, source) for source, target in forward]
        low = lax.ppermute(
            lax.slice_in_dim(block, block.shape[dim] - width, None, axis=dim), axis, forward
        )
        high = lax.ppermute(lax.slice_in_dim(block, 0, width, axis=dim), axis, backward)
        block = jnp.concatenate([low, block, high], axis=dim)
    return block


def routing(random_device, random_block, own_index, seq_size, blocks_dev, capacity):
    entries = blocks_dev * RAND
    wanted_from = random_device.reshape(seq_size, entries)
    wanted_block = random_block.reshape(seq_size, entries)
    from_me = (wanted_from == own_index).astype(jnp.int32)
    rank_out = jnp.cumsum(from_me, axis=1) - from_me
    slot_hits = from_me[:, None, :] * (
        rank_out[:, None, :] == jnp.arange(capacity, dtype=jnp.int32)[None, :, None]
    ).astype(jnp.int32)
    block_hits = (
        wanted_block[:, :, None] == jnp.arange(blocks_dev, dtype=jnp.int32)[None, None, :]
    ).astype(jnp.float32)
    selector = jnp.einsum("sce,sej->scj", slot_hits.astype(jnp.float32), block_hits)
    selector = selector.reshape(seq_size * capacity, blocks_dev).astype(jnp.bfloat16)
    own_sources = lax.dynamic_slice_in_dim(
        random_device, own_index * blocks_dev, blocks_dev, 0
    ).reshape(entries)
    peer_hits = (own_sources[:, None] == jnp.arange(seq_size, dtype=jnp.int32)[None, :]).astype(
        jnp.int32
    )
    earlier = jnp.cumsum(peer_hits, axis=0) - peer_hits
    rank_in = jnp.sum(earlier * peer_hits, axis=1)
    slot_index = own_sources * capacity + rank_in
    return (selector, slot_index)


def far_context(arrived, slot_index, blocks_dev):
    picked = jnp.take(arrived, slot_index, axis=0)
    return picked.reshape(blocks_dev, RAND, arrived.shape[1], arrived.shape[2])


def usable_mask(own_index, seq_size, blocks_dev):
    block_ids = jnp.arange(blocks_dev, dtype=jnp.int32)[:, None]
    slot_ids = jnp.arange(3 + RAND, dtype=jnp.int32)[None, :]
    global_block = own_index * blocks_dev + block_ids
    missing = (slot_ids == 0) & (global_block == 0) | (slot_ids == 2) & (
        global_block == seq_size * blocks_dev - 1
    )
    return jnp.repeat(jnp.logical_not(missing), BLOCK, axis=1)


def slot_pieces(haloed, far_blocks, blocks_dev, start_col):
    pieces = []
    for slot in range(3):
        pieces.append(haloed[slot : slot + blocks_dev, :, start_col : start_col + DH])
    far_part = far_blocks[:, :, :, start_col : start_col + DH]
    return (pieces, far_part)


def forward_head(query_tiles, key_pieces, key_far, value_pieces, value_far, usable):
    blocks_dev = query_tiles.shape[0]
    logit_parts = [
        jnp.einsum("bje,bxe->bjx", query_tiles, piece, preferred_element_type=jnp.float32)
        for piece in key_pieces
    ]
    far_logits = jnp.einsum(
        "bje,brxe->bjrx", query_tiles, key_far, preferred_element_type=jnp.float32
    )
    logit_parts.append(far_logits.reshape(blocks_dev, BLOCK, RAND * BLOCK))
    attention_logits = jnp.concatenate(logit_parts, axis=-1) * (1.0 / math.sqrt(DH))
    attention_logits = jnp.where(usable[:, None, :], attention_logits, -jnp.inf)
    row_max = jnp.max(attention_logits, axis=-1, keepdims=True)
    exponent = jnp.exp(attention_logits - row_max)
    row_total = jnp.sum(exponent, axis=-1, keepdims=True)
    probability = exponent / row_total
    softmax_weights = probability.astype(jnp.bfloat16)
    attended = jnp.einsum(
        "bjx,bxe->bje",
        softmax_weights[:, :, :BLOCK],
        value_pieces[0],
        preferred_element_type=jnp.float32,
    )
    for slot in range(1, 3):
        attended = attended + jnp.einsum(
            "bjx,bxe->bje",
            softmax_weights[:, :, slot * BLOCK : (slot + 1) * BLOCK],
            value_pieces[slot],
            preferred_element_type=jnp.float32,
        )
    far_weights = softmax_weights[:, :, 3 * BLOCK :].reshape(blocks_dev, BLOCK, RAND, BLOCK)
    attended = attended + jnp.einsum(
        "bjrx,brxe->bje", far_weights, value_far, preferred_element_type=jnp.float32
    )
    return (probability, attended.astype(jnp.bfloat16))


def backward_head(
    query_tiles, key_pieces, key_far, value_pieces, value_far, gradient_tiles, forward_state
):
    probability, attended_output = forward_state
    blocks_dev = query_tiles.shape[0]
    logit_scale = 1.0 / math.sqrt(DH)
    softmax_weights = probability.astype(jnp.bfloat16)
    row_delta = jnp.sum(
        gradient_tiles.astype(jnp.float32) * attended_output.astype(jnp.float32),
        axis=-1,
        keepdims=True,
    )
    grad_parts = [
        jnp.einsum("bje,bxe->bjx", gradient_tiles, piece, preferred_element_type=jnp.float32)
        for piece in value_pieces
    ]
    far_grad = jnp.einsum(
        "bje,brxe->bjrx", gradient_tiles, value_far, preferred_element_type=jnp.float32
    )
    grad_parts.append(far_grad.reshape(blocks_dev, BLOCK, RAND * BLOCK))
    probability_gradient = jnp.concatenate(grad_parts, axis=-1)
    score_gradient = (probability * (probability_gradient - row_delta)).astype(jnp.bfloat16)
    query_sum = jnp.einsum(
        "bjx,bxe->bje",
        score_gradient[:, :, :BLOCK],
        key_pieces[0],
        preferred_element_type=jnp.float32,
    )
    for slot in range(1, 3):
        query_sum = query_sum + jnp.einsum(
            "bjx,bxe->bje",
            score_gradient[:, :, slot * BLOCK : (slot + 1) * BLOCK],
            key_pieces[slot],
            preferred_element_type=jnp.float32,
        )
    far_scores = score_gradient[:, :, 3 * BLOCK :].reshape(blocks_dev, BLOCK, RAND, BLOCK)
    query_sum = query_sum + jnp.einsum(
        "bjrx,brxe->bje", far_scores, key_far, preferred_element_type=jnp.float32
    )
    query_gradient = (logit_scale * query_sum).astype(jnp.bfloat16)
    key_window, value_window = ([], [])
    for slot in range(3):
        columns = slice(slot * BLOCK, (slot + 1) * BLOCK)
        key_window.append(
            logit_scale
            * jnp.einsum(
                "bjx,bje->bxe",
                score_gradient[:, :, columns],
                query_tiles,
                preferred_element_type=jnp.float32,
            )
        )
        value_window.append(
            jnp.einsum(
                "bjx,bje->bxe",
                softmax_weights[:, :, columns],
                gradient_tiles,
                preferred_element_type=jnp.float32,
            )
        )
    far_weights = softmax_weights[:, :, 3 * BLOCK :].reshape(blocks_dev, BLOCK, RAND, BLOCK)
    key_far_terms = (
        logit_scale
        * jnp.einsum("bjrx,bje->brxe", far_scores, query_tiles, preferred_element_type=jnp.float32)
    ).astype(jnp.bfloat16)
    value_far_terms = jnp.einsum(
        "bjrx,bje->brxe", far_weights, gradient_tiles, preferred_element_type=jnp.float32
    ).astype(jnp.bfloat16)
    return (query_gradient, key_window, value_window, key_far_terms, value_far_terms)


def exchanged_shards(queries, key_rows, value_rows, out_grad, random_device, random_block):
    seq_size = lax.axis_size("seq")
    own_index = lax.axis_index("seq")
    tokens, row_width = queries.shape
    blocks_dev = tokens // BLOCK
    heads_dev = row_width // DH
    capacity = max(2, 3 * blocks_dev // seq_size)
    selector, slot_index = routing(
        random_device, random_block, own_index, seq_size, blocks_dev, capacity
    )
    packed = jnp.concatenate([key_rows, value_rows], axis=1).reshape(
        blocks_dev, BLOCK, 2 * row_width
    )
    flattened = packed.reshape(blocks_dev, BLOCK * 2 * row_width)
    outgoing_blocks = jnp.dot(selector, flattened, preferred_element_type=jnp.float32).astype(
        jnp.bfloat16
    )
    outgoing_blocks = outgoing_blocks.reshape(seq_size * capacity, BLOCK, 2 * row_width)
    haloed = extended(packed, (("seq", 0),), 1)
    arrived = lax.all_to_all(outgoing_blocks, "seq", split_axis=0, concat_axis=0, tiled=True)
    far_blocks = far_context(arrived, slot_index, blocks_dev)
    usable = usable_mask(own_index, seq_size, blocks_dev)
    query_tiles = queries.reshape(blocks_dev, BLOCK, row_width)
    gradient_tiles = out_grad.reshape(blocks_dev, BLOCK, row_width)
    states = []
    for head_index in range(heads_dev):
        key_pieces, key_far = slot_pieces(haloed, far_blocks, blocks_dev, head_index * DH)
        value_pieces, value_far = slot_pieces(
            haloed, far_blocks, blocks_dev, row_width + head_index * DH
        )
        query_head = query_tiles[:, :, head_index * DH : (head_index + 1) * DH]
        states.append(
            forward_head(query_head, key_pieces, key_far, value_pieces, value_far, usable)
        )
    query_parts = []
    window_lists = [[], [], []]
    value_lists = [[], [], []]
    far_keys, far_values = ([], [])
    for head_index in range(heads_dev):
        key_pieces, key_far = slot_pieces(haloed, far_blocks, blocks_dev, head_index * DH)
        value_pieces, value_far = slot_pieces(
            haloed, far_blocks, blocks_dev, row_width + head_index * DH
        )
        query_head = query_tiles[:, :, head_index * DH : (head_index + 1) * DH]
        gradient_head = gradient_tiles[:, :, head_index * DH : (head_index + 1) * DH]
        query_gradient, key_window, value_window, key_far_terms, value_far_terms = backward_head(
            query_head,
            key_pieces,
            key_far,
            value_pieces,
            value_far,
            gradient_head,
            states[head_index],
        )
        query_parts.append(query_gradient)
        for slot in range(3):
            window_lists[slot].append(key_window[slot])
            value_lists[slot].append(value_window[slot])
        far_keys.append(key_far_terms)
        far_values.append(value_far_terms)
    slot_terms = [
        jnp.concatenate(window_lists[slot] + value_lists[slot], axis=-1) for slot in range(3)
    ]
    left_terms = slot_terms[0]
    right_terms = slot_terms[2]
    far_terms = jnp.concatenate(far_keys + far_values, axis=-1).reshape(
        blocks_dev * RAND, BLOCK, 2 * row_width
    )
    edge_terms = jnp.stack([left_terms[0], right_terms[-1]])
    edge_haloed = extended(edge_terms.astype(jnp.bfloat16), (("seq", 0),), 1).astype(
        edge_terms.dtype
    )
    summed = (
        slot_terms[1]
        + jnp.concatenate([left_terms[1:], edge_haloed[3:]], axis=0)
        + jnp.concatenate([edge_haloed[:1], right_terms[:-1]], axis=0)
    )
    returning = (
        jnp.zeros((seq_size * capacity, BLOCK, 2 * row_width), jnp.bfloat16)
        .at[slot_index]
        .set(far_terms)
    )
    returned = lax.all_to_all(returning, "seq", split_axis=0, concat_axis=0, tiled=True)
    gathered_terms = jnp.dot(
        selector.T,
        returned.reshape(seq_size * capacity, BLOCK * 2 * row_width),
        preferred_element_type=jnp.float32,
    )
    summed = summed + gathered_terms.reshape(blocks_dev, BLOCK, 2 * row_width)
    summed = summed.reshape(tokens, 2 * row_width)
    query_out = jnp.concatenate(query_parts, axis=-1).reshape(tokens, row_width)
    return (
        query_out,
        summed[:, :row_width].astype(jnp.bfloat16),
        summed[:, row_width:].astype(jnp.bfloat16),
    )


SLOTS = 3 + RAND


def block_kernel(ids_ref, write_ref, valid_ref, first_ref, q_ref, g_ref, *rest):
    kv_refs = rest[:SLOTS]
    own_ref, spread_ref, dq_ref, acc_ref = rest[SLOTS:]
    step = pl.program_id(0)
    steps = pl.num_programs(0)
    width = q_ref.shape[1]
    blocks_dev = own_ref.shape[0]
    logit_scale = 1.0 / math.sqrt(DH)

    @pl.when(step == 0)
    def _():
        acc_ref[...] = jnp.zeros(acc_ref.shape, jnp.float32)

    context = jnp.concatenate([ref[0] for ref in kv_refs], axis=0)
    slot_of = lax.broadcasted_iota(jnp.int32, (1, SLOTS * BLOCK), 1) // BLOCK
    usable = slot_of < 0
    for slot in range(SLOTS):
        usable = usable | ((slot_of == slot) & (valid_ref[step * SLOTS + slot] > 0))
    key_parts, value_parts = [], []
    for head in range(width // DH):
        cols = slice(head * DH, (head + 1) * DH)
        vcols = slice(width + head * DH, width + (head + 1) * DH)
        query = q_ref[:, cols]
        grad = g_ref[:, cols]
        keys = context[:, cols]
        values = context[:, vcols]
        logits = lax.dot_general(
            query, keys, (((1,), (1,)), ((), ())), preferred_element_type=jnp.float32
        ) * logit_scale
        logits = jnp.where(usable, logits, -jnp.inf)
        row_max = jnp.max(logits, axis=-1, keepdims=True)
        exponent = jnp.exp(logits - row_max)
        row_total = jnp.sum(exponent, axis=-1, keepdims=True)
        probability = exponent / row_total
        weights = probability.astype(jnp.bfloat16)
        attended = jnp.dot(weights, values, preferred_element_type=jnp.float32).astype(
            jnp.bfloat16
        )
        row_delta = jnp.sum(
            grad.astype(jnp.float32) * attended.astype(jnp.float32), axis=-1, keepdims=True
        )
        prob_grad = lax.dot_general(
            grad, values, (((1,), (1,)), ((), ())), preferred_element_type=jnp.float32
        )
        score_grad = (probability * (prob_grad - row_delta)).astype(jnp.bfloat16)
        query_grad = logit_scale * jnp.dot(score_grad, keys, preferred_element_type=jnp.float32)
        dq_ref[:, cols] = query_grad.astype(jnp.bfloat16)
        key_parts.append(
            logit_scale
            * lax.dot_general(
                score_grad, query, (((0,), (0,)), ((), ())), preferred_element_type=jnp.float32
            )
        )
        value_parts.append(
            lax.dot_general(
                weights, grad, (((0,), (0,)), ((), ())), preferred_element_type=jnp.float32
            )
        )
    terms = jnp.concatenate(key_parts + value_parts, axis=1)
    for slot in range(SLOTS):
        piece = terms[slot * BLOCK : (slot + 1) * BLOCK]
        if slot >= 3:
            piece = piece.astype(jnp.bfloat16).astype(jnp.float32)
        target = write_ref[step * SLOTS + slot]
        acc_ref[target] = acc_ref[target] + piece

    @pl.when(step == steps - 1)
    def _():
        first = first_ref[0]
        spread_ref[...] = acc_ref[...].astype(jnp.bfloat16)
        for block in range(blocks_dev):
            own_ref[block] = acc_ref[first + block].astype(jnp.bfloat16)
            spread_ref[first + block] = jnp.zeros(spread_ref.shape[1:], jnp.bfloat16)


def block_attention(ids, write_ids, valid, first, queries, out_grad, source, chunk, width, total):
    tokens = queries.shape[0]
    blocks_dev = tokens // BLOCK

    def context_spec(slot):
        return pl.BlockSpec(
            (1, BLOCK, 2 * width), lambda i, ids, write_ids, valid, first: (ids[i * SLOTS + slot], 0, 0)
        )

    column_spec = pl.BlockSpec((BLOCK, width), lambda i, ids, write_ids, valid, first: (i, chunk))
    row_spec = pl.BlockSpec((BLOCK, width), lambda i, ids, write_ids, valid, first: (i, 0))
    grid_spec = pltpu.PrefetchScalarGridSpec(
        num_scalar_prefetch=4,
        grid=(blocks_dev,),
        in_specs=[column_spec, column_spec] + [context_spec(s) for s in range(SLOTS)],
        out_specs=[
            pl.BlockSpec(
                (blocks_dev, BLOCK, 2 * width), lambda i, ids, write_ids, valid, first: (0, 0, 0)
            ),
            pl.BlockSpec((total, BLOCK, 2 * width), lambda i, ids, write_ids, valid, first: (0, 0, 0)),
            row_spec,
        ],
        scratch_shapes=[pltpu.VMEM((total, BLOCK, 2 * width), jnp.float32)],
    )
    return pl.pallas_call(
        block_kernel,
        grid_spec=grid_spec,
        out_shape=[
            jax.ShapeDtypeStruct((blocks_dev, BLOCK, 2 * width), jnp.bfloat16),
            jax.ShapeDtypeStruct((total, BLOCK, 2 * width), jnp.bfloat16),
            jax.ShapeDtypeStruct((tokens, width), jnp.bfloat16),
        ],
        compiler_params=pltpu.CompilerParams(vmem_limit_bytes=60 * 1024 * 1024),
    )(ids, write_ids, valid, first, queries, out_grad, *([source] * SLOTS))


def finish_kernel(target_ref, returned_ref, own_b_ref, left_ref, right_ref, own_a_ref,
                  rs_a_ref, key_ref, value_ref, sum_ref):
    blocks_dev = own_b_ref.shape[0]
    half = own_b_ref.shape[2] // 2
    sum_ref[...] = own_b_ref[...].astype(jnp.float32)
    sum_ref[0] = sum_ref[0] + left_ref[...].astype(jnp.float32)
    sum_ref[blocks_dev - 1] = sum_ref[blocks_dev - 1] + right_ref[...].astype(jnp.float32)
    for slot in range(returned_ref.shape[0]):
        target = target_ref[slot]

        @pl.when(target >= 0)
        def _():
            sum_ref[target] = sum_ref[target] + returned_ref[slot].astype(jnp.float32)

    for block in range(blocks_dev):
        rows = pl.ds(block * BLOCK, BLOCK)
        first = own_a_ref[block].astype(jnp.float32) + rs_a_ref[rows, :].astype(jnp.float32)
        second = sum_ref[block]
        key_ref[rows, pl.ds(0, half)] = first[:, :half].astype(jnp.bfloat16)
        key_ref[rows, pl.ds(half, half)] = second[:, :half].astype(jnp.bfloat16)
        value_ref[rows, pl.ds(0, half)] = first[:, half:].astype(jnp.bfloat16)
        value_ref[rows, pl.ds(half, half)] = second[:, half:].astype(jnp.bfloat16)


def finish(target, returned, own_b, left, right, own_a, rs_a):
    blocks_dev, _, width = own_b.shape
    tokens = blocks_dev * BLOCK
    vmem = pltpu.MemorySpace.VMEM if hasattr(pltpu, "MemorySpace") else pltpu.VMEM
    smem_spec = pl.BlockSpec(memory_space=pltpu.SMEM)
    vmem_spec = pl.BlockSpec(memory_space=vmem)
    return pl.pallas_call(
        finish_kernel,
        in_specs=[smem_spec] + [vmem_spec] * 6,
        out_specs=[vmem_spec, vmem_spec],
        out_shape=[
            jax.ShapeDtypeStruct((tokens, width), jnp.bfloat16),
            jax.ShapeDtypeStruct((tokens, width), jnp.bfloat16),
        ],
        scratch_shapes=[pltpu.VMEM(own_b.shape, jnp.float32)],
    )(target, returned, own_b, left, right, own_a, rs_a)


def gathered_shards(queries, key_rows, value_rows, out_grad, random_device, random_block):
    seq_size = lax.axis_size("seq")
    own_index = lax.axis_index("seq")
    tokens, width = queries.shape
    blocks_dev = tokens // BLOCK
    total = seq_size * blocks_dev
    first = own_index * blocks_dev
    capacity = max(2, 3 * blocks_dev // seq_size)
    selector, slot_index = routing(
        random_device, random_block, own_index, seq_size, blocks_dev, capacity
    )
    block_ids = first + jnp.arange(blocks_dev, dtype=jnp.int32)
    local_ids = jnp.arange(blocks_dev, dtype=jnp.int32)
    own_device = lax.dynamic_slice_in_dim(random_device, first, blocks_dev, 0)
    own_block = lax.dynamic_slice_in_dim(random_block, first, blocks_dev, 0)
    chosen = (own_device * blocks_dev + own_block).astype(jnp.int32)
    window = jnp.stack(
        [jnp.clip(block_ids - 1, 0, total - 1), block_ids, jnp.clip(block_ids + 1, 0, total - 1)],
        axis=1,
    )
    write_ids = jnp.concatenate([window, chosen], axis=1).reshape(-1)
    read_window = jnp.stack([local_ids, local_ids + 1, local_ids + 2], axis=1)
    read_far = (slot_index + blocks_dev + 2).reshape(blocks_dev, RAND).astype(jnp.int32)
    read_ids = jnp.concatenate([read_window, read_far], axis=1).reshape(-1)
    always = jnp.ones_like(block_ids, dtype=jnp.bool_)
    valid = jnp.stack([block_ids > 0, always, block_ids < total - 1] + [always] * RAND, axis=1)
    valid = valid.astype(jnp.int32).reshape(-1)
    first_table = first.reshape(1).astype(jnp.int32)
    chunks = 2 if (width // DH) % 2 == 0 else 1
    part = width // chunks
    global_ids = write_ids
    results = []
    link = None
    for chunk in range(chunks):
        cols = slice(chunk * part, (chunk + 1) * part)
        packed = jnp.concatenate([key_rows[:, cols], value_rows[:, cols]], axis=1)
        if chunk == 0:
            source = lax.all_gather(packed, "seq", axis=0, tiled=True)
            source = source.reshape(total, BLOCK, 2 * part)
            table_ids = global_ids
            link = source[0, 0, :1]
        else:
            packed = packed.reshape(blocks_dev, BLOCK, 2 * part)
            wanted_from = random_device.reshape(seq_size, blocks_dev * RAND)
            wanted_block = random_block.reshape(seq_size, blocks_dev * RAND)
            from_me = (wanted_from == own_index).astype(jnp.int32)
            rank = jnp.cumsum(from_me, axis=1) - from_me
            hit = (from_me[:, None, :] > 0) & (
                rank[:, None, :] == jnp.arange(capacity, dtype=jnp.int32)[None, :, None]
            )
            picked = jnp.sum(jnp.where(hit, wanted_block[:, None, :], 0), axis=2)
            picked = picked.reshape(-1).astype(jnp.int32)
            outgoing = jnp.take(packed, picked, axis=0, mode="clip")
            haloed = extended(packed, (("seq", 0),), 1)
            arrived = lax.all_to_all(outgoing, "seq", split_axis=0, concat_axis=0, tiled=True)
            source = jnp.concatenate([haloed, arrived], axis=0)
            table_ids = read_ids
        results.append((source, table_ids))
    query_parts, key_parts, value_parts = [], [], []
    after = results[-1][0][blocks_dev + 2 :] if chunks > 1 else None
    for chunk in range(chunks):
        source, table_ids = results[chunk]
        table = first_table
        if after is not None:
            table = table + (after[0, 0, :1] * 0.0).astype(jnp.int32)
        if chunk == 0:
            own_sum, spread, query_out = block_attention(
                table_ids, global_ids, valid, table, queries, out_grad, source, chunk, part, total,
            )
            returned = lax.psum_scatter(
                spread.reshape(total * BLOCK, 2 * part), "seq", scatter_dimension=0, tiled=True
            )
            first_half = (own_sum, returned)
        else:
            slots = seq_size * capacity
            far_rows = slot_index.reshape(blocks_dev, RAND).astype(jnp.int32)
            near = window - first + 1 + slots
            far_write = jnp.concatenate([near, far_rows], axis=1).reshape(-1)
            own_sum, spread, query_out = block_attention(
                table_ids, far_write, valid, table - first + 1 + slots, queries, out_grad, source,
                chunk, part, slots + blocks_dev + 2,
            )
            returned = lax.all_to_all(
                spread[:slots], "seq", split_axis=0, concat_axis=0, tiled=True
            )
            spread = spread[slots:]

            left_edge = spread[0]
            right_edge = spread[blocks_dev + 1]
            from_right = lax.ppermute(left_edge, "seq", [(i, i - 1) for i in range(1, seq_size)])
            from_left = lax.ppermute(right_edge, "seq", [(i, i + 1) for i in range(seq_size - 1)])
            hits = selector > 0
            target = jnp.where(
                jnp.any(hits, axis=1), jnp.argmax(hits, axis=1).astype(jnp.int32), -1
            )
            finished = (target, returned, own_sum, from_left, from_right)
        after = own_sum
        query_parts.append(query_out)
    key_out, value_out = finish(*finished, *first_half)
    return (jnp.concatenate(query_parts, axis=1), key_out, value_out)


def shards(queries, key_rows, value_rows, out_grad, random_device, random_block):
    if lax.axis_size("seq") <= 8 and (queries.shape[1] // DH) % 2 == 0:
        return gathered_shards(queries, key_rows, value_rows, out_grad, random_device, random_block)
    return exchanged_shards(queries, key_rows, value_rows, out_grad, random_device, random_block)


def solution(mesh):
    return jax.shard_map(
        shards,
        mesh=mesh,
        in_specs=(
            P(("groups", "seq"), ("heads", "pair")),
            P(("groups", "seq"), ("heads", "pair")),
            P(("groups", "seq"), ("heads", "pair")),
            P(("groups", "seq"), ("heads", "pair")),
            P("groups", None),
            P("groups", None),
        ),
        out_specs=(
            P(("groups", "seq"), ("heads", "pair")),
            P(("groups", "seq"), ("heads", "pair")),
            P(("groups", "seq"), ("heads", "pair")),
        ),
        check_vma=False,
    )
```
